32 devices in a mesh: views: 4 (over y, x), depth: 4 (over z), lat: 2 (over core).
Axes of the slice: x: 2, y: 2, z: 4, core: 2. Of those that a mesh axis runs over, the one named last changes fastest.
Arguments:
- density: bfloat16 [64, 2, 16, 1024], P(None, None, 'depth', 'lat'), may hold values from 0 to 3, as said below
- measured: float32 [16, 64, 1024], P('views', None, 'lat'), may hold values from 0 to 4
- shear_shift: int32 [16, 16], P('views', 'depth'), may hold values from -64 to 63
- shear_frac: float32 [16, 16], P('views', 'depth'), may hold values from 0 to 1
- spectrum: float32 [64], replicated, may hold values from 0.05 to 1
- attenuation: float32 [2, 64], replicated, may hold values from 0.3 to 6
Outputs:
- density_gradient: float32 [64, 2, 16, 1024], P('views', None, 'depth', 'lat')
The draws below stay inside these ranges and needn't reach their ends.
Inputs may be any that keep to these rules, and one draw needn't show every extreme that they name: `density`: densities are non-negative.
All inputs are finite; a program needn't handle non-finite values.
Results may differ from the reference program's by a relative error of at most 0.0016.
Values may be sent and summed in bfloat16 or wider, within the bound.
No kernel may reach another device: no remote copies, remote signals or barrier semaphores. Data moves between devices by JAX's collectives and lax.ppermute only.
A program may use at most 64 MiB of HBM per device.

```python
import math
import jax
import jax.numpy as jnp
from jax import lax

M = 2
E = 64
Y = 64
HALO = 64
VIEWS = 16
Z = 16
X = 1024


def draw_density(key, part):
    key_cells, key_columns = jax.random.split(key)
    voxels = jax.random.uniform(key_cells, (Y, M, Z, X), jnp.float32, 0.0, 1.0)
    column_scale = jnp.exp(jax.random.uniform(key_columns, (Y, M, 1, X), jnp.float32, math.log(0.2), math.log(2.0)))
    return (voxels * column_scale).astype(jnp.bfloat16)


def with_ends(array, key, low, high):
    extent = array.shape
    place = [jax.random.randint(jax.random.fold_in(key, axis), (), 0, extent[axis]) for axis in range(len(extent))]
    array = array.at[tuple(place)].set(low)
    longest = extent.index(max(extent))
    place[longest] = (place[longest] + 1) % extent[longest]
    return array.at[tuple(place)].set(high)


def level_of(own_key, dims, cuts, low, largest):
    factor_of = 1.0
    for position, parts in cuts:
        draws = jax.random.uniform(jax.random.fold_in(jax.random.fold_in(own_key, 6), position), (parts,), jnp.float32, low / len(cuts), largest / len(cuts))
        factor_of = factor_of * jnp.repeat(jnp.exp(draws), dims[position] // parts).reshape((-1,) + (1,) * (len(dims) - 1 - position))
    return factor_of


def setup_inputs(seed: int = 0) -> dict:
    key_of = jax.random.split(jax.random.key(seed), 7)
    density = draw_density(jax.random.fold_in(key_of[6], 71), 0)
    measured = jnp.clip(4.0 * jax.random.uniform(key_of[1], (VIEWS, Y, X), jnp.float32) ** level_of(key_of[1], (VIEWS, Y, X), ((0, 4), (2, 2)), -0.2, 0.2), 0.0, 4.0)
    shear_shift = with_ends(jax.random.randint(key_of[2], (VIEWS, Z), 0 - HALO, HALO), jax.random.fold_in(key_of[2], 1), 0 - HALO, HALO - 1).astype(jnp.int32)
    shear_frac = jnp.clip(1.0 * jax.random.uniform(key_of[3], (VIEWS, Z), jnp.float32) ** level_of(key_of[3], (VIEWS, Z), ((0, 4), (1, 4)), -0.2, 0.2), 0.0, 1.0)
    spectrum = jnp.clip(jnp.exp(jax.random.uniform(key_of[4], (E,), jnp.float32, math.log(0.05), math.log(1.0))), 0.05, 1.0)
    attenuation = jnp.clip(jnp.exp(jax.random.uniform(key_of[5], (M, E), jnp.float32, math.log(0.3), math.log(6.0))), 0.3, 6.0)
    return {"density": density, "measured": measured, "shear_shift": shear_shift, "shear_frac": shear_frac, "spectrum": spectrum, "attenuation": attenuation}


def spectral_grad(path_water, path_bone, observed, spectrum, attenuation, views_all):
    coefficients = jnp.concatenate([jnp.ones((1, spectrum.shape[0]), jnp.float32), attenuation], axis=0)
    exponent = attenuation[0][:, None, None] * path_water[None] + attenuation[1][:, None, None] * path_bone[None]
    counts = spectrum[:, None, None] * jnp.exp(-exponent)
    moments = jnp.einsum('ke,eyx->kyx', coefficients, counts, precision=lax.Precision.HIGHEST)
    intensity = moments[0]
    residual = jnp.log(jnp.sum(spectrum)) - jnp.log(intensity) - observed
    factor = residual / intensity / views_all
    return (moments[1:] * factor[None]).astype(jnp.bfloat16)

def reference(density, measured, shear_shift, shear_frac, spectrum, attenuation):
    views_all = measured.shape[0]
    row_total, materials, depth_all, width_all = density.shape
    lower_weight = lax.optimization_barrier((1.0 - shear_frac).astype(jnp.bfloat16)).astype(jnp.float32)
    upper_weight = lax.optimization_barrier(shear_frac.astype(jnp.bfloat16)).astype(jnp.float32)
    padded = jnp.pad(density, ((0, 0), (0, 0), (0, 0), (HALO, HALO)))
    positions = jnp.arange(depth_all, dtype=jnp.int32)

    def forward_step(running, depth_pos):
        slab_plane = lax.dynamic_index_in_dim(padded, depth_pos, 2, keepdims=False).astype(jnp.float32)

        def one_view(offset, lower_tap_weight, upper_tap_weight):
            lower_tap = lax.dynamic_slice_in_dim(slab_plane, offset + HALO, width_all, 2)
            upper_tap = lax.dynamic_slice_in_dim(slab_plane, offset + HALO + 1, width_all, 2)
            return lower_tap_weight * lower_tap + upper_tap_weight * upper_tap
        sheared = jax.vmap(one_view)(shear_shift[:, depth_pos], lower_weight[:, depth_pos], upper_weight[:, depth_pos])
        return (running + sheared, None)
    initial = jnp.zeros((views_all, row_total, materials, width_all), jnp.float32)
    path_sums, _ = lax.scan(forward_step, initial, positions)
    path_sums = path_sums / depth_all

    def per_view(inputs):
        return spectral_grad(inputs[0], inputs[1], inputs[2], spectrum, attenuation, views_all)
    path_grads = lax.map(per_view, (path_sums[:, :, 0, :], path_sums[:, :, 1, :], measured))
    path_grads = lax.optimization_barrier(jnp.transpose(path_grads, (0, 2, 1, 3)))
    padded_grads = jnp.pad(path_grads, ((0, 0), (0, 0), (0, 0), (HALO, HALO))).astype(jnp.float32)

    def back_step(carry, depth_pos):

        def one_view(grid, offset, lower_tap_weight, upper_tap_weight):
            lower_tap = lax.dynamic_slice_in_dim(grid, HALO - offset, width_all, 2)
            upper_tap = lax.dynamic_slice_in_dim(grid, HALO - offset - 1, width_all, 2)
            return lower_tap_weight * lower_tap + upper_tap_weight * upper_tap
        layer = lax.optimization_barrier(jnp.sum(jax.vmap(one_view)(padded_grads, shear_shift[:, depth_pos], lower_weight[:, depth_pos], upper_weight[:, depth_pos]), axis=0))
        return (carry, layer)
    _, layers = lax.scan(back_step, jnp.zeros((), jnp.float32), positions)
    return jnp.transpose(layers, (1, 2, 0, 3))
```

```python
import jax
import jax.numpy as jnp
from jax import lax
from jax.sharding import PartitionSpec as P
from jax.experimental import pallas as pl
from jax.experimental.pallas import tpu as pltpu

HALO = 64


def with_halo(x, sides, width):
    for axis, dim in sides:
        size, length = (lax.axis_size(axis), x.shape[dim])
        up = [(i, (i + 1) % size) for i in range(size - 1)]
        down = [(j, i) for i, j in up]
        last = lax.slice_in_dim(x, length - width, length, axis=dim)
        first = lax.slice_in_dim(x, 0, width, axis=dim)
        before = lax.ppermute(last, axis, up)
        after = lax.ppermute(first, axis, down)
        x = jnp.concatenate([before, x, after], axis=dim)
    return x


def band_forward(shear_shift, lower_weight, upper_weight, window, block_width):
    band_shape = (shear_shift.shape[1], window, shear_shift.shape[0], block_width)
    tap_index = lax.broadcasted_iota(jnp.int32, band_shape, 1)
    column = lax.broadcasted_iota(jnp.int32, band_shape, 3)
    anchor = (shear_shift.T + HALO)[:, None, :, None]
    nothing = jnp.zeros((), jnp.bfloat16)
    lower_part = jnp.where(tap_index == column + anchor, lower_weight.T[:, None, :, None], nothing)
    upper_part = jnp.where(
        tap_index == column + anchor + 1, upper_weight.T[:, None, :, None], nothing
    )
    return lower_part + upper_part


def band_backward(shear_shift, lower_weight, upper_weight, window, block_width):
    band_shape = (shear_shift.shape[0], window, shear_shift.shape[1], block_width)
    tap_index = lax.broadcasted_iota(jnp.int32, band_shape, 1)
    column = lax.broadcasted_iota(jnp.int32, band_shape, 3)
    anchor = (HALO - shear_shift)[:, None, :, None]
    nothing = jnp.zeros((), jnp.bfloat16)
    lower_part = jnp.where(tap_index == column + anchor, lower_weight[:, None, :, None], nothing)
    upper_part = jnp.where(
        tap_index == column + anchor - 1, upper_weight[:, None, :, None], nothing
    )
    return lower_part + upper_part


def spectral(path_sums, observed, spectrum, attenuation, views_all):
    view_count, row_count, materials, tile_width = path_sums.shape
    block_pixels = 4096
    path_water = path_sums[:, :, 0, :].reshape(-1, block_pixels)
    path_bone = path_sums[:, :, 1, :].reshape(-1, block_pixels)
    target_flat = observed.reshape(-1, block_pixels)
    coefficients = jnp.concatenate(
        [jnp.ones((1, spectrum.shape[0]), jnp.float32), attenuation], axis=0
    )
    emitted = jnp.log(jnp.sum(spectrum))

    def one_block(inputs):
        water_block, bone_block, target_block = inputs
        exponent = (
            attenuation[0][:, None] * water_block[None, :]
            + attenuation[1][:, None] * bone_block[None, :]
        )
        counts = spectrum[:, None] * jnp.exp(-exponent)
        moments = jnp.dot(coefficients, counts, precision=lax.Precision.HIGHEST)
        intensity = moments[0]
        residual = emitted - jnp.log(intensity) - target_block
        factor = residual / intensity / views_all
        return (moments[1:] * factor[None, :]).astype(jnp.bfloat16)

    stacked = lax.map(one_block, (path_water, path_bone, target_flat))
    gradients = jnp.swapaxes(stacked, 0, 1).reshape(materials, view_count, row_count, tile_width)
    return jnp.transpose(gradients, (1, 2, 0, 3))


def per_device(density, measured, shear_shift, shear_frac, spectrum, attenuation):
    row_total, materials, depth_here, tile_width = density.shape
    block_width = min(128, tile_width)
    block_count = tile_width // block_width
    window = block_width + 2 * HALO
    views_all = measured.shape[0] * lax.axis_size("views")
    depth_all = depth_here * lax.axis_size("depth")
    rows_out = row_total // lax.axis_size("views")
    lower_weight = (1.0 - shear_frac).astype(jnp.bfloat16)
    upper_weight = shear_frac.astype(jnp.bfloat16)
    rows_here = density.shape[0]
    padded = with_halo(density, (("lat", 3),), HALO)
    framed = jnp.stack(
        [
            padded[:, :, :, number * block_width : number * block_width + window]
            for number in range(block_count)
        ],
        axis=2,
    )
    forward_band = band_forward(shear_shift, lower_weight, upper_weight, window, block_width)
    partial_value = jnp.einsum(
        "ymnzi,zivc->vymnc", framed, forward_band, preferred_element_type=jnp.float32
    )
    partial_value = partial_value.reshape(shear_shift.shape[0], rows_here, materials, tile_width)
    shares = lax.psum_scatter(partial_value, "depth", scatter_dimension=3, tiled=True) / depth_all
    share_cols = shares.shape[3]
    observed = lax.dynamic_slice_in_dim(
        measured, lax.axis_index("depth") * share_cols, share_cols, 2
    )
    share_grads = spectral(shares, observed, spectrum, attenuation, views_all)
    path_grads = lax.all_gather(share_grads, "depth", axis=3, tiled=True)
    padded_grads = with_halo(path_grads, (("lat", 3),), HALO)
    framed_grads = jnp.stack(
        [
            padded_grads[:, :, :, number * block_width : number * block_width + window]
            for number in range(block_count)
        ],
        axis=3,
    )
    backward_band = band_backward(shear_shift, lower_weight, upper_weight, window, block_width)
    product = jnp.einsum(
        "vymni,vizc->ymznc", framed_grads, backward_band, preferred_element_type=jnp.float32
    )
    return lax.psum_scatter(
        product.reshape(rows_out * lax.axis_size("views"), materials, depth_here, tile_width),
        "views",
        scatter_dimension=0,
        tiled=True,
    )


LANES = 128
INTERPRET = False


def shear_kernel(rot_ref, thr_ref, wa_ref, wb_ref, src_ref, out_ref):
    outer_count, channels, width = src_ref.shape
    inner_count, _, out_width = out_ref.shape
    pieces = width // LANES
    out_pieces = out_width // LANES
    out_ref[...] = jnp.zeros(out_ref.shape, jnp.float32)
    lane = lax.broadcasted_iota(jnp.int32, (channels, LANES), 1)

    def outer(o, carry):
        cols = [src_ref[o, :, k * LANES : (k + 1) * LANES] for k in range(pieces)]
        turned = [pltpu.roll(c, LANES - 1, 1) for c in cols]
        nexts = [
            jnp.where(lane < LANES - 1, turned[k], turned[k + 1]) for k in range(pieces - 1)
        ] + [turned[pieces - 1]]
        for i in range(inner_count):
            wa = wa_ref[o, i]
            wb = wb_ref[o, i]
            mixed = [wa * cols[k] + wb * nexts[k] for k in range(pieces)]
            rolled = [pltpu.roll(m, rot_ref[o, i], 1) for m in mixed]
            keep = lane < thr_ref[o, i]
            for j in range(out_pieces):
                out_ref[i, :, j * LANES : (j + 1) * LANES] += jnp.where(
                    keep, rolled[j], rolled[j + 1]
                )
        return carry

    lax.fori_loop(0, outer_count, outer, 0)


def shear_apply(offset, wa, wb, src, out_width):
    outer_count, channels, width = src.shape
    inner_count = offset.shape[1]
    rot = (LANES - offset) % LANES
    thr = LANES - offset
    smem = pl.BlockSpec(memory_space=pltpu.SMEM)
    vmem = pl.BlockSpec(memory_space=pltpu.VMEM)
    return pl.pallas_call(
        shear_kernel,
        out_shape=jax.ShapeDtypeStruct((inner_count, channels, out_width), jnp.float32),
        in_specs=[smem, smem, smem, smem, vmem],
        out_specs=vmem,
        interpret=INTERPRET,
    )(rot.astype(jnp.int32), thr.astype(jnp.int32), wa, wb, src)


def rows_fit(density, measured):
    rows = density.shape[0]
    groups = lax.axis_size("views")
    depth = lax.axis_size("depth")
    tile_width = density.shape[3]
    return (
        rows % groups == 0
        and (rows // groups) % depth == 0
        and tile_width % LANES == 0
        and 2 * HALO <= LANES
        and tile_width >= HALO
    )


def per_device_rows(density, measured, shear_shift, shear_frac, spectrum, attenuation):
    row_total, materials, depth_here, tile_width = density.shape
    groups = lax.axis_size("views")
    depth_count = lax.axis_size("depth")
    views_here = measured.shape[0]
    views_all = views_here * groups
    depth_all = depth_here * depth_count
    rows_group = row_total // groups
    rows_here = rows_group // depth_count
    group = lax.axis_index("views")
    slab = lax.axis_index("depth")

    lower_weight = (1.0 - shear_frac).astype(jnp.bfloat16).astype(jnp.float32)
    upper_weight = shear_frac.astype(jnp.bfloat16).astype(jnp.float32)
    table = jnp.stack([shear_shift.astype(jnp.float32), lower_weight, upper_weight])
    table = lax.all_gather(table, ("views", "depth"), axis=0, tiled=False)
    table = table.reshape(groups, depth_count, 3, views_here, depth_here)
    table = jnp.transpose(table, (2, 0, 3, 1, 4)).reshape(3, views_all, depth_all)
    shift_all = table[0].astype(jnp.int32)
    lower_all = table[1]
    upper_all = table[2]

    observed = measured.reshape(views_here, groups, rows_group, tile_width)
    observed = lax.dynamic_slice_in_dim(observed, slab * rows_here, rows_here, 2)
    observed = lax.all_to_all(observed, "views", 1, 0, tiled=True)
    observed = observed.reshape(views_all, rows_here, tile_width)

    mine = lax.dynamic_slice_in_dim(density, group * rows_group, rows_group, 0)
    mine = jnp.transpose(mine, (2, 0, 1, 3))
    mine = lax.all_to_all(mine, "depth", 1, 0, tiled=True)
    mine = mine.reshape(depth_all, rows_here * materials, tile_width)
    padded = with_halo(mine, (("lat", 2),), HALO).astype(jnp.float32)

    sums = shear_apply(
        (shift_all + HALO).T, lower_all.T, upper_all.T, padded, tile_width
    )
    sums = (sums / depth_all).reshape(views_all, rows_here, materials, tile_width)
    grads = spectral(sums, observed, spectrum, attenuation, views_all)
    grads = grads.reshape(views_all, rows_here * materials, tile_width)
    padded_grads = with_halo(grads, (("lat", 2),), HALO).astype(jnp.float32)
    layers = shear_apply(
        HALO - 1 - shift_all, upper_all, lower_all, padded_grads, tile_width
    )
    layers = layers.reshape(depth_all, rows_here, materials, tile_width)
    layers = lax.all_to_all(layers, "depth", 0, 1, tiled=True)
    return jnp.transpose(layers, (1, 2, 0, 3))


def per_device_any(density, measured, shear_shift, shear_frac, spectrum, attenuation):
    if rows_fit(density, measured):
        return per_device_rows(density, measured, shear_shift, shear_frac, spectrum, attenuation)
    return per_device(density, measured, shear_shift, shear_frac, spectrum, attenuation)


def solution(mesh):
    in_specs = (
        P(None, None, "depth", "lat"),
        P("views", None, "lat"),
        P("views", "depth"),
        P("views", "depth"),
        P(),
        P(),
    )
    out_specs = P("views", None, "depth", "lat")
    return jax.shard_map(
        per_device_any, mesh=mesh, in_specs=in_specs, out_specs=out_specs, check_vma=False
    )
```

```python
import jax
import jax.numpy as jnp
from jax import lax
from jax.sharding import PartitionSpec as P
from jax.experimental import pallas as pl
from jax.experimental.pallas import tpu as pltpu

HALO = 64


def with_halo(x, sides, width):
    for axis, dim in sides:
        size, length = (lax.axis_size(axis), x.shape[dim])
        up = [(i, (i + 1) % size) for i in range(size - 1)]
        down = [(j, i) for i, j in up]
        last = lax.slice_in_dim(x, length - width, length, axis=dim)
        first = lax.slice_in_dim(x, 0, width, axis=dim)
        before = lax.ppermute(last, axis, up)
        after = lax.ppermute(first, axis, down)
        x = jnp.concatenate([before, x, after], axis=dim)
    return x


def band_forward(shear_shift, lower_weight, upper_weight, window, block_width):
    band_shape = (shear_shift.shape[1], window, shear_shift.shape[0], block_width)
    tap_index = lax.broadcasted_iota(jnp.int32, band_shape, 1)
    column = lax.broadcasted_iota(jnp.int32, band_shape, 3)
    anchor = (shear_shift.T + HALO)[:, None, :, None]
    nothing = jnp.zeros((), jnp.bfloat16)
    lower_part = jnp.where(tap_index == column + anchor, lower_weight.T[:, None, :, None], nothing)
    upper_part = jnp.where(
        tap_index == column + anchor + 1, upper_weight.T[:, None, :, None], nothing
    )
    return lower_part + upper_part


def band_backward(shear_shift, lower_weight, upper_weight, window, block_width):
    band_shape = (shear_shift.shape[0], window, shear_shift.shape[1], block_width)
    tap_index = lax.broadcasted_iota(jnp.int32, band_shape, 1)
    column = lax.broadcasted_iota(jnp.int32, band_shape, 3)
    anchor = (HALO - shear_shift)[:, None, :, None]
    nothing = jnp.zeros((), jnp.bfloat16)
    lower_part = jnp.where(tap_index == column + anchor, lower_weight[:, None, :, None], nothing)
    upper_part = jnp.where(
        tap_index == column + anchor - 1, upper_weight[:, None, :, None], nothing
    )
    return lower_part + upper_part


def spectral(path_sums, observed, spectrum, attenuation, views_all):
    view_count, row_count, materials, tile_width = path_sums.shape
    block_pixels = 4096
    path_water = path_sums[:, :, 0, :].reshape(-1, block_pixels)
    path_bone = path_sums[:, :, 1, :].reshape(-1, block_pixels)
    target_flat = observed.reshape(-1, block_pixels)
    coefficients = jnp.concatenate(
        [jnp.ones((1, spectrum.shape[0]), jnp.float32), attenuation], axis=0
    )
    emitted = jnp.log(jnp.sum(spectrum))

    def one_block(inputs):
        water_block, bone_block, target_block = inputs
        exponent = (
            attenuation[0][:, None] * water_block[None, :]
            + attenuation[1][:, None] * bone_block[None, :]
        )
        counts = spectrum[:, None] * jnp.exp(-exponent)
        moments = jnp.dot(coefficients, counts, precision=lax.Precision.HIGHEST)
        intensity = moments[0]
        residual = emitted - jnp.log(intensity) - target_block
        factor = residual / intensity / views_all
        return (moments[1:] * factor[None, :]).astype(jnp.bfloat16)

    stacked = lax.map(one_block, (path_water, path_bone, target_flat))
    gradients = jnp.swapaxes(stacked, 0, 1).reshape(materials, view_count, row_count, tile_width)
    return jnp.transpose(gradients, (1, 2, 0, 3))


def per_device(density, measured, shear_shift, shear_frac, spectrum, attenuation):
    row_total, materials, depth_here, tile_width = density.shape
    block_width = min(128, tile_width)
    block_count = tile_width // block_width
    window = block_width + 2 * HALO
    views_all = measured.shape[0] * lax.axis_size("views")
    depth_all = depth_here * lax.axis_size("depth")
    rows_out = row_total // lax.axis_size("views")
    lower_weight = (1.0 - shear_frac).astype(jnp.bfloat16)
    upper_weight = shear_frac.astype(jnp.bfloat16)
    rows_here = density.shape[0]
    padded = with_halo(density, (("lat", 3),), HALO)
    framed = jnp.stack(
        [
            padded[:, :, :, number * block_width : number * block_width + window]
            for number in range(block_count)
        ],
        axis=2,
    )
    forward_band = band_forward(shear_shift, lower_weight, upper_weight, window, block_width)
    partial_value = jnp.einsum(
        "ymnzi,zivc->vymnc", framed, forward_band, preferred_element_type=jnp.float32
    )
    partial_value = partial_value.reshape(shear_shift.shape[0], rows_here, materials, tile_width)
    shares = lax.psum_scatter(partial_value, "depth", scatter_dimension=3, tiled=True) / depth_all
    share_cols = shares.shape[3]
    observed = lax.dynamic_slice_in_dim(
        measured, lax.axis_index("depth") * share_cols, share_cols, 2
    )
    share_grads = spectral(shares, observed, spectrum, attenuation, views_all)
    path_grads = lax.all_gather(share_grads, "depth", axis=3, tiled=True)
    padded_grads = with_halo(path_grads, (("lat", 3),), HALO)
    framed_grads = jnp.stack(
        [
            padded_grads[:, :, :, number * block_width : number * block_width + window]
            for number in range(block_count)
        ],
        axis=3,
    )
    backward_band = band_backward(shear_shift, lower_weight, upper_weight, window, block_width)
    product = jnp.einsum(
        "vymni,vizc->ymznc", framed_grads, backward_band, preferred_element_type=jnp.float32
    )
    return lax.psum_scatter(
        product.reshape(rows_out * lax.axis_size("views"), materials, depth_here, tile_width),
        "views",
        scatter_dimension=0,
        tiled=True,
    )


LANES = 128
INTERPRET = False


def shear_kernel(rot_ref, thr_ref, wa_ref, wb_ref, src_ref, out_ref):
    outer_count, channels, width = src_ref.shape
    inner_count, _, out_width = out_ref.shape
    pieces = width // LANES
    out_pieces = out_width // LANES
    out_ref[...] = jnp.zeros(out_ref.shape, jnp.float32)
    lane = lax.broadcasted_iota(jnp.int32, (channels, LANES), 1)

    def outer(o, carry):
        cols = [src_ref[o, :, k * LANES : (k + 1) * LANES] for k in range(pieces)]
        turned = [pltpu.roll(c, LANES - 1, 1) for c in cols]
        nexts = [
            jnp.where(lane < LANES - 1, turned[k], turned[k + 1]) for k in range(pieces - 1)
        ] + [turned[pieces - 1]]
        for i in range(inner_count):
            wa = wa_ref[o, i]
            wb = wb_ref[o, i]
            mixed = [wa * cols[k] + wb * nexts[k] for k in range(pieces)]
            rolled = [pltpu.roll(m, rot_ref[o, i], 1) for m in mixed]
            keep = lane < thr_ref[o, i]
            for j in range(out_pieces):
                out_ref[i, :, j * LANES : (j + 1) * LANES] += jnp.where(
                    keep, rolled[j], rolled[j + 1]
                )
        return carry

    lax.fori_loop(0, outer_count, outer, 0)


def shear_apply(offset, wa, wb, src, out_width):
    outer_count, channels, width = src.shape
    inner_count = offset.shape[1]
    rot = (LANES - offset) % LANES
    thr = LANES - offset
    smem = pl.BlockSpec(memory_space=pltpu.SMEM)
    vmem = pl.BlockSpec(memory_space=pltpu.VMEM)
    return pl.pallas_call(
        shear_kernel,
        out_shape=jax.ShapeDtypeStruct((inner_count, channels, out_width), jnp.float32),
        in_specs=[smem, smem, smem, smem, vmem],
        out_specs=vmem,
        interpret=INTERPRET,
    )(rot.astype(jnp.int32), thr.astype(jnp.int32), wa, wb, src)


def rows_fit(density, measured):
    rows = density.shape[0]
    groups = lax.axis_size("views")
    depth = lax.axis_size("depth")
    tile_width = density.shape[3]
    return (
        rows % groups == 0
        and (rows // groups) % depth == 0
        and tile_width % LANES == 0
        and 2 * HALO <= LANES
        and tile_width >= HALO
        and tile_width >= 3 * measured.shape[0] * density.shape[2] * groups
    )


def per_device_rows(density, measured, shear_shift, shear_frac, spectrum, attenuation):
    row_total, materials, depth_here, tile_width = density.shape
    groups = lax.axis_size("views")
    depth_count = lax.axis_size("depth")
    views_here = measured.shape[0]
    views_all = views_here * groups
    depth_all = depth_here * depth_count
    rows_group = row_total // groups
    rows_here = rows_group // depth_count
    group = lax.axis_index("views")
    slab = lax.axis_index("depth")

    lower_weight = (1.0 - shear_frac).astype(jnp.bfloat16).astype(jnp.float32)
    upper_weight = shear_frac.astype(jnp.bfloat16).astype(jnp.float32)
    table = jnp.stack([shear_shift.astype(jnp.float32), lower_weight, upper_weight])
    entries = table.size
    observed = measured.reshape(views_here, groups, rows_group, tile_width)
    observed = lax.dynamic_slice_in_dim(observed, slab * rows_here, rows_here, 2)
    observed = jnp.transpose(observed, (1, 0, 2, 3)).reshape(groups, views_here * rows_here, tile_width)
    extra = jnp.pad(table.reshape(1, entries), ((0, 0), (0, tile_width - entries)))
    extra = jnp.broadcast_to(extra[None], (groups, 1, tile_width))
    observed = jnp.concatenate([observed, extra], axis=1)
    observed = lax.all_to_all(observed, "views", 0, 0, tiled=True)
    table = observed[:, views_here * rows_here, :entries].reshape(groups, 3, views_here, depth_here)
    table = jnp.transpose(table, (1, 0, 2, 3)).reshape(3, views_all, depth_here)
    observed = observed[:, : views_here * rows_here].reshape(views_all, rows_here, tile_width)

    channels = rows_here * materials
    mine = lax.dynamic_slice_in_dim(density, group * rows_group, rows_group, 0)
    mine = mine.reshape(depth_count, rows_here, materials, depth_here, tile_width)
    mine = jnp.transpose(mine, (0, 3, 1, 2, 4)).reshape(depth_count, depth_here * channels, tile_width)
    wide = table.size
    extra = jnp.pad(table.reshape(1, wide), ((0, 0), (0, tile_width - wide))).astype(jnp.bfloat16)
    extra = jnp.broadcast_to(extra[None], (depth_count, 1, tile_width))
    mine = jnp.concatenate([mine, extra], axis=1)
    mine = lax.all_to_all(mine, "depth", 0, 0, tiled=True)
    table = mine[:, depth_here * channels, :wide].astype(jnp.float32)
    table = table.reshape(depth_count, 3, views_all, depth_here)
    table = jnp.transpose(table, (1, 2, 0, 3)).reshape(3, views_all, depth_all)
    shift_all = table[0].astype(jnp.int32)
    lower_all = table[1]
    upper_all = table[2]
    mine = mine[:, : depth_here * channels].reshape(depth_all, channels, tile_width)
    padded = with_halo(mine, (("lat", 2),), HALO).astype(jnp.float32)

    sums = shear_apply(
        (shift_all + HALO).T, lower_all.T, upper_all.T, padded, tile_width
    )
    sums = (sums / depth_all).reshape(views_all, rows_here, materials, tile_width)
    grads = spectral(sums, observed, spectrum, attenuation, views_all)
    grads = grads.reshape(views_all, rows_here * materials, tile_width)
    padded_grads = with_halo(grads, (("lat", 2),), HALO).astype(jnp.float32)
    layers = shear_apply(
        HALO - 1 - shift_all, upper_all, lower_all, padded_grads, tile_width
    )
    layers = layers.reshape(depth_all, rows_here, materials, tile_width)
    layers = lax.all_to_all(layers, "depth", 0, 1, tiled=True)
    return jnp.transpose(layers, (1, 2, 0, 3))


def per_device_any(density, measured, shear_shift, shear_frac, spectrum, attenuation):
    if rows_fit(density, measured):
        return per_device_rows(density, measured, shear_shift, shear_frac, spectrum, attenuation)
    return per_device(density, measured, shear_shift, shear_frac, spectrum, attenuation)


def solution(mesh):
    in_specs = (
        P(None, None, "depth", "lat"),
        P("views", None, "lat"),
        P("views", "depth"),
        P("views", "depth"),
        P(),
        P(),
    )
    out_specs = P("views", None, "depth", "lat")
    return jax.shard_map(
        per_device_any, mesh=mesh, in_specs=in_specs, out_specs=out_specs, check_vma=False
    )
```

```python
import jax
import jax.numpy as jnp
from jax import lax
from jax.sharding import PartitionSpec as P
from jax.experimental import pallas as pl
from jax.experimental.pallas import tpu as pltpu

HALO = 64


def with_halo(x, sides, width):
    for axis, dim in sides:
        size, length = (lax.axis_size(axis), x.shape[dim])
        up = [(i, (i + 1) % size) for i in range(size - 1)]
        down = [(j, i) for i, j in up]
        last = lax.slice_in_dim(x, length - width, length, axis=dim)
        first = lax.slice_in_dim(x, 0, width, axis=dim)
        before = lax.ppermute(last, axis, up)
        after = lax.ppermute(first, axis, down)
        x = jnp.concatenate([before, x, after], axis=dim)
    return x


def exchange(x, axis):
    count = lax.axis_size(axis)
    me = lax.axis_index(axis)
    result = x
    for step in range(1, count):
        pairs = [(i, (i + step) % count) for i in range(count)]
        part = lax.dynamic_index_in_dim(x, (me + step) % count, 0, keepdims=True)
        part = lax.ppermute(part, axis, pairs)
        result = lax.dynamic_update_index_in_dim(result, part, (me - step) % count, 0)
    return result


def band_forward(shear_shift, lower_weight, upper_weight, window, block_width):
    band_shape = (shear_shift.shape[1], window, shear_shift.shape[0], block_width)
    tap_index = lax.broadcasted_iota(jnp.int32, band_shape, 1)
    column = lax.broadcasted_iota(jnp.int32, band_shape, 3)
    anchor = (shear_shift.T + HALO)[:, None, :, None]
    nothing = jnp.zeros((), jnp.bfloat16)
    lower_part = jnp.where(tap_index == column + anchor, lower_weight.T[:, None, :, None], nothing)
    upper_part = jnp.where(
        tap_index == column + anchor + 1, upper_weight.T[:, None, :, None], nothing
    )
    return lower_part + upper_part


def band_backward(shear_shift, lower_weight, upper_weight, window, block_width):
    band_shape = (shear_shift.shape[0], window, shear_shift.shape[1], block_width)
    tap_index = lax.broadcasted_iota(jnp.int32, band_shape, 1)
    column = lax.broadcasted_iota(jnp.int32, band_shape, 3)
    anchor = (HALO - shear_shift)[:, None, :, None]
    nothing = jnp.zeros((), jnp.bfloat16)
    lower_part = jnp.where(tap_index == column + anchor, lower_weight[:, None, :, None], nothing)
    upper_part = jnp.where(
        tap_index == column + anchor - 1, upper_weight[:, None, :, None], nothing
    )
    return lower_part + upper_part


def spectral(path_sums, observed, spectrum, attenuation, views_all):
    view_count, row_count, materials, tile_width = path_sums.shape
    block_pixels = 4096
    path_water = path_sums[:, :, 0, :].reshape(-1, block_pixels)
    path_bone = path_sums[:, :, 1, :].reshape(-1, block_pixels)
    target_flat = observed.reshape(-1, block_pixels)
    coefficients = jnp.concatenate(
        [jnp.ones((1, spectrum.shape[0]), jnp.float32), attenuation], axis=0
    )
    emitted = jnp.log(jnp.sum(spectrum))

    def one_block(inputs):
        water_block, bone_block, target_block = inputs
        exponent = (
            attenuation[0][:, None] * water_block[None, :]
            + attenuation[1][:, None] * bone_block[None, :]
        )
        counts = spectrum[:, None] * jnp.exp(-exponent)
        moments = jnp.dot(coefficients, counts, precision=lax.Precision.HIGHEST)
        intensity = moments[0]
        residual = emitted - jnp.log(intensity) - target_block
        factor = residual / intensity / views_all
        return (moments[1:] * factor[None, :]).astype(jnp.bfloat16)

    stacked = lax.map(one_block, (path_water, path_bone, target_flat))
    gradients = jnp.swapaxes(stacked, 0, 1).reshape(materials, view_count, row_count, tile_width)
    return jnp.transpose(gradients, (1, 2, 0, 3))


def per_device(density, measured, shear_shift, shear_frac, spectrum, attenuation):
    row_total, materials, depth_here, tile_width = density.shape
    block_width = min(128, tile_width)
    block_count = tile_width // block_width
    window = block_width + 2 * HALO
    views_all = measured.shape[0] * lax.axis_size("views")
    depth_all = depth_here * lax.axis_size("depth")
    rows_out = row_total // lax.axis_size("views")
    lower_weight = (1.0 - shear_frac).astype(jnp.bfloat16)
    upper_weight = shear_frac.astype(jnp.bfloat16)
    rows_here = density.shape[0]
    padded = with_halo(density, (("lat", 3),), HALO)
    framed = jnp.stack(
        [
            padded[:, :, :, number * block_width : number * block_width + window]
            for number in range(block_count)
        ],
        axis=2,
    )
    forward_band = band_forward(shear_shift, lower_weight, upper_weight, window, block_width)
    partial_value = jnp.einsum(
        "ymnzi,zivc->vymnc", framed, forward_band, preferred_element_type=jnp.float32
    )
    partial_value = partial_value.reshape(shear_shift.shape[0], rows_here, materials, tile_width)
    shares = lax.psum_scatter(partial_value, "depth", scatter_dimension=3, tiled=True) / depth_all
    share_cols = shares.shape[3]
    observed = lax.dynamic_slice_in_dim(
        measured, lax.axis_index("depth") * share_cols, share_cols, 2
    )
    share_grads = spectral(shares, observed, spectrum, attenuation, views_all)
    path_grads = lax.all_gather(share_grads, "depth", axis=3, tiled=True)
    padded_grads = with_halo(path_grads, (("lat", 3),), HALO)
    framed_grads = jnp.stack(
        [
            padded_grads[:, :, :, number * block_width : number * block_width + window]
            for number in range(block_count)
        ],
        axis=3,
    )
    backward_band = band_backward(shear_shift, lower_weight, upper_weight, window, block_width)
    product = jnp.einsum(
        "vymni,vizc->ymznc", framed_grads, backward_band, preferred_element_type=jnp.float32
    )
    return lax.psum_scatter(
        product.reshape(rows_out * lax.axis_size("views"), materials, depth_here, tile_width),
        "views",
        scatter_dimension=0,
        tiled=True,
    )


LANES = 128
INTERPRET = False


def shear_kernel(rot_ref, thr_ref, wa_ref, wb_ref, src_ref, out_ref):
    outer_count, channels, width = src_ref.shape
    inner_count, _, out_width = out_ref.shape
    pieces = width // LANES
    out_pieces = out_width // LANES
    out_ref[...] = jnp.zeros(out_ref.shape, jnp.float32)
    lane = lax.broadcasted_iota(jnp.int32, (channels, LANES), 1)

    def outer(o, carry):
        cols = [src_ref[o, :, k * LANES : (k + 1) * LANES] for k in range(pieces)]
        turned = [pltpu.roll(c, LANES - 1, 1) for c in cols]
        nexts = [
            jnp.where(lane < LANES - 1, turned[k], turned[k + 1]) for k in range(pieces - 1)
        ] + [turned[pieces - 1]]
        for i in range(inner_count):
            wa = wa_ref[o, i]
            wb = wb_ref[o, i]
            mixed = [wa * cols[k] + wb * nexts[k] for k in range(pieces)]
            rolled = [pltpu.roll(m, rot_ref[o, i], 1) for m in mixed]
            keep = lane < thr_ref[o, i]
            for j in range(out_pieces):
                out_ref[i, :, j * LANES : (j + 1) * LANES] += jnp.where(
                    keep, rolled[j], rolled[j + 1]
                )
        return carry

    lax.fori_loop(0, outer_count, outer, 0)


def shear_apply(offset, wa, wb, src, out_width):
    outer_count, channels, width = src.shape
    inner_count = offset.shape[1]
    rot = (LANES - offset) % LANES
    thr = LANES - offset
    smem = pl.BlockSpec(memory_space=pltpu.SMEM)
    vmem = pl.BlockSpec(memory_space=pltpu.VMEM)
    return pl.pallas_call(
        shear_kernel,
        out_shape=jax.ShapeDtypeStruct((inner_count, channels, out_width), jnp.float32),
        in_specs=[smem, smem, smem, smem, vmem],
        out_specs=vmem,
        interpret=INTERPRET,
    )(rot.astype(jnp.int32), thr.astype(jnp.int32), wa, wb, src)


def rows_fit(density, measured):
    rows = density.shape[0]
    groups = lax.axis_size("views")
    depth = lax.axis_size("depth")
    tile_width = density.shape[3]
    return (
        rows % groups == 0
        and (rows // groups) % depth == 0
        and tile_width % LANES == 0
        and 2 * HALO <= LANES
        and tile_width >= HALO
        and tile_width >= 3 * measured.shape[0] * density.shape[2] * groups
    )


def per_device_rows(density, measured, shear_shift, shear_frac, spectrum, attenuation):
    row_total, materials, depth_here, tile_width = density.shape
    groups = lax.axis_size("views")
    depth_count = lax.axis_size("depth")
    views_here = measured.shape[0]
    views_all = views_here * groups
    depth_all = depth_here * depth_count
    rows_group = row_total // groups
    rows_here = rows_group // depth_count
    group = lax.axis_index("views")
    slab = lax.axis_index("depth")

    lower_weight = (1.0 - shear_frac).astype(jnp.bfloat16).astype(jnp.float32)
    upper_weight = shear_frac.astype(jnp.bfloat16).astype(jnp.float32)
    table = jnp.stack([shear_shift.astype(jnp.float32), lower_weight, upper_weight])
    entries = table.size
    observed = measured.reshape(views_here, groups, rows_group, tile_width)
    observed = lax.dynamic_slice_in_dim(observed, slab * rows_here, rows_here, 2)
    observed = jnp.transpose(observed, (1, 0, 2, 3)).reshape(groups, views_here * rows_here, tile_width)
    extra = jnp.pad(table.reshape(1, entries), ((0, 0), (0, tile_width - entries)))
    extra = jnp.broadcast_to(extra[None], (groups, 1, tile_width))
    observed = jnp.concatenate([observed, extra], axis=1)
    observed = lax.all_to_all(observed, "views", 0, 0, tiled=True)
    table = observed[:, views_here * rows_here, :entries].reshape(groups, 3, views_here, depth_here)
    table = jnp.transpose(table, (1, 0, 2, 3)).reshape(3, views_all, depth_here)
    observed = observed[:, : views_here * rows_here].reshape(views_all, rows_here, tile_width)

    channels = rows_here * materials
    mine = lax.dynamic_slice_in_dim(density, group * rows_group, rows_group, 0)
    mine = mine.reshape(depth_count, rows_here, materials, depth_here, tile_width)
    mine = jnp.transpose(mine, (0, 3, 1, 2, 4)).reshape(depth_count, depth_here * channels, tile_width)
    wide = table.size
    extra = jnp.pad(table.reshape(1, wide), ((0, 0), (0, tile_width - wide))).astype(jnp.bfloat16)
    extra = jnp.broadcast_to(extra[None], (depth_count, 1, tile_width))
    mine = jnp.concatenate([mine, extra], axis=1)
    mine = lax.all_to_all(mine, "depth", 0, 0, tiled=True)
    table = mine[:, depth_here * channels, :wide].astype(jnp.float32)
    table = table.reshape(depth_count, 3, views_all, depth_here)
    table = jnp.transpose(table, (1, 2, 0, 3)).reshape(3, views_all, depth_all)
    shift_all = table[0].astype(jnp.int32)
    lower_all = table[1]
    upper_all = table[2]
    mine = mine[:, : depth_here * channels].reshape(depth_all, channels, tile_width)
    padded = with_halo(mine, (("lat", 2),), HALO).astype(jnp.float32)

    sums = shear_apply(
        (shift_all + HALO).T, lower_all.T, upper_all.T, padded, tile_width
    )
    sums = (sums / depth_all).reshape(views_all, rows_here, materials, tile_width)
    grads = spectral(sums, observed, spectrum, attenuation, views_all)
    grads = grads.reshape(views_all, rows_here * materials, tile_width)
    padded_grads = with_halo(grads, (("lat", 2),), HALO).astype(jnp.float32)
    layers = shear_apply(
        HALO - 1 - shift_all, upper_all, lower_all, padded_grads, tile_width
    )
    layers = layers.reshape(depth_count, depth_here, rows_here, materials, tile_width)
    layers = exchange(layers, "depth")
    return jnp.transpose(layers, (0, 2, 3, 1, 4)).reshape(rows_group, materials, depth_here, tile_width)


def per_device_any(density, measured, shear_shift, shear_frac, spectrum, attenuation):
    if rows_fit(density, measured):
        return per_device_rows(density, measured, shear_shift, shear_frac, spectrum, attenuation)
    return per_device(density, measured, shear_shift, shear_frac, spectrum, attenuation)


def solution(mesh):
    in_specs = (
        P(None, None, "depth", "lat"),
        P("views", None, "lat"),
        P("views", "depth"),
        P("views", "depth"),
        P(),
        P(),
    )
    out_specs = P("views", None, "depth", "lat")
    return jax.shard_map(
        per_device_any, mesh=mesh, in_specs=in_specs, out_specs=out_specs, check_vma=False
    )
```

```python
import jax
import jax.numpy as jnp
from jax import lax
from jax.sharding import PartitionSpec as P
from jax.experimental import pallas as pl
from jax.experimental.pallas import tpu as pltpu

HALO = 64


def with_halo(x, sides, width):
    for axis, dim in sides:
        size, length = (lax.axis_size(axis), x.shape[dim])
        up = [(i, (i + 1) % size) for i in range(size - 1)]
        down = [(j, i) for i, j in up]
        last = lax.slice_in_dim(x, length - width, length, axis=dim)
        first = lax.slice_in_dim(x, 0, width, axis=dim)
        before = lax.ppermute(last, axis, up)
        after = lax.ppermute(first, axis, down)
        x = jnp.concatenate([before, x, after], axis=dim)
    return x


def exchange(x, axis):
    count = lax.axis_size(axis)
    me = lax.axis_index(axis)
    result = x
    for step in range(1, count):
        pairs = [(i, (i + step) % count) for i in range(count)]
        part = lax.dynamic_index_in_dim(x, (me + step) % count, 0, keepdims=True)
        part = lax.ppermute(part, axis, pairs)
        result = lax.dynamic_update_index_in_dim(result, part, (me - step) % count, 0)
    return result


def band_forward(shear_shift, lower_weight, upper_weight, window, block_width):
    band_shape = (shear_shift.shape[1], window, shear_shift.shape[0], block_width)
    tap_index = lax.broadcasted_iota(jnp.int32, band_shape, 1)
    column = lax.broadcasted_iota(jnp.int32, band_shape, 3)
    anchor = (shear_shift.T + HALO)[:, None, :, None]
    nothing = jnp.zeros((), jnp.bfloat16)
    lower_part = jnp.where(tap_index == column + anchor, lower_weight.T[:, None, :, None], nothing)
    upper_part = jnp.where(
        tap_index == column + anchor + 1, upper_weight.T[:, None, :, None], nothing
    )
    return lower_part + upper_part


def band_backward(shear_shift, lower_weight, upper_weight, window, block_width):
    band_shape = (shear_shift.shape[0], window, shear_shift.shape[1], block_width)
    tap_index = lax.broadcasted_iota(jnp.int32, band_shape, 1)
    column = lax.broadcasted_iota(jnp.int32, band_shape, 3)
    anchor = (HALO - shear_shift)[:, None, :, None]
    nothing = jnp.zeros((), jnp.bfloat16)
    lower_part = jnp.where(tap_index == column + anchor, lower_weight[:, None, :, None], nothing)
    upper_part = jnp.where(
        tap_index == column + anchor - 1, upper_weight[:, None, :, None], nothing
    )
    return lower_part + upper_part


def spectral(path_sums, observed, spectrum, attenuation, views_all):
    view_count, row_count, materials, tile_width = path_sums.shape
    block_pixels = 4096
    path_water = path_sums[:, :, 0, :].reshape(-1, block_pixels)
    path_bone = path_sums[:, :, 1, :].reshape(-1, block_pixels)
    target_flat = observed.reshape(-1, block_pixels)
    coefficients = jnp.concatenate(
        [jnp.ones((1, spectrum.shape[0]), jnp.float32), attenuation], axis=0
    )
    emitted = jnp.log(jnp.sum(spectrum))

    def one_block(inputs):
        water_block, bone_block, target_block = inputs
        exponent = (
            attenuation[0][:, None] * water_block[None, :]
            + attenuation[1][:, None] * bone_block[None, :]
        )
        counts = spectrum[:, None] * jnp.exp(-exponent)
        moments = jnp.dot(coefficients, counts, precision=lax.Precision.HIGHEST)
        intensity = moments[0]
        residual = emitted - jnp.log(intensity) - target_block
        factor = residual / intensity / views_all
        return (moments[1:] * factor[None, :]).astype(jnp.bfloat16)

    stacked = lax.map(one_block, (path_water, path_bone, target_flat))
    gradients = jnp.swapaxes(stacked, 0, 1).reshape(materials, view_count, row_count, tile_width)
    return jnp.transpose(gradients, (1, 2, 0, 3))


def per_device(density, measured, shear_shift, shear_frac, spectrum, attenuation):
    row_total, materials, depth_here, tile_width = density.shape
    block_width = min(128, tile_width)
    block_count = tile_width // block_width
    window = block_width + 2 * HALO
    views_all = measured.shape[0] * lax.axis_size("views")
    depth_all = depth_here * lax.axis_size("depth")
    rows_out = row_total // lax.axis_size("views")
    lower_weight = (1.0 - shear_frac).astype(jnp.bfloat16)
    upper_weight = shear_frac.astype(jnp.bfloat16)
    rows_here = density.shape[0]
    padded = with_halo(density, (("lat", 3),), HALO)
    framed = jnp.stack(
        [
            padded[:, :, :, number * block_width : number * block_width + window]
            for number in range(block_count)
        ],
        axis=2,
    )
    forward_band = band_forward(shear_shift, lower_weight, upper_weight, window, block_width)
    partial_value = jnp.einsum(
        "ymnzi,zivc->vymnc", framed, forward_band, preferred_element_type=jnp.float32
    )
    partial_value = partial_value.reshape(shear_shift.shape[0], rows_here, materials, tile_width)
    shares = lax.psum_scatter(partial_value, "depth", scatter_dimension=3, tiled=True) / depth_all
    share_cols = shares.shape[3]
    observed = lax.dynamic_slice_in_dim(
        measured, lax.axis_index("depth") * share_cols, share_cols, 2
    )
    share_grads = spectral(shares, observed, spectrum, attenuation, views_all)
    path_grads = lax.all_gather(share_grads, "depth", axis=3, tiled=True)
    padded_grads = with_halo(path_grads, (("lat", 3),), HALO)
    framed_grads = jnp.stack(
        [
            padded_grads[:, :, :, number * block_width : number * block_width + window]
            for number in range(block_count)
        ],
        axis=3,
    )
    backward_band = band_backward(shear_shift, lower_weight, upper_weight, window, block_width)
    product = jnp.einsum(
        "vymni,vizc->ymznc", framed_grads, backward_band, preferred_element_type=jnp.float32
    )
    return lax.psum_scatter(
        product.reshape(rows_out * lax.axis_size("views"), materials, depth_here, tile_width),
        "views",
        scatter_dimension=0,
        tiled=True,
    )


LANES = 128
INTERPRET = False


def shear_kernel(rot_ref, thr_ref, wa_ref, wb_ref, src_ref, out_ref):
    outer_count, channels, width = src_ref.shape
    inner_count, _, out_width = out_ref.shape
    pieces = width // LANES
    out_pieces = out_width // LANES
    out_ref[...] = jnp.zeros(out_ref.shape, jnp.float32)
    lane = lax.broadcasted_iota(jnp.int32, (channels, LANES), 1)

    def outer(o, carry):
        cols = [src_ref[o, :, k * LANES : (k + 1) * LANES] for k in range(pieces)]
        turned = [pltpu.roll(c, LANES - 1, 1) for c in cols]
        nexts = [
            jnp.where(lane < LANES - 1, turned[k], turned[k + 1]) for k in range(pieces - 1)
        ] + [turned[pieces - 1]]
        for i in range(inner_count):
            wa = wa_ref[o, i]
            wb = wb_ref[o, i]
            mixed = [wa * cols[k] + wb * nexts[k] for k in range(pieces)]
            rolled = [pltpu.roll(m, rot_ref[o, i], 1) for m in mixed]
            keep = lane < thr_ref[o, i]
            for j in range(out_pieces):
                out_ref[i, :, j * LANES : (j + 1) * LANES] += jnp.where(
                    keep, rolled[j], rolled[j + 1]
                )
        return carry

    lax.fori_loop(0, outer_count, outer, 0)


def shear_apply(offset, wa, wb, src, out_width):
    outer_count, channels, width = src.shape
    inner_count = offset.shape[1]
    rot = (LANES - offset) % LANES
    thr = LANES - offset
    smem = pl.BlockSpec(memory_space=pltpu.SMEM)
    vmem = pl.BlockSpec(memory_space=pltpu.VMEM)
    return pl.pallas_call(
        shear_kernel,
        out_shape=jax.ShapeDtypeStruct((inner_count, channels, out_width), jnp.float32),
        in_specs=[smem, smem, smem, smem, vmem],
        out_specs=vmem,
        interpret=INTERPRET,
    )(rot.astype(jnp.int32), thr.astype(jnp.int32), wa, wb, src)


def rows_fit(density, measured):
    rows = density.shape[0]
    groups = lax.axis_size("views")
    depth = lax.axis_size("depth")
    tile_width = density.shape[3]
    return (
        rows % groups == 0
        and (rows // groups) % depth == 0
        and tile_width % LANES == 0
        and 2 * HALO <= LANES
        and tile_width >= HALO
        and tile_width >= 3 * measured.shape[0] * density.shape[2] * groups
    )


def per_device_rows(density, measured, shear_shift, shear_frac, spectrum, attenuation):
    row_total, materials, depth_here, tile_width = density.shape
    groups = lax.axis_size("views")
    depth_count = lax.axis_size("depth")
    views_here = measured.shape[0]
    views_all = views_here * groups
    depth_all = depth_here * depth_count
    rows_group = row_total // groups
    rows_here = rows_group // depth_count
    group = lax.axis_index("views")
    slab = lax.axis_index("depth")

    lower_weight = (1.0 - shear_frac).astype(jnp.bfloat16).astype(jnp.float32)
    upper_weight = shear_frac.astype(jnp.bfloat16).astype(jnp.float32)
    table = jnp.stack([shear_shift.astype(jnp.float32), lower_weight, upper_weight])
    entries = table.size
    observed = measured.reshape(views_here, groups, rows_group, tile_width)
    observed = lax.dynamic_slice_in_dim(observed, slab * rows_here, rows_here, 2)
    observed = jnp.transpose(observed, (1, 0, 2, 3)).reshape(groups, views_here * rows_here, tile_width)
    extra = jnp.pad(table.reshape(1, entries), ((0, 0), (0, tile_width - entries)))
    extra = jnp.broadcast_to(extra[None], (groups, 1, tile_width))
    observed = jnp.concatenate([observed, extra], axis=1)
    observed = lax.all_to_all(observed, "views", 0, 0, tiled=True)
    table = observed[:, views_here * rows_here, :entries].reshape(groups, 3, views_here, depth_here)
    table = jnp.transpose(table, (1, 0, 2, 3)).reshape(3, views_all, depth_here)
    observed = observed[:, : views_here * rows_here].reshape(views_all, rows_here, tile_width)

    channels = rows_here * materials
    mine = lax.dynamic_slice_in_dim(density, group * rows_group, rows_group, 0)
    mine = mine.reshape(depth_count, rows_here, materials, depth_here, tile_width)
    mine = jnp.transpose(mine, (0, 3, 1, 2, 4)).reshape(depth_count, depth_here * channels, tile_width)
    wide = table.size
    extra = jnp.pad(table.reshape(1, wide), ((0, 0), (0, tile_width - wide))).astype(jnp.bfloat16)
    extra = jnp.broadcast_to(extra[None], (depth_count, 1, tile_width))
    mine = jnp.concatenate([mine, extra], axis=1)
    mine = lax.all_to_all(mine, "depth", 0, 0, tiled=True)
    table = mine[:, depth_here * channels, :wide].astype(jnp.float32)
    table = table.reshape(depth_count, 3, views_all, depth_here)
    table = jnp.transpose(table, (1, 2, 0, 3)).reshape(3, views_all, depth_all)
    shift_all = table[0].astype(jnp.int32)
    lower_all = table[1]
    upper_all = table[2]
    mine = mine[:, : depth_here * channels].reshape(depth_all, channels, tile_width)
    padded = with_halo(mine, (("lat", 2),), HALO).astype(jnp.float32)

    sums = shear_apply(
        (shift_all + HALO).T, lower_all.T, upper_all.T, padded, tile_width
    )
    sums = (sums / depth_all).reshape(views_all, rows_here, materials, tile_width)
    grads = spectral(sums, observed, spectrum, attenuation, views_all)
    grads = grads.reshape(views_all, rows_here * materials, tile_width)
    padded_grads = with_halo(grads, (("lat", 2),), HALO).astype(jnp.float32)
    layers = shear_apply(
        HALO - 1 - shift_all, upper_all, lower_all, padded_grads, tile_width
    )
    layers = layers.reshape(depth_count, depth_here, rows_here, materials, tile_width)
    layers = exchange(layers, "depth")
    return jnp.transpose(layers, (0, 2, 3, 1, 4)).reshape(rows_group, materials, depth_here, tile_width)


def rows_fit_wide(density, measured):
    rows = density.shape[0]
    groups = lax.axis_size("views")
    parts = lax.axis_size("depth") * lax.axis_size("lat")
    tile_width = density.shape[3]
    return (
        rows % groups == 0
        and (rows // groups) % parts == 0
        and tile_width % LANES == 0
        and 2 * HALO <= LANES
        and tile_width >= HALO
        and tile_width >= 3 * measured.shape[0] * density.shape[2] * groups
    )


def stack_halves(values, halves, tile_width):
    count, rows, materials, _ = values.shape
    padded = jnp.pad(values, ((0, 0), (0, 0), (0, 0), (HALO, HALO)))
    parts = [
        padded[..., h * tile_width : h * tile_width + tile_width + 2 * HALO] for h in range(halves)
    ]
    return jnp.stack(parts, axis=1).reshape(count, halves * rows * materials, tile_width + 2 * HALO)


def join_halves(values, halves, rows, materials):
    count, _, tile_width = values.shape
    values = values.reshape(count, halves, rows, materials, tile_width)
    return jnp.transpose(values, (0, 2, 3, 1, 4)).reshape(count, rows, materials, halves * tile_width)


def per_device_wide(density, measured, shear_shift, shear_frac, spectrum, attenuation):
    row_total, materials, depth_here, tile_width = density.shape
    groups = lax.axis_size("views")
    depth_count = lax.axis_size("depth")
    halves = lax.axis_size("lat")
    parts = depth_count * halves
    views_here = measured.shape[0]
    views_all = views_here * groups
    depth_all = depth_here * depth_count
    rows_group = row_total // groups
    rows_here = rows_group // parts
    group = lax.axis_index("views")
    slab = lax.axis_index("depth")
    half = lax.axis_index("lat")

    lower_weight = (1.0 - shear_frac).astype(jnp.bfloat16).astype(jnp.float32)
    upper_weight = shear_frac.astype(jnp.bfloat16).astype(jnp.float32)
    table = jnp.stack([shear_shift.astype(jnp.float32), lower_weight, upper_weight])
    entries = table.size
    observed = measured.reshape(views_here, groups, depth_count, halves, rows_here, tile_width)
    observed = lax.dynamic_index_in_dim(observed, slab, 2, keepdims=False)
    observed = jnp.transpose(observed, (1, 2, 0, 3, 4)).reshape(
        groups * halves, views_here * rows_here, tile_width
    )
    extra = jnp.pad(table.reshape(1, entries), ((0, 0), (0, tile_width - entries)))
    extra = jnp.broadcast_to(extra[None], (groups * halves, 1, tile_width))
    observed = jnp.concatenate([observed, extra], axis=1)
    observed = lax.all_to_all(observed, ("views", "lat"), 0, 0, tiled=True)
    observed = observed.reshape(groups, halves, views_here * rows_here + 1, tile_width)
    table = observed[:, 0, views_here * rows_here, :entries].reshape(groups, 3, views_here, depth_here)
    table = jnp.transpose(table, (1, 0, 2, 3)).reshape(3, views_all, depth_here)
    observed = observed[:, :, : views_here * rows_here].reshape(groups, halves, views_here, rows_here, tile_width)
    observed = jnp.transpose(observed, (0, 2, 3, 1, 4)).reshape(views_all, rows_here, halves * tile_width)

    mine = lax.dynamic_slice_in_dim(density, group * rows_group, rows_group, 0)
    mine = mine.reshape(parts, rows_here * materials * depth_here, tile_width)
    wide = table.size
    extra = jnp.pad(table.reshape(1, wide), ((0, 0), (0, tile_width - wide))).astype(jnp.bfloat16)
    extra = jnp.broadcast_to(extra[None], (parts, 1, tile_width))
    mine = jnp.concatenate([mine, extra], axis=1)
    mine = lax.all_to_all(mine, ("depth", "lat"), 0, 0, tiled=True)
    mine = mine.reshape(depth_count, halves, rows_here * materials * depth_here + 1, tile_width)
    table = mine[:, 0, rows_here * materials * depth_here, :wide].astype(jnp.float32)
    table = table.reshape(depth_count, 3, views_all, depth_here)
    table = jnp.transpose(table, (1, 2, 0, 3)).reshape(3, views_all, depth_all)
    shift_all = table[0].astype(jnp.int32)
    lower_all = table[1]
    upper_all = table[2]
    mine = mine[:, :, : rows_here * materials * depth_here]
    mine = mine.reshape(depth_count, halves, rows_here, materials, depth_here, tile_width)
    mine = jnp.transpose(mine, (0, 4, 2, 3, 1, 5)).reshape(
        depth_all, rows_here, materials, halves * tile_width
    )
    stacked = stack_halves(mine.astype(jnp.float32), halves, tile_width)

    sums = shear_apply((shift_all + HALO).T, lower_all.T, upper_all.T, stacked, tile_width)
    sums = join_halves(sums, halves, rows_here, materials) / depth_all
    grads = spectral(sums, observed, spectrum, attenuation, views_all)
    stacked_grads = stack_halves(grads.astype(jnp.float32), halves, tile_width)
    layers = shear_apply(HALO - 1 - shift_all, upper_all, lower_all, stacked_grads, tile_width)
    layers = join_halves(layers, halves, rows_here, materials)
    layers = layers.reshape(depth_count, depth_here, rows_here, materials, halves, tile_width)
    layers = jnp.transpose(layers, (0, 4, 2, 3, 1, 5)).reshape(
        parts, rows_here, materials, depth_here, tile_width
    )
    layers = lax.all_to_all(layers, ("depth", "lat"), 0, 0, tiled=True)
    return layers.reshape(rows_group, materials, depth_here, tile_width)


def per_device_any(density, measured, shear_shift, shear_frac, spectrum, attenuation):
    if rows_fit_wide(density, measured):
        return per_device_wide(density, measured, shear_shift, shear_frac, spectrum, attenuation)
    if rows_fit(density, measured):
        return per_device_rows(density, measured, shear_shift, shear_frac, spectrum, attenuation)
    return per_device(density, measured, shear_shift, shear_frac, spectrum, attenuation)


def solution(mesh):
    in_specs = (
        P(None, None, "depth", "lat"),
        P("views", None, "lat"),
        P("views", "depth"),
        P("views", "depth"),
        P(),
        P(),
    )
    out_specs = P("views", None, "depth", "lat")
    return jax.shard_map(
        per_device_any, mesh=mesh, in_specs=in_specs, out_specs=out_specs, check_vma=False
    )
```

```python
import functools
import jax
import jax.numpy as jnp
from jax import lax
from jax.sharding import PartitionSpec as P
from jax.experimental import pallas as pl
from jax.experimental.pallas import tpu as pltpu

HALO = 64


def with_halo(x, sides, width):
    for axis, dim in sides:
        size, length = (lax.axis_size(axis), x.shape[dim])
        up = [(i, (i + 1) % size) for i in range(size - 1)]
        down = [(j, i) for i, j in up]
        last = lax.slice_in_dim(x, length - width, length, axis=dim)
        first = lax.slice_in_dim(x, 0, width, axis=dim)
        before = lax.ppermute(last, axis, up)
        after = lax.ppermute(first, axis, down)
        x = jnp.concatenate([before, x, after], axis=dim)
    return x


def exchange(x, axis):
    count = lax.axis_size(axis)
    me = lax.axis_index(axis)
    result = x
    for step in range(1, count):
        pairs = [(i, (i + step) % count) for i in range(count)]
        part = lax.dynamic_index_in_dim(x, (me + step) % count, 0, keepdims=True)
        part = lax.ppermute(part, axis, pairs)
        result = lax.dynamic_update_index_in_dim(result, part, (me - step) % count, 0)
    return result


def band_forward(shear_shift, lower_weight, upper_weight, window, block_width):
    band_shape = (shear_shift.shape[1], window, shear_shift.shape[0], block_width)
    tap_index = lax.broadcasted_iota(jnp.int32, band_shape, 1)
    column = lax.broadcasted_iota(jnp.int32, band_shape, 3)
    anchor = (shear_shift.T + HALO)[:, None, :, None]
    nothing = jnp.zeros((), jnp.bfloat16)
    lower_part = jnp.where(tap_index == column + anchor, lower_weight.T[:, None, :, None], nothing)
    upper_part = jnp.where(
        tap_index == column + anchor + 1, upper_weight.T[:, None, :, None], nothing
    )
    return lower_part + upper_part


def band_backward(shear_shift, lower_weight, upper_weight, window, block_width):
    band_shape = (shear_shift.shape[0], window, shear_shift.shape[1], block_width)
    tap_index = lax.broadcasted_iota(jnp.int32, band_shape, 1)
    column = lax.broadcasted_iota(jnp.int32, band_shape, 3)
    anchor = (HALO - shear_shift)[:, None, :, None]
    nothing = jnp.zeros((), jnp.bfloat16)
    lower_part = jnp.where(tap_index == column + anchor, lower_weight[:, None, :, None], nothing)
    upper_part = jnp.where(
        tap_index == column + anchor - 1, upper_weight[:, None, :, None], nothing
    )
    return lower_part + upper_part


def spectral(path_sums, observed, spectrum, attenuation, views_all):
    view_count, row_count, materials, tile_width = path_sums.shape
    block_pixels = 4096
    path_water = path_sums[:, :, 0, :].reshape(-1, block_pixels)
    path_bone = path_sums[:, :, 1, :].reshape(-1, block_pixels)
    target_flat = observed.reshape(-1, block_pixels)
    coefficients = jnp.concatenate(
        [jnp.ones((1, spectrum.shape[0]), jnp.float32), attenuation], axis=0
    )
    emitted = jnp.log(jnp.sum(spectrum))

    def one_block(inputs):
        water_block, bone_block, target_block = inputs
        exponent = (
            attenuation[0][:, None] * water_block[None, :]
            + attenuation[1][:, None] * bone_block[None, :]
        )
        counts = spectrum[:, None] * jnp.exp(-exponent)
        moments = jnp.dot(coefficients, counts, precision=lax.Precision.HIGHEST)
        intensity = moments[0]
        residual = emitted - jnp.log(intensity) - target_block
        factor = residual / intensity / views_all
        return (moments[1:] * factor[None, :]).astype(jnp.bfloat16)

    stacked = lax.map(one_block, (path_water, path_bone, target_flat))
    gradients = jnp.swapaxes(stacked, 0, 1).reshape(materials, view_count, row_count, tile_width)
    return jnp.transpose(gradients, (1, 2, 0, 3))


def per_device(density, measured, shear_shift, shear_frac, spectrum, attenuation):
    row_total, materials, depth_here, tile_width = density.shape
    block_width = min(128, tile_width)
    block_count = tile_width // block_width
    window = block_width + 2 * HALO
    views_all = measured.shape[0] * lax.axis_size("views")
    depth_all = depth_here * lax.axis_size("depth")
    rows_out = row_total // lax.axis_size("views")
    lower_weight = (1.0 - shear_frac).astype(jnp.bfloat16)
    upper_weight = shear_frac.astype(jnp.bfloat16)
    rows_here = density.shape[0]
    padded = with_halo(density, (("lat", 3),), HALO)
    framed = jnp.stack(
        [
            padded[:, :, :, number * block_width : number * block_width + window]
            for number in range(block_count)
        ],
        axis=2,
    )
    forward_band = band_forward(shear_shift, lower_weight, upper_weight, window, block_width)
    partial_value = jnp.einsum(
        "ymnzi,zivc->vymnc", framed, forward_band, preferred_element_type=jnp.float32
    )
    partial_value = partial_value.reshape(shear_shift.shape[0], rows_here, materials, tile_width)
    shares = lax.psum_scatter(partial_value, "depth", scatter_dimension=3, tiled=True) / depth_all
    share_cols = shares.shape[3]
    observed = lax.dynamic_slice_in_dim(
        measured, lax.axis_index("depth") * share_cols, share_cols, 2
    )
    share_grads = spectral(shares, observed, spectrum, attenuation, views_all)
    path_grads = lax.all_gather(share_grads, "depth", axis=3, tiled=True)
    padded_grads = with_halo(path_grads, (("lat", 3),), HALO)
    framed_grads = jnp.stack(
        [
            padded_grads[:, :, :, number * block_width : number * block_width + window]
            for number in range(block_count)
        ],
        axis=3,
    )
    backward_band = band_backward(shear_shift, lower_weight, upper_weight, window, block_width)
    product = jnp.einsum(
        "vymni,vizc->ymznc", framed_grads, backward_band, preferred_element_type=jnp.float32
    )
    return lax.psum_scatter(
        product.reshape(rows_out * lax.axis_size("views"), materials, depth_here, tile_width),
        "views",
        scatter_dimension=0,
        tiled=True,
    )


LANES = 128
INTERPRET = False


def shear_kernel(rot_ref, thr_ref, wa_ref, wb_ref, src_ref, out_ref):
    outer_count, channels, width = src_ref.shape
    inner_count, _, out_width = out_ref.shape
    pieces = width // LANES
    out_pieces = out_width // LANES
    out_ref[...] = jnp.zeros(out_ref.shape, jnp.float32)
    lane = lax.broadcasted_iota(jnp.int32, (channels, LANES), 1)

    def outer(o, carry):
        cols = [src_ref[o, :, k * LANES : (k + 1) * LANES] for k in range(pieces)]
        turned = [pltpu.roll(c, LANES - 1, 1) for c in cols]
        nexts = [
            jnp.where(lane < LANES - 1, turned[k], turned[k + 1]) for k in range(pieces - 1)
        ] + [turned[pieces - 1]]
        for i in range(inner_count):
            wa = wa_ref[o, i]
            wb = wb_ref[o, i]
            mixed = [wa * cols[k] + wb * nexts[k] for k in range(pieces)]
            rolled = [pltpu.roll(m, rot_ref[o, i], 1) for m in mixed]
            keep = lane < thr_ref[o, i]
            for j in range(out_pieces):
                out_ref[i, :, j * LANES : (j + 1) * LANES] += jnp.where(
                    keep, rolled[j], rolled[j + 1]
                )
        return carry

    lax.fori_loop(0, outer_count, outer, 0)


def shear_table_kernel(forward, tab_ref, src_ref, out_ref):
    outer_count, channels, width = src_ref.shape
    inner_count, _, out_width = out_ref.shape
    pieces = width // LANES
    out_pieces = out_width // LANES
    out_ref[...] = jnp.zeros(out_ref.shape, jnp.float32)
    lane = lax.broadcasted_iota(jnp.int32, (channels, LANES), 1)

    def outer(o, carry):
        cols = [src_ref[o, :, k * LANES : (k + 1) * LANES] for k in range(pieces)]
        turned = [pltpu.roll(c, LANES - 1, 1) for c in cols]
        nexts = [
            jnp.where(lane < LANES - 1, turned[k], turned[k + 1]) for k in range(pieces - 1)
        ] + [turned[pieces - 1]]
        for i in range(inner_count):
            if forward:
                shift = tab_ref[0, i, o].astype(jnp.int32)
                wa = tab_ref[1, i, o]
                wb = tab_ref[2, i, o]
                offset = shift + HALO
            else:
                shift = tab_ref[0, o, i].astype(jnp.int32)
                wa = tab_ref[2, o, i]
                wb = tab_ref[1, o, i]
                offset = HALO - 1 - shift
            limit = LANES - offset
            amount = jnp.where(limit == LANES, 0, limit)
            mixed = [wa * cols[k] + wb * nexts[k] for k in range(pieces)]
            rolled = [pltpu.roll(m, amount, 1) for m in mixed]
            keep = lane < limit
            for j in range(out_pieces):
                out_ref[i, :, j * LANES : (j + 1) * LANES] += jnp.where(
                    keep, rolled[j], rolled[j + 1]
                )
        return carry

    lax.fori_loop(0, outer_count, outer, 0)


def shear_table(forward, table, src, inner_count, out_width):
    _, channels, _ = src.shape
    smem = pl.BlockSpec(memory_space=pltpu.SMEM)
    vmem = pl.BlockSpec(memory_space=pltpu.VMEM)
    return pl.pallas_call(
        functools.partial(shear_table_kernel, forward),
        out_shape=jax.ShapeDtypeStruct((inner_count, channels, out_width), jnp.float32),
        in_specs=[smem, vmem],
        out_specs=vmem,
        interpret=INTERPRET,
    )(table, src)


def shear_apply(offset, wa, wb, src, out_width):
    outer_count, channels, width = src.shape
    inner_count = offset.shape[1]
    rot = (LANES - offset) % LANES
    thr = LANES - offset
    smem = pl.BlockSpec(memory_space=pltpu.SMEM)
    vmem = pl.BlockSpec(memory_space=pltpu.VMEM)
    return pl.pallas_call(
        shear_kernel,
        out_shape=jax.ShapeDtypeStruct((inner_count, channels, out_width), jnp.float32),
        in_specs=[smem, smem, smem, smem, vmem],
        out_specs=vmem,
        interpret=INTERPRET,
    )(rot.astype(jnp.int32), thr.astype(jnp.int32), wa, wb, src)


def rows_fit(density, measured):
    rows = density.shape[0]
    groups = lax.axis_size("views")
    depth = lax.axis_size("depth")
    tile_width = density.shape[3]
    return (
        rows % groups == 0
        and (rows // groups) % depth == 0
        and tile_width % LANES == 0
        and 2 * HALO <= LANES
        and tile_width >= HALO
        and tile_width >= 3 * measured.shape[0] * density.shape[2] * groups
    )


def per_device_rows(density, measured, shear_shift, shear_frac, spectrum, attenuation):
    row_total, materials, depth_here, tile_width = density.shape
    groups = lax.axis_size("views")
    depth_count = lax.axis_size("depth")
    views_here = measured.shape[0]
    views_all = views_here * groups
    depth_all = depth_here * depth_count
    rows_group = row_total // groups
    rows_here = rows_group // depth_count
    group = lax.axis_index("views")
    slab = lax.axis_index("depth")

    lower_weight = (1.0 - shear_frac).astype(jnp.bfloat16).astype(jnp.float32)
    upper_weight = shear_frac.astype(jnp.bfloat16).astype(jnp.float32)
    table = jnp.stack([shear_shift.astype(jnp.float32), lower_weight, upper_weight])
    entries = table.size
    observed = measured.reshape(views_here, groups, rows_group, tile_width)
    observed = lax.dynamic_slice_in_dim(observed, slab * rows_here, rows_here, 2)
    observed = jnp.transpose(observed, (1, 0, 2, 3)).reshape(groups, views_here * rows_here, tile_width)
    extra = jnp.pad(table.reshape(1, entries), ((0, 0), (0, tile_width - entries)))
    extra = jnp.broadcast_to(extra[None], (groups, 1, tile_width))
    observed = jnp.concatenate([observed, extra], axis=1)
    observed = lax.all_to_all(observed, "views", 0, 0, tiled=True)
    table = observed[:, views_here * rows_here, :entries].reshape(groups, 3, views_here, depth_here)
    table = jnp.transpose(table, (1, 0, 2, 3)).reshape(3, views_all, depth_here)
    observed = observed[:, : views_here * rows_here].reshape(views_all, rows_here, tile_width)

    channels = rows_here * materials
    mine = lax.dynamic_slice_in_dim(density, group * rows_group, rows_group, 0)
    mine = mine.reshape(depth_count, rows_here, materials, depth_here, tile_width)
    mine = jnp.transpose(mine, (0, 3, 1, 2, 4)).reshape(depth_count, depth_here * channels, tile_width)
    wide = table.size
    extra = jnp.pad(table.reshape(1, wide), ((0, 0), (0, tile_width - wide))).astype(jnp.bfloat16)
    extra = jnp.broadcast_to(extra[None], (depth_count, 1, tile_width))
    mine = jnp.concatenate([mine, extra], axis=1)
    mine = lax.all_to_all(mine, "depth", 0, 0, tiled=True)
    table = mine[:, depth_here * channels, :wide].astype(jnp.float32)
    table = table.reshape(depth_count, 3, views_all, depth_here)
    table = jnp.transpose(table, (1, 2, 0, 3)).reshape(3, views_all, depth_all)
    shift_all = table[0].astype(jnp.int32)
    lower_all = table[1]
    upper_all = table[2]
    mine = mine[:, : depth_here * channels].reshape(depth_all, channels, tile_width)
    padded = with_halo(mine, (("lat", 2),), HALO).astype(jnp.float32)

    sums = shear_apply(
        (shift_all + HALO).T, lower_all.T, upper_all.T, padded, tile_width
    )
    sums = (sums / depth_all).reshape(views_all, rows_here, materials, tile_width)
    grads = spectral(sums, observed, spectrum, attenuation, views_all)
    grads = grads.reshape(views_all, rows_here * materials, tile_width)
    padded_grads = with_halo(grads, (("lat", 2),), HALO).astype(jnp.float32)
    layers = shear_apply(
        HALO - 1 - shift_all, upper_all, lower_all, padded_grads, tile_width
    )
    layers = layers.reshape(depth_count, depth_here, rows_here, materials, tile_width)
    layers = exchange(layers, "depth")
    return jnp.transpose(layers, (0, 2, 3, 1, 4)).reshape(rows_group, materials, depth_here, tile_width)


def rows_fit_wide(density, measured):
    rows = density.shape[0]
    groups = lax.axis_size("views")
    parts = lax.axis_size("depth") * lax.axis_size("lat")
    tile_width = density.shape[3]
    return (
        rows % groups == 0
        and (rows // groups) % parts == 0
        and tile_width % LANES == 0
        and 2 * HALO <= LANES
        and tile_width >= HALO
        and tile_width >= 3 * measured.shape[0] * density.shape[2] * groups
    )


def stack_halves(values, halves, tile_width):
    count, rows, materials, _ = values.shape
    padded = jnp.pad(values, ((0, 0), (0, 0), (0, 0), (HALO, HALO)))
    parts = [
        padded[..., h * tile_width : h * tile_width + tile_width + 2 * HALO] for h in range(halves)
    ]
    return jnp.stack(parts, axis=1).reshape(count, halves * rows * materials, tile_width + 2 * HALO)


def join_halves(values, halves, rows, materials):
    count, _, tile_width = values.shape
    values = values.reshape(count, halves, rows, materials, tile_width)
    return jnp.transpose(values, (0, 2, 3, 1, 4)).reshape(count, rows, materials, halves * tile_width)


def per_device_wide(density, measured, shear_shift, shear_frac, spectrum, attenuation):
    row_total, materials, depth_here, tile_width = density.shape
    groups = lax.axis_size("views")
    depth_count = lax.axis_size("depth")
    halves = lax.axis_size("lat")
    parts = depth_count * halves
    views_here = measured.shape[0]
    views_all = views_here * groups
    depth_all = depth_here * depth_count
    rows_group = row_total // groups
    rows_here = rows_group // parts
    group = lax.axis_index("views")
    slab = lax.axis_index("depth")
    half = lax.axis_index("lat")

    lower_weight = (1.0 - shear_frac).astype(jnp.bfloat16).astype(jnp.float32)
    upper_weight = shear_frac.astype(jnp.bfloat16).astype(jnp.float32)
    block = jnp.stack([shear_shift.astype(jnp.float32), lower_weight, upper_weight])
    table = jnp.zeros((3, views_all, depth_all), jnp.float32)
    table = lax.dynamic_update_slice(table, block, (0, group * views_here, slab * depth_here))
    table = lax.psum(table, ("views", "depth"))
    observed = measured.reshape(views_here, groups, depth_count, halves, rows_here, tile_width)
    observed = lax.dynamic_index_in_dim(observed, slab, 2, keepdims=False)
    observed = jnp.transpose(observed, (1, 2, 0, 3, 4)).reshape(
        groups * halves, views_here * rows_here, tile_width
    )
    observed = lax.all_to_all(observed, ("views", "lat"), 0, 0, tiled=True)
    observed = observed.reshape(groups, halves, views_here, rows_here, tile_width)
    observed = jnp.transpose(observed, (0, 2, 3, 1, 4)).reshape(views_all, rows_here, halves * tile_width)

    mine = lax.dynamic_slice_in_dim(density, group * rows_group, rows_group, 0)
    mine = mine.reshape(parts, rows_here * materials * depth_here, tile_width)
    mine = lax.all_to_all(mine, ("depth", "lat"), 0, 0, tiled=True)
    mine = mine.reshape(depth_count, halves, rows_here, materials, depth_here, tile_width)
    mine = jnp.transpose(mine, (0, 4, 2, 3, 1, 5)).reshape(
        depth_all, rows_here, materials, halves * tile_width
    )
    stacked = stack_halves(mine.astype(jnp.float32), halves, tile_width)

    sums = shear_table(True, table, stacked, views_all, tile_width)
    sums = join_halves(sums, halves, rows_here, materials) / depth_all
    grads = spectral(sums, observed, spectrum, attenuation, views_all)
    stacked_grads = stack_halves(grads.astype(jnp.float32), halves, tile_width)
    layers = shear_table(False, table, stacked_grads, depth_all, tile_width)
    layers = join_halves(layers, halves, rows_here, materials)
    layers = layers.reshape(depth_count, depth_here, rows_here, materials, halves, tile_width)
    layers = jnp.transpose(layers, (0, 4, 2, 3, 1, 5)).reshape(
        parts, rows_here, materials, depth_here, tile_width
    )
    layers = lax.all_to_all(layers, ("depth", "lat"), 0, 0, tiled=True)
    return layers.reshape(rows_group, materials, depth_here, tile_width)


def per_device_any(density, measured, shear_shift, shear_frac, spectrum, attenuation):
    if rows_fit_wide(density, measured):
        return per_device_wide(density, measured, shear_shift, shear_frac, spectrum, attenuation)
    if rows_fit(density, measured):
        return per_device_rows(density, measured, shear_shift, shear_frac, spectrum, attenuation)
    return per_device(density, measured, shear_shift, shear_frac, spectrum, attenuation)


def solution(mesh):
    in_specs = (
        P(None, None, "depth", "lat"),
        P("views", None, "lat"),
        P("views", "depth"),
        P("views", "depth"),
        P(),
        P(),
    )
    out_specs = P("views", None, "depth", "lat")
    return jax.shard_map(
        per_device_any, mesh=mesh, in_specs=in_specs, out_specs=out_specs, check_vma=False
    )
```

```python
import functools
import jax
import jax.numpy as jnp
from jax import lax
from jax.sharding import PartitionSpec as P
from jax.experimental import pallas as pl
from jax.experimental.pallas import tpu as pltpu

HALO = 64


def with_halo(x, sides, width):
    for axis, dim in sides:
        size, length = (lax.axis_size(axis), x.shape[dim])
        up = [(i, (i + 1) % size) for i in range(size - 1)]
        down = [(j, i) for i, j in up]
        last = lax.slice_in_dim(x, length - width, length, axis=dim)
        first = lax.slice_in_dim(x, 0, width, axis=dim)
        before = lax.ppermute(last, axis, up)
        after = lax.ppermute(first, axis, down)
        x = jnp.concatenate([before, x, after], axis=dim)
    return x


def exchange(x, axis):
    count = lax.axis_size(axis)
    me = lax.axis_index(axis)
    result = x
    for step in range(1, count):
        pairs = [(i, (i + step) % count) for i in range(count)]
        part = lax.dynamic_index_in_dim(x, (me + step) % count, 0, keepdims=True)
        part = lax.ppermute(part, axis, pairs)
        result = lax.dynamic_update_index_in_dim(result, part, (me - step) % count, 0)
    return result


def band_forward(shear_shift, lower_weight, upper_weight, window, block_width):
    band_shape = (shear_shift.shape[1], window, shear_shift.shape[0], block_width)
    tap_index = lax.broadcasted_iota(jnp.int32, band_shape, 1)
    column = lax.broadcasted_iota(jnp.int32, band_shape, 3)
    anchor = (shear_shift.T + HALO)[:, None, :, None]
    nothing = jnp.zeros((), jnp.bfloat16)
    lower_part = jnp.where(tap_index == column + anchor, lower_weight.T[:, None, :, None], nothing)
    upper_part = jnp.where(
        tap_index == column + anchor + 1, upper_weight.T[:, None, :, None], nothing
    )
    return lower_part + upper_part


def band_backward(shear_shift, lower_weight, upper_weight, window, block_width):
    band_shape = (shear_shift.shape[0], window, shear_shift.shape[1], block_width)
    tap_index = lax.broadcasted_iota(jnp.int32, band_shape, 1)
    column = lax.broadcasted_iota(jnp.int32, band_shape, 3)
    anchor = (HALO - shear_shift)[:, None, :, None]
    nothing = jnp.zeros((), jnp.bfloat16)
    lower_part = jnp.where(tap_index == column + anchor, lower_weight[:, None, :, None], nothing)
    upper_part = jnp.where(
        tap_index == column + anchor - 1, upper_weight[:, None, :, None], nothing
    )
    return lower_part + upper_part


def spectral(path_sums, observed, spectrum, attenuation, views_all):
    view_count, row_count, materials, tile_width = path_sums.shape
    block_pixels = 4096
    path_water = path_sums[:, :, 0, :].reshape(-1, block_pixels)
    path_bone = path_sums[:, :, 1, :].reshape(-1, block_pixels)
    target_flat = observed.reshape(-1, block_pixels)
    coefficients = jnp.concatenate(
        [jnp.ones((1, spectrum.shape[0]), jnp.float32), attenuation], axis=0
    )
    emitted = jnp.log(jnp.sum(spectrum))

    def one_block(inputs):
        water_block, bone_block, target_block = inputs
        exponent = (
            attenuation[0][:, None] * water_block[None, :]
            + attenuation[1][:, None] * bone_block[None, :]
        )
        counts = spectrum[:, None] * jnp.exp(-exponent)
        moments = jnp.dot(coefficients, counts, precision=lax.Precision.HIGHEST)
        intensity = moments[0]
        residual = emitted - jnp.log(intensity) - target_block
        factor = residual / intensity / views_all
        return (moments[1:] * factor[None, :]).astype(jnp.bfloat16)

    stacked = lax.map(one_block, (path_water, path_bone, target_flat))
    gradients = jnp.swapaxes(stacked, 0, 1).reshape(materials, view_count, row_count, tile_width)
    return jnp.transpose(gradients, (1, 2, 0, 3))


def per_device(density, measured, shear_shift, shear_frac, spectrum, attenuation):
    row_total, materials, depth_here, tile_width = density.shape
    block_width = min(128, tile_width)
    block_count = tile_width // block_width
    window = block_width + 2 * HALO
    views_all = measured.shape[0] * lax.axis_size("views")
    depth_all = depth_here * lax.axis_size("depth")
    rows_out = row_total // lax.axis_size("views")
    lower_weight = (1.0 - shear_frac).astype(jnp.bfloat16)
    upper_weight = shear_frac.astype(jnp.bfloat16)
    rows_here = density.shape[0]
    padded = with_halo(density, (("lat", 3),), HALO)
    framed = jnp.stack(
        [
            padded[:, :, :, number * block_width : number * block_width + window]
            for number in range(block_count)
        ],
        axis=2,
    )
    forward_band = band_forward(shear_shift, lower_weight, upper_weight, window, block_width)
    partial_value = jnp.einsum(
        "ymnzi,zivc->vymnc", framed, forward_band, preferred_element_type=jnp.float32
    )
    partial_value = partial_value.reshape(shear_shift.shape[0], rows_here, materials, tile_width)
    shares = lax.psum_scatter(partial_value, "depth", scatter_dimension=3, tiled=True) / depth_all
    share_cols = shares.shape[3]
    observed = lax.dynamic_slice_in_dim(
        measured, lax.axis_index("depth") * share_cols, share_cols, 2
    )
    share_grads = spectral(shares, observed, spectrum, attenuation, views_all)
    path_grads = lax.all_gather(share_grads, "depth", axis=3, tiled=True)
    padded_grads = with_halo(path_grads, (("lat", 3),), HALO)
    framed_grads = jnp.stack(
        [
            padded_grads[:, :, :, number * block_width : number * block_width + window]
            for number in range(block_count)
        ],
        axis=3,
    )
    backward_band = band_backward(shear_shift, lower_weight, upper_weight, window, block_width)
    product = jnp.einsum(
        "vymni,vizc->ymznc", framed_grads, backward_band, preferred_element_type=jnp.float32
    )
    return lax.psum_scatter(
        product.reshape(rows_out * lax.axis_size("views"), materials, depth_here, tile_width),
        "views",
        scatter_dimension=0,
        tiled=True,
    )


LANES = 128
INTERPRET = False


def shear_kernel(rot_ref, thr_ref, wa_ref, wb_ref, src_ref, out_ref):
    outer_count, channels, width = src_ref.shape
    inner_count, _, out_width = out_ref.shape
    pieces = width // LANES
    out_pieces = out_width // LANES
    out_ref[...] = jnp.zeros(out_ref.shape, jnp.float32)
    lane = lax.broadcasted_iota(jnp.int32, (channels, LANES), 1)

    def outer(o, carry):
        cols = [src_ref[o, :, k * LANES : (k + 1) * LANES] for k in range(pieces)]
        turned = [pltpu.roll(c, LANES - 1, 1) for c in cols]
        nexts = [
            jnp.where(lane < LANES - 1, turned[k], turned[k + 1]) for k in range(pieces - 1)
        ] + [turned[pieces - 1]]
        for i in range(inner_count):
            wa = wa_ref[o, i]
            wb = wb_ref[o, i]
            mixed = [wa * cols[k] + wb * nexts[k] for k in range(pieces)]
            rolled = [pltpu.roll(m, rot_ref[o, i], 1) for m in mixed]
            keep = lane < thr_ref[o, i]
            for j in range(out_pieces):
                out_ref[i, :, j * LANES : (j + 1) * LANES] += jnp.where(
                    keep, rolled[j], rolled[j + 1]
                )
        return carry

    lax.fori_loop(0, outer_count, outer, 0)


def shear_table_kernel(forward, tab_ref, src_ref, out_ref):
    outer_count, channels, width = src_ref.shape
    inner_count, _, out_width = out_ref.shape
    pieces = width // LANES
    out_pieces = out_width // LANES
    out_ref[...] = jnp.zeros(out_ref.shape, jnp.float32)
    lane = lax.broadcasted_iota(jnp.int32, (channels, LANES), 1)

    def outer(o, carry):
        cols = [src_ref[o, :, k * LANES : (k + 1) * LANES] for k in range(pieces)]
        turned = [pltpu.roll(c, LANES - 1, 1) for c in cols]
        nexts = [
            jnp.where(lane < LANES - 1, turned[k], turned[k + 1]) for k in range(pieces - 1)
        ] + [turned[pieces - 1]]
        for i in range(inner_count):
            if forward:
                shift = tab_ref[0, i, o].astype(jnp.int32)
                wa = tab_ref[1, i, o]
                wb = tab_ref[2, i, o]
                offset = shift + HALO
            else:
                shift = tab_ref[0, o, i].astype(jnp.int32)
                wa = tab_ref[2, o, i]
                wb = tab_ref[1, o, i]
                offset = HALO - 1 - shift
            limit = LANES - offset
            amount = jnp.where(limit == LANES, 0, limit)
            mixed = [wa * cols[k] + wb * nexts[k] for k in range(pieces)]
            rolled = [pltpu.roll(m, amount, 1) for m in mixed]
            keep = lane < limit
            for j in range(out_pieces):
                out_ref[i, :, j * LANES : (j + 1) * LANES] += jnp.where(
                    keep, rolled[j], rolled[j + 1]
                )
        return carry

    lax.fori_loop(0, outer_count, outer, 0)


def shear_table(forward, table, src, inner_count, out_width):
    _, channels, _ = src.shape
    smem = pl.BlockSpec(memory_space=pltpu.SMEM)
    vmem = pl.BlockSpec(memory_space=pltpu.VMEM)
    return pl.pallas_call(
        functools.partial(shear_table_kernel, forward),
        out_shape=jax.ShapeDtypeStruct((inner_count, channels, out_width), jnp.float32),
        in_specs=[smem, vmem],
        out_specs=vmem,
        interpret=INTERPRET,
    )(table, src)


def shear_apply(offset, wa, wb, src, out_width):
    outer_count, channels, width = src.shape
    inner_count = offset.shape[1]
    rot = (LANES - offset) % LANES
    thr = LANES - offset
    smem = pl.BlockSpec(memory_space=pltpu.SMEM)
    vmem = pl.BlockSpec(memory_space=pltpu.VMEM)
    return pl.pallas_call(
        shear_kernel,
        out_shape=jax.ShapeDtypeStruct((inner_count, channels, out_width), jnp.float32),
        in_specs=[smem, smem, smem, smem, vmem],
        out_specs=vmem,
        interpret=INTERPRET,
    )(rot.astype(jnp.int32), thr.astype(jnp.int32), wa, wb, src)


def rows_fit(density, measured):
    rows = density.shape[0]
    groups = lax.axis_size("views")
    depth = lax.axis_size("depth")
    tile_width = density.shape[3]
    return (
        rows % groups == 0
        and (rows // groups) % depth == 0
        and tile_width % LANES == 0
        and 2 * HALO <= LANES
        and tile_width >= HALO
        and tile_width >= 3 * measured.shape[0] * density.shape[2] * groups
    )


def per_device_rows(density, measured, shear_shift, shear_frac, spectrum, attenuation):
    row_total, materials, depth_here, tile_width = density.shape
    groups = lax.axis_size("views")
    depth_count = lax.axis_size("depth")
    views_here = measured.shape[0]
    views_all = views_here * groups
    depth_all = depth_here * depth_count
    rows_group = row_total // groups
    rows_here = rows_group // depth_count
    group = lax.axis_index("views")
    slab = lax.axis_index("depth")

    lower_weight = (1.0 - shear_frac).astype(jnp.bfloat16).astype(jnp.float32)
    upper_weight = shear_frac.astype(jnp.bfloat16).astype(jnp.float32)
    table = jnp.stack([shear_shift.astype(jnp.float32), lower_weight, upper_weight])
    entries = table.size
    observed = measured.reshape(views_here, groups, rows_group, tile_width)
    observed = lax.dynamic_slice_in_dim(observed, slab * rows_here, rows_here, 2)
    observed = jnp.transpose(observed, (1, 0, 2, 3)).reshape(groups, views_here * rows_here, tile_width)
    extra = jnp.pad(table.reshape(1, entries), ((0, 0), (0, tile_width - entries)))
    extra = jnp.broadcast_to(extra[None], (groups, 1, tile_width))
    observed = jnp.concatenate([observed, extra], axis=1)
    observed = lax.all_to_all(observed, "views", 0, 0, tiled=True)
    table = observed[:, views_here * rows_here, :entries].reshape(groups, 3, views_here, depth_here)
    table = jnp.transpose(table, (1, 0, 2, 3)).reshape(3, views_all, depth_here)
    observed = observed[:, : views_here * rows_here].reshape(views_all, rows_here, tile_width)

    channels = rows_here * materials
    mine = lax.dynamic_slice_in_dim(density, group * rows_group, rows_group, 0)
    mine = mine.reshape(depth_count, rows_here, materials, depth_here, tile_width)
    mine = jnp.transpose(mine, (0, 3, 1, 2, 4)).reshape(depth_count, depth_here * channels, tile_width)
    wide = table.size
    extra = jnp.pad(table.reshape(1, wide), ((0, 0), (0, tile_width - wide))).astype(jnp.bfloat16)
    extra = jnp.broadcast_to(extra[None], (depth_count, 1, tile_width))
    mine = jnp.concatenate([mine, extra], axis=1)
    mine = lax.all_to_all(mine, "depth", 0, 0, tiled=True)
    table = mine[:, depth_here * channels, :wide].astype(jnp.float32)
    table = table.reshape(depth_count, 3, views_all, depth_here)
    table = jnp.transpose(table, (1, 2, 0, 3)).reshape(3, views_all, depth_all)
    shift_all = table[0].astype(jnp.int32)
    lower_all = table[1]
    upper_all = table[2]
    mine = mine[:, : depth_here * channels].reshape(depth_all, channels, tile_width)
    padded = with_halo(mine, (("lat", 2),), HALO).astype(jnp.float32)

    sums = shear_apply(
        (shift_all + HALO).T, lower_all.T, upper_all.T, padded, tile_width
    )
    sums = (sums / depth_all).reshape(views_all, rows_here, materials, tile_width)
    grads = spectral(sums, observed, spectrum, attenuation, views_all)
    grads = grads.reshape(views_all, rows_here * materials, tile_width)
    padded_grads = with_halo(grads, (("lat", 2),), HALO).astype(jnp.float32)
    layers = shear_apply(
        HALO - 1 - shift_all, upper_all, lower_all, padded_grads, tile_width
    )
    layers = layers.reshape(depth_count, depth_here, rows_here, materials, tile_width)
    layers = exchange(layers, "depth")
    return jnp.transpose(layers, (0, 2, 3, 1, 4)).reshape(rows_group, materials, depth_here, tile_width)


def rows_fit_wide(density, measured):
    rows = density.shape[0]
    groups = lax.axis_size("views")
    parts = lax.axis_size("depth") * lax.axis_size("lat")
    tile_width = density.shape[3]
    return (
        rows % groups == 0
        and (rows // groups) % parts == 0
        and tile_width % LANES == 0
        and 2 * HALO <= LANES
        and tile_width >= HALO
        and tile_width >= 3 * measured.shape[0] * density.shape[2]
        and ((rows // groups // parts) * density.shape[1] * density.shape[2]) % groups == 0
    )


def stack_halves(values, halves, tile_width):
    count, rows, materials, _ = values.shape
    padded = jnp.pad(values, ((0, 0), (0, 0), (0, 0), (HALO, HALO)))
    parts = [
        padded[..., h * tile_width : h * tile_width + tile_width + 2 * HALO] for h in range(halves)
    ]
    return jnp.stack(parts, axis=1).reshape(count, halves * rows * materials, tile_width + 2 * HALO)


def join_halves(values, halves, rows, materials):
    count, _, tile_width = values.shape
    values = values.reshape(count, halves, rows, materials, tile_width)
    return jnp.transpose(values, (0, 2, 3, 1, 4)).reshape(count, rows, materials, halves * tile_width)


def per_device_wide(density, measured, shear_shift, shear_frac, spectrum, attenuation):
    row_total, materials, depth_here, tile_width = density.shape
    groups = lax.axis_size("views")
    depth_count = lax.axis_size("depth")
    halves = lax.axis_size("lat")
    parts = depth_count * halves
    views_here = measured.shape[0]
    views_all = views_here * groups
    depth_all = depth_here * depth_count
    rows_group = row_total // groups
    rows_here = rows_group // parts
    group = lax.axis_index("views")
    slab = lax.axis_index("depth")
    half = lax.axis_index("lat")

    lower_weight = (1.0 - shear_frac).astype(jnp.bfloat16).astype(jnp.float32)
    upper_weight = shear_frac.astype(jnp.bfloat16).astype(jnp.float32)
    block = jnp.stack([shear_shift.astype(jnp.float32), lower_weight, upper_weight])
    entries = block.size
    observed = measured.reshape(views_here, groups, depth_count, halves, rows_here, tile_width)
    observed = lax.dynamic_index_in_dim(observed, slab, 2, keepdims=False)
    observed = jnp.transpose(observed, (1, 2, 0, 3, 4)).reshape(
        groups * halves, views_here * rows_here, tile_width
    )
    observed = lax.all_to_all(observed, ("views", "lat"), 0, 0, tiled=True)
    observed = observed.reshape(groups, halves, views_here, rows_here, tile_width)
    observed = jnp.transpose(observed, (0, 2, 3, 1, 4)).reshape(views_all, rows_here, halves * tile_width)

    chunk = rows_here * materials * depth_here * tile_width
    piece = chunk // groups
    mine = density.reshape(groups * parts, groups, piece)
    mine = lax.dynamic_index_in_dim(mine, group, 1, keepdims=False)
    mine = mine.reshape(groups * parts, piece // tile_width, tile_width)
    extra = jnp.pad(block.reshape(1, entries), ((0, 0), (0, tile_width - entries))).astype(jnp.bfloat16)
    extra = jnp.broadcast_to(extra[None], (groups * parts, 1, tile_width))
    mine = jnp.concatenate([mine, extra], axis=1)
    mine = lax.all_to_all(mine, ("views", "depth", "lat"), 0, 0, tiled=True)
    mine = mine.reshape(groups, depth_count, halves, piece // tile_width + 1, tile_width)
    table = mine[:, :, 0, piece // tile_width, :entries].astype(jnp.float32)
    table = table.reshape(groups, depth_count, 3, views_here, depth_here)
    table = jnp.transpose(table, (2, 0, 3, 1, 4)).reshape(3, views_all, depth_all)
    mine = mine[:, :, :, : piece // tile_width].reshape(groups, depth_count, halves, piece)
    mine = jnp.transpose(mine, (1, 2, 0, 3)).reshape(
        depth_count, halves, rows_here, materials, depth_here, tile_width
    )
    mine = jnp.transpose(mine, (0, 4, 2, 3, 1, 5)).reshape(
        depth_all, rows_here, materials, halves * tile_width
    )
    stacked = stack_halves(mine.astype(jnp.float32), halves, tile_width)

    sums = shear_table(True, table, stacked, views_all, tile_width)
    sums = join_halves(sums, halves, rows_here, materials) / depth_all
    grads = spectral(sums, observed, spectrum, attenuation, views_all)
    stacked_grads = stack_halves(grads.astype(jnp.float32), halves, tile_width)
    layers = shear_table(False, table, stacked_grads, depth_all, tile_width)
    layers = join_halves(layers, halves, rows_here, materials)
    layers = layers.reshape(depth_count, depth_here, rows_here, materials, halves, tile_width)
    layers = jnp.transpose(layers, (0, 4, 2, 3, 1, 5)).reshape(
        parts, rows_here, materials, depth_here, tile_width
    )
    layers = lax.all_to_all(layers, ("depth", "lat"), 0, 0, tiled=True)
    return layers.reshape(rows_group, materials, depth_here, tile_width)


def per_device_any(density, measured, shear_shift, shear_frac, spectrum, attenuation):
    if rows_fit_wide(density, measured):
        return per_device_wide(density, measured, shear_shift, shear_frac, spectrum, attenuation)
    if rows_fit(density, measured):
        return per_device_rows(density, measured, shear_shift, shear_frac, spectrum, attenuation)
    return per_device(density, measured, shear_shift, shear_frac, spectrum, attenuation)


def solution(mesh):
    in_specs = (
        P(None, None, "depth", "lat"),
        P("views", None, "lat"),
        P("views", "depth"),
        P("views", "depth"),
        P(),
        P(),
    )
    out_specs = P("views", None, "depth", "lat")
    return jax.shard_map(
        per_device_any, mesh=mesh, in_specs=in_specs, out_specs=out_specs, check_vma=False
    )
```

```python
import functools
import jax
import jax.numpy as jnp
from jax import lax
from jax.sharding import PartitionSpec as P
from jax.experimental import pallas as pl
from jax.experimental.pallas import tpu as pltpu

HALO = 64


def with_halo(x, sides, width):
    for axis, dim in sides:
        size, length = (lax.axis_size(axis), x.shape[dim])
        up = [(i, (i + 1) % size) for i in range(size - 1)]
        down = [(j, i) for i, j in up]
        last = lax.slice_in_dim(x, length - width, length, axis=dim)
        first = lax.slice_in_dim(x, 0, width, axis=dim)
        before = lax.ppermute(last, axis, up)
        after = lax.ppermute(first, axis, down)
        x = jnp.concatenate([before, x, after], axis=dim)
    return x


def exchange(x, axis):
    count = lax.axis_size(axis)
    me = lax.axis_index(axis)
    result = x
    for step in range(1, count):
        pairs = [(i, (i + step) % count) for i in range(count)]
        part = lax.dynamic_index_in_dim(x, (me + step) % count, 0, keepdims=True)
        part = lax.ppermute(part, axis, pairs)
        result = lax.dynamic_update_index_in_dim(result, part, (me - step) % count, 0)
    return result


def band_forward(shear_shift, lower_weight, upper_weight, window, block_width):
    band_shape = (shear_shift.shape[1], window, shear_shift.shape[0], block_width)
    tap_index = lax.broadcasted_iota(jnp.int32, band_shape, 1)
    column = lax.broadcasted_iota(jnp.int32, band_shape, 3)
    anchor = (shear_shift.T + HALO)[:, None, :, None]
    nothing = jnp.zeros((), jnp.bfloat16)
    lower_part = jnp.where(tap_index == column + anchor, lower_weight.T[:, None, :, None], nothing)
    upper_part = jnp.where(
        tap_index == column + anchor + 1, upper_weight.T[:, None, :, None], nothing
    )
    return lower_part + upper_part


def band_backward(shear_shift, lower_weight, upper_weight, window, block_width):
    band_shape = (shear_shift.shape[0], window, shear_shift.shape[1], block_width)
    tap_index = lax.broadcasted_iota(jnp.int32, band_shape, 1)
    column = lax.broadcasted_iota(jnp.int32, band_shape, 3)
    anchor = (HALO - shear_shift)[:, None, :, None]
    nothing = jnp.zeros((), jnp.bfloat16)
    lower_part = jnp.where(tap_index == column + anchor, lower_weight[:, None, :, None], nothing)
    upper_part = jnp.where(
        tap_index == column + anchor - 1, upper_weight[:, None, :, None], nothing
    )
    return lower_part + upper_part


def spectral(path_sums, observed, spectrum, attenuation, views_all):
    view_count, row_count, materials, tile_width = path_sums.shape
    block_pixels = 4096
    path_water = path_sums[:, :, 0, :].reshape(-1, block_pixels)
    path_bone = path_sums[:, :, 1, :].reshape(-1, block_pixels)
    target_flat = observed.reshape(-1, block_pixels)
    coefficients = jnp.concatenate(
        [jnp.ones((1, spectrum.shape[0]), jnp.float32), attenuation], axis=0
    )
    emitted = jnp.log(jnp.sum(spectrum))

    def one_block(inputs):
        water_block, bone_block, target_block = inputs
        exponent = (
            attenuation[0][:, None] * water_block[None, :]
            + attenuation[1][:, None] * bone_block[None, :]
        )
        counts = spectrum[:, None] * jnp.exp(-exponent)
        moments = jnp.dot(coefficients, counts, precision=lax.Precision.HIGHEST)
        intensity = moments[0]
        residual = emitted - jnp.log(intensity) - target_block
        factor = residual / intensity / views_all
        return (moments[1:] * factor[None, :]).astype(jnp.bfloat16)

    stacked = lax.map(one_block, (path_water, path_bone, target_flat))
    gradients = jnp.swapaxes(stacked, 0, 1).reshape(materials, view_count, row_count, tile_width)
    return jnp.transpose(gradients, (1, 2, 0, 3))


def per_device(density, measured, shear_shift, shear_frac, spectrum, attenuation):
    row_total, materials, depth_here, tile_width = density.shape
    block_width = min(128, tile_width)
    block_count = tile_width // block_width
    window = block_width + 2 * HALO
    views_all = measured.shape[0] * lax.axis_size("views")
    depth_all = depth_here * lax.axis_size("depth")
    rows_out = row_total // lax.axis_size("views")
    lower_weight = (1.0 - shear_frac).astype(jnp.bfloat16)
    upper_weight = shear_frac.astype(jnp.bfloat16)
    rows_here = density.shape[0]
    padded = with_halo(density, (("lat", 3),), HALO)
    framed = jnp.stack(
        [
            padded[:, :, :, number * block_width : number * block_width + window]
            for number in range(block_count)
        ],
        axis=2,
    )
    forward_band = band_forward(shear_shift, lower_weight, upper_weight, window, block_width)
    partial_value = jnp.einsum(
        "ymnzi,zivc->vymnc", framed, forward_band, preferred_element_type=jnp.float32
    )
    partial_value = partial_value.reshape(shear_shift.shape[0], rows_here, materials, tile_width)
    shares = lax.psum_scatter(partial_value, "depth", scatter_dimension=3, tiled=True) / depth_all
    share_cols = shares.shape[3]
    observed = lax.dynamic_slice_in_dim(
        measured, lax.axis_index("depth") * share_cols, share_cols, 2
    )
    share_grads = spectral(shares, observed, spectrum, attenuation, views_all)
    path_grads = lax.all_gather(share_grads, "depth", axis=3, tiled=True)
    padded_grads = with_halo(path_grads, (("lat", 3),), HALO)
    framed_grads = jnp.stack(
        [
            padded_grads[:, :, :, number * block_width : number * block_width + window]
            for number in range(block_count)
        ],
        axis=3,
    )
    backward_band = band_backward(shear_shift, lower_weight, upper_weight, window, block_width)
    product = jnp.einsum(
        "vymni,vizc->ymznc", framed_grads, backward_band, preferred_element_type=jnp.float32
    )
    return lax.psum_scatter(
        product.reshape(rows_out * lax.axis_size("views"), materials, depth_here, tile_width),
        "views",
        scatter_dimension=0,
        tiled=True,
    )


LANES = 128
INTERPRET = False


def shear_kernel(rot_ref, thr_ref, wa_ref, wb_ref, src_ref, out_ref):
    outer_count, channels, width = src_ref.shape
    inner_count, _, out_width = out_ref.shape
    pieces = width // LANES
    out_pieces = out_width // LANES
    out_ref[...] = jnp.zeros(out_ref.shape, jnp.float32)
    lane = lax.broadcasted_iota(jnp.int32, (channels, LANES), 1)

    def outer(o, carry):
        cols = [src_ref[o, :, k * LANES : (k + 1) * LANES] for k in range(pieces)]
        turned = [pltpu.roll(c, LANES - 1, 1) for c in cols]
        nexts = [
            jnp.where(lane < LANES - 1, turned[k], turned[k + 1]) for k in range(pieces - 1)
        ] + [turned[pieces - 1]]
        for i in range(inner_count):
            wa = wa_ref[o, i]
            wb = wb_ref[o, i]
            mixed = [wa * cols[k] + wb * nexts[k] for k in range(pieces)]
            rolled = [pltpu.roll(m, rot_ref[o, i], 1) for m in mixed]
            keep = lane < thr_ref[o, i]
            for j in range(out_pieces):
                out_ref[i, :, j * LANES : (j + 1) * LANES] += jnp.where(
                    keep, rolled[j], rolled[j + 1]
                )
        return carry

    lax.fori_loop(0, outer_count, outer, 0)


def shear_table_kernel(forward, tab_ref, src_ref, out_ref):
    outer_count, channels, width = src_ref.shape
    inner_count, _, out_width = out_ref.shape
    pieces = width // LANES
    out_pieces = out_width // LANES
    out_ref[...] = jnp.zeros(out_ref.shape, jnp.float32)
    lane = lax.broadcasted_iota(jnp.int32, (channels, LANES), 1)

    def outer(o, carry):
        cols = [src_ref[o, :, k * LANES : (k + 1) * LANES] for k in range(pieces)]
        turned = [pltpu.roll(c, LANES - 1, 1) for c in cols]
        nexts = [
            jnp.where(lane < LANES - 1, turned[k], turned[k + 1]) for k in range(pieces - 1)
        ] + [turned[pieces - 1]]
        for i in range(inner_count):
            if forward:
                shift = tab_ref[0, i, o].astype(jnp.int32)
                wa = tab_ref[1, i, o]
                wb = tab_ref[2, i, o]
                offset = shift + HALO
            else:
                shift = tab_ref[0, o, i].astype(jnp.int32)
                wa = tab_ref[2, o, i]
                wb = tab_ref[1, o, i]
                offset = HALO - 1 - shift
            limit = LANES - offset
            amount = jnp.where(limit == LANES, 0, limit)
            mixed = [wa * cols[k] + wb * nexts[k] for k in range(pieces)]
            rolled = [pltpu.roll(m, amount, 1) for m in mixed]
            keep = lane < limit
            for j in range(out_pieces):
                out_ref[i, :, j * LANES : (j + 1) * LANES] += jnp.where(
                    keep, rolled[j], rolled[j + 1]
                )
        return carry

    lax.fori_loop(0, outer_count, outer, 0)


def shear_table(forward, table, src, inner_count, out_width):
    _, channels, _ = src.shape
    smem = pl.BlockSpec(memory_space=pltpu.SMEM)
    vmem = pl.BlockSpec(memory_space=pltpu.VMEM)
    return pl.pallas_call(
        functools.partial(shear_table_kernel, forward),
        out_shape=jax.ShapeDtypeStruct((inner_count, channels, out_width), jnp.float32),
        in_specs=[smem, vmem],
        out_specs=vmem,
        interpret=INTERPRET,
    )(table, src)


def shear_apply(offset, wa, wb, src, out_width):
    outer_count, channels, width = src.shape
    inner_count = offset.shape[1]
    rot = (LANES - offset) % LANES
    thr = LANES - offset
    smem = pl.BlockSpec(memory_space=pltpu.SMEM)
    vmem = pl.BlockSpec(memory_space=pltpu.VMEM)
    return pl.pallas_call(
        shear_kernel,
        out_shape=jax.ShapeDtypeStruct((inner_count, channels, out_width), jnp.float32),
        in_specs=[smem, smem, smem, smem, vmem],
        out_specs=vmem,
        interpret=INTERPRET,
    )(rot.astype(jnp.int32), thr.astype(jnp.int32), wa, wb, src)


def rows_fit(density, measured):
    rows = density.shape[0]
    groups = lax.axis_size("views")
    depth = lax.axis_size("depth")
    tile_width = density.shape[3]
    return (
        rows % groups == 0
        and (rows // groups) % depth == 0
        and tile_width % LANES == 0
        and 2 * HALO <= LANES
        and tile_width >= HALO
        and tile_width >= 3 * measured.shape[0] * density.shape[2] * groups
    )


def per_device_rows(density, measured, shear_shift, shear_frac, spectrum, attenuation):
    row_total, materials, depth_here, tile_width = density.shape
    groups = lax.axis_size("views")
    depth_count = lax.axis_size("depth")
    views_here = measured.shape[0]
    views_all = views_here * groups
    depth_all = depth_here * depth_count
    rows_group = row_total // groups
    rows_here = rows_group // depth_count
    group = lax.axis_index("views")
    slab = lax.axis_index("depth")

    lower_weight = (1.0 - shear_frac).astype(jnp.bfloat16).astype(jnp.float32)
    upper_weight = shear_frac.astype(jnp.bfloat16).astype(jnp.float32)
    table = jnp.stack([shear_shift.astype(jnp.float32), lower_weight, upper_weight])
    entries = table.size
    observed = measured.reshape(views_here, groups, rows_group, tile_width)
    observed = lax.dynamic_slice_in_dim(observed, slab * rows_here, rows_here, 2)
    observed = jnp.transpose(observed, (1, 0, 2, 3)).reshape(groups, views_here * rows_here, tile_width)
    extra = jnp.pad(table.reshape(1, entries), ((0, 0), (0, tile_width - entries)))
    extra = jnp.broadcast_to(extra[None], (groups, 1, tile_width))
    observed = jnp.concatenate([observed, extra], axis=1)
    observed = lax.all_to_all(observed, "views", 0, 0, tiled=True)
    table = observed[:, views_here * rows_here, :entries].reshape(groups, 3, views_here, depth_here)
    table = jnp.transpose(table, (1, 0, 2, 3)).reshape(3, views_all, depth_here)
    observed = observed[:, : views_here * rows_here].reshape(views_all, rows_here, tile_width)

    channels = rows_here * materials
    mine = lax.dynamic_slice_in_dim(density, group * rows_group, rows_group, 0)
    mine = mine.reshape(depth_count, rows_here, materials, depth_here, tile_width)
    mine = jnp.transpose(mine, (0, 3, 1, 2, 4)).reshape(depth_count, depth_here * channels, tile_width)
    wide = table.size
    extra = jnp.pad(table.reshape(1, wide), ((0, 0), (0, tile_width - wide))).astype(jnp.bfloat16)
    extra = jnp.broadcast_to(extra[None], (depth_count, 1, tile_width))
    mine = jnp.concatenate([mine, extra], axis=1)
    mine = lax.all_to_all(mine, "depth", 0, 0, tiled=True)
    table = mine[:, depth_here * channels, :wide].astype(jnp.float32)
    table = table.reshape(depth_count, 3, views_all, depth_here)
    table = jnp.transpose(table, (1, 2, 0, 3)).reshape(3, views_all, depth_all)
    shift_all = table[0].astype(jnp.int32)
    lower_all = table[1]
    upper_all = table[2]
    mine = mine[:, : depth_here * channels].reshape(depth_all, channels, tile_width)
    padded = with_halo(mine, (("lat", 2),), HALO).astype(jnp.float32)

    sums = shear_apply(
        (shift_all + HALO).T, lower_all.T, upper_all.T, padded, tile_width
    )
    sums = (sums / depth_all).reshape(views_all, rows_here, materials, tile_width)
    grads = spectral(sums, observed, spectrum, attenuation, views_all)
    grads = grads.reshape(views_all, rows_here * materials, tile_width)
    padded_grads = with_halo(grads, (("lat", 2),), HALO).astype(jnp.float32)
    layers = shear_apply(
        HALO - 1 - shift_all, upper_all, lower_all, padded_grads, tile_width
    )
    layers = layers.reshape(depth_count, depth_here, rows_here, materials, tile_width)
    layers = exchange(layers, "depth")
    return jnp.transpose(layers, (0, 2, 3, 1, 4)).reshape(rows_group, materials, depth_here, tile_width)


def rows_fit_wide(density, measured):
    rows = density.shape[0]
    groups = lax.axis_size("views")
    parts = lax.axis_size("depth") * lax.axis_size("lat")
    tile_width = density.shape[3]
    return (
        rows % groups == 0
        and (rows // groups) % parts == 0
        and tile_width % LANES == 0
        and 2 * HALO <= LANES
        and tile_width >= HALO
        and tile_width >= 3 * measured.shape[0] * density.shape[2]
        and ((rows // groups // parts) * density.shape[1] * density.shape[2]) % groups == 0
        and (measured.shape[0] * (rows // groups // parts)) % lax.axis_size("depth") == 0
    )


def stack_halves(values, halves, tile_width):
    count, rows, materials, _ = values.shape
    padded = jnp.pad(values, ((0, 0), (0, 0), (0, 0), (HALO, HALO)))
    parts = [
        padded[..., h * tile_width : h * tile_width + tile_width + 2 * HALO] for h in range(halves)
    ]
    return jnp.stack(parts, axis=1).reshape(count, halves * rows * materials, tile_width + 2 * HALO)


def join_halves(values, halves, rows, materials):
    count, _, tile_width = values.shape
    values = values.reshape(count, halves, rows, materials, tile_width)
    return jnp.transpose(values, (0, 2, 3, 1, 4)).reshape(count, rows, materials, halves * tile_width)


def per_device_wide(density, measured, shear_shift, shear_frac, spectrum, attenuation):
    row_total, materials, depth_here, tile_width = density.shape
    groups = lax.axis_size("views")
    depth_count = lax.axis_size("depth")
    halves = lax.axis_size("lat")
    parts = depth_count * halves
    views_here = measured.shape[0]
    views_all = views_here * groups
    depth_all = depth_here * depth_count
    rows_group = row_total // groups
    rows_here = rows_group // parts
    group = lax.axis_index("views")
    slab = lax.axis_index("depth")
    half = lax.axis_index("lat")

    lower_weight = (1.0 - shear_frac).astype(jnp.bfloat16).astype(jnp.float32)
    upper_weight = shear_frac.astype(jnp.bfloat16).astype(jnp.float32)
    block = jnp.stack([shear_shift.astype(jnp.float32), lower_weight, upper_weight])
    entries = block.size
    parts_all = groups * parts
    chunk = rows_here * materials * depth_here * tile_width
    piece = chunk // groups
    dens_rows = piece // tile_width
    mine = density.reshape(parts_all, groups, piece)
    mine = lax.dynamic_index_in_dim(mine, group, 1, keepdims=False)
    mine = mine.reshape(parts_all, dens_rows, tile_width).astype(jnp.float32)
    meas_rows = views_here * rows_here // depth_count
    observed = measured.reshape(views_here, parts_all, rows_here, tile_width)
    observed = jnp.transpose(observed, (1, 0, 2, 3)).reshape(parts_all, depth_count, meas_rows * tile_width)
    observed = lax.dynamic_index_in_dim(observed, slab, 1, keepdims=False)
    observed = observed.reshape(parts_all, meas_rows, tile_width)
    extra = jnp.pad(block.reshape(1, entries), ((0, 0), (0, tile_width - entries)))
    extra = jnp.broadcast_to(extra[None], (parts_all, 1, tile_width))
    packed = jnp.concatenate([mine, observed, extra], axis=1)
    packed = lax.all_to_all(packed, ("views", "depth", "lat"), 0, 0, tiled=True)
    packed = packed.reshape(groups, depth_count, halves, dens_rows + meas_rows + 1, tile_width)
    table = packed[:, :, 0, dens_rows + meas_rows, :entries]
    table = table.reshape(groups, depth_count, 3, views_here, depth_here)
    table = jnp.transpose(table, (2, 0, 3, 1, 4)).reshape(3, views_all, depth_all)
    observed = packed[:, :, :, dens_rows : dens_rows + meas_rows]
    observed = jnp.transpose(observed, (0, 2, 1, 3, 4)).reshape(
        groups, halves, views_here, rows_here, tile_width
    )
    observed = jnp.transpose(observed, (0, 2, 3, 1, 4)).reshape(views_all, rows_here, halves * tile_width)
    mine = packed[:, :, :, :dens_rows].reshape(groups, depth_count, halves, piece)
    mine = jnp.transpose(mine, (1, 2, 0, 3)).reshape(
        depth_count, halves, rows_here, materials, depth_here, tile_width
    )
    mine = jnp.transpose(mine, (0, 4, 2, 3, 1, 5)).reshape(
        depth_all, rows_here, materials, halves * tile_width
    )
    stacked = stack_halves(mine, halves, tile_width)

    sums = shear_table(True, table, stacked, views_all, tile_width)
    sums = join_halves(sums, halves, rows_here, materials) / depth_all
    grads = spectral(sums, observed, spectrum, attenuation, views_all)
    stacked_grads = stack_halves(grads.astype(jnp.float32), halves, tile_width)
    layers = shear_table(False, table, stacked_grads, depth_all, tile_width)
    layers = join_halves(layers, halves, rows_here, materials)
    layers = layers.reshape(depth_count, depth_here, rows_here, materials, halves, tile_width)
    layers = jnp.transpose(layers, (0, 4, 2, 3, 1, 5)).reshape(
        parts, rows_here, materials, depth_here, tile_width
    )
    layers = lax.all_to_all(layers, ("depth", "lat"), 0, 0, tiled=True)
    return layers.reshape(rows_group, materials, depth_here, tile_width)


def per_device_any(density, measured, shear_shift, shear_frac, spectrum, attenuation):
    if rows_fit_wide(density, measured):
        return per_device_wide(density, measured, shear_shift, shear_frac, spectrum, attenuation)
    if rows_fit(density, measured):
        return per_device_rows(density, measured, shear_shift, shear_frac, spectrum, attenuation)
    return per_device(density, measured, shear_shift, shear_frac, spectrum, attenuation)


def solution(mesh):
    in_specs = (
        P(None, None, "depth", "lat"),
        P("views", None, "lat"),
        P("views", "depth"),
        P("views", "depth"),
        P(),
        P(),
    )
    out_specs = P("views", None, "depth", "lat")
    return jax.shard_map(
        per_device_any, mesh=mesh, in_specs=in_specs, out_specs=out_specs, check_vma=False
    )
```

```python
import functools
import jax
import jax.numpy as jnp
from jax import lax
from jax.sharding import PartitionSpec as P
from jax.experimental import pallas as pl
from jax.experimental.pallas import tpu as pltpu

HALO = 64


def with_halo(x, sides, width):
    for axis, dim in sides:
        size, length = (lax.axis_size(axis), x.shape[dim])
        up = [(i, (i + 1) % size) for i in range(size - 1)]
        down = [(j, i) for i, j in up]
        last = lax.slice_in_dim(x, length - width, length, axis=dim)
        first = lax.slice_in_dim(x, 0, width, axis=dim)
        before = lax.ppermute(last, axis, up)
        after = lax.ppermute(first, axis, down)
        x = jnp.concatenate([before, x, after], axis=dim)
    return x


def exchange(x, axis):
    count = lax.axis_size(axis)
    me = lax.axis_index(axis)
    result = x
    for step in range(1, count):
        pairs = [(i, (i + step) % count) for i in range(count)]
        part = lax.dynamic_index_in_dim(x, (me + step) % count, 0, keepdims=True)
        part = lax.ppermute(part, axis, pairs)
        result = lax.dynamic_update_index_in_dim(result, part, (me - step) % count, 0)
    return result


def band_forward(shear_shift, lower_weight, upper_weight, window, block_width):
    band_shape = (shear_shift.shape[1], window, shear_shift.shape[0], block_width)
    tap_index = lax.broadcasted_iota(jnp.int32, band_shape, 1)
    column = lax.broadcasted_iota(jnp.int32, band_shape, 3)
    anchor = (shear_shift.T + HALO)[:, None, :, None]
    nothing = jnp.zeros((), jnp.bfloat16)
    lower_part = jnp.where(tap_index == column + anchor, lower_weight.T[:, None, :, None], nothing)
    upper_part = jnp.where(
        tap_index == column + anchor + 1, upper_weight.T[:, None, :, None], nothing
    )
    return lower_part + upper_part


def band_backward(shear_shift, lower_weight, upper_weight, window, block_width):
    band_shape = (shear_shift.shape[0], window, shear_shift.shape[1], block_width)
    tap_index = lax.broadcasted_iota(jnp.int32, band_shape, 1)
    column = lax.broadcasted_iota(jnp.int32, band_shape, 3)
    anchor = (HALO - shear_shift)[:, None, :, None]
    nothing = jnp.zeros((), jnp.bfloat16)
    lower_part = jnp.where(tap_index == column + anchor, lower_weight[:, None, :, None], nothing)
    upper_part = jnp.where(
        tap_index == column + anchor - 1, upper_weight[:, None, :, None], nothing
    )
    return lower_part + upper_part


def spectral(path_sums, observed, spectrum, attenuation, views_all):
    view_count, row_count, materials, tile_width = path_sums.shape
    block_pixels = 4096
    path_water = path_sums[:, :, 0, :].reshape(-1, block_pixels)
    path_bone = path_sums[:, :, 1, :].reshape(-1, block_pixels)
    target_flat = observed.reshape(-1, block_pixels)
    coefficients = jnp.concatenate(
        [jnp.ones((1, spectrum.shape[0]), jnp.float32), attenuation], axis=0
    )
    emitted = jnp.log(jnp.sum(spectrum))

    def one_block(inputs):
        water_block, bone_block, target_block = inputs
        exponent = (
            attenuation[0][:, None] * water_block[None, :]
            + attenuation[1][:, None] * bone_block[None, :]
        )
        counts = spectrum[:, None] * jnp.exp(-exponent)
        moments = jnp.dot(coefficients, counts, precision=lax.Precision.HIGHEST)
        intensity = moments[0]
        residual = emitted - jnp.log(intensity) - target_block
        factor = residual / intensity / views_all
        return (moments[1:] * factor[None, :]).astype(jnp.bfloat16)

    stacked = lax.map(one_block, (path_water, path_bone, target_flat))
    gradients = jnp.swapaxes(stacked, 0, 1).reshape(materials, view_count, row_count, tile_width)
    return jnp.transpose(gradients, (1, 2, 0, 3))


def spectral_kernel(views_all, emitted_ref, spectrum_ref, attenuation_ref, water_ref, bone_ref, target_ref, out0_ref, out1_ref):
    rows, width = water_ref.shape
    energies = spectrum_ref.shape[0]
    block = 8

    def one_block(b, carry):
        lo = pl.multiple_of(b * block, block)
        water = water_ref[pl.ds(lo, block), :]
        bone = bone_ref[pl.ds(lo, block), :]

        def one_energy(e, sums):
            intensity, first, second = sums
            a0 = attenuation_ref[0, e]
            a1 = attenuation_ref[1, e]
            counts = spectrum_ref[e] * jnp.exp(-(a0 * water + a1 * bone))
            return (intensity + counts, first + a0 * counts, second + a1 * counts)

        zero = jnp.zeros((block, width), jnp.float32)
        intensity, first, second = lax.fori_loop(0, energies, one_energy, (zero, zero, zero), unroll=8)
        residual = emitted_ref[0] - jnp.log(intensity) - target_ref[pl.ds(lo, block), :]
        factor = residual / intensity / views_all
        out0_ref[pl.ds(lo, block), :] = (first * factor).astype(out0_ref.dtype)
        out1_ref[pl.ds(lo, block), :] = (second * factor).astype(out1_ref.dtype)
        return carry

    lax.fori_loop(0, rows // block, one_block, 0)


def spectral_pallas(path_sums, observed, spectrum, attenuation, views_all):
    view_count, row_count, materials, width_all = path_sums.shape
    pixels = view_count * row_count * width_all
    rows = pixels // LANES // 4
    water = path_sums[:, :, 0, :].reshape(rows, 4 * LANES)
    bone = path_sums[:, :, 1, :].reshape(rows, 4 * LANES)
    target = observed.reshape(rows, 4 * LANES)
    emitted = jnp.log(jnp.sum(spectrum)).reshape(1)
    smem = pl.BlockSpec(memory_space=pltpu.SMEM)
    vmem = pl.BlockSpec(memory_space=pltpu.VMEM)
    first, second = pl.pallas_call(
        functools.partial(spectral_kernel, views_all),
        out_shape=(
            jax.ShapeDtypeStruct((rows, 4 * LANES), jnp.bfloat16),
            jax.ShapeDtypeStruct((rows, 4 * LANES), jnp.bfloat16),
        ),
        in_specs=[smem, smem, smem, vmem, vmem, vmem],
        out_specs=(vmem, vmem),
        interpret=INTERPRET,
    )(emitted, spectrum, attenuation, water, bone, target)
    shape = (view_count, row_count, width_all)
    return jnp.stack([first.reshape(shape), second.reshape(shape)], axis=2)


def per_device(density, measured, shear_shift, shear_frac, spectrum, attenuation):
    row_total, materials, depth_here, tile_width = density.shape
    block_width = min(128, tile_width)
    block_count = tile_width // block_width
    window = block_width + 2 * HALO
    views_all = measured.shape[0] * lax.axis_size("views")
    depth_all = depth_here * lax.axis_size("depth")
    rows_out = row_total // lax.axis_size("views")
    lower_weight = (1.0 - shear_frac).astype(jnp.bfloat16)
    upper_weight = shear_frac.astype(jnp.bfloat16)
    rows_here = density.shape[0]
    padded = with_halo(density, (("lat", 3),), HALO)
    framed = jnp.stack(
        [
            padded[:, :, :, number * block_width : number * block_width + window]
            for number in range(block_count)
        ],
        axis=2,
    )
    forward_band = band_forward(shear_shift, lower_weight, upper_weight, window, block_width)
    partial_value = jnp.einsum(
        "ymnzi,zivc->vymnc", framed, forward_band, preferred_element_type=jnp.float32
    )
    partial_value = partial_value.reshape(shear_shift.shape[0], rows_here, materials, tile_width)
    shares = lax.psum_scatter(partial_value, "depth", scatter_dimension=3, tiled=True) / depth_all
    share_cols = shares.shape[3]
    observed = lax.dynamic_slice_in_dim(
        measured, lax.axis_index("depth") * share_cols, share_cols, 2
    )
    share_grads = spectral(shares, observed, spectrum, attenuation, views_all)
    path_grads = lax.all_gather(share_grads, "depth", axis=3, tiled=True)
    padded_grads = with_halo(path_grads, (("lat", 3),), HALO)
    framed_grads = jnp.stack(
        [
            padded_grads[:, :, :, number * block_width : number * block_width + window]
            for number in range(block_count)
        ],
        axis=3,
    )
    backward_band = band_backward(shear_shift, lower_weight, upper_weight, window, block_width)
    product = jnp.einsum(
        "vymni,vizc->ymznc", framed_grads, backward_band, preferred_element_type=jnp.float32
    )
    return lax.psum_scatter(
        product.reshape(rows_out * lax.axis_size("views"), materials, depth_here, tile_width),
        "views",
        scatter_dimension=0,
        tiled=True,
    )


LANES = 128
INTERPRET = False


def shear_kernel(rot_ref, thr_ref, wa_ref, wb_ref, src_ref, out_ref):
    outer_count, channels, width = src_ref.shape
    inner_count, _, out_width = out_ref.shape
    pieces = width // LANES
    out_pieces = out_width // LANES
    out_ref[...] = jnp.zeros(out_ref.shape, jnp.float32)
    lane = lax.broadcasted_iota(jnp.int32, (channels, LANES), 1)

    def outer(o, carry):
        cols = [src_ref[o, :, k * LANES : (k + 1) * LANES] for k in range(pieces)]
        turned = [pltpu.roll(c, LANES - 1, 1) for c in cols]
        nexts = [
            jnp.where(lane < LANES - 1, turned[k], turned[k + 1]) for k in range(pieces - 1)
        ] + [turned[pieces - 1]]
        for i in range(inner_count):
            wa = wa_ref[o, i]
            wb = wb_ref[o, i]
            mixed = [wa * cols[k] + wb * nexts[k] for k in range(pieces)]
            rolled = [pltpu.roll(m, rot_ref[o, i], 1) for m in mixed]
            keep = lane < thr_ref[o, i]
            for j in range(out_pieces):
                out_ref[i, :, j * LANES : (j + 1) * LANES] += jnp.where(
                    keep, rolled[j], rolled[j + 1]
                )
        return carry

    lax.fori_loop(0, outer_count, outer, 0)


def shear_table_kernel(forward, tab_ref, src_ref, out_ref):
    outer_count, channels, width = src_ref.shape
    inner_count, _, out_width = out_ref.shape
    pieces = width // LANES
    out_pieces = out_width // LANES
    out_ref[...] = jnp.zeros(out_ref.shape, jnp.float32)
    lane = lax.broadcasted_iota(jnp.int32, (channels, LANES), 1)

    def outer(o, carry):
        cols = [src_ref[o, :, k * LANES : (k + 1) * LANES] for k in range(pieces)]
        turned = [pltpu.roll(c, LANES - 1, 1) for c in cols]
        nexts = [
            jnp.where(lane < LANES - 1, turned[k], turned[k + 1]) for k in range(pieces - 1)
        ] + [turned[pieces - 1]]
        for i in range(inner_count):
            if forward:
                shift = tab_ref[0, i, o].astype(jnp.int32)
                wa = tab_ref[1, i, o]
                wb = tab_ref[2, i, o]
                offset = shift + HALO
            else:
                shift = tab_ref[0, o, i].astype(jnp.int32)
                wa = tab_ref[2, o, i]
                wb = tab_ref[1, o, i]
                offset = HALO - 1 - shift
            limit = LANES - offset
            amount = jnp.where(limit == LANES, 0, limit)
            mixed = [wa * cols[k] + wb * nexts[k] for k in range(pieces)]
            rolled = [pltpu.roll(m, amount, 1) for m in mixed]
            keep = lane < limit
            for j in range(out_pieces):
                out_ref[i, :, j * LANES : (j + 1) * LANES] += jnp.where(
                    keep, rolled[j], rolled[j + 1]
                )
        return carry

    lax.fori_loop(0, outer_count, outer, 0)


def shear_table(forward, table, src, inner_count, out_width):
    _, channels, _ = src.shape
    smem = pl.BlockSpec(memory_space=pltpu.SMEM)
    vmem = pl.BlockSpec(memory_space=pltpu.VMEM)
    return pl.pallas_call(
        functools.partial(shear_table_kernel, forward),
        out_shape=jax.ShapeDtypeStruct((inner_count, channels, out_width), jnp.float32),
        in_specs=[smem, vmem],
        out_specs=vmem,
        interpret=INTERPRET,
    )(table, src)


def shear_apply(offset, wa, wb, src, out_width):
    outer_count, channels, width = src.shape
    inner_count = offset.shape[1]
    rot = (LANES - offset) % LANES
    thr = LANES - offset
    smem = pl.BlockSpec(memory_space=pltpu.SMEM)
    vmem = pl.BlockSpec(memory_space=pltpu.VMEM)
    return pl.pallas_call(
        shear_kernel,
        out_shape=jax.ShapeDtypeStruct((inner_count, channels, out_width), jnp.float32),
        in_specs=[smem, smem, smem, smem, vmem],
        out_specs=vmem,
        interpret=INTERPRET,
    )(rot.astype(jnp.int32), thr.astype(jnp.int32), wa, wb, src)


def rows_fit(density, measured):
    rows = density.shape[0]
    groups = lax.axis_size("views")
    depth = lax.axis_size("depth")
    tile_width = density.shape[3]
    return (
        rows % groups == 0
        and (rows // groups) % depth == 0
        and tile_width % LANES == 0
        and 2 * HALO <= LANES
        and tile_width >= HALO
        and tile_width >= 3 * measured.shape[0] * density.shape[2] * groups
    )


def per_device_rows(density, measured, shear_shift, shear_frac, spectrum, attenuation):
    row_total, materials, depth_here, tile_width = density.shape
    groups = lax.axis_size("views")
    depth_count = lax.axis_size("depth")
    views_here = measured.shape[0]
    views_all = views_here * groups
    depth_all = depth_here * depth_count
    rows_group = row_total // groups
    rows_here = rows_group // depth_count
    group = lax.axis_index("views")
    slab = lax.axis_index("depth")

    lower_weight = (1.0 - shear_frac).astype(jnp.bfloat16).astype(jnp.float32)
    upper_weight = shear_frac.astype(jnp.bfloat16).astype(jnp.float32)
    table = jnp.stack([shear_shift.astype(jnp.float32), lower_weight, upper_weight])
    entries = table.size
    observed = measured.reshape(views_here, groups, rows_group, tile_width)
    observed = lax.dynamic_slice_in_dim(observed, slab * rows_here, rows_here, 2)
    observed = jnp.transpose(observed, (1, 0, 2, 3)).reshape(groups, views_here * rows_here, tile_width)
    extra = jnp.pad(table.reshape(1, entries), ((0, 0), (0, tile_width - entries)))
    extra = jnp.broadcast_to(extra[None], (groups, 1, tile_width))
    observed = jnp.concatenate([observed, extra], axis=1)
    observed = lax.all_to_all(observed, "views", 0, 0, tiled=True)
    table = observed[:, views_here * rows_here, :entries].reshape(groups, 3, views_here, depth_here)
    table = jnp.transpose(table, (1, 0, 2, 3)).reshape(3, views_all, depth_here)
    observed = observed[:, : views_here * rows_here].reshape(views_all, rows_here, tile_width)

    channels = rows_here * materials
    mine = lax.dynamic_slice_in_dim(density, group * rows_group, rows_group, 0)
    mine = mine.reshape(depth_count, rows_here, materials, depth_here, tile_width)
    mine = jnp.transpose(mine, (0, 3, 1, 2, 4)).reshape(depth_count, depth_here * channels, tile_width)
    wide = table.size
    extra = jnp.pad(table.reshape(1, wide), ((0, 0), (0, tile_width - wide))).astype(jnp.bfloat16)
    extra = jnp.broadcast_to(extra[None], (depth_count, 1, tile_width))
    mine = jnp.concatenate([mine, extra], axis=1)
    mine = lax.all_to_all(mine, "depth", 0, 0, tiled=True)
    table = mine[:, depth_here * channels, :wide].astype(jnp.float32)
    table = table.reshape(depth_count, 3, views_all, depth_here)
    table = jnp.transpose(table, (1, 2, 0, 3)).reshape(3, views_all, depth_all)
    shift_all = table[0].astype(jnp.int32)
    lower_all = table[1]
    upper_all = table[2]
    mine = mine[:, : depth_here * channels].reshape(depth_all, channels, tile_width)
    padded = with_halo(mine, (("lat", 2),), HALO).astype(jnp.float32)

    sums = shear_apply(
        (shift_all + HALO).T, lower_all.T, upper_all.T, padded, tile_width
    )
    sums = (sums / depth_all).reshape(views_all, rows_here, materials, tile_width)
    grads = spectral(sums, observed, spectrum, attenuation, views_all)
    grads = grads.reshape(views_all, rows_here * materials, tile_width)
    padded_grads = with_halo(grads, (("lat", 2),), HALO).astype(jnp.float32)
    layers = shear_apply(
        HALO - 1 - shift_all, upper_all, lower_all, padded_grads, tile_width
    )
    layers = layers.reshape(depth_count, depth_here, rows_here, materials, tile_width)
    layers = exchange(layers, "depth")
    return jnp.transpose(layers, (0, 2, 3, 1, 4)).reshape(rows_group, materials, depth_here, tile_width)


def rows_fit_wide(density, measured):
    rows = density.shape[0]
    groups = lax.axis_size("views")
    parts = lax.axis_size("depth") * lax.axis_size("lat")
    tile_width = density.shape[3]
    return (
        rows % groups == 0
        and (rows // groups) % parts == 0
        and tile_width % LANES == 0
        and 2 * HALO <= LANES
        and tile_width >= HALO
        and tile_width >= 3 * measured.shape[0] * density.shape[2]
        and ((rows // groups // parts) * density.shape[1] * density.shape[2]) % groups == 0
    )


def stack_halves(values, halves, tile_width):
    count, rows, materials, _ = values.shape
    padded = jnp.pad(values, ((0, 0), (0, 0), (0, 0), (HALO, HALO)))
    parts = [
        padded[..., h * tile_width : h * tile_width + tile_width + 2 * HALO] for h in range(halves)
    ]
    return jnp.stack(parts, axis=1).reshape(count, halves * rows * materials, tile_width + 2 * HALO)


def join_halves(values, halves, rows, materials):
    count, _, tile_width = values.shape
    values = values.reshape(count, halves, rows, materials, tile_width)
    return jnp.transpose(values, (0, 2, 3, 1, 4)).reshape(count, rows, materials, halves * tile_width)


def per_device_wide(density, measured, shear_shift, shear_frac, spectrum, attenuation):
    row_total, materials, depth_here, tile_width = density.shape
    groups = lax.axis_size("views")
    depth_count = lax.axis_size("depth")
    halves = lax.axis_size("lat")
    parts = depth_count * halves
    views_here = measured.shape[0]
    views_all = views_here * groups
    depth_all = depth_here * depth_count
    rows_group = row_total // groups
    rows_here = rows_group // parts
    group = lax.axis_index("views")
    slab = lax.axis_index("depth")
    half = lax.axis_index("lat")

    lower_weight = (1.0 - shear_frac).astype(jnp.bfloat16).astype(jnp.float32)
    upper_weight = shear_frac.astype(jnp.bfloat16).astype(jnp.float32)
    block = jnp.stack([shear_shift.astype(jnp.float32), lower_weight, upper_weight])
    entries = block.size
    observed = measured.reshape(views_here, groups, depth_count, halves, rows_here, tile_width)
    observed = lax.dynamic_index_in_dim(observed, slab, 2, keepdims=False)
    observed = jnp.transpose(observed, (1, 2, 0, 3, 4)).reshape(
        groups * halves, views_here * rows_here, tile_width
    )
    observed = lax.all_to_all(observed, ("views", "lat"), 0, 0, tiled=True)
    observed = observed.reshape(groups, halves, views_here, rows_here, tile_width)
    observed = jnp.transpose(observed, (0, 2, 3, 1, 4)).reshape(views_all, rows_here, halves * tile_width)

    chunk = rows_here * materials * depth_here * tile_width
    piece = chunk // groups
    mine = density.reshape(groups * parts, groups, piece)
    mine = lax.dynamic_index_in_dim(mine, group, 1, keepdims=False)
    mine = mine.reshape(groups * parts, piece // tile_width, tile_width)
    extra = jnp.pad(block.reshape(1, entries), ((0, 0), (0, tile_width - entries))).astype(jnp.bfloat16)
    extra = jnp.broadcast_to(extra[None], (groups * parts, 1, tile_width))
    mine = jnp.concatenate([mine, extra], axis=1)
    mine = lax.all_to_all(mine, ("views", "depth", "lat"), 0, 0, tiled=True)
    mine = mine.reshape(groups, depth_count, halves, piece // tile_width + 1, tile_width)
    table = mine[:, :, 0, piece // tile_width, :entries].astype(jnp.float32)
    table = table.reshape(groups, depth_count, 3, views_here, depth_here)
    table = jnp.transpose(table, (2, 0, 3, 1, 4)).reshape(3, views_all, depth_all)
    mine = mine[:, :, :, : piece // tile_width].reshape(groups, depth_count, halves, piece)
    mine = jnp.transpose(mine, (1, 2, 0, 3)).reshape(
        depth_count, halves, rows_here, materials, depth_here, tile_width
    )
    mine = jnp.transpose(mine, (0, 4, 2, 3, 1, 5)).reshape(
        depth_all, rows_here, materials, halves * tile_width
    )
    stacked = stack_halves(mine.astype(jnp.float32), halves, tile_width)

    sums = shear_table(True, table, stacked, views_all, tile_width)
    sums = join_halves(sums, halves, rows_here, materials) / depth_all
    grads = spectral_pallas(sums, observed, spectrum, attenuation, views_all)
    stacked_grads = stack_halves(grads.astype(jnp.float32), halves, tile_width)
    layers = shear_table(False, table, stacked_grads, depth_all, tile_width)
    layers = join_halves(layers, halves, rows_here, materials)
    layers = layers.reshape(depth_count, depth_here, rows_here, materials, halves, tile_width)
    layers = jnp.transpose(layers, (0, 4, 2, 3, 1, 5)).reshape(
        parts, rows_here, materials, depth_here, tile_width
    )
    layers = lax.all_to_all(layers, ("depth", "lat"), 0, 0, tiled=True)
    return layers.reshape(rows_group, materials, depth_here, tile_width)


def per_device_any(density, measured, shear_shift, shear_frac, spectrum, attenuation):
    if rows_fit_wide(density, measured):
        return per_device_wide(density, measured, shear_shift, shear_frac, spectrum, attenuation)
    if rows_fit(density, measured):
        return per_device_rows(density, measured, shear_shift, shear_frac, spectrum, attenuation)
    return per_device(density, measured, shear_shift, shear_frac, spectrum, attenuation)


def solution(mesh):
    in_specs = (
        P(None, None, "depth", "lat"),
        P("views", None, "lat"),
        P("views", "depth"),
        P("views", "depth"),
        P(),
        P(),
    )
    out_specs = P("views", None, "depth", "lat")
    return jax.shard_map(
        per_device_any, mesh=mesh, in_specs=in_specs, out_specs=out_specs, check_vma=False
    )
```

```python
import functools
import jax
import jax.numpy as jnp
from jax import lax
from jax.sharding import PartitionSpec as P
from jax.experimental import pallas as pl
from jax.experimental.pallas import tpu as pltpu

HALO = 64


def with_halo(x, sides, width):
    for axis, dim in sides:
        size, length = (lax.axis_size(axis), x.shape[dim])
        up = [(i, (i + 1) % size) for i in range(size - 1)]
        down = [(j, i) for i, j in up]
        last = lax.slice_in_dim(x, length - width, length, axis=dim)
        first = lax.slice_in_dim(x, 0, width, axis=dim)
        before = lax.ppermute(last, axis, up)
        after = lax.ppermute(first, axis, down)
        x = jnp.concatenate([before, x, after], axis=dim)
    return x


def exchange(x, axis):
    count = lax.axis_size(axis)
    me = lax.axis_index(axis)
    result = x
    for step in range(1, count):
        pairs = [(i, (i + step) % count) for i in range(count)]
        part = lax.dynamic_index_in_dim(x, (me + step) % count, 0, keepdims=True)
        part = lax.ppermute(part, axis, pairs)
        result = lax.dynamic_update_index_in_dim(result, part, (me - step) % count, 0)
    return result


def band_forward(shear_shift, lower_weight, upper_weight, window, block_width):
    band_shape = (shear_shift.shape[1], window, shear_shift.shape[0], block_width)
    tap_index = lax.broadcasted_iota(jnp.int32, band_shape, 1)
    column = lax.broadcasted_iota(jnp.int32, band_shape, 3)
    anchor = (shear_shift.T + HALO)[:, None, :, None]
    nothing = jnp.zeros((), jnp.bfloat16)
    lower_part = jnp.where(tap_index == column + anchor, lower_weight.T[:, None, :, None], nothing)
    upper_part = jnp.where(
        tap_index == column + anchor + 1, upper_weight.T[:, None, :, None], nothing
    )
    return lower_part + upper_part


def band_backward(shear_shift, lower_weight, upper_weight, window, block_width):
    band_shape = (shear_shift.shape[0], window, shear_shift.shape[1], block_width)
    tap_index = lax.broadcasted_iota(jnp.int32, band_shape, 1)
    column = lax.broadcasted_iota(jnp.int32, band_shape, 3)
    anchor = (HALO - shear_shift)[:, None, :, None]
    nothing = jnp.zeros((), jnp.bfloat16)
    lower_part = jnp.where(tap_index == column + anchor, lower_weight[:, None, :, None], nothing)
    upper_part = jnp.where(
        tap_index == column + anchor - 1, upper_weight[:, None, :, None], nothing
    )
    return lower_part + upper_part


def spectral(path_sums, observed, spectrum, attenuation, views_all):
    view_count, row_count, materials, tile_width = path_sums.shape
    block_pixels = 4096
    path_water = path_sums[:, :, 0, :].reshape(-1, block_pixels)
    path_bone = path_sums[:, :, 1, :].reshape(-1, block_pixels)
    target_flat = observed.reshape(-1, block_pixels)
    coefficients = jnp.concatenate(
        [jnp.ones((1, spectrum.shape[0]), jnp.float32), attenuation], axis=0
    )
    emitted = jnp.log(jnp.sum(spectrum))

    def one_block(inputs):
        water_block, bone_block, target_block = inputs
        exponent = (
            attenuation[0][:, None] * water_block[None, :]
            + attenuation[1][:, None] * bone_block[None, :]
        )
        counts = spectrum[:, None] * jnp.exp(-exponent)
        moments = jnp.dot(coefficients, counts, precision=lax.Precision.HIGHEST)
        intensity = moments[0]
        residual = emitted - jnp.log(intensity) - target_block
        factor = residual / intensity / views_all
        return (moments[1:] * factor[None, :]).astype(jnp.bfloat16)

    stacked = lax.map(one_block, (path_water, path_bone, target_flat))
    gradients = jnp.swapaxes(stacked, 0, 1).reshape(materials, view_count, row_count, tile_width)
    return jnp.transpose(gradients, (1, 2, 0, 3))


def spectral_kernel(views_all, emitted_ref, spectrum_ref, attenuation_ref, water_ref, bone_ref, target_ref, out0_ref, out1_ref):
    rows, width = water_ref.shape
    energies = spectrum_ref.shape[0]
    block = 8

    def one_block(b, carry):
        lo = pl.multiple_of(b * block, block)
        water = water_ref[pl.ds(lo, block), :]
        bone = bone_ref[pl.ds(lo, block), :]

        def one_energy(e, sums):
            intensity, first, second = sums
            a0 = attenuation_ref[0, e]
            a1 = attenuation_ref[1, e]
            counts = spectrum_ref[e] * jnp.exp(-(a0 * water + a1 * bone))
            return (intensity + counts, first + a0 * counts, second + a1 * counts)

        zero = jnp.zeros((block, width), jnp.float32)
        intensity, first, second = lax.fori_loop(0, energies, one_energy, (zero, zero, zero), unroll=8)
        residual = emitted_ref[0] - jnp.log(intensity) - target_ref[pl.ds(lo, block), :]
        factor = residual / intensity / views_all
        out0_ref[pl.ds(lo, block), :] = (first * factor).astype(out0_ref.dtype)
        out1_ref[pl.ds(lo, block), :] = (second * factor).astype(out1_ref.dtype)
        return carry

    lax.fori_loop(0, rows // block, one_block, 0)


def spectral_pallas(path_sums, observed, spectrum, attenuation, views_all):
    view_count, row_count, materials, width_all = path_sums.shape
    pixels = view_count * row_count * width_all
    rows = pixels // LANES // 4
    water = path_sums[:, :, 0, :].reshape(rows, 4 * LANES)
    bone = path_sums[:, :, 1, :].reshape(rows, 4 * LANES)
    target = observed.reshape(rows, 4 * LANES)
    emitted = jnp.log(jnp.sum(spectrum)).reshape(1)
    smem = pl.BlockSpec(memory_space=pltpu.SMEM)
    vmem = pl.BlockSpec(memory_space=pltpu.VMEM)
    first, second = pl.pallas_call(
        functools.partial(spectral_kernel, views_all),
        out_shape=(
            jax.ShapeDtypeStruct((rows, 4 * LANES), jnp.bfloat16),
            jax.ShapeDtypeStruct((rows, 4 * LANES), jnp.bfloat16),
        ),
        in_specs=[smem, smem, smem, vmem, vmem, vmem],
        out_specs=(vmem, vmem),
        interpret=INTERPRET,
    )(emitted, spectrum, attenuation, water, bone, target)
    shape = (view_count, row_count, width_all)
    return jnp.stack([first.reshape(shape), second.reshape(shape)], axis=2)


def per_device(density, measured, shear_shift, shear_frac, spectrum, attenuation):
    row_total, materials, depth_here, tile_width = density.shape
    block_width = min(128, tile_width)
    block_count = tile_width // block_width
    window = block_width + 2 * HALO
    views_all = measured.shape[0] * lax.axis_size("views")
    depth_all = depth_here * lax.axis_size("depth")
    rows_out = row_total // lax.axis_size("views")
    lower_weight = (1.0 - shear_frac).astype(jnp.bfloat16)
    upper_weight = shear_frac.astype(jnp.bfloat16)
    rows_here = density.shape[0]
    padded = with_halo(density, (("lat", 3),), HALO)
    framed = jnp.stack(
        [
            padded[:, :, :, number * block_width : number * block_width + window]
            for number in range(block_count)
        ],
        axis=2,
    )
    forward_band = band_forward(shear_shift, lower_weight, upper_weight, window, block_width)
    partial_value = jnp.einsum(
        "ymnzi,zivc->vymnc", framed, forward_band, preferred_element_type=jnp.float32
    )
    partial_value = partial_value.reshape(shear_shift.shape[0], rows_here, materials, tile_width)
    shares = lax.psum_scatter(partial_value, "depth", scatter_dimension=3, tiled=True) / depth_all
    share_cols = shares.shape[3]
    observed = lax.dynamic_slice_in_dim(
        measured, lax.axis_index("depth") * share_cols, share_cols, 2
    )
    share_grads = spectral(shares, observed, spectrum, attenuation, views_all)
    path_grads = lax.all_gather(share_grads, "depth", axis=3, tiled=True)
    padded_grads = with_halo(path_grads, (("lat", 3),), HALO)
    framed_grads = jnp.stack(
        [
            padded_grads[:, :, :, number * block_width : number * block_width + window]
            for number in range(block_count)
        ],
        axis=3,
    )
    backward_band = band_backward(shear_shift, lower_weight, upper_weight, window, block_width)
    product = jnp.einsum(
        "vymni,vizc->ymznc", framed_grads, backward_band, preferred_element_type=jnp.float32
    )
    return lax.psum_scatter(
        product.reshape(rows_out * lax.axis_size("views"), materials, depth_here, tile_width),
        "views",
        scatter_dimension=0,
        tiled=True,
    )


LANES = 128
INTERPRET = False


def shear_kernel(rot_ref, thr_ref, wa_ref, wb_ref, src_ref, out_ref):
    outer_count, channels, width = src_ref.shape
    inner_count, _, out_width = out_ref.shape
    pieces = width // LANES
    out_pieces = out_width // LANES
    out_ref[...] = jnp.zeros(out_ref.shape, jnp.float32)
    lane = lax.broadcasted_iota(jnp.int32, (channels, LANES), 1)

    def outer(o, carry):
        cols = [src_ref[o, :, k * LANES : (k + 1) * LANES] for k in range(pieces)]
        turned = [pltpu.roll(c, LANES - 1, 1) for c in cols]
        nexts = [
            jnp.where(lane < LANES - 1, turned[k], turned[k + 1]) for k in range(pieces - 1)
        ] + [turned[pieces - 1]]
        for i in range(inner_count):
            wa = wa_ref[o, i]
            wb = wb_ref[o, i]
            mixed = [wa * cols[k] + wb * nexts[k] for k in range(pieces)]
            rolled = [pltpu.roll(m, rot_ref[o, i], 1) for m in mixed]
            keep = lane < thr_ref[o, i]
            for j in range(out_pieces):
                out_ref[i, :, j * LANES : (j + 1) * LANES] += jnp.where(
                    keep, rolled[j], rolled[j + 1]
                )
        return carry

    lax.fori_loop(0, outer_count, outer, 0)


def shear_table_kernel(forward, tab_ref, src_ref, out_ref):
    outer_count, channels, width = src_ref.shape
    inner_count, _, out_width = out_ref.shape
    pieces = width // LANES
    out_pieces = out_width // LANES
    out_ref[...] = jnp.zeros(out_ref.shape, jnp.float32)
    lane = lax.broadcasted_iota(jnp.int32, (channels, LANES), 1)

    def outer(o, carry):
        cols = [src_ref[o, :, k * LANES : (k + 1) * LANES] for k in range(pieces)]
        turned = [pltpu.roll(c, LANES - 1, 1) for c in cols]
        nexts = [
            jnp.where(lane < LANES - 1, turned[k], turned[k + 1]) for k in range(pieces - 1)
        ] + [turned[pieces - 1]]
        for i in range(inner_count):
            if forward:
                shift = tab_ref[0, i, o].astype(jnp.int32)
                wa = tab_ref[1, i, o]
                wb = tab_ref[2, i, o]
                offset = shift + HALO
            else:
                shift = tab_ref[0, o, i].astype(jnp.int32)
                wa = tab_ref[2, o, i]
                wb = tab_ref[1, o, i]
                offset = HALO - 1 - shift
            limit = LANES - offset
            amount = jnp.where(limit == LANES, 0, limit)
            mixed = [wa * cols[k] + wb * nexts[k] for k in range(pieces)]
            rolled = [pltpu.roll(m, amount, 1) for m in mixed]
            keep = lane < limit
            for j in range(out_pieces):
                out_ref[i, :, j * LANES : (j + 1) * LANES] += jnp.where(
                    keep, rolled[j], rolled[j + 1]
                )
        return carry

    lax.fori_loop(0, outer_count, outer, 0)


def shear_table(forward, table, src, inner_count, out_width):
    _, channels, _ = src.shape
    smem = pl.BlockSpec(memory_space=pltpu.SMEM)
    vmem = pl.BlockSpec(memory_space=pltpu.VMEM)
    return pl.pallas_call(
        functools.partial(shear_table_kernel, forward),
        out_shape=jax.ShapeDtypeStruct((inner_count, channels, out_width), jnp.float32),
        in_specs=[smem, vmem],
        out_specs=vmem,
        interpret=INTERPRET,
    )(table, src)


def halo_columns(ys, lane, half_of, rows_here, halves, channels):
    count = len(ys)
    turned = [pltpu.roll(y, HALO, 1) for y in ys]
    zero = jnp.zeros_like(ys[0])
    left = jnp.where(half_of >= 1, pltpu.roll(turned[count - 1], rows_here, 0), zero)
    right = jnp.where(half_of <= halves - 2, pltpu.roll(turned[0], channels - rows_here, 0), zero)
    edge = lane < HALO
    cols = [jnp.where(edge, left, turned[0])]
    cols += [jnp.where(edge, turned[k - 1], turned[k]) for k in range(1, count)]
    cols += [jnp.where(edge, turned[count - 1], right)]
    return cols


def shear_pass(forward, rows_here, halves, tab_ref, src_ref, acc_ref):
    outer_count, channels, width = src_ref.shape
    inner_count = acc_ref.shape[0]
    pieces = width // LANES
    lane = lax.broadcasted_iota(jnp.int32, (channels, LANES), 1)
    half_of = (lax.broadcasted_iota(jnp.int32, (channels, LANES), 0) // rows_here) % halves
    acc_ref[...] = jnp.zeros(acc_ref.shape, jnp.float32)

    def outer(o, carry):
        ys = [src_ref[o, :, k * LANES : (k + 1) * LANES] for k in range(pieces)]
        cols = halo_columns(ys, lane, half_of, rows_here, halves, channels)
        turned = [pltpu.roll(c, LANES - 1, 1) for c in cols]
        nexts = [jnp.where(lane < LANES - 1, turned[k], turned[k + 1]) for k in range(pieces)]
        nexts.append(turned[pieces])
        for i in range(inner_count):
            if forward:
                shift = tab_ref[0, i, o].astype(jnp.int32)
                wa = tab_ref[1, i, o]
                wb = tab_ref[2, i, o]
                offset = shift + HALO
            else:
                shift = tab_ref[0, o, i].astype(jnp.int32)
                wa = tab_ref[2, o, i]
                wb = tab_ref[1, o, i]
                offset = HALO - 1 - shift
            limit = LANES - offset
            amount = jnp.where(limit == LANES, 0, limit)
            mixed = [wa * cols[k] + wb * nexts[k] for k in range(pieces + 1)]
            rolled = [pltpu.roll(m, amount, 1) for m in mixed]
            keep = lane < limit
            for j in range(pieces):
                acc_ref[i, :, j * LANES : (j + 1) * LANES] += jnp.where(keep, rolled[j], rolled[j + 1])
        return carry

    lax.fori_loop(0, outer_count, outer, 0)


def forward_kernel(rows_here, halves, depth_all, views_all, tab_ref, emitted_ref, spectrum_ref,
                   attenuation_ref, src_ref, target_ref, out_ref, sums_ref):
    shear_pass(True, rows_here, halves, tab_ref, src_ref, sums_ref)
    _, channels, width = sums_ref.shape
    energies = spectrum_ref.shape[0]
    split = channels // 2
    low = lax.broadcasted_iota(jnp.int32, (channels, width), 0) < split

    def one_pair(p, carry):
        first_view = sums_ref[2 * p] / depth_all
        second_view = sums_ref[2 * p + 1] / depth_all
        water = jnp.where(low, first_view, pltpu.roll(second_view, split, 0))
        bone = jnp.where(low, pltpu.roll(first_view, split, 0), second_view)

        def one_energy(e, sums):
            intensity, first, second = sums
            a0 = attenuation_ref[0, e]
            a1 = attenuation_ref[1, e]
            counts = spectrum_ref[e] * jnp.exp(-(a0 * water + a1 * bone))
            return (intensity + counts, first + a0 * counts, second + a1 * counts)

        zero = jnp.zeros((channels, width), jnp.float32)
        intensity, first, second = lax.fori_loop(0, energies, one_energy, (zero, zero, zero), unroll=8)
        residual = emitted_ref[0] - jnp.log(intensity) - target_ref[p]
        factor = residual / intensity / views_all
        first = (first * factor).astype(jnp.bfloat16).astype(jnp.float32)
        second = (second * factor).astype(jnp.bfloat16).astype(jnp.float32)
        out_ref[2 * p] = jnp.where(low, first, pltpu.roll(second, split, 0))
        out_ref[2 * p + 1] = jnp.where(low, pltpu.roll(first, split, 0), second)
        return carry

    lax.fori_loop(0, out_ref.shape[0] // 2, one_pair, 0)


def backward_kernel(rows_here, halves, tab_ref, src_ref, out_ref):
    shear_pass(False, rows_here, halves, tab_ref, src_ref, out_ref)


def shear_apply(offset, wa, wb, src, out_width):
    outer_count, channels, width = src.shape
    inner_count = offset.shape[1]
    rot = (LANES - offset) % LANES
    thr = LANES - offset
    smem = pl.BlockSpec(memory_space=pltpu.SMEM)
    vmem = pl.BlockSpec(memory_space=pltpu.VMEM)
    return pl.pallas_call(
        shear_kernel,
        out_shape=jax.ShapeDtypeStruct((inner_count, channels, out_width), jnp.float32),
        in_specs=[smem, smem, smem, smem, vmem],
        out_specs=vmem,
        interpret=INTERPRET,
    )(rot.astype(jnp.int32), thr.astype(jnp.int32), wa, wb, src)


def rows_fit(density, measured):
    rows = density.shape[0]
    groups = lax.axis_size("views")
    depth = lax.axis_size("depth")
    tile_width = density.shape[3]
    return (
        rows % groups == 0
        and (rows // groups) % depth == 0
        and tile_width % LANES == 0
        and 2 * HALO == LANES
        and density.shape[1] == 2
        and measured.shape[0] * groups % 2 == 0
        and tile_width >= 3 * measured.shape[0] * density.shape[2] * groups
    )


def per_device_rows(density, measured, shear_shift, shear_frac, spectrum, attenuation):
    row_total, materials, depth_here, tile_width = density.shape
    groups = lax.axis_size("views")
    depth_count = lax.axis_size("depth")
    views_here = measured.shape[0]
    views_all = views_here * groups
    depth_all = depth_here * depth_count
    rows_group = row_total // groups
    rows_here = rows_group // depth_count
    group = lax.axis_index("views")
    slab = lax.axis_index("depth")

    lower_weight = (1.0 - shear_frac).astype(jnp.bfloat16).astype(jnp.float32)
    upper_weight = shear_frac.astype(jnp.bfloat16).astype(jnp.float32)
    table = jnp.stack([shear_shift.astype(jnp.float32), lower_weight, upper_weight])
    entries = table.size
    observed = measured.reshape(views_here, groups, rows_group, tile_width)
    observed = lax.dynamic_slice_in_dim(observed, slab * rows_here, rows_here, 2)
    observed = jnp.transpose(observed, (1, 0, 2, 3)).reshape(groups, views_here * rows_here, tile_width)
    extra = jnp.pad(table.reshape(1, entries), ((0, 0), (0, tile_width - entries)))
    extra = jnp.broadcast_to(extra[None], (groups, 1, tile_width))
    observed = jnp.concatenate([observed, extra], axis=1)
    observed = lax.all_to_all(observed, "views", 0, 0, tiled=True)
    table = observed[:, views_here * rows_here, :entries].reshape(groups, 3, views_here, depth_here)
    table = jnp.transpose(table, (1, 0, 2, 3)).reshape(3, views_all, depth_here)
    observed = observed[:, : views_here * rows_here].reshape(views_all, rows_here, tile_width)

    channels = rows_here * materials
    mine = lax.dynamic_slice_in_dim(density, group * rows_group, rows_group, 0)
    mine = mine.reshape(depth_count, rows_here, materials, depth_here, tile_width)
    mine = jnp.transpose(mine, (0, 3, 1, 2, 4)).reshape(depth_count, depth_here * channels, tile_width)
    wide = table.size
    extra = jnp.pad(table.reshape(1, wide), ((0, 0), (0, tile_width - wide))).astype(jnp.bfloat16)
    extra = jnp.broadcast_to(extra[None], (depth_count, 1, tile_width))
    mine = jnp.concatenate([mine, extra], axis=1)
    mine = lax.all_to_all(mine, "depth", 0, 0, tiled=True)
    table = mine[:, depth_here * channels, :wide].astype(jnp.float32)
    table = table.reshape(depth_count, 3, views_all, depth_here)
    table = jnp.transpose(table, (1, 2, 0, 3)).reshape(3, views_all, depth_all)
    shift_all = table[0].astype(jnp.int32)
    lower_all = table[1]
    upper_all = table[2]
    mine = mine[:, : depth_here * channels].reshape(depth_all, channels, tile_width)
    padded = with_halo(mine, (("lat", 2),), HALO).astype(jnp.float32)

    sums = shear_apply(
        (shift_all + HALO).T, lower_all.T, upper_all.T, padded, tile_width
    )
    sums = (sums / depth_all).reshape(views_all, rows_here, materials, tile_width)
    grads = spectral(sums, observed, spectrum, attenuation, views_all)
    grads = grads.reshape(views_all, rows_here * materials, tile_width)
    padded_grads = with_halo(grads, (("lat", 2),), HALO).astype(jnp.float32)
    layers = shear_apply(
        HALO - 1 - shift_all, upper_all, lower_all, padded_grads, tile_width
    )
    layers = layers.reshape(depth_count, depth_here, rows_here, materials, tile_width)
    layers = exchange(layers, "depth")
    return jnp.transpose(layers, (0, 2, 3, 1, 4)).reshape(rows_group, materials, depth_here, tile_width)


def rows_fit_wide(density, measured):
    rows = density.shape[0]
    groups = lax.axis_size("views")
    parts = lax.axis_size("depth") * lax.axis_size("lat")
    tile_width = density.shape[3]
    return (
        rows % groups == 0
        and (rows // groups) % parts == 0
        and tile_width % LANES == 0
        and 2 * HALO == LANES
        and density.shape[1] == 2
        and measured.shape[0] * groups % 2 == 0
        and tile_width >= 3 * measured.shape[0] * density.shape[2]
        and ((rows // groups // parts) * density.shape[1] * density.shape[2]) % groups == 0
    )


def stack_halves(values, halves, tile_width):
    count, rows, materials, _ = values.shape
    padded = jnp.pad(values, ((0, 0), (0, 0), (0, 0), (HALO, HALO)))
    parts = [
        padded[..., h * tile_width : h * tile_width + tile_width + 2 * HALO] for h in range(halves)
    ]
    return jnp.stack(parts, axis=1).reshape(count, halves * rows * materials, tile_width + 2 * HALO)


def join_halves(values, halves, rows, materials):
    count, _, tile_width = values.shape
    values = values.reshape(count, halves, rows, materials, tile_width)
    return jnp.transpose(values, (0, 2, 3, 1, 4)).reshape(count, rows, materials, halves * tile_width)


def per_device_wide(density, measured, shear_shift, shear_frac, spectrum, attenuation):
    row_total, materials, depth_here, tile_width = density.shape
    groups = lax.axis_size("views")
    depth_count = lax.axis_size("depth")
    halves = lax.axis_size("lat")
    parts = depth_count * halves
    views_here = measured.shape[0]
    views_all = views_here * groups
    depth_all = depth_here * depth_count
    rows_group = row_total // groups
    rows_here = rows_group // parts
    group = lax.axis_index("views")
    slab = lax.axis_index("depth")
    half = lax.axis_index("lat")

    lower_weight = (1.0 - shear_frac).astype(jnp.bfloat16).astype(jnp.float32)
    upper_weight = shear_frac.astype(jnp.bfloat16).astype(jnp.float32)
    block = jnp.stack([shear_shift.astype(jnp.float32), lower_weight, upper_weight])
    entries = block.size
    observed = measured.reshape(views_here, groups, depth_count, halves, rows_here, tile_width)
    observed = lax.dynamic_index_in_dim(observed, slab, 2, keepdims=False)
    observed = jnp.transpose(observed, (1, 2, 0, 3, 4)).reshape(
        groups * halves, views_here * rows_here, tile_width
    )
    observed = lax.all_to_all(observed, ("views", "lat"), 0, 0, tiled=True)
    observed = observed.reshape(groups, halves, views_here, rows_here, tile_width)
    observed = jnp.transpose(observed, (0, 2, 3, 1, 4)).reshape(views_all, rows_here, halves * tile_width)

    chunk = rows_here * materials * depth_here * tile_width
    piece = chunk // groups
    mine = density.reshape(groups * parts, groups, piece)
    mine = lax.dynamic_index_in_dim(mine, group, 1, keepdims=False)
    mine = mine.reshape(groups * parts, piece // tile_width, tile_width)
    extra = jnp.pad(block.reshape(1, entries), ((0, 0), (0, tile_width - entries))).astype(jnp.bfloat16)
    extra = jnp.broadcast_to(extra[None], (groups * parts, 1, tile_width))
    mine = jnp.concatenate([mine, extra], axis=1)
    mine = lax.all_to_all(mine, ("views", "depth", "lat"), 0, 0, tiled=True)
    mine = mine.reshape(groups, depth_count, halves, piece // tile_width + 1, tile_width)
    table = mine[:, :, 0, piece // tile_width, :entries].astype(jnp.float32)
    table = table.reshape(groups, depth_count, 3, views_here, depth_here)
    table = jnp.transpose(table, (2, 0, 3, 1, 4)).reshape(3, views_all, depth_all)
    mine = mine[:, :, :, : piece // tile_width].reshape(groups, depth_count, halves, piece)
    mine = jnp.transpose(mine, (1, 2, 0, 3)).reshape(
        depth_count, halves, rows_here, materials, depth_here, tile_width
    )
    channels = materials * halves * rows_here
    mine = jnp.transpose(mine, (0, 4, 3, 1, 2, 5)).reshape(depth_all, channels, tile_width)
    mine = mine.astype(jnp.float32)
    target = observed.reshape(views_all // 2, 2, rows_here, halves, tile_width)
    target = jnp.transpose(target, (0, 1, 3, 2, 4)).reshape(views_all // 2, 2 * halves * rows_here, tile_width)
    emitted = jnp.log(jnp.sum(spectrum)).reshape(1)
    smem = pl.BlockSpec(memory_space=pltpu.SMEM)
    vmem = pl.BlockSpec(memory_space=pltpu.VMEM)
    grads = pl.pallas_call(
        functools.partial(forward_kernel, rows_here, halves, depth_all, views_all),
        out_shape=jax.ShapeDtypeStruct((views_all, channels, tile_width), jnp.float32),
        in_specs=[smem, smem, smem, smem, vmem, vmem],
        out_specs=vmem,
        scratch_shapes=[pltpu.VMEM((views_all, channels, tile_width), jnp.float32)],
        interpret=INTERPRET,
    )(table, emitted, spectrum, attenuation, mine, target)
    layers = pl.pallas_call(
        functools.partial(backward_kernel, rows_here, halves),
        out_shape=jax.ShapeDtypeStruct((depth_all, channels, tile_width), jnp.float32),
        in_specs=[smem, vmem],
        out_specs=vmem,
        interpret=INTERPRET,
    )(table, grads)
    layers = layers.reshape(depth_count, depth_here, materials, halves, rows_here, tile_width)
    layers = jnp.transpose(layers, (0, 3, 4, 2, 1, 5)).reshape(
        parts, rows_here, materials, depth_here, tile_width
    )
    layers = lax.all_to_all(layers, ("depth", "lat"), 0, 0, tiled=True)
    return layers.reshape(rows_group, materials, depth_here, tile_width)


def per_device_any(density, measured, shear_shift, shear_frac, spectrum, attenuation):
    if rows_fit_wide(density, measured):
        return per_device_wide(density, measured, shear_shift, shear_frac, spectrum, attenuation)
    if rows_fit(density, measured):
        return per_device_rows(density, measured, shear_shift, shear_frac, spectrum, attenuation)
    return per_device(density, measured, shear_shift, shear_frac, spectrum, attenuation)


def solution(mesh):
    in_specs = (
        P(None, None, "depth", "lat"),
        P("views", None, "lat"),
        P("views", "depth"),
        P("views", "depth"),
        P(),
        P(),
    )
    out_specs = P("views", None, "depth", "lat")
    return jax.shard_map(
        per_device_any, mesh=mesh, in_specs=in_specs, out_specs=out_specs, check_vma=False
    )
```

```python
import functools
import jax
import jax.numpy as jnp
from jax import lax
from jax.sharding import PartitionSpec as P
from jax.experimental import pallas as pl
from jax.experimental.pallas import tpu as pltpu

HALO = 64


def with_halo(x, sides, width):
    for axis, dim in sides:
        size, length = (lax.axis_size(axis), x.shape[dim])
        up = [(i, (i + 1) % size) for i in range(size - 1)]
        down = [(j, i) for i, j in up]
        last = lax.slice_in_dim(x, length - width, length, axis=dim)
        first = lax.slice_in_dim(x, 0, width, axis=dim)
        before = lax.ppermute(last, axis, up)
        after = lax.ppermute(first, axis, down)
        x = jnp.concatenate([before, x, after], axis=dim)
    return x


def exchange(x, axis):
    count = lax.axis_size(axis)
    me = lax.axis_index(axis)
    result = x
    for step in range(1, count):
        pairs = [(i, (i + step) % count) for i in range(count)]
        part = lax.dynamic_index_in_dim(x, (me + step) % count, 0, keepdims=True)
        part = lax.ppermute(part, axis, pairs)
        result = lax.dynamic_update_index_in_dim(result, part, (me - step) % count, 0)
    return result


def band_forward(shear_shift, lower_weight, upper_weight, window, block_width):
    band_shape = (shear_shift.shape[1], window, shear_shift.shape[0], block_width)
    tap_index = lax.broadcasted_iota(jnp.int32, band_shape, 1)
    column = lax.broadcasted_iota(jnp.int32, band_shape, 3)
    anchor = (shear_shift.T + HALO)[:, None, :, None]
    nothing = jnp.zeros((), jnp.bfloat16)
    lower_part = jnp.where(tap_index == column + anchor, lower_weight.T[:, None, :, None], nothing)
    upper_part = jnp.where(
        tap_index == column + anchor + 1, upper_weight.T[:, None, :, None], nothing
    )
    return lower_part + upper_part


def band_backward(shear_shift, lower_weight, upper_weight, window, block_width):
    band_shape = (shear_shift.shape[0], window, shear_shift.shape[1], block_width)
    tap_index = lax.broadcasted_iota(jnp.int32, band_shape, 1)
    column = lax.broadcasted_iota(jnp.int32, band_shape, 3)
    anchor = (HALO - shear_shift)[:, None, :, None]
    nothing = jnp.zeros((), jnp.bfloat16)
    lower_part = jnp.where(tap_index == column + anchor, lower_weight[:, None, :, None], nothing)
    upper_part = jnp.where(
        tap_index == column + anchor - 1, upper_weight[:, None, :, None], nothing
    )
    return lower_part + upper_part


def spectral(path_sums, observed, spectrum, attenuation, views_all):
    view_count, row_count, materials, tile_width = path_sums.shape
    block_pixels = 4096
    path_water = path_sums[:, :, 0, :].reshape(-1, block_pixels)
    path_bone = path_sums[:, :, 1, :].reshape(-1, block_pixels)
    target_flat = observed.reshape(-1, block_pixels)
    coefficients = jnp.concatenate(
        [jnp.ones((1, spectrum.shape[0]), jnp.float32), attenuation], axis=0
    )
    emitted = jnp.log(jnp.sum(spectrum))

    def one_block(inputs):
        water_block, bone_block, target_block = inputs
        exponent = (
            attenuation[0][:, None] * water_block[None, :]
            + attenuation[1][:, None] * bone_block[None, :]
        )
        counts = spectrum[:, None] * jnp.exp(-exponent)
        moments = jnp.dot(coefficients, counts, precision=lax.Precision.HIGHEST)
        intensity = moments[0]
        residual = emitted - jnp.log(intensity) - target_block
        factor = residual / intensity / views_all
        return (moments[1:] * factor[None, :]).astype(jnp.bfloat16)

    stacked = lax.map(one_block, (path_water, path_bone, target_flat))
    gradients = jnp.swapaxes(stacked, 0, 1).reshape(materials, view_count, row_count, tile_width)
    return jnp.transpose(gradients, (1, 2, 0, 3))


def spectral_kernel(views_all, emitted_ref, spectrum_ref, attenuation_ref, water_ref, bone_ref, target_ref, out0_ref, out1_ref):
    rows, width = water_ref.shape
    energies = spectrum_ref.shape[0]
    block = 8

    def one_block(b, carry):
        lo = pl.multiple_of(b * block, block)
        water = water_ref[pl.ds(lo, block), :]
        bone = bone_ref[pl.ds(lo, block), :]

        def one_energy(e, sums):
            intensity, first, second = sums
            a0 = attenuation_ref[0, e]
            a1 = attenuation_ref[1, e]
            counts = spectrum_ref[e] * jnp.exp(-(a0 * water + a1 * bone))
            return (intensity + counts, first + a0 * counts, second + a1 * counts)

        zero = jnp.zeros((block, width), jnp.float32)
        intensity, first, second = lax.fori_loop(0, energies, one_energy, (zero, zero, zero), unroll=8)
        residual = emitted_ref[0] - jnp.log(intensity) - target_ref[pl.ds(lo, block), :]
        factor = residual / intensity / views_all
        out0_ref[pl.ds(lo, block), :] = (first * factor).astype(out0_ref.dtype)
        out1_ref[pl.ds(lo, block), :] = (second * factor).astype(out1_ref.dtype)
        return carry

    lax.fori_loop(0, rows // block, one_block, 0)


def spectral_pallas(path_sums, observed, spectrum, attenuation, views_all):
    view_count, row_count, materials, width_all = path_sums.shape
    pixels = view_count * row_count * width_all
    rows = pixels // LANES // 4
    water = path_sums[:, :, 0, :].reshape(rows, 4 * LANES)
    bone = path_sums[:, :, 1, :].reshape(rows, 4 * LANES)
    target = observed.reshape(rows, 4 * LANES)
    emitted = jnp.log(jnp.sum(spectrum)).reshape(1)
    smem = pl.BlockSpec(memory_space=pltpu.SMEM)
    vmem = pl.BlockSpec(memory_space=pltpu.VMEM)
    first, second = pl.pallas_call(
        functools.partial(spectral_kernel, views_all),
        out_shape=(
            jax.ShapeDtypeStruct((rows, 4 * LANES), jnp.bfloat16),
            jax.ShapeDtypeStruct((rows, 4 * LANES), jnp.bfloat16),
        ),
        in_specs=[smem, smem, smem, vmem, vmem, vmem],
        out_specs=(vmem, vmem),
        interpret=INTERPRET,
    )(emitted, spectrum, attenuation, water, bone, target)
    shape = (view_count, row_count, width_all)
    return jnp.stack([first.reshape(shape), second.reshape(shape)], axis=2)


def per_device(density, measured, shear_shift, shear_frac, spectrum, attenuation):
    row_total, materials, depth_here, tile_width = density.shape
    block_width = min(128, tile_width)
    block_count = tile_width // block_width
    window = block_width + 2 * HALO
    views_all = measured.shape[0] * lax.axis_size("views")
    depth_all = depth_here * lax.axis_size("depth")
    rows_out = row_total // lax.axis_size("views")
    lower_weight = (1.0 - shear_frac).astype(jnp.bfloat16)
    upper_weight = shear_frac.astype(jnp.bfloat16)
    rows_here = density.shape[0]
    padded = with_halo(density, (("lat", 3),), HALO)
    framed = jnp.stack(
        [
            padded[:, :, :, number * block_width : number * block_width + window]
            for number in range(block_count)
        ],
        axis=2,
    )
    forward_band = band_forward(shear_shift, lower_weight, upper_weight, window, block_width)
    partial_value = jnp.einsum(
        "ymnzi,zivc->vymnc", framed, forward_band, preferred_element_type=jnp.float32
    )
    partial_value = partial_value.reshape(shear_shift.shape[0], rows_here, materials, tile_width)
    shares = lax.psum_scatter(partial_value, "depth", scatter_dimension=3, tiled=True) / depth_all
    share_cols = shares.shape[3]
    observed = lax.dynamic_slice_in_dim(
        measured, lax.axis_index("depth") * share_cols, share_cols, 2
    )
    share_grads = spectral(shares, observed, spectrum, attenuation, views_all)
    path_grads = lax.all_gather(share_grads, "depth", axis=3, tiled=True)
    padded_grads = with_halo(path_grads, (("lat", 3),), HALO)
    framed_grads = jnp.stack(
        [
            padded_grads[:, :, :, number * block_width : number * block_width + window]
            for number in range(block_count)
        ],
        axis=3,
    )
    backward_band = band_backward(shear_shift, lower_weight, upper_weight, window, block_width)
    product = jnp.einsum(
        "vymni,vizc->ymznc", framed_grads, backward_band, preferred_element_type=jnp.float32
    )
    return lax.psum_scatter(
        product.reshape(rows_out * lax.axis_size("views"), materials, depth_here, tile_width),
        "views",
        scatter_dimension=0,
        tiled=True,
    )


LANES = 128
INTERPRET = False


def shear_kernel(rot_ref, thr_ref, wa_ref, wb_ref, src_ref, out_ref):
    outer_count, channels, width = src_ref.shape
    inner_count, _, out_width = out_ref.shape
    pieces = width // LANES
    out_pieces = out_width // LANES
    out_ref[...] = jnp.zeros(out_ref.shape, jnp.float32)
    lane = lax.broadcasted_iota(jnp.int32, (channels, LANES), 1)

    def outer(o, carry):
        cols = [src_ref[o, :, k * LANES : (k + 1) * LANES] for k in range(pieces)]
        turned = [pltpu.roll(c, LANES - 1, 1) for c in cols]
        nexts = [
            jnp.where(lane < LANES - 1, turned[k], turned[k + 1]) for k in range(pieces - 1)
        ] + [turned[pieces - 1]]
        for i in range(inner_count):
            wa = wa_ref[o, i]
            wb = wb_ref[o, i]
            mixed = [wa * cols[k] + wb * nexts[k] for k in range(pieces)]
            rolled = [pltpu.roll(m, rot_ref[o, i], 1) for m in mixed]
            keep = lane < thr_ref[o, i]
            for j in range(out_pieces):
                out_ref[i, :, j * LANES : (j + 1) * LANES] += jnp.where(
                    keep, rolled[j], rolled[j + 1]
                )
        return carry

    lax.fori_loop(0, outer_count, outer, 0)


def shear_table_kernel(forward, tab_ref, src_ref, out_ref):
    outer_count, channels, width = src_ref.shape
    inner_count, _, out_width = out_ref.shape
    pieces = width // LANES
    out_pieces = out_width // LANES
    out_ref[...] = jnp.zeros(out_ref.shape, jnp.float32)
    lane = lax.broadcasted_iota(jnp.int32, (channels, LANES), 1)

    def outer(o, carry):
        cols = [src_ref[o, :, k * LANES : (k + 1) * LANES] for k in range(pieces)]
        turned = [pltpu.roll(c, LANES - 1, 1) for c in cols]
        nexts = [
            jnp.where(lane < LANES - 1, turned[k], turned[k + 1]) for k in range(pieces - 1)
        ] + [turned[pieces - 1]]
        for i in range(inner_count):
            if forward:
                shift = tab_ref[0, i, o].astype(jnp.int32)
                wa = tab_ref[1, i, o]
                wb = tab_ref[2, i, o]
                offset = shift + HALO
            else:
                shift = tab_ref[0, o, i].astype(jnp.int32)
                wa = tab_ref[2, o, i]
                wb = tab_ref[1, o, i]
                offset = HALO - 1 - shift
            limit = LANES - offset
            amount = jnp.where(limit == LANES, 0, limit)
            mixed = [wa * cols[k] + wb * nexts[k] for k in range(pieces)]
            rolled = [pltpu.roll(m, amount, 1) for m in mixed]
            keep = lane < limit
            for j in range(out_pieces):
                out_ref[i, :, j * LANES : (j + 1) * LANES] += jnp.where(
                    keep, rolled[j], rolled[j + 1]
                )
        return carry

    lax.fori_loop(0, outer_count, outer, 0)


def shear_table(forward, table, src, inner_count, out_width):
    _, channels, _ = src.shape
    smem = pl.BlockSpec(memory_space=pltpu.SMEM)
    vmem = pl.BlockSpec(memory_space=pltpu.VMEM)
    return pl.pallas_call(
        functools.partial(shear_table_kernel, forward),
        out_shape=jax.ShapeDtypeStruct((inner_count, channels, out_width), jnp.float32),
        in_specs=[smem, vmem],
        out_specs=vmem,
        interpret=INTERPRET,
    )(table, src)


def halo_columns(ys, lane, half_of, rows_here, halves, channels):
    count = len(ys)
    turned = [pltpu.roll(y, HALO, 1) for y in ys]
    zero = jnp.zeros_like(ys[0])
    left = jnp.where(half_of >= 1, pltpu.roll(turned[count - 1], rows_here, 0), zero)
    right = jnp.where(half_of <= halves - 2, pltpu.roll(turned[0], channels - rows_here, 0), zero)
    edge = lane < HALO
    cols = [jnp.where(edge, left, turned[0])]
    cols += [jnp.where(edge, turned[k - 1], turned[k]) for k in range(1, count)]
    cols += [jnp.where(edge, turned[count - 1], right)]
    return cols


def shear_pass(forward, rows_here, halves, tab_ref, src_ref, acc_ref, cols_ref, nexts_ref):
    outer_count, channels, width = src_ref.shape
    inner_count = acc_ref.shape[0]
    pieces = width // LANES
    lane = lax.broadcasted_iota(jnp.int32, (channels, LANES), 1)
    half_of = (lax.broadcasted_iota(jnp.int32, (channels, LANES), 0) // rows_here) % halves

    def prepare(o, carry):
        ys = [src_ref[o, :, k * LANES : (k + 1) * LANES] for k in range(pieces)]
        cols = halo_columns(ys, lane, half_of, rows_here, halves, channels)
        turned = [pltpu.roll(c, LANES - 1, 1) for c in cols]
        nexts = [jnp.where(lane < LANES - 1, turned[k], turned[k + 1]) for k in range(pieces)]
        nexts.append(turned[pieces])
        for k in range(pieces + 1):
            cols_ref[o, :, k * LANES : (k + 1) * LANES] = cols[k]
            nexts_ref[o, :, k * LANES : (k + 1) * LANES] = nexts[k]
        return carry

    lax.fori_loop(0, outer_count, prepare, 0)

    def inner(i, carry):
        acc = [jnp.zeros((channels, LANES), jnp.float32) for _ in range(pieces)]
        for o in range(outer_count):
            if forward:
                shift = tab_ref[0, i, o].astype(jnp.int32)
                wa = tab_ref[1, i, o]
                wb = tab_ref[2, i, o]
                offset = shift + HALO
            else:
                shift = tab_ref[0, o, i].astype(jnp.int32)
                wa = tab_ref[2, o, i]
                wb = tab_ref[1, o, i]
                offset = HALO - 1 - shift
            limit = LANES - offset
            amount = jnp.where(limit == LANES, 0, limit)
            mixed = [
                wa * cols_ref[o, :, k * LANES : (k + 1) * LANES]
                + wb * nexts_ref[o, :, k * LANES : (k + 1) * LANES]
                for k in range(pieces + 1)
            ]
            rolled = [pltpu.roll(m, amount, 1) for m in mixed]
            keep = lane < limit
            acc = [acc[j] + jnp.where(keep, rolled[j], rolled[j + 1]) for j in range(pieces)]
        for j in range(pieces):
            acc_ref[i, :, j * LANES : (j + 1) * LANES] = acc[j]
        return carry

    lax.fori_loop(0, inner_count, inner, 0)


def forward_kernel(rows_here, halves, depth_all, views_all, tab_ref, emitted_ref, spectrum_ref,
                   attenuation_ref, src_ref, target_ref, out_ref, sums_ref, cols_ref, nexts_ref):
    shear_pass(True, rows_here, halves, tab_ref, src_ref, sums_ref, cols_ref, nexts_ref)
    _, channels, width = sums_ref.shape
    energies = spectrum_ref.shape[0]
    split = channels // 2
    low = lax.broadcasted_iota(jnp.int32, (channels, width), 0) < split

    def one_pair(p, carry):
        first_view = sums_ref[2 * p] / depth_all
        second_view = sums_ref[2 * p + 1] / depth_all
        water = jnp.where(low, first_view, pltpu.roll(second_view, split, 0))
        bone = jnp.where(low, pltpu.roll(first_view, split, 0), second_view)

        def one_energy(e, sums):
            intensity, first, second = sums
            a0 = attenuation_ref[0, e]
            a1 = attenuation_ref[1, e]
            counts = spectrum_ref[e] * jnp.exp(-(a0 * water + a1 * bone))
            return (intensity + counts, first + a0 * counts, second + a1 * counts)

        zero = jnp.zeros((channels, width), jnp.float32)
        intensity, first, second = lax.fori_loop(0, energies, one_energy, (zero, zero, zero), unroll=8)
        residual = emitted_ref[0] - jnp.log(intensity) - target_ref[p]
        factor = residual / intensity / views_all
        first = (first * factor).astype(jnp.bfloat16).astype(jnp.float32)
        second = (second * factor).astype(jnp.bfloat16).astype(jnp.float32)
        out_ref[2 * p] = jnp.where(low, first, pltpu.roll(second, split, 0))
        out_ref[2 * p + 1] = jnp.where(low, pltpu.roll(first, split, 0), second)
        return carry

    lax.fori_loop(0, out_ref.shape[0] // 2, one_pair, 0)


def backward_kernel(rows_here, halves, tab_ref, src_ref, out_ref, cols_ref, nexts_ref):
    shear_pass(False, rows_here, halves, tab_ref, src_ref, out_ref, cols_ref, nexts_ref)


def shear_apply(offset, wa, wb, src, out_width):
    outer_count, channels, width = src.shape
    inner_count = offset.shape[1]
    rot = (LANES - offset) % LANES
    thr = LANES - offset
    smem = pl.BlockSpec(memory_space=pltpu.SMEM)
    vmem = pl.BlockSpec(memory_space=pltpu.VMEM)
    return pl.pallas_call(
        shear_kernel,
        out_shape=jax.ShapeDtypeStruct((inner_count, channels, out_width), jnp.float32),
        in_specs=[smem, smem, smem, smem, vmem],
        out_specs=vmem,
        interpret=INTERPRET,
    )(rot.astype(jnp.int32), thr.astype(jnp.int32), wa, wb, src)


def rows_fit(density, measured):
    rows = density.shape[0]
    groups = lax.axis_size("views")
    depth = lax.axis_size("depth")
    tile_width = density.shape[3]
    return (
        rows % groups == 0
        and (rows // groups) % depth == 0
        and tile_width % LANES == 0
        and 2 * HALO == LANES
        and density.shape[1] == 2
        and measured.shape[0] * groups % 2 == 0
        and tile_width >= 3 * measured.shape[0] * density.shape[2] * groups
    )


def per_device_rows(density, measured, shear_shift, shear_frac, spectrum, attenuation):
    row_total, materials, depth_here, tile_width = density.shape
    groups = lax.axis_size("views")
    depth_count = lax.axis_size("depth")
    views_here = measured.shape[0]
    views_all = views_here * groups
    depth_all = depth_here * depth_count
    rows_group = row_total // groups
    rows_here = rows_group // depth_count
    group = lax.axis_index("views")
    slab = lax.axis_index("depth")

    lower_weight = (1.0 - shear_frac).astype(jnp.bfloat16).astype(jnp.float32)
    upper_weight = shear_frac.astype(jnp.bfloat16).astype(jnp.float32)
    table = jnp.stack([shear_shift.astype(jnp.float32), lower_weight, upper_weight])
    entries = table.size
    observed = measured.reshape(views_here, groups, rows_group, tile_width)
    observed = lax.dynamic_slice_in_dim(observed, slab * rows_here, rows_here, 2)
    observed = jnp.transpose(observed, (1, 0, 2, 3)).reshape(groups, views_here * rows_here, tile_width)
    extra = jnp.pad(table.reshape(1, entries), ((0, 0), (0, tile_width - entries)))
    extra = jnp.broadcast_to(extra[None], (groups, 1, tile_width))
    observed = jnp.concatenate([observed, extra], axis=1)
    observed = lax.all_to_all(observed, "views", 0, 0, tiled=True)
    table = observed[:, views_here * rows_here, :entries].reshape(groups, 3, views_here, depth_here)
    table = jnp.transpose(table, (1, 0, 2, 3)).reshape(3, views_all, depth_here)
    observed = observed[:, : views_here * rows_here].reshape(views_all, rows_here, tile_width)

    channels = rows_here * materials
    mine = lax.dynamic_slice_in_dim(density, group * rows_group, rows_group, 0)
    mine = mine.reshape(depth_count, rows_here, materials, depth_here, tile_width)
    mine = jnp.transpose(mine, (0, 3, 1, 2, 4)).reshape(depth_count, depth_here * channels, tile_width)
    wide = table.size
    extra = jnp.pad(table.reshape(1, wide), ((0, 0), (0, tile_width - wide))).astype(jnp.bfloat16)
    extra = jnp.broadcast_to(extra[None], (depth_count, 1, tile_width))
    mine = jnp.concatenate([mine, extra], axis=1)
    mine = lax.all_to_all(mine, "depth", 0, 0, tiled=True)
    table = mine[:, depth_here * channels, :wide].astype(jnp.float32)
    table = table.reshape(depth_count, 3, views_all, depth_here)
    table = jnp.transpose(table, (1, 2, 0, 3)).reshape(3, views_all, depth_all)
    shift_all = table[0].astype(jnp.int32)
    lower_all = table[1]
    upper_all = table[2]
    mine = mine[:, : depth_here * channels].reshape(depth_all, channels, tile_width)
    padded = with_halo(mine, (("lat", 2),), HALO).astype(jnp.float32)

    sums = shear_apply(
        (shift_all + HALO).T, lower_all.T, upper_all.T, padded, tile_width
    )
    sums = (sums / depth_all).reshape(views_all, rows_here, materials, tile_width)
    grads = spectral(sums, observed, spectrum, attenuation, views_all)
    grads = grads.reshape(views_all, rows_here * materials, tile_width)
    padded_grads = with_halo(grads, (("lat", 2),), HALO).astype(jnp.float32)
    layers = shear_apply(
        HALO - 1 - shift_all, upper_all, lower_all, padded_grads, tile_width
    )
    layers = layers.reshape(depth_count, depth_here, rows_here, materials, tile_width)
    layers = exchange(layers, "depth")
    return jnp.transpose(layers, (0, 2, 3, 1, 4)).reshape(rows_group, materials, depth_here, tile_width)


def rows_fit_wide(density, measured):
    rows = density.shape[0]
    groups = lax.axis_size("views")
    parts = lax.axis_size("depth") * lax.axis_size("lat")
    tile_width = density.shape[3]
    return (
        rows % groups == 0
        and (rows // groups) % parts == 0
        and tile_width % LANES == 0
        and 2 * HALO == LANES
        and density.shape[1] == 2
        and measured.shape[0] * groups % 2 == 0
        and tile_width >= 3 * measured.shape[0] * density.shape[2]
        and ((rows // groups // parts) * density.shape[1] * density.shape[2]) % groups == 0
    )


def stack_halves(values, halves, tile_width):
    count, rows, materials, _ = values.shape
    padded = jnp.pad(values, ((0, 0), (0, 0), (0, 0), (HALO, HALO)))
    parts = [
        padded[..., h * tile_width : h * tile_width + tile_width + 2 * HALO] for h in range(halves)
    ]
    return jnp.stack(parts, axis=1).reshape(count, halves * rows * materials, tile_width + 2 * HALO)


def join_halves(values, halves, rows, materials):
    count, _, tile_width = values.shape
    values = values.reshape(count, halves, rows, materials, tile_width)
    return jnp.transpose(values, (0, 2, 3, 1, 4)).reshape(count, rows, materials, halves * tile_width)


def per_device_wide(density, measured, shear_shift, shear_frac, spectrum, attenuation):
    row_total, materials, depth_here, tile_width = density.shape
    groups = lax.axis_size("views")
    depth_count = lax.axis_size("depth")
    halves = lax.axis_size("lat")
    parts = depth_count * halves
    views_here = measured.shape[0]
    views_all = views_here * groups
    depth_all = depth_here * depth_count
    rows_group = row_total // groups
    rows_here = rows_group // parts
    group = lax.axis_index("views")
    slab = lax.axis_index("depth")
    half = lax.axis_index("lat")

    lower_weight = (1.0 - shear_frac).astype(jnp.bfloat16).astype(jnp.float32)
    upper_weight = shear_frac.astype(jnp.bfloat16).astype(jnp.float32)
    block = jnp.stack([shear_shift.astype(jnp.float32), lower_weight, upper_weight])
    entries = block.size
    observed = measured.reshape(views_here, groups, depth_count, halves, rows_here, tile_width)
    observed = lax.dynamic_index_in_dim(observed, slab, 2, keepdims=False)
    observed = jnp.transpose(observed, (1, 2, 0, 3, 4)).reshape(
        groups * halves, views_here * rows_here, tile_width
    )
    observed = lax.all_to_all(observed, ("views", "lat"), 0, 0, tiled=True)
    observed = observed.reshape(groups, halves, views_here, rows_here, tile_width)
    observed = jnp.transpose(observed, (0, 2, 3, 1, 4)).reshape(views_all, rows_here, halves * tile_width)

    chunk = rows_here * materials * depth_here * tile_width
    piece = chunk // groups
    mine = density.reshape(groups * parts, groups, piece)
    mine = lax.dynamic_index_in_dim(mine, group, 1, keepdims=False)
    mine = mine.reshape(groups * parts, piece // tile_width, tile_width)
    extra = jnp.pad(block.reshape(1, entries), ((0, 0), (0, tile_width - entries))).astype(jnp.bfloat16)
    extra = jnp.broadcast_to(extra[None], (groups * parts, 1, tile_width))
    mine = jnp.concatenate([mine, extra], axis=1)
    mine = lax.all_to_all(mine, ("views", "depth", "lat"), 0, 0, tiled=True)
    mine = mine.reshape(groups, depth_count, halves, piece // tile_width + 1, tile_width)
    table = mine[:, :, 0, piece // tile_width, :entries].astype(jnp.float32)
    table = table.reshape(groups, depth_count, 3, views_here, depth_here)
    table = jnp.transpose(table, (2, 0, 3, 1, 4)).reshape(3, views_all, depth_all)
    mine = mine[:, :, :, : piece // tile_width].reshape(groups, depth_count, halves, piece)
    mine = jnp.transpose(mine, (1, 2, 0, 3)).reshape(
        depth_count, halves, rows_here, materials, depth_here, tile_width
    )
    channels = materials * halves * rows_here
    mine = jnp.transpose(mine, (0, 4, 3, 1, 2, 5)).reshape(depth_all, channels, tile_width)
    mine = mine.astype(jnp.float32)
    target = observed.reshape(views_all // 2, 2, rows_here, halves, tile_width)
    target = jnp.transpose(target, (0, 1, 3, 2, 4)).reshape(views_all // 2, 2 * halves * rows_here, tile_width)
    emitted = jnp.log(jnp.sum(spectrum)).reshape(1)
    smem = pl.BlockSpec(memory_space=pltpu.SMEM)
    vmem = pl.BlockSpec(memory_space=pltpu.VMEM)
    grads = pl.pallas_call(
        functools.partial(forward_kernel, rows_here, halves, depth_all, views_all),
        out_shape=jax.ShapeDtypeStruct((views_all, channels, tile_width), jnp.float32),
        in_specs=[smem, smem, smem, smem, vmem, vmem],
        out_specs=vmem,
        scratch_shapes=[
            pltpu.VMEM((views_all, channels, tile_width), jnp.float32),
            pltpu.VMEM((depth_all, channels, tile_width + LANES), jnp.float32),
            pltpu.VMEM((depth_all, channels, tile_width + LANES), jnp.float32),
        ],
        interpret=INTERPRET,
    )(table, emitted, spectrum, attenuation, mine, target)
    layers = pl.pallas_call(
        functools.partial(backward_kernel, rows_here, halves),
        out_shape=jax.ShapeDtypeStruct((depth_all, channels, tile_width), jnp.float32),
        in_specs=[smem, vmem],
        out_specs=vmem,
        scratch_shapes=[
            pltpu.VMEM((views_all, channels, tile_width + LANES), jnp.float32),
            pltpu.VMEM((views_all, channels, tile_width + LANES), jnp.float32),
        ],
        interpret=INTERPRET,
    )(table, grads)
    layers = layers.reshape(depth_count, depth_here, materials, halves, rows_here, tile_width)
    layers = jnp.transpose(layers, (0, 3, 4, 2, 1, 5)).reshape(
        parts, rows_here, materials, depth_here, tile_width
    )
    layers = lax.all_to_all(layers, ("depth", "lat"), 0, 0, tiled=True)
    return layers.reshape(rows_group, materials, depth_here, tile_width)


def per_device_any(density, measured, shear_shift, shear_frac, spectrum, attenuation):
    if rows_fit_wide(density, measured):
        return per_device_wide(density, measured, shear_shift, shear_frac, spectrum, attenuation)
    if rows_fit(density, measured):
        return per_device_rows(density, measured, shear_shift, shear_frac, spectrum, attenuation)
    return per_device(density, measured, shear_shift, shear_frac, spectrum, attenuation)


def solution(mesh):
    in_specs = (
        P(None, None, "depth", "lat"),
        P("views", None, "lat"),
        P("views", "depth"),
        P("views", "depth"),
        P(),
        P(),
    )
    out_specs = P("views", None, "depth", "lat")
    return jax.shard_map(
        per_device_any, mesh=mesh, in_specs=in_specs, out_specs=out_specs, check_vma=False
    )
```

```python
import functools
import jax
import jax.numpy as jnp
from jax import lax
from jax.sharding import PartitionSpec as P
from jax.experimental import pallas as pl
from jax.experimental.pallas import tpu as pltpu

HALO = 64


def with_halo(x, sides, width):
    for axis, dim in sides:
        size, length = (lax.axis_size(axis), x.shape[dim])
        up = [(i, (i + 1) % size) for i in range(size - 1)]
        down = [(j, i) for i, j in up]
        last = lax.slice_in_dim(x, length - width, length, axis=dim)
        first = lax.slice_in_dim(x, 0, width, axis=dim)
        before = lax.ppermute(last, axis, up)
        after = lax.ppermute(first, axis, down)
        x = jnp.concatenate([before, x, after], axis=dim)
    return x


def exchange(x, axis):
    count = lax.axis_size(axis)
    me = lax.axis_index(axis)
    result = x
    for step in range(1, count):
        pairs = [(i, (i + step) % count) for i in range(count)]
        part = lax.dynamic_index_in_dim(x, (me + step) % count, 0, keepdims=True)
        part = lax.ppermute(part, axis, pairs)
        result = lax.dynamic_update_index_in_dim(result, part, (me - step) % count, 0)
    return result


def band_forward(shear_shift, lower_weight, upper_weight, window, block_width):
    band_shape = (shear_shift.shape[1], window, shear_shift.shape[0], block_width)
    tap_index = lax.broadcasted_iota(jnp.int32, band_shape, 1)
    column = lax.broadcasted_iota(jnp.int32, band_shape, 3)
    anchor = (shear_shift.T + HALO)[:, None, :, None]
    nothing = jnp.zeros((), jnp.bfloat16)
    lower_part = jnp.where(tap_index == column + anchor, lower_weight.T[:, None, :, None], nothing)
    upper_part = jnp.where(
        tap_index == column + anchor + 1, upper_weight.T[:, None, :, None], nothing
    )
    return lower_part + upper_part


def band_backward(shear_shift, lower_weight, upper_weight, window, block_width):
    band_shape = (shear_shift.shape[0], window, shear_shift.shape[1], block_width)
    tap_index = lax.broadcasted_iota(jnp.int32, band_shape, 1)
    column = lax.broadcasted_iota(jnp.int32, band_shape, 3)
    anchor = (HALO - shear_shift)[:, None, :, None]
    nothing = jnp.zeros((), jnp.bfloat16)
    lower_part = jnp.where(tap_index == column + anchor, lower_weight[:, None, :, None], nothing)
    upper_part = jnp.where(
        tap_index == column + anchor - 1, upper_weight[:, None, :, None], nothing
    )
    return lower_part + upper_part


def spectral(path_sums, observed, spectrum, attenuation, views_all):
    view_count, row_count, materials, tile_width = path_sums.shape
    block_pixels = 4096
    path_water = path_sums[:, :, 0, :].reshape(-1, block_pixels)
    path_bone = path_sums[:, :, 1, :].reshape(-1, block_pixels)
    target_flat = observed.reshape(-1, block_pixels)
    coefficients = jnp.concatenate(
        [jnp.ones((1, spectrum.shape[0]), jnp.float32), attenuation], axis=0
    )
    emitted = jnp.log(jnp.sum(spectrum))

    def one_block(inputs):
        water_block, bone_block, target_block = inputs
        exponent = (
            attenuation[0][:, None] * water_block[None, :]
            + attenuation[1][:, None] * bone_block[None, :]
        )
        counts = spectrum[:, None] * jnp.exp(-exponent)
        moments = jnp.dot(coefficients, counts, precision=lax.Precision.HIGHEST)
        intensity = moments[0]
        residual = emitted - jnp.log(intensity) - target_block
        factor = residual / intensity / views_all
        return (moments[1:] * factor[None, :]).astype(jnp.bfloat16)

    stacked = lax.map(one_block, (path_water, path_bone, target_flat))
    gradients = jnp.swapaxes(stacked, 0, 1).reshape(materials, view_count, row_count, tile_width)
    return jnp.transpose(gradients, (1, 2, 0, 3))


def spectral_kernel(views_all, emitted_ref, spectrum_ref, attenuation_ref, water_ref, bone_ref, target_ref, out0_ref, out1_ref):
    rows, width = water_ref.shape
    energies = spectrum_ref.shape[0]
    block = 8

    def one_block(b, carry):
        lo = pl.multiple_of(b * block, block)
        water = water_ref[pl.ds(lo, block), :]
        bone = bone_ref[pl.ds(lo, block), :]

        def one_energy(e, sums):
            intensity, first, second = sums
            a0 = attenuation_ref[0, e]
            a1 = attenuation_ref[1, e]
            counts = spectrum_ref[e] * jnp.exp(-(a0 * water + a1 * bone))
            return (intensity + counts, first + a0 * counts, second + a1 * counts)

        zero = jnp.zeros((block, width), jnp.float32)
        intensity, first, second = lax.fori_loop(0, energies, one_energy, (zero, zero, zero), unroll=8)
        residual = emitted_ref[0] - jnp.log(intensity) - target_ref[pl.ds(lo, block), :]
        factor = residual / intensity / views_all
        out0_ref[pl.ds(lo, block), :] = (first * factor).astype(out0_ref.dtype)
        out1_ref[pl.ds(lo, block), :] = (second * factor).astype(out1_ref.dtype)
        return carry

    lax.fori_loop(0, rows // block, one_block, 0)


def spectral_pallas(path_sums, observed, spectrum, attenuation, views_all):
    view_count, row_count, materials, width_all = path_sums.shape
    pixels = view_count * row_count * width_all
    rows = pixels // LANES // 4
    water = path_sums[:, :, 0, :].reshape(rows, 4 * LANES)
    bone = path_sums[:, :, 1, :].reshape(rows, 4 * LANES)
    target = observed.reshape(rows, 4 * LANES)
    emitted = jnp.log(jnp.sum(spectrum)).reshape(1)
    smem = pl.BlockSpec(memory_space=pltpu.SMEM)
    vmem = pl.BlockSpec(memory_space=pltpu.VMEM)
    first, second = pl.pallas_call(
        functools.partial(spectral_kernel, views_all),
        out_shape=(
            jax.ShapeDtypeStruct((rows, 4 * LANES), jnp.bfloat16),
            jax.ShapeDtypeStruct((rows, 4 * LANES), jnp.bfloat16),
        ),
        in_specs=[smem, smem, smem, vmem, vmem, vmem],
        out_specs=(vmem, vmem),
        interpret=INTERPRET,
    )(emitted, spectrum, attenuation, water, bone, target)
    shape = (view_count, row_count, width_all)
    return jnp.stack([first.reshape(shape), second.reshape(shape)], axis=2)


def per_device(density, measured, shear_shift, shear_frac, spectrum, attenuation):
    row_total, materials, depth_here, tile_width = density.shape
    block_width = min(128, tile_width)
    block_count = tile_width // block_width
    window = block_width + 2 * HALO
    views_all = measured.shape[0] * lax.axis_size("views")
    depth_all = depth_here * lax.axis_size("depth")
    rows_out = row_total // lax.axis_size("views")
    lower_weight = (1.0 - shear_frac).astype(jnp.bfloat16)
    upper_weight = shear_frac.astype(jnp.bfloat16)
    rows_here = density.shape[0]
    padded = with_halo(density, (("lat", 3),), HALO)
    framed = jnp.stack(
        [
            padded[:, :, :, number * block_width : number * block_width + window]
            for number in range(block_count)
        ],
        axis=2,
    )
    forward_band = band_forward(shear_shift, lower_weight, upper_weight, window, block_width)
    partial_value = jnp.einsum(
        "ymnzi,zivc->vymnc", framed, forward_band, preferred_element_type=jnp.float32
    )
    partial_value = partial_value.reshape(shear_shift.shape[0], rows_here, materials, tile_width)
    shares = lax.psum_scatter(partial_value, "depth", scatter_dimension=3, tiled=True) / depth_all
    share_cols = shares.shape[3]
    observed = lax.dynamic_slice_in_dim(
        measured, lax.axis_index("depth") * share_cols, share_cols, 2
    )
    share_grads = spectral(shares, observed, spectrum, attenuation, views_all)
    path_grads = lax.all_gather(share_grads, "depth", axis=3, tiled=True)
    padded_grads = with_halo(path_grads, (("lat", 3),), HALO)
    framed_grads = jnp.stack(
        [
            padded_grads[:, :, :, number * block_width : number * block_width + window]
            for number in range(block_count)
        ],
        axis=3,
    )
    backward_band = band_backward(shear_shift, lower_weight, upper_weight, window, block_width)
    product = jnp.einsum(
        "vymni,vizc->ymznc", framed_grads, backward_band, preferred_element_type=jnp.float32
    )
    return lax.psum_scatter(
        product.reshape(rows_out * lax.axis_size("views"), materials, depth_here, tile_width),
        "views",
        scatter_dimension=0,
        tiled=True,
    )


LANES = 128
INTERPRET = False


def shear_kernel(rot_ref, thr_ref, wa_ref, wb_ref, src_ref, out_ref):
    outer_count, channels, width = src_ref.shape
    inner_count, _, out_width = out_ref.shape
    pieces = width // LANES
    out_pieces = out_width // LANES
    out_ref[...] = jnp.zeros(out_ref.shape, jnp.float32)
    lane = lax.broadcasted_iota(jnp.int32, (channels, LANES), 1)

    def outer(o, carry):
        cols = [src_ref[o, :, k * LANES : (k + 1) * LANES] for k in range(pieces)]
        turned = [pltpu.roll(c, LANES - 1, 1) for c in cols]
        nexts = [
            jnp.where(lane < LANES - 1, turned[k], turned[k + 1]) for k in range(pieces - 1)
        ] + [turned[pieces - 1]]
        for i in range(inner_count):
            wa = wa_ref[o, i]
            wb = wb_ref[o, i]
            mixed = [wa * cols[k] + wb * nexts[k] for k in range(pieces)]
            rolled = [pltpu.roll(m, rot_ref[o, i], 1) for m in mixed]
            keep = lane < thr_ref[o, i]
            for j in range(out_pieces):
                out_ref[i, :, j * LANES : (j + 1) * LANES] += jnp.where(
                    keep, rolled[j], rolled[j + 1]
                )
        return carry

    lax.fori_loop(0, outer_count, outer, 0)


def shear_table_kernel(forward, tab_ref, src_ref, out_ref):
    outer_count, channels, width = src_ref.shape
    inner_count, _, out_width = out_ref.shape
    pieces = width // LANES
    out_pieces = out_width // LANES
    out_ref[...] = jnp.zeros(out_ref.shape, jnp.float32)
    lane = lax.broadcasted_iota(jnp.int32, (channels, LANES), 1)

    def outer(o, carry):
        cols = [src_ref[o, :, k * LANES : (k + 1) * LANES] for k in range(pieces)]
        turned = [pltpu.roll(c, LANES - 1, 1) for c in cols]
        nexts = [
            jnp.where(lane < LANES - 1, turned[k], turned[k + 1]) for k in range(pieces - 1)
        ] + [turned[pieces - 1]]
        for i in range(inner_count):
            if forward:
                shift = tab_ref[0, i, o].astype(jnp.int32)
                wa = tab_ref[1, i, o]
                wb = tab_ref[2, i, o]
                offset = shift + HALO
            else:
                shift = tab_ref[0, o, i].astype(jnp.int32)
                wa = tab_ref[2, o, i]
                wb = tab_ref[1, o, i]
                offset = HALO - 1 - shift
            limit = LANES - offset
            amount = jnp.where(limit == LANES, 0, limit)
            mixed = [wa * cols[k] + wb * nexts[k] for k in range(pieces)]
            rolled = [pltpu.roll(m, amount, 1) for m in mixed]
            keep = lane < limit
            for j in range(out_pieces):
                out_ref[i, :, j * LANES : (j + 1) * LANES] += jnp.where(
                    keep, rolled[j], rolled[j + 1]
                )
        return carry

    lax.fori_loop(0, outer_count, outer, 0)


def shear_table(forward, table, src, inner_count, out_width):
    _, channels, _ = src.shape
    smem = pl.BlockSpec(memory_space=pltpu.SMEM)
    vmem = pl.BlockSpec(memory_space=pltpu.VMEM)
    return pl.pallas_call(
        functools.partial(shear_table_kernel, forward),
        out_shape=jax.ShapeDtypeStruct((inner_count, channels, out_width), jnp.float32),
        in_specs=[smem, vmem],
        out_specs=vmem,
        interpret=INTERPRET,
    )(table, src)


def halo_columns(ys, lane, half_of, rows_here, halves, channels):
    count = len(ys)
    turned = [pltpu.roll(y, HALO, 1) for y in ys]
    zero = jnp.zeros_like(ys[0])
    left = jnp.where(half_of >= 1, pltpu.roll(turned[count - 1], rows_here, 0), zero)
    right = jnp.where(half_of <= halves - 2, pltpu.roll(turned[0], channels - rows_here, 0), zero)
    edge = lane < HALO
    cols = [jnp.where(edge, left, turned[0])]
    cols += [jnp.where(edge, turned[k - 1], turned[k]) for k in range(1, count)]
    cols += [jnp.where(edge, turned[count - 1], right)]
    return cols


def shear_pass(forward, rows_here, halves, tab_ref, src_ref, acc_ref, cols_ref, nexts_ref):
    outer_count, channels, width = src_ref.shape
    inner_count = acc_ref.shape[0]
    pieces = width // LANES
    lane = lax.broadcasted_iota(jnp.int32, (channels, LANES), 1)
    half_of = (lax.broadcasted_iota(jnp.int32, (channels, LANES), 0) // rows_here) % halves

    def prepare(o, carry):
        ys = [src_ref[o, :, k * LANES : (k + 1) * LANES] for k in range(pieces)]
        cols = halo_columns(ys, lane, half_of, rows_here, halves, channels)
        turned = [pltpu.roll(c, LANES - 1, 1) for c in cols]
        nexts = [jnp.where(lane < LANES - 1, turned[k], turned[k + 1]) for k in range(pieces)]
        nexts.append(turned[pieces])
        for k in range(pieces + 1):
            cols_ref[o, :, k * LANES : (k + 1) * LANES] = cols[k]
            nexts_ref[o, :, k * LANES : (k + 1) * LANES] = nexts[k]
        return carry

    lax.fori_loop(0, outer_count, prepare, 0)

    def inner(i, carry):
        acc = [jnp.zeros((channels, LANES), jnp.float32) for _ in range(pieces)]
        for o in range(outer_count):
            if forward:
                shift = tab_ref[0, i, o].astype(jnp.int32)
                wa = tab_ref[1, i, o]
                wb = tab_ref[2, i, o]
                offset = shift + HALO
            else:
                shift = tab_ref[0, o, i].astype(jnp.int32)
                wa = tab_ref[2, o, i]
                wb = tab_ref[1, o, i]
                offset = HALO - 1 - shift
            limit = LANES - offset
            amount = jnp.where(limit == LANES, 0, limit)
            mixed = [
                wa * cols_ref[o, :, k * LANES : (k + 1) * LANES]
                + wb * nexts_ref[o, :, k * LANES : (k + 1) * LANES]
                for k in range(pieces + 1)
            ]
            rolled = [pltpu.roll(m, amount, 1) for m in mixed]
            keep = lane < limit
            acc = [acc[j] + jnp.where(keep, rolled[j], rolled[j + 1]) for j in range(pieces)]
        for j in range(pieces):
            acc_ref[i, :, j * LANES : (j + 1) * LANES] = acc[j]
        return carry

    lax.fori_loop(0, inner_count, inner, 0)


def scatter_pass(rows_here, halves, tab_ref, src_ref, out_ref, cols_ref, nexts_ref):
    outer_count, channels, width = src_ref.shape
    _, depth_here, _ = out_ref.shape
    materials = channels // (halves * rows_here)
    pieces = width // LANES
    lane = lax.broadcasted_iota(jnp.int32, (channels, LANES), 1)
    half_of = (lax.broadcasted_iota(jnp.int32, (channels, LANES), 0) // rows_here) % halves

    def prepare(o, carry):
        ys = [src_ref[o, :, k * LANES : (k + 1) * LANES] for k in range(pieces)]
        cols = halo_columns(ys, lane, half_of, rows_here, halves, channels)
        turned = [pltpu.roll(c, LANES - 1, 1) for c in cols]
        nexts = [jnp.where(lane < LANES - 1, turned[k], turned[k + 1]) for k in range(pieces)]
        nexts.append(turned[pieces])
        for k in range(pieces + 1):
            cols_ref[o, :, k * LANES : (k + 1) * LANES] = cols[k]
            nexts_ref[o, :, k * LANES : (k + 1) * LANES] = nexts[k]
        return carry

    lax.fori_loop(0, outer_count, prepare, 0)
    inner_count = tab_ref.shape[2]

    for i in range(inner_count):
        slab, level = divmod(i, depth_here)

        def one_view(o, acc):
            shift = tab_ref[0, o, i].astype(jnp.int32)
            wa = tab_ref[2, o, i]
            wb = tab_ref[1, o, i]
            offset = HALO - 1 - shift
            limit = LANES - offset
            amount = jnp.where(limit == LANES, 0, limit)
            mixed = [
                wa * cols_ref[o, :, k * LANES : (k + 1) * LANES]
                + wb * nexts_ref[o, :, k * LANES : (k + 1) * LANES]
                for k in range(pieces + 1)
            ]
            rolled = [pltpu.roll(m, amount, 1) for m in mixed]
            keep = lane < limit
            return tuple(acc[j] + jnp.where(keep, rolled[j], rolled[j + 1]) for j in range(pieces))

        zero = jnp.zeros((channels, LANES), jnp.float32)
        acc = lax.fori_loop(0, outer_count, one_view, tuple(zero for _ in range(pieces)), unroll=True)
        value = jnp.concatenate(acc, axis=1)
        for c in range(channels):
            material, rest = divmod(c, halves * rows_here)
            half, row = divmod(rest, rows_here)
            target = ((slab * halves + half) * rows_here + row) * materials + material
            out_ref[target, level : level + 1, :] = value[c : c + 1, :]


def forward_kernel(rows_here, halves, depth_all, views_all, tab_ref, emitted_ref, spectrum_ref,
                   attenuation_ref, src_ref, target_ref, out_ref, sums_ref, cols_ref, nexts_ref):
    shear_pass(True, rows_here, halves, tab_ref, src_ref, sums_ref, cols_ref, nexts_ref)
    _, channels, width = sums_ref.shape
    energies = spectrum_ref.shape[0]
    split = channels // 2
    low = lax.broadcasted_iota(jnp.int32, (channels, width), 0) < split

    def one_pair(p, carry):
        first_view = sums_ref[2 * p] / depth_all
        second_view = sums_ref[2 * p + 1] / depth_all
        water = jnp.where(low, first_view, pltpu.roll(second_view, split, 0))
        bone = jnp.where(low, pltpu.roll(first_view, split, 0), second_view)

        def one_energy(e, sums):
            intensity, first, second = sums
            a0 = attenuation_ref[0, e]
            a1 = attenuation_ref[1, e]
            counts = spectrum_ref[e] * jnp.exp(-(a0 * water + a1 * bone))
            return (intensity + counts, first + a0 * counts, second + a1 * counts)

        zero = jnp.zeros((channels, width), jnp.float32)
        intensity, first, second = lax.fori_loop(0, energies, one_energy, (zero, zero, zero), unroll=8)
        residual = emitted_ref[0] - jnp.log(intensity) - target_ref[p]
        factor = residual / intensity / views_all
        first = (first * factor).astype(jnp.bfloat16).astype(jnp.float32)
        second = (second * factor).astype(jnp.bfloat16).astype(jnp.float32)
        out_ref[2 * p] = jnp.where(low, first, pltpu.roll(second, split, 0))
        out_ref[2 * p + 1] = jnp.where(low, pltpu.roll(first, split, 0), second)
        return carry

    lax.fori_loop(0, out_ref.shape[0] // 2, one_pair, 0)


def backward_kernel(rows_here, halves, tab_ref, src_ref, out_ref, cols_ref, nexts_ref):
    scatter_pass(rows_here, halves, tab_ref, src_ref, out_ref, cols_ref, nexts_ref)


def shear_apply(offset, wa, wb, src, out_width):
    outer_count, channels, width = src.shape
    inner_count = offset.shape[1]
    rot = (LANES - offset) % LANES
    thr = LANES - offset
    smem = pl.BlockSpec(memory_space=pltpu.SMEM)
    vmem = pl.BlockSpec(memory_space=pltpu.VMEM)
    return pl.pallas_call(
        shear_kernel,
        out_shape=jax.ShapeDtypeStruct((inner_count, channels, out_width), jnp.float32),
        in_specs=[smem, smem, smem, smem, vmem],
        out_specs=vmem,
        interpret=INTERPRET,
    )(rot.astype(jnp.int32), thr.astype(jnp.int32), wa, wb, src)


def rows_fit(density, measured):
    rows = density.shape[0]
    groups = lax.axis_size("views")
    depth = lax.axis_size("depth")
    tile_width = density.shape[3]
    return (
        rows % groups == 0
        and (rows // groups) % depth == 0
        and tile_width % LANES == 0
        and 2 * HALO == LANES
        and density.shape[1] == 2
        and measured.shape[0] * groups % 2 == 0
        and tile_width >= 3 * measured.shape[0] * density.shape[2] * groups
    )


def per_device_rows(density, measured, shear_shift, shear_frac, spectrum, attenuation):
    row_total, materials, depth_here, tile_width = density.shape
    groups = lax.axis_size("views")
    depth_count = lax.axis_size("depth")
    views_here = measured.shape[0]
    views_all = views_here * groups
    depth_all = depth_here * depth_count
    rows_group = row_total // groups
    rows_here = rows_group // depth_count
    group = lax.axis_index("views")
    slab = lax.axis_index("depth")

    lower_weight = (1.0 - shear_frac).astype(jnp.bfloat16).astype(jnp.float32)
    upper_weight = shear_frac.astype(jnp.bfloat16).astype(jnp.float32)
    table = jnp.stack([shear_shift.astype(jnp.float32), lower_weight, upper_weight])
    entries = table.size
    observed = measured.reshape(views_here, groups, rows_group, tile_width)
    observed = lax.dynamic_slice_in_dim(observed, slab * rows_here, rows_here, 2)
    observed = jnp.transpose(observed, (1, 0, 2, 3)).reshape(groups, views_here * rows_here, tile_width)
    extra = jnp.pad(table.reshape(1, entries), ((0, 0), (0, tile_width - entries)))
    extra = jnp.broadcast_to(extra[None], (groups, 1, tile_width))
    observed = jnp.concatenate([observed, extra], axis=1)
    observed = lax.all_to_all(observed, "views", 0, 0, tiled=True)
    table = observed[:, views_here * rows_here, :entries].reshape(groups, 3, views_here, depth_here)
    table = jnp.transpose(table, (1, 0, 2, 3)).reshape(3, views_all, depth_here)
    observed = observed[:, : views_here * rows_here].reshape(views_all, rows_here, tile_width)

    channels = rows_here * materials
    mine = lax.dynamic_slice_in_dim(density, group * rows_group, rows_group, 0)
    mine = mine.reshape(depth_count, rows_here, materials, depth_here, tile_width)
    mine = jnp.transpose(mine, (0, 3, 1, 2, 4)).reshape(depth_count, depth_here * channels, tile_width)
    wide = table.size
    extra = jnp.pad(table.reshape(1, wide), ((0, 0), (0, tile_width - wide))).astype(jnp.bfloat16)
    extra = jnp.broadcast_to(extra[None], (depth_count, 1, tile_width))
    mine = jnp.concatenate([mine, extra], axis=1)
    mine = lax.all_to_all(mine, "depth", 0, 0, tiled=True)
    table = mine[:, depth_here * channels, :wide].astype(jnp.float32)
    table = table.reshape(depth_count, 3, views_all, depth_here)
    table = jnp.transpose(table, (1, 2, 0, 3)).reshape(3, views_all, depth_all)
    shift_all = table[0].astype(jnp.int32)
    lower_all = table[1]
    upper_all = table[2]
    mine = mine[:, : depth_here * channels].reshape(depth_all, channels, tile_width)
    padded = with_halo(mine, (("lat", 2),), HALO).astype(jnp.float32)

    sums = shear_apply(
        (shift_all + HALO).T, lower_all.T, upper_all.T, padded, tile_width
    )
    sums = (sums / depth_all).reshape(views_all, rows_here, materials, tile_width)
    grads = spectral(sums, observed, spectrum, attenuation, views_all)
    grads = grads.reshape(views_all, rows_here * materials, tile_width)
    padded_grads = with_halo(grads, (("lat", 2),), HALO).astype(jnp.float32)
    layers = shear_apply(
        HALO - 1 - shift_all, upper_all, lower_all, padded_grads, tile_width
    )
    layers = layers.reshape(depth_count, depth_here, rows_here, materials, tile_width)
    layers = exchange(layers, "depth")
    return jnp.transpose(layers, (0, 2, 3, 1, 4)).reshape(rows_group, materials, depth_here, tile_width)


def rows_fit_wide(density, measured):
    rows = density.shape[0]
    groups = lax.axis_size("views")
    parts = lax.axis_size("depth") * lax.axis_size("lat")
    tile_width = density.shape[3]
    return (
        rows % groups == 0
        and (rows // groups) % parts == 0
        and tile_width % LANES == 0
        and 2 * HALO == LANES
        and density.shape[1] == 2
        and measured.shape[0] * groups % 2 == 0
        and tile_width >= 3 * measured.shape[0] * density.shape[2]
        and ((rows // groups // parts) * density.shape[1] * density.shape[2]) % groups == 0
    )


def stack_halves(values, halves, tile_width):
    count, rows, materials, _ = values.shape
    padded = jnp.pad(values, ((0, 0), (0, 0), (0, 0), (HALO, HALO)))
    parts = [
        padded[..., h * tile_width : h * tile_width + tile_width + 2 * HALO] for h in range(halves)
    ]
    return jnp.stack(parts, axis=1).reshape(count, halves * rows * materials, tile_width + 2 * HALO)


def join_halves(values, halves, rows, materials):
    count, _, tile_width = values.shape
    values = values.reshape(count, halves, rows, materials, tile_width)
    return jnp.transpose(values, (0, 2, 3, 1, 4)).reshape(count, rows, materials, halves * tile_width)


def per_device_wide(density, measured, shear_shift, shear_frac, spectrum, attenuation):
    row_total, materials, depth_here, tile_width = density.shape
    groups = lax.axis_size("views")
    depth_count = lax.axis_size("depth")
    halves = lax.axis_size("lat")
    parts = depth_count * halves
    views_here = measured.shape[0]
    views_all = views_here * groups
    depth_all = depth_here * depth_count
    rows_group = row_total // groups
    rows_here = rows_group // parts
    group = lax.axis_index("views")
    slab = lax.axis_index("depth")
    half = lax.axis_index("lat")

    lower_weight = (1.0 - shear_frac).astype(jnp.bfloat16).astype(jnp.float32)
    upper_weight = shear_frac.astype(jnp.bfloat16).astype(jnp.float32)
    block = jnp.stack([shear_shift.astype(jnp.float32), lower_weight, upper_weight])
    entries = block.size
    observed = measured.reshape(views_here, groups, depth_count, halves, rows_here, tile_width)
    observed = lax.dynamic_index_in_dim(observed, slab, 2, keepdims=False)
    observed = jnp.transpose(observed, (1, 2, 0, 3, 4)).reshape(
        groups * halves, views_here * rows_here, tile_width
    )
    observed = lax.all_to_all(observed, ("views", "lat"), 0, 0, tiled=True)
    observed = observed.reshape(groups, halves, views_here, rows_here, tile_width)
    observed = jnp.transpose(observed, (0, 2, 3, 1, 4)).reshape(views_all, rows_here, halves * tile_width)

    chunk = rows_here * materials * depth_here * tile_width
    piece = chunk // groups
    mine = density.reshape(groups * parts, groups, piece)
    mine = lax.dynamic_index_in_dim(mine, group, 1, keepdims=False)
    mine = mine.reshape(groups * parts, piece // tile_width, tile_width)
    extra = jnp.pad(block.reshape(1, entries), ((0, 0), (0, tile_width - entries))).astype(jnp.bfloat16)
    extra = jnp.broadcast_to(extra[None], (groups * parts, 1, tile_width))
    mine = jnp.concatenate([mine, extra], axis=1)
    mine = lax.all_to_all(mine, ("views", "depth", "lat"), 0, 0, tiled=True)
    mine = mine.reshape(groups, depth_count, halves, piece // tile_width + 1, tile_width)
    table = mine[:, :, 0, piece // tile_width, :entries].astype(jnp.float32)
    table = table.reshape(groups, depth_count, 3, views_here, depth_here)
    table = jnp.transpose(table, (2, 0, 3, 1, 4)).reshape(3, views_all, depth_all)
    mine = mine[:, :, :, : piece // tile_width].reshape(groups, depth_count, halves, piece)
    mine = jnp.transpose(mine, (1, 2, 0, 3)).reshape(
        depth_count, halves, rows_here, materials, depth_here, tile_width
    )
    channels = materials * halves * rows_here
    mine = jnp.transpose(mine, (0, 4, 3, 1, 2, 5)).reshape(depth_all, channels, tile_width)
    mine = mine.astype(jnp.float32)
    target = observed.reshape(views_all // 2, 2, rows_here, halves, tile_width)
    target = jnp.transpose(target, (0, 1, 3, 2, 4)).reshape(views_all // 2, 2 * halves * rows_here, tile_width)
    emitted = jnp.log(jnp.sum(spectrum)).reshape(1)
    smem = pl.BlockSpec(memory_space=pltpu.SMEM)
    vmem = pl.BlockSpec(memory_space=pltpu.VMEM)
    grads = pl.pallas_call(
        functools.partial(forward_kernel, rows_here, halves, depth_all, views_all),
        out_shape=jax.ShapeDtypeStruct((views_all, channels, tile_width), jnp.float32),
        in_specs=[smem, smem, smem, smem, vmem, vmem],
        out_specs=vmem,
        scratch_shapes=[
            pltpu.VMEM((views_all, channels, tile_width), jnp.float32),
            pltpu.VMEM((depth_all, channels, tile_width + LANES), jnp.float32),
            pltpu.VMEM((depth_all, channels, tile_width + LANES), jnp.float32),
        ],
        interpret=INTERPRET,
    )(table, emitted, spectrum, attenuation, mine, target)
    layers = pl.pallas_call(
        functools.partial(backward_kernel, rows_here, halves),
        out_shape=jax.ShapeDtypeStruct((parts * rows_here * materials, depth_here, tile_width), jnp.float32),
        in_specs=[smem, vmem],
        out_specs=vmem,
        scratch_shapes=[
            pltpu.VMEM((views_all, channels, tile_width + LANES), jnp.float32),
            pltpu.VMEM((views_all, channels, tile_width + LANES), jnp.float32),
        ],
        interpret=INTERPRET,
    )(table, grads)
    layers = layers.reshape(parts, rows_here, materials, depth_here, tile_width)
    layers = lax.all_to_all(layers, ("depth", "lat"), 0, 0, tiled=True)
    return layers.reshape(rows_group, materials, depth_here, tile_width)


def per_device_any(density, measured, shear_shift, shear_frac, spectrum, attenuation):
    if rows_fit_wide(density, measured):
        return per_device_wide(density, measured, shear_shift, shear_frac, spectrum, attenuation)
    if rows_fit(density, measured):
        return per_device_rows(density, measured, shear_shift, shear_frac, spectrum, attenuation)
    return per_device(density, measured, shear_shift, shear_frac, spectrum, attenuation)


def solution(mesh):
    in_specs = (
        P(None, None, "depth", "lat"),
        P("views", None, "lat"),
        P("views", "depth"),
        P("views", "depth"),
        P(),
        P(),
    )
    out_specs = P("views", None, "depth", "lat")
    return jax.shard_map(
        per_device_any, mesh=mesh, in_specs=in_specs, out_specs=out_specs, check_vma=False
    )
```

```python
import functools
import jax
import jax.numpy as jnp
from jax import lax
from jax.sharding import PartitionSpec as P
from jax.experimental import pallas as pl
from jax.experimental.pallas import tpu as pltpu

HALO = 64


def with_halo(x, sides, width):
    for axis, dim in sides:
        size, length = (lax.axis_size(axis), x.shape[dim])
        up = [(i, (i + 1) % size) for i in range(size - 1)]
        down = [(j, i) for i, j in up]
        last = lax.slice_in_dim(x, length - width, length, axis=dim)
        first = lax.slice_in_dim(x, 0, width, axis=dim)
        before = lax.ppermute(last, axis, up)
        after = lax.ppermute(first, axis, down)
        x = jnp.concatenate([before, x, after], axis=dim)
    return x


def exchange(x, axis):
    count = lax.axis_size(axis)
    me = lax.axis_index(axis)
    result = x
    for step in range(1, count):
        pairs = [(i, (i + step) % count) for i in range(count)]
        part = lax.dynamic_index_in_dim(x, (me + step) % count, 0, keepdims=True)
        part = lax.ppermute(part, axis, pairs)
        result = lax.dynamic_update_index_in_dim(result, part, (me - step) % count, 0)
    return result


def band_forward(shear_shift, lower_weight, upper_weight, window, block_width):
    band_shape = (shear_shift.shape[1], window, shear_shift.shape[0], block_width)
    tap_index = lax.broadcasted_iota(jnp.int32, band_shape, 1)
    column = lax.broadcasted_iota(jnp.int32, band_shape, 3)
    anchor = (shear_shift.T + HALO)[:, None, :, None]
    nothing = jnp.zeros((), jnp.bfloat16)
    lower_part = jnp.where(tap_index == column + anchor, lower_weight.T[:, None, :, None], nothing)
    upper_part = jnp.where(
        tap_index == column + anchor + 1, upper_weight.T[:, None, :, None], nothing
    )
    return lower_part + upper_part


def band_backward(shear_shift, lower_weight, upper_weight, window, block_width):
    band_shape = (shear_shift.shape[0], window, shear_shift.shape[1], block_width)
    tap_index = lax.broadcasted_iota(jnp.int32, band_shape, 1)
    column = lax.broadcasted_iota(jnp.int32, band_shape, 3)
    anchor = (HALO - shear_shift)[:, None, :, None]
    nothing = jnp.zeros((), jnp.bfloat16)
    lower_part = jnp.where(tap_index == column + anchor, lower_weight[:, None, :, None], nothing)
    upper_part = jnp.where(
        tap_index == column + anchor - 1, upper_weight[:, None, :, None], nothing
    )
    return lower_part + upper_part


def spectral(path_sums, observed, spectrum, attenuation, views_all):
    view_count, row_count, materials, tile_width = path_sums.shape
    block_pixels = 4096
    path_water = path_sums[:, :, 0, :].reshape(-1, block_pixels)
    path_bone = path_sums[:, :, 1, :].reshape(-1, block_pixels)
    target_flat = observed.reshape(-1, block_pixels)
    coefficients = jnp.concatenate(
        [jnp.ones((1, spectrum.shape[0]), jnp.float32), attenuation], axis=0
    )
    emitted = jnp.log(jnp.sum(spectrum))

    def one_block(inputs):
        water_block, bone_block, target_block = inputs
        exponent = (
            attenuation[0][:, None] * water_block[None, :]
            + attenuation[1][:, None] * bone_block[None, :]
        )
        counts = spectrum[:, None] * jnp.exp(-exponent)
        moments = jnp.dot(coefficients, counts, precision=lax.Precision.HIGHEST)
        intensity = moments[0]
        residual = emitted - jnp.log(intensity) - target_block
        factor = residual / intensity / views_all
        return (moments[1:] * factor[None, :]).astype(jnp.bfloat16)

    stacked = lax.map(one_block, (path_water, path_bone, target_flat))
    gradients = jnp.swapaxes(stacked, 0, 1).reshape(materials, view_count, row_count, tile_width)
    return jnp.transpose(gradients, (1, 2, 0, 3))


def spectral_kernel(views_all, emitted_ref, spectrum_ref, attenuation_ref, water_ref, bone_ref, target_ref, out0_ref, out1_ref):
    rows, width = water_ref.shape
    energies = spectrum_ref.shape[0]
    block = 8

    def one_block(b, carry):
        lo = pl.multiple_of(b * block, block)
        water = water_ref[pl.ds(lo, block), :]
        bone = bone_ref[pl.ds(lo, block), :]

        def one_energy(e, sums):
            intensity, first, second = sums
            a0 = attenuation_ref[0, e]
            a1 = attenuation_ref[1, e]
            counts = spectrum_ref[e] * jnp.exp(-(a0 * water + a1 * bone))
            return (intensity + counts, first + a0 * counts, second + a1 * counts)

        zero = jnp.zeros((block, width), jnp.float32)
        intensity, first, second = lax.fori_loop(0, energies, one_energy, (zero, zero, zero), unroll=8)
        residual = emitted_ref[0] - jnp.log(intensity) - target_ref[pl.ds(lo, block), :]
        factor = residual / intensity / views_all
        out0_ref[pl.ds(lo, block), :] = (first * factor).astype(out0_ref.dtype)
        out1_ref[pl.ds(lo, block), :] = (second * factor).astype(out1_ref.dtype)
        return carry

    lax.fori_loop(0, rows // block, one_block, 0)


def spectral_pallas(path_sums, observed, spectrum, attenuation, views_all):
    view_count, row_count, materials, width_all = path_sums.shape
    pixels = view_count * row_count * width_all
    rows = pixels // LANES // 4
    water = path_sums[:, :, 0, :].reshape(rows, 4 * LANES)
    bone = path_sums[:, :, 1, :].reshape(rows, 4 * LANES)
    target = observed.reshape(rows, 4 * LANES)
    emitted = jnp.log(jnp.sum(spectrum)).reshape(1)
    smem = pl.BlockSpec(memory_space=pltpu.SMEM)
    vmem = pl.BlockSpec(memory_space=pltpu.VMEM)
    first, second = pl.pallas_call(
        functools.partial(spectral_kernel, views_all),
        out_shape=(
            jax.ShapeDtypeStruct((rows, 4 * LANES), jnp.bfloat16),
            jax.ShapeDtypeStruct((rows, 4 * LANES), jnp.bfloat16),
        ),
        in_specs=[smem, smem, smem, vmem, vmem, vmem],
        out_specs=(vmem, vmem),
        interpret=INTERPRET,
    )(emitted, spectrum, attenuation, water, bone, target)
    shape = (view_count, row_count, width_all)
    return jnp.stack([first.reshape(shape), second.reshape(shape)], axis=2)


def per_device(density, measured, shear_shift, shear_frac, spectrum, attenuation):
    row_total, materials, depth_here, tile_width = density.shape
    block_width = min(128, tile_width)
    block_count = tile_width // block_width
    window = block_width + 2 * HALO
    views_all = measured.shape[0] * lax.axis_size("views")
    depth_all = depth_here * lax.axis_size("depth")
    rows_out = row_total // lax.axis_size("views")
    lower_weight = (1.0 - shear_frac).astype(jnp.bfloat16)
    upper_weight = shear_frac.astype(jnp.bfloat16)
    rows_here = density.shape[0]
    padded = with_halo(density, (("lat", 3),), HALO)
    framed = jnp.stack(
        [
            padded[:, :, :, number * block_width : number * block_width + window]
            for number in range(block_count)
        ],
        axis=2,
    )
    forward_band = band_forward(shear_shift, lower_weight, upper_weight, window, block_width)
    partial_value = jnp.einsum(
        "ymnzi,zivc->vymnc", framed, forward_band, preferred_element_type=jnp.float32
    )
    partial_value = partial_value.reshape(shear_shift.shape[0], rows_here, materials, tile_width)
    shares = lax.psum_scatter(partial_value, "depth", scatter_dimension=3, tiled=True) / depth_all
    share_cols = shares.shape[3]
    observed = lax.dynamic_slice_in_dim(
        measured, lax.axis_index("depth") * share_cols, share_cols, 2
    )
    share_grads = spectral(shares, observed, spectrum, attenuation, views_all)
    path_grads = lax.all_gather(share_grads, "depth", axis=3, tiled=True)
    padded_grads = with_halo(path_grads, (("lat", 3),), HALO)
    framed_grads = jnp.stack(
        [
            padded_grads[:, :, :, number * block_width : number * block_width + window]
            for number in range(block_count)
        ],
        axis=3,
    )
    backward_band = band_backward(shear_shift, lower_weight, upper_weight, window, block_width)
    product = jnp.einsum(
        "vymni,vizc->ymznc", framed_grads, backward_band, preferred_element_type=jnp.float32
    )
    return lax.psum_scatter(
        product.reshape(rows_out * lax.axis_size("views"), materials, depth_here, tile_width),
        "views",
        scatter_dimension=0,
        tiled=True,
    )


LANES = 128
INTERPRET = False


def shear_kernel(rot_ref, thr_ref, wa_ref, wb_ref, src_ref, out_ref):
    outer_count, channels, width = src_ref.shape
    inner_count, _, out_width = out_ref.shape
    pieces = width // LANES
    out_pieces = out_width // LANES
    out_ref[...] = jnp.zeros(out_ref.shape, jnp.float32)
    lane = lax.broadcasted_iota(jnp.int32, (channels, LANES), 1)

    def outer(o, carry):
        cols = [src_ref[o, :, k * LANES : (k + 1) * LANES] for k in range(pieces)]
        turned = [pltpu.roll(c, LANES - 1, 1) for c in cols]
        nexts = [
            jnp.where(lane < LANES - 1, turned[k], turned[k + 1]) for k in range(pieces - 1)
        ] + [turned[pieces - 1]]
        for i in range(inner_count):
            wa = wa_ref[o, i]
            wb = wb_ref[o, i]
            mixed = [wa * cols[k] + wb * nexts[k] for k in range(pieces)]
            rolled = [pltpu.roll(m, rot_ref[o, i], 1) for m in mixed]
            keep = lane < thr_ref[o, i]
            for j in range(out_pieces):
                out_ref[i, :, j * LANES : (j + 1) * LANES] += jnp.where(
                    keep, rolled[j], rolled[j + 1]
                )
        return carry

    lax.fori_loop(0, outer_count, outer, 0)


def shear_table_kernel(forward, tab_ref, src_ref, out_ref):
    outer_count, channels, width = src_ref.shape
    inner_count, _, out_width = out_ref.shape
    pieces = width // LANES
    out_pieces = out_width // LANES
    out_ref[...] = jnp.zeros(out_ref.shape, jnp.float32)
    lane = lax.broadcasted_iota(jnp.int32, (channels, LANES), 1)

    def outer(o, carry):
        cols = [src_ref[o, :, k * LANES : (k + 1) * LANES] for k in range(pieces)]
        turned = [pltpu.roll(c, LANES - 1, 1) for c in cols]
        nexts = [
            jnp.where(lane < LANES - 1, turned[k], turned[k + 1]) for k in range(pieces - 1)
        ] + [turned[pieces - 1]]
        for i in range(inner_count):
            if forward:
                shift = tab_ref[0, i, o].astype(jnp.int32)
                wa = tab_ref[1, i, o]
                wb = tab_ref[2, i, o]
                offset = shift + HALO
            else:
                shift = tab_ref[0, o, i].astype(jnp.int32)
                wa = tab_ref[2, o, i]
                wb = tab_ref[1, o, i]
                offset = HALO - 1 - shift
            limit = LANES - offset
            amount = jnp.where(limit == LANES, 0, limit)
            mixed = [wa * cols[k] + wb * nexts[k] for k in range(pieces)]
            rolled = [pltpu.roll(m, amount, 1) for m in mixed]
            keep = lane < limit
            for j in range(out_pieces):
                out_ref[i, :, j * LANES : (j + 1) * LANES] += jnp.where(
                    keep, rolled[j], rolled[j + 1]
                )
        return carry

    lax.fori_loop(0, outer_count, outer, 0)


def shear_table(forward, table, src, inner_count, out_width):
    _, channels, _ = src.shape
    smem = pl.BlockSpec(memory_space=pltpu.SMEM)
    vmem = pl.BlockSpec(memory_space=pltpu.VMEM)
    return pl.pallas_call(
        functools.partial(shear_table_kernel, forward),
        out_shape=jax.ShapeDtypeStruct((inner_count, channels, out_width), jnp.float32),
        in_specs=[smem, vmem],
        out_specs=vmem,
        interpret=INTERPRET,
    )(table, src)


def halo_columns(ys, lane, half_of, rows_here, halves, channels):
    count = len(ys)
    turned = [pltpu.roll(y, HALO, 1) for y in ys]
    zero = jnp.zeros_like(ys[0])
    left = jnp.where(half_of >= 1, pltpu.roll(turned[count - 1], rows_here, 0), zero)
    right = jnp.where(half_of <= halves - 2, pltpu.roll(turned[0], channels - rows_here, 0), zero)
    edge = lane < HALO
    cols = [jnp.where(edge, left, turned[0])]
    cols += [jnp.where(edge, turned[k - 1], turned[k]) for k in range(1, count)]
    cols += [jnp.where(edge, turned[count - 1], right)]
    return cols


def shear_pass(forward, rows_here, halves, tab_ref, src_ref, acc_ref, cols_ref, nexts_ref):
    outer_count, channels, width = src_ref.shape
    inner_count = acc_ref.shape[0]
    pieces = width // LANES
    lane = lax.broadcasted_iota(jnp.int32, (channels, LANES), 1)
    half_of = (lax.broadcasted_iota(jnp.int32, (channels, LANES), 0) // rows_here) % halves

    def prepare(o, carry):
        ys = [src_ref[o, :, k * LANES : (k + 1) * LANES] for k in range(pieces)]
        cols = halo_columns(ys, lane, half_of, rows_here, halves, channels)
        turned = [pltpu.roll(c, LANES - 1, 1) for c in cols]
        nexts = [jnp.where(lane < LANES - 1, turned[k], turned[k + 1]) for k in range(pieces)]
        nexts.append(turned[pieces])
        for k in range(pieces + 1):
            cols_ref[o, :, k * LANES : (k + 1) * LANES] = cols[k]
            nexts_ref[o, :, k * LANES : (k + 1) * LANES] = nexts[k]
        return carry

    lax.fori_loop(0, outer_count, prepare, 0)

    for i in range(inner_count):

        def one_input(o, acc):
            if forward:
                shift = tab_ref[0, i, o].astype(jnp.int32)
                wa = tab_ref[1, i, o]
                wb = tab_ref[2, i, o]
                offset = shift + HALO
            else:
                shift = tab_ref[0, o, i].astype(jnp.int32)
                wa = tab_ref[2, o, i]
                wb = tab_ref[1, o, i]
                offset = HALO - 1 - shift
            limit = LANES - offset
            amount = jnp.where(limit == LANES, 0, limit)
            mixed = [
                wa * cols_ref[o, :, k * LANES : (k + 1) * LANES]
                + wb * nexts_ref[o, :, k * LANES : (k + 1) * LANES]
                for k in range(pieces + 1)
            ]
            rolled = [pltpu.roll(m, amount, 1) for m in mixed]
            keep = lane < limit
            return tuple(acc[j] + jnp.where(keep, rolled[j], rolled[j + 1]) for j in range(pieces))

        zero = jnp.zeros((channels, LANES), jnp.float32)
        acc = lax.fori_loop(0, outer_count, one_input, tuple(zero for _ in range(pieces)), unroll=True)
        for j in range(pieces):
            acc_ref[i, :, j * LANES : (j + 1) * LANES] = acc[j]


def scatter_pass(rows_here, halves, tab_ref, src_ref, out_ref, cols_ref, nexts_ref):
    outer_count, channels, width = src_ref.shape
    _, depth_here, _ = out_ref.shape
    materials = channels // (halves * rows_here)
    pieces = width // LANES
    lane = lax.broadcasted_iota(jnp.int32, (channels, LANES), 1)
    half_of = (lax.broadcasted_iota(jnp.int32, (channels, LANES), 0) // rows_here) % halves

    def prepare(o, carry):
        ys = [src_ref[o, :, k * LANES : (k + 1) * LANES] for k in range(pieces)]
        cols = halo_columns(ys, lane, half_of, rows_here, halves, channels)
        turned = [pltpu.roll(c, LANES - 1, 1) for c in cols]
        nexts = [jnp.where(lane < LANES - 1, turned[k], turned[k + 1]) for k in range(pieces)]
        nexts.append(turned[pieces])
        for k in range(pieces + 1):
            cols_ref[o, :, k * LANES : (k + 1) * LANES] = cols[k]
            nexts_ref[o, :, k * LANES : (k + 1) * LANES] = nexts[k]
        return carry

    lax.fori_loop(0, outer_count, prepare, 0)
    inner_count = tab_ref.shape[2]

    for i in range(inner_count):
        slab, level = divmod(i, depth_here)

        def one_view(o, acc):
            shift = tab_ref[0, o, i].astype(jnp.int32)
            wa = tab_ref[2, o, i]
            wb = tab_ref[1, o, i]
            offset = HALO - 1 - shift
            limit = LANES - offset
            amount = jnp.where(limit == LANES, 0, limit)
            mixed = [
                wa * cols_ref[o, :, k * LANES : (k + 1) * LANES]
                + wb * nexts_ref[o, :, k * LANES : (k + 1) * LANES]
                for k in range(pieces + 1)
            ]
            rolled = [pltpu.roll(m, amount, 1) for m in mixed]
            keep = lane < limit
            return tuple(acc[j] + jnp.where(keep, rolled[j], rolled[j + 1]) for j in range(pieces))

        zero = jnp.zeros((channels, LANES), jnp.float32)
        acc = lax.fori_loop(0, outer_count, one_view, tuple(zero for _ in range(pieces)), unroll=True)
        value = jnp.concatenate(acc, axis=1)
        for c in range(channels):
            material, rest = divmod(c, halves * rows_here)
            half, row = divmod(rest, rows_here)
            target = ((slab * halves + half) * rows_here + row) * materials + material
            out_ref[target, level : level + 1, :] = value[c : c + 1, :]


def forward_kernel(rows_here, halves, depth_all, views_all, tab_ref, emitted_ref, spectrum_ref,
                   attenuation_ref, src_ref, target_ref, out_ref, sums_ref, cols_ref, nexts_ref):
    shear_pass(True, rows_here, halves, tab_ref, src_ref, sums_ref, cols_ref, nexts_ref)
    _, channels, width = sums_ref.shape
    energies = spectrum_ref.shape[0]
    split = channels // 2
    low = lax.broadcasted_iota(jnp.int32, (channels, width), 0) < split

    def one_pair(p, carry):
        first_view = sums_ref[2 * p] / depth_all
        second_view = sums_ref[2 * p + 1] / depth_all
        water = jnp.where(low, first_view, pltpu.roll(second_view, split, 0))
        bone = jnp.where(low, pltpu.roll(first_view, split, 0), second_view)

        def one_energy(e, sums):
            intensity, first, second = sums
            a0 = attenuation_ref[0, e]
            a1 = attenuation_ref[1, e]
            counts = spectrum_ref[e] * jnp.exp(-(a0 * water + a1 * bone))
            return (intensity + counts, first + a0 * counts, second + a1 * counts)

        zero = jnp.zeros((channels, width), jnp.float32)
        intensity, first, second = lax.fori_loop(0, energies, one_energy, (zero, zero, zero), unroll=8)
        residual = emitted_ref[0] - jnp.log(intensity) - target_ref[p]
        factor = residual / intensity / views_all
        first = (first * factor).astype(jnp.bfloat16).astype(jnp.float32)
        second = (second * factor).astype(jnp.bfloat16).astype(jnp.float32)
        out_ref[2 * p] = jnp.where(low, first, pltpu.roll(second, split, 0))
        out_ref[2 * p + 1] = jnp.where(low, pltpu.roll(first, split, 0), second)
        return carry

    lax.fori_loop(0, out_ref.shape[0] // 2, one_pair, 0)


def backward_kernel(rows_here, halves, tab_ref, src_ref, out_ref, cols_ref, nexts_ref):
    scatter_pass(rows_here, halves, tab_ref, src_ref, out_ref, cols_ref, nexts_ref)


def shear_apply(offset, wa, wb, src, out_width):
    outer_count, channels, width = src.shape
    inner_count = offset.shape[1]
    rot = (LANES - offset) % LANES
    thr = LANES - offset
    smem = pl.BlockSpec(memory_space=pltpu.SMEM)
    vmem = pl.BlockSpec(memory_space=pltpu.VMEM)
    return pl.pallas_call(
        shear_kernel,
        out_shape=jax.ShapeDtypeStruct((inner_count, channels, out_width), jnp.float32),
        in_specs=[smem, smem, smem, smem, vmem],
        out_specs=vmem,
        interpret=INTERPRET,
    )(rot.astype(jnp.int32), thr.astype(jnp.int32), wa, wb, src)


def rows_fit(density, measured):
    rows = density.shape[0]
    groups = lax.axis_size("views")
    depth = lax.axis_size("depth")
    tile_width = density.shape[3]
    return (
        rows % groups == 0
        and (rows // groups) % depth == 0
        and tile_width % LANES == 0
        and 2 * HALO == LANES
        and density.shape[1] == 2
        and measured.shape[0] * groups % 2 == 0
        and tile_width >= 3 * measured.shape[0] * density.shape[2] * groups
    )


def per_device_rows(density, measured, shear_shift, shear_frac, spectrum, attenuation):
    row_total, materials, depth_here, tile_width = density.shape
    groups = lax.axis_size("views")
    depth_count = lax.axis_size("depth")
    views_here = measured.shape[0]
    views_all = views_here * groups
    depth_all = depth_here * depth_count
    rows_group = row_total // groups
    rows_here = rows_group // depth_count
    group = lax.axis_index("views")
    slab = lax.axis_index("depth")

    lower_weight = (1.0 - shear_frac).astype(jnp.bfloat16).astype(jnp.float32)
    upper_weight = shear_frac.astype(jnp.bfloat16).astype(jnp.float32)
    table = jnp.stack([shear_shift.astype(jnp.float32), lower_weight, upper_weight])
    entries = table.size
    observed = measured.reshape(views_here, groups, rows_group, tile_width)
    observed = lax.dynamic_slice_in_dim(observed, slab * rows_here, rows_here, 2)
    observed = jnp.transpose(observed, (1, 0, 2, 3)).reshape(groups, views_here * rows_here, tile_width)
    extra = jnp.pad(table.reshape(1, entries), ((0, 0), (0, tile_width - entries)))
    extra = jnp.broadcast_to(extra[None], (groups, 1, tile_width))
    observed = jnp.concatenate([observed, extra], axis=1)
    observed = lax.all_to_all(observed, "views", 0, 0, tiled=True)
    table = observed[:, views_here * rows_here, :entries].reshape(groups, 3, views_here, depth_here)
    table = jnp.transpose(table, (1, 0, 2, 3)).reshape(3, views_all, depth_here)
    observed = observed[:, : views_here * rows_here].reshape(views_all, rows_here, tile_width)

    channels = rows_here * materials
    mine = lax.dynamic_slice_in_dim(density, group * rows_group, rows_group, 0)
    mine = mine.reshape(depth_count, rows_here, materials, depth_here, tile_width)
    mine = jnp.transpose(mine, (0, 3, 1, 2, 4)).reshape(depth_count, depth_here * channels, tile_width)
    wide = table.size
    extra = jnp.pad(table.reshape(1, wide), ((0, 0), (0, tile_width - wide))).astype(jnp.bfloat16)
    extra = jnp.broadcast_to(extra[None], (depth_count, 1, tile_width))
    mine = jnp.concatenate([mine, extra], axis=1)
    mine = lax.all_to_all(mine, "depth", 0, 0, tiled=True)
    table = mine[:, depth_here * channels, :wide].astype(jnp.float32)
    table = table.reshape(depth_count, 3, views_all, depth_here)
    table = jnp.transpose(table, (1, 2, 0, 3)).reshape(3, views_all, depth_all)
    shift_all = table[0].astype(jnp.int32)
    lower_all = table[1]
    upper_all = table[2]
    mine = mine[:, : depth_here * channels].reshape(depth_all, channels, tile_width)
    padded = with_halo(mine, (("lat", 2),), HALO).astype(jnp.float32)

    sums = shear_apply(
        (shift_all + HALO).T, lower_all.T, upper_all.T, padded, tile_width
    )
    sums = (sums / depth_all).reshape(views_all, rows_here, materials, tile_width)
    grads = spectral(sums, observed, spectrum, attenuation, views_all)
    grads = grads.reshape(views_all, rows_here * materials, tile_width)
    padded_grads = with_halo(grads, (("lat", 2),), HALO).astype(jnp.float32)
    layers = shear_apply(
        HALO - 1 - shift_all, upper_all, lower_all, padded_grads, tile_width
    )
    layers = layers.reshape(depth_count, depth_here, rows_here, materials, tile_width)
    layers = exchange(layers, "depth")
    return jnp.transpose(layers, (0, 2, 3, 1, 4)).reshape(rows_group, materials, depth_here, tile_width)


def rows_fit_wide(density, measured):
    rows = density.shape[0]
    groups = lax.axis_size("views")
    parts = lax.axis_size("depth") * lax.axis_size("lat")
    tile_width = density.shape[3]
    return (
        rows % groups == 0
        and (rows // groups) % parts == 0
        and tile_width % LANES == 0
        and 2 * HALO == LANES
        and density.shape[1] == 2
        and measured.shape[0] * groups % 2 == 0
        and tile_width >= 3 * measured.shape[0] * density.shape[2]
        and ((rows // groups // parts) * density.shape[1] * density.shape[2]) % groups == 0
    )


def stack_halves(values, halves, tile_width):
    count, rows, materials, _ = values.shape
    padded = jnp.pad(values, ((0, 0), (0, 0), (0, 0), (HALO, HALO)))
    parts = [
        padded[..., h * tile_width : h * tile_width + tile_width + 2 * HALO] for h in range(halves)
    ]
    return jnp.stack(parts, axis=1).reshape(count, halves * rows * materials, tile_width + 2 * HALO)


def join_halves(values, halves, rows, materials):
    count, _, tile_width = values.shape
    values = values.reshape(count, halves, rows, materials, tile_width)
    return jnp.transpose(values, (0, 2, 3, 1, 4)).reshape(count, rows, materials, halves * tile_width)


def per_device_wide(density, measured, shear_shift, shear_frac, spectrum, attenuation):
    row_total, materials, depth_here, tile_width = density.shape
    groups = lax.axis_size("views")
    depth_count = lax.axis_size("depth")
    halves = lax.axis_size("lat")
    parts = depth_count * halves
    views_here = measured.shape[0]
    views_all = views_here * groups
    depth_all = depth_here * depth_count
    rows_group = row_total // groups
    rows_here = rows_group // parts
    group = lax.axis_index("views")
    slab = lax.axis_index("depth")
    half = lax.axis_index("lat")

    lower_weight = (1.0 - shear_frac).astype(jnp.bfloat16).astype(jnp.float32)
    upper_weight = shear_frac.astype(jnp.bfloat16).astype(jnp.float32)
    block = jnp.stack([shear_shift.astype(jnp.float32), lower_weight, upper_weight])
    entries = block.size
    observed = measured.reshape(views_here, groups, depth_count, halves, rows_here, tile_width)
    observed = lax.dynamic_index_in_dim(observed, slab, 2, keepdims=False)
    observed = jnp.transpose(observed, (1, 2, 0, 3, 4)).reshape(
        groups * halves, views_here * rows_here, tile_width
    )
    observed = lax.all_to_all(observed, ("views", "lat"), 0, 0, tiled=True)
    observed = observed.reshape(groups, halves, views_here, rows_here, tile_width)
    observed = jnp.transpose(observed, (0, 2, 3, 1, 4)).reshape(views_all, rows_here, halves * tile_width)

    chunk = rows_here * materials * depth_here * tile_width
    piece = chunk // groups
    mine = density.reshape(groups * parts, groups, piece)
    mine = lax.dynamic_index_in_dim(mine, group, 1, keepdims=False)
    mine = mine.reshape(groups * parts, piece // tile_width, tile_width)
    extra = jnp.pad(block.reshape(1, entries), ((0, 0), (0, tile_width - entries))).astype(jnp.bfloat16)
    extra = jnp.broadcast_to(extra[None], (groups * parts, 1, tile_width))
    mine = jnp.concatenate([mine, extra], axis=1)
    mine = lax.all_to_all(mine, ("views", "depth", "lat"), 0, 0, tiled=True)
    mine = mine.reshape(groups, depth_count, halves, piece // tile_width + 1, tile_width)
    table = mine[:, :, 0, piece // tile_width, :entries].astype(jnp.float32)
    table = table.reshape(groups, depth_count, 3, views_here, depth_here)
    table = jnp.transpose(table, (2, 0, 3, 1, 4)).reshape(3, views_all, depth_all)
    mine = mine[:, :, :, : piece // tile_width].reshape(groups, depth_count, halves, piece)
    mine = jnp.transpose(mine, (1, 2, 0, 3)).reshape(
        depth_count, halves, rows_here, materials, depth_here, tile_width
    )
    channels = materials * halves * rows_here
    mine = jnp.transpose(mine, (0, 4, 3, 1, 2, 5)).reshape(depth_all, channels, tile_width)
    mine = mine.astype(jnp.float32)
    target = observed.reshape(views_all // 2, 2, rows_here, halves, tile_width)
    target = jnp.transpose(target, (0, 1, 3, 2, 4)).reshape(views_all // 2, 2 * halves * rows_here, tile_width)
    emitted = jnp.log(jnp.sum(spectrum)).reshape(1)
    smem = pl.BlockSpec(memory_space=pltpu.SMEM)
    vmem = pl.BlockSpec(memory_space=pltpu.VMEM)
    grads = pl.pallas_call(
        functools.partial(forward_kernel, rows_here, halves, depth_all, views_all),
        out_shape=jax.ShapeDtypeStruct((views_all, channels, tile_width), jnp.float32),
        in_specs=[smem, smem, smem, smem, vmem, vmem],
        out_specs=vmem,
        scratch_shapes=[
            pltpu.VMEM((views_all, channels, tile_width), jnp.float32),
            pltpu.VMEM((depth_all, channels, tile_width + LANES), jnp.float32),
            pltpu.VMEM((depth_all, channels, tile_width + LANES), jnp.float32),
        ],
        interpret=INTERPRET,
    )(table, emitted, spectrum, attenuation, mine, target)
    layers = pl.pallas_call(
        functools.partial(backward_kernel, rows_here, halves),
        out_shape=jax.ShapeDtypeStruct((parts * rows_here * materials, depth_here, tile_width), jnp.float32),
        in_specs=[smem, vmem],
        out_specs=vmem,
        scratch_shapes=[
            pltpu.VMEM((views_all, channels, tile_width + LANES), jnp.float32),
            pltpu.VMEM((views_all, channels, tile_width + LANES), jnp.float32),
        ],
        interpret=INTERPRET,
    )(table, grads)
    layers = layers.reshape(parts, rows_here, materials, depth_here, tile_width)
    layers = lax.all_to_all(layers, ("depth", "lat"), 0, 0, tiled=True)
    return layers.reshape(rows_group, materials, depth_here, tile_width)


def per_device_any(density, measured, shear_shift, shear_frac, spectrum, attenuation):
    if rows_fit_wide(density, measured):
        return per_device_wide(density, measured, shear_shift, shear_frac, spectrum, attenuation)
    if rows_fit(density, measured):
        return per_device_rows(density, measured, shear_shift, shear_frac, spectrum, attenuation)
    return per_device(density, measured, shear_shift, shear_frac, spectrum, attenuation)


def solution(mesh):
    in_specs = (
        P(None, None, "depth", "lat"),
        P("views", None, "lat"),
        P("views", "depth"),
        P("views", "depth"),
        P(),
        P(),
    )
    out_specs = P("views", None, "depth", "lat")
    return jax.shard_map(
        per_device_any, mesh=mesh, in_specs=in_specs, out_specs=out_specs, check_vma=False
    )
```

```python
import functools
import jax
import jax.numpy as jnp
from jax import lax
from jax.sharding import PartitionSpec as P
from jax.experimental import pallas as pl
from jax.experimental.pallas import tpu as pltpu

HALO = 64


def with_halo(x, sides, width):
    for axis, dim in sides:
        size, length = (lax.axis_size(axis), x.shape[dim])
        up = [(i, (i + 1) % size) for i in range(size - 1)]
        down = [(j, i) for i, j in up]
        last = lax.slice_in_dim(x, length - width, length, axis=dim)
        first = lax.slice_in_dim(x, 0, width, axis=dim)
        before = lax.ppermute(last, axis, up)
        after = lax.ppermute(first, axis, down)
        x = jnp.concatenate([before, x, after], axis=dim)
    return x


def exchange(x, axis):
    count = lax.axis_size(axis)
    me = lax.axis_index(axis)
    result = x
    for step in range(1, count):
        pairs = [(i, (i + step) % count) for i in range(count)]
        part = lax.dynamic_index_in_dim(x, (me + step) % count, 0, keepdims=True)
        part = lax.ppermute(part, axis, pairs)
        result = lax.dynamic_update_index_in_dim(result, part, (me - step) % count, 0)
    return result


def band_forward(shear_shift, lower_weight, upper_weight, window, block_width):
    band_shape = (shear_shift.shape[1], window, shear_shift.shape[0], block_width)
    tap_index = lax.broadcasted_iota(jnp.int32, band_shape, 1)
    column = lax.broadcasted_iota(jnp.int32, band_shape, 3)
    anchor = (shear_shift.T + HALO)[:, None, :, None]
    nothing = jnp.zeros((), jnp.bfloat16)
    lower_part = jnp.where(tap_index == column + anchor, lower_weight.T[:, None, :, None], nothing)
    upper_part = jnp.where(
        tap_index == column + anchor + 1, upper_weight.T[:, None, :, None], nothing
    )
    return lower_part + upper_part


def band_backward(shear_shift, lower_weight, upper_weight, window, block_width):
    band_shape = (shear_shift.shape[0], window, shear_shift.shape[1], block_width)
    tap_index = lax.broadcasted_iota(jnp.int32, band_shape, 1)
    column = lax.broadcasted_iota(jnp.int32, band_shape, 3)
    anchor = (HALO - shear_shift)[:, None, :, None]
    nothing = jnp.zeros((), jnp.bfloat16)
    lower_part = jnp.where(tap_index == column + anchor, lower_weight[:, None, :, None], nothing)
    upper_part = jnp.where(
        tap_index == column + anchor - 1, upper_weight[:, None, :, None], nothing
    )
    return lower_part + upper_part


def spectral(path_sums, observed, spectrum, attenuation, views_all):
    view_count, row_count, materials, tile_width = path_sums.shape
    block_pixels = 4096
    path_water = path_sums[:, :, 0, :].reshape(-1, block_pixels)
    path_bone = path_sums[:, :, 1, :].reshape(-1, block_pixels)
    target_flat = observed.reshape(-1, block_pixels)
    coefficients = jnp.concatenate(
        [jnp.ones((1, spectrum.shape[0]), jnp.float32), attenuation], axis=0
    )
    emitted = jnp.log(jnp.sum(spectrum))

    def one_block(inputs):
        water_block, bone_block, target_block = inputs
        exponent = (
            attenuation[0][:, None] * water_block[None, :]
            + attenuation[1][:, None] * bone_block[None, :]
        )
        counts = spectrum[:, None] * jnp.exp(-exponent)
        moments = jnp.dot(coefficients, counts, precision=lax.Precision.HIGHEST)
        intensity = moments[0]
        residual = emitted - jnp.log(intensity) - target_block
        factor = residual / intensity / views_all
        return (moments[1:] * factor[None, :]).astype(jnp.bfloat16)

    stacked = lax.map(one_block, (path_water, path_bone, target_flat))
    gradients = jnp.swapaxes(stacked, 0, 1).reshape(materials, view_count, row_count, tile_width)
    return jnp.transpose(gradients, (1, 2, 0, 3))


def spectral_kernel(views_all, emitted_ref, spectrum_ref, attenuation_ref, water_ref, bone_ref, target_ref, out0_ref, out1_ref):
    rows, width = water_ref.shape
    energies = spectrum_ref.shape[0]
    block = 8

    def one_block(b, carry):
        lo = pl.multiple_of(b * block, block)
        water = water_ref[pl.ds(lo, block), :]
        bone = bone_ref[pl.ds(lo, block), :]

        def one_energy(e, sums):
            intensity, first, second = sums
            a0 = attenuation_ref[0, e]
            a1 = attenuation_ref[1, e]
            counts = spectrum_ref[e] * jnp.exp(-(a0 * water + a1 * bone))
            return (intensity + counts, first + a0 * counts, second + a1 * counts)

        zero = jnp.zeros((block, width), jnp.float32)
        intensity, first, second = lax.fori_loop(0, energies, one_energy, (zero, zero, zero), unroll=8)
        residual = emitted_ref[0] - jnp.log(intensity) - target_ref[pl.ds(lo, block), :]
        factor = residual / intensity / views_all
        out0_ref[pl.ds(lo, block), :] = (first * factor).astype(out0_ref.dtype)
        out1_ref[pl.ds(lo, block), :] = (second * factor).astype(out1_ref.dtype)
        return carry

    lax.fori_loop(0, rows // block, one_block, 0)


def spectral_pallas(path_sums, observed, spectrum, attenuation, views_all):
    view_count, row_count, materials, width_all = path_sums.shape
    pixels = view_count * row_count * width_all
    rows = pixels // LANES // 4
    water = path_sums[:, :, 0, :].reshape(rows, 4 * LANES)
    bone = path_sums[:, :, 1, :].reshape(rows, 4 * LANES)
    target = observed.reshape(rows, 4 * LANES)
    emitted = jnp.log(jnp.sum(spectrum)).reshape(1)
    smem = pl.BlockSpec(memory_space=pltpu.SMEM)
    vmem = pl.BlockSpec(memory_space=pltpu.VMEM)
    first, second = pl.pallas_call(
        functools.partial(spectral_kernel, views_all),
        out_shape=(
            jax.ShapeDtypeStruct((rows, 4 * LANES), jnp.bfloat16),
            jax.ShapeDtypeStruct((rows, 4 * LANES), jnp.bfloat16),
        ),
        in_specs=[smem, smem, smem, vmem, vmem, vmem],
        out_specs=(vmem, vmem),
        interpret=INTERPRET,
    )(emitted, spectrum, attenuation, water, bone, target)
    shape = (view_count, row_count, width_all)
    return jnp.stack([first.reshape(shape), second.reshape(shape)], axis=2)


def per_device(density, measured, shear_shift, shear_frac, spectrum, attenuation):
    row_total, materials, depth_here, tile_width = density.shape
    block_width = min(128, tile_width)
    block_count = tile_width // block_width
    window = block_width + 2 * HALO
    views_all = measured.shape[0] * lax.axis_size("views")
    depth_all = depth_here * lax.axis_size("depth")
    rows_out = row_total // lax.axis_size("views")
    lower_weight = (1.0 - shear_frac).astype(jnp.bfloat16)
    upper_weight = shear_frac.astype(jnp.bfloat16)
    rows_here = density.shape[0]
    padded = with_halo(density, (("lat", 3),), HALO)
    framed = jnp.stack(
        [
            padded[:, :, :, number * block_width : number * block_width + window]
            for number in range(block_count)
        ],
        axis=2,
    )
    forward_band = band_forward(shear_shift, lower_weight, upper_weight, window, block_width)
    partial_value = jnp.einsum(
        "ymnzi,zivc->vymnc", framed, forward_band, preferred_element_type=jnp.float32
    )
    partial_value = partial_value.reshape(shear_shift.shape[0], rows_here, materials, tile_width)
    shares = lax.psum_scatter(partial_value, "depth", scatter_dimension=3, tiled=True) / depth_all
    share_cols = shares.shape[3]
    observed = lax.dynamic_slice_in_dim(
        measured, lax.axis_index("depth") * share_cols, share_cols, 2
    )
    share_grads = spectral(shares, observed, spectrum, attenuation, views_all)
    path_grads = lax.all_gather(share_grads, "depth", axis=3, tiled=True)
    padded_grads = with_halo(path_grads, (("lat", 3),), HALO)
    framed_grads = jnp.stack(
        [
            padded_grads[:, :, :, number * block_width : number * block_width + window]
            for number in range(block_count)
        ],
        axis=3,
    )
    backward_band = band_backward(shear_shift, lower_weight, upper_weight, window, block_width)
    product = jnp.einsum(
        "vymni,vizc->ymznc", framed_grads, backward_band, preferred_element_type=jnp.float32
    )
    return lax.psum_scatter(
        product.reshape(rows_out * lax.axis_size("views"), materials, depth_here, tile_width),
        "views",
        scatter_dimension=0,
        tiled=True,
    )


LANES = 128
INTERPRET = False


def shear_kernel(rot_ref, thr_ref, wa_ref, wb_ref, src_ref, out_ref):
    outer_count, channels, width = src_ref.shape
    inner_count, _, out_width = out_ref.shape
    pieces = width // LANES
    out_pieces = out_width // LANES
    out_ref[...] = jnp.zeros(out_ref.shape, jnp.float32)
    lane = lax.broadcasted_iota(jnp.int32, (channels, LANES), 1)

    def outer(o, carry):
        cols = [src_ref[o, :, k * LANES : (k + 1) * LANES] for k in range(pieces)]
        turned = [pltpu.roll(c, LANES - 1, 1) for c in cols]
        nexts = [
            jnp.where(lane < LANES - 1, turned[k], turned[k + 1]) for k in range(pieces - 1)
        ] + [turned[pieces - 1]]
        for i in range(inner_count):
            wa = wa_ref[o, i]
            wb = wb_ref[o, i]
            mixed = [wa * cols[k] + wb * nexts[k] for k in range(pieces)]
            rolled = [pltpu.roll(m, rot_ref[o, i], 1) for m in mixed]
            keep = lane < thr_ref[o, i]
            for j in range(out_pieces):
                out_ref[i, :, j * LANES : (j + 1) * LANES] += jnp.where(
                    keep, rolled[j], rolled[j + 1]
                )
        return carry

    lax.fori_loop(0, outer_count, outer, 0)


def shear_table_kernel(forward, tab_ref, src_ref, out_ref):
    outer_count, channels, width = src_ref.shape
    inner_count, _, out_width = out_ref.shape
    pieces = width // LANES
    out_pieces = out_width // LANES
    out_ref[...] = jnp.zeros(out_ref.shape, jnp.float32)
    lane = lax.broadcasted_iota(jnp.int32, (channels, LANES), 1)

    def outer(o, carry):
        cols = [src_ref[o, :, k * LANES : (k + 1) * LANES] for k in range(pieces)]
        turned = [pltpu.roll(c, LANES - 1, 1) for c in cols]
        nexts = [
            jnp.where(lane < LANES - 1, turned[k], turned[k + 1]) for k in range(pieces - 1)
        ] + [turned[pieces - 1]]
        for i in range(inner_count):
            if forward:
                shift = tab_ref[0, i, o].astype(jnp.int32)
                wa = tab_ref[1, i, o]
                wb = tab_ref[2, i, o]
                offset = shift + HALO
            else:
                shift = tab_ref[0, o, i].astype(jnp.int32)
                wa = tab_ref[2, o, i]
                wb = tab_ref[1, o, i]
                offset = HALO - 1 - shift
            limit = LANES - offset
            amount = jnp.where(limit == LANES, 0, limit)
            mixed = [wa * cols[k] + wb * nexts[k] for k in range(pieces)]
            rolled = [pltpu.roll(m, amount, 1) for m in mixed]
            keep = lane < limit
            for j in range(out_pieces):
                out_ref[i, :, j * LANES : (j + 1) * LANES] += jnp.where(
                    keep, rolled[j], rolled[j + 1]
                )
        return carry

    lax.fori_loop(0, outer_count, outer, 0)


def shear_table(forward, table, src, inner_count, out_width):
    _, channels, _ = src.shape
    smem = pl.BlockSpec(memory_space=pltpu.SMEM)
    vmem = pl.BlockSpec(memory_space=pltpu.VMEM)
    return pl.pallas_call(
        functools.partial(shear_table_kernel, forward),
        out_shape=jax.ShapeDtypeStruct((inner_count, channels, out_width), jnp.float32),
        in_specs=[smem, vmem],
        out_specs=vmem,
        interpret=INTERPRET,
    )(table, src)


def halo_columns(ys, lane, half_of, rows_here, halves, channels):
    count = len(ys)
    turned = [pltpu.roll(y, HALO, 1) for y in ys]
    zero = jnp.zeros_like(ys[0])
    left = jnp.where(half_of >= 1, pltpu.roll(turned[count - 1], rows_here, 0), zero)
    right = jnp.where(half_of <= halves - 2, pltpu.roll(turned[0], channels - rows_here, 0), zero)
    edge = lane < HALO
    cols = [jnp.where(edge, left, turned[0])]
    cols += [jnp.where(edge, turned[k - 1], turned[k]) for k in range(1, count)]
    cols += [jnp.where(edge, turned[count - 1], right)]
    return cols


def shear_pass(forward, rows_here, halves, tab_ref, src_ref, acc_ref, cols_ref, nexts_ref):
    outer_count, channels, width = src_ref.shape
    inner_count = acc_ref.shape[0]
    pieces = width // LANES
    lane = lax.broadcasted_iota(jnp.int32, (channels, LANES), 1)
    half_of = (lax.broadcasted_iota(jnp.int32, (channels, LANES), 0) // rows_here) % halves

    def prepare(o, carry):
        ys = [src_ref[o, :, k * LANES : (k + 1) * LANES] for k in range(pieces)]
        cols = halo_columns(ys, lane, half_of, rows_here, halves, channels)
        turned = [pltpu.roll(c, LANES - 1, 1) for c in cols]
        nexts = [jnp.where(lane < LANES - 1, turned[k], turned[k + 1]) for k in range(pieces)]
        nexts.append(turned[pieces])
        for k in range(pieces + 1):
            cols_ref[o, :, k * LANES : (k + 1) * LANES] = cols[k]
            nexts_ref[o, :, k * LANES : (k + 1) * LANES] = nexts[k]
        return carry

    lax.fori_loop(0, outer_count, prepare, 0)

    for i in range(inner_count):

        def one_input(o, acc):
            if forward:
                shift = tab_ref[0, i, o].astype(jnp.int32)
                wa = tab_ref[1, i, o]
                wb = tab_ref[2, i, o]
                offset = shift + HALO
            else:
                shift = tab_ref[0, o, i].astype(jnp.int32)
                wa = tab_ref[2, o, i]
                wb = tab_ref[1, o, i]
                offset = HALO - 1 - shift
            limit = LANES - offset
            amount = jnp.where(limit == LANES, 0, limit)
            mixed = [
                wa * cols_ref[o, :, k * LANES : (k + 1) * LANES]
                + wb * nexts_ref[o, :, k * LANES : (k + 1) * LANES]
                for k in range(pieces + 1)
            ]
            rolled = [pltpu.roll(m, amount, 1) for m in mixed]
            keep = lane < limit
            return tuple(acc[j] + jnp.where(keep, rolled[j], rolled[j + 1]) for j in range(pieces))

        zero = jnp.zeros((channels, LANES), jnp.float32)
        acc = lax.fori_loop(0, outer_count, one_input, tuple(zero for _ in range(pieces)), unroll=True)
        for j in range(pieces):
            acc_ref[i, :, j * LANES : (j + 1) * LANES] = acc[j]


def scatter_pass(rows_here, halves, tab_ref, src_ref, out_ref, cols_ref, nexts_ref):
    outer_count, channels, width = src_ref.shape
    _, depth_here, _ = out_ref.shape
    materials = channels // (halves * rows_here)
    pieces = width // LANES
    lane = lax.broadcasted_iota(jnp.int32, (channels, LANES), 1)
    half_of = (lax.broadcasted_iota(jnp.int32, (channels, LANES), 0) // rows_here) % halves

    def prepare(o, carry):
        ys = [src_ref[o, :, k * LANES : (k + 1) * LANES] for k in range(pieces)]
        cols = halo_columns(ys, lane, half_of, rows_here, halves, channels)
        turned = [pltpu.roll(c, LANES - 1, 1) for c in cols]
        nexts = [jnp.where(lane < LANES - 1, turned[k], turned[k + 1]) for k in range(pieces)]
        nexts.append(turned[pieces])
        for k in range(pieces + 1):
            cols_ref[o, :, k * LANES : (k + 1) * LANES] = cols[k]
            nexts_ref[o, :, k * LANES : (k + 1) * LANES] = nexts[k]
        return carry

    lax.fori_loop(0, outer_count, prepare, 0)
    inner_count = tab_ref.shape[2]

    for i in range(inner_count):
        slab, level = divmod(i, depth_here)

        def one_view(o, acc):
            shift = tab_ref[0, o, i].astype(jnp.int32)
            wa = tab_ref[2, o, i]
            wb = tab_ref[1, o, i]
            offset = HALO - 1 - shift
            limit = LANES - offset
            amount = jnp.where(limit == LANES, 0, limit)
            mixed = [
                wa * cols_ref[o, :, k * LANES : (k + 1) * LANES]
                + wb * nexts_ref[o, :, k * LANES : (k + 1) * LANES]
                for k in range(pieces + 1)
            ]
            rolled = [pltpu.roll(m, amount, 1) for m in mixed]
            keep = lane < limit
            return tuple(acc[j] + jnp.where(keep, rolled[j], rolled[j + 1]) for j in range(pieces))

        zero = jnp.zeros((channels, LANES), jnp.float32)
        acc = lax.fori_loop(0, outer_count, one_view, tuple(zero for _ in range(pieces)), unroll=True)
        value = jnp.concatenate(acc, axis=1)
        for c in range(channels):
            material, rest = divmod(c, halves * rows_here)
            half, row = divmod(rest, rows_here)
            target = ((slab * halves + half) * rows_here + row) * materials + material
            out_ref[target, level : level + 1, :] = value[c : c + 1, :]


def forward_kernel(rows_here, halves, depth_all, views_all, tab_ref, emitted_ref, spectrum_ref,
                   attenuation_ref, src_ref, target_ref, out_ref, sums_ref, cols_ref, nexts_ref):
    shear_pass(True, rows_here, halves, tab_ref, src_ref, sums_ref, cols_ref, nexts_ref)
    _, channels, width = sums_ref.shape
    energies = spectrum_ref.shape[0]
    split = channels // 2
    low = lax.broadcasted_iota(jnp.int32, (channels, width), 0) < split

    def one_pair(p, carry):
        first_view = sums_ref[2 * p] / depth_all
        second_view = sums_ref[2 * p + 1] / depth_all
        water = jnp.where(low, first_view, pltpu.roll(second_view, split, 0))
        bone = jnp.where(low, pltpu.roll(first_view, split, 0), second_view)

        def one_energy(e, sums):
            intensity, first, second = sums
            a0 = attenuation_ref[0, e]
            a1 = attenuation_ref[1, e]
            counts = spectrum_ref[e] * jnp.exp(-(a0 * water + a1 * bone))
            return (intensity + counts, first + a0 * counts, second + a1 * counts)

        zero = jnp.zeros((channels, width), jnp.float32)
        intensity, first, second = lax.fori_loop(0, energies, one_energy, (zero, zero, zero), unroll=True)
        residual = emitted_ref[0] - jnp.log(intensity) - target_ref[p]
        factor = residual / intensity / views_all
        first = (first * factor).astype(jnp.bfloat16).astype(jnp.float32)
        second = (second * factor).astype(jnp.bfloat16).astype(jnp.float32)
        out_ref[2 * p] = jnp.where(low, first, pltpu.roll(second, split, 0))
        out_ref[2 * p + 1] = jnp.where(low, pltpu.roll(first, split, 0), second)
        return carry

    lax.fori_loop(0, out_ref.shape[0] // 2, one_pair, 0)


def backward_kernel(rows_here, halves, tab_ref, src_ref, out_ref, cols_ref, nexts_ref):
    scatter_pass(rows_here, halves, tab_ref, src_ref, out_ref, cols_ref, nexts_ref)


def shear_apply(offset, wa, wb, src, out_width):
    outer_count, channels, width = src.shape
    inner_count = offset.shape[1]
    rot = (LANES - offset) % LANES
    thr = LANES - offset
    smem = pl.BlockSpec(memory_space=pltpu.SMEM)
    vmem = pl.BlockSpec(memory_space=pltpu.VMEM)
    return pl.pallas_call(
        shear_kernel,
        out_shape=jax.ShapeDtypeStruct((inner_count, channels, out_width), jnp.float32),
        in_specs=[smem, smem, smem, smem, vmem],
        out_specs=vmem,
        interpret=INTERPRET,
    )(rot.astype(jnp.int32), thr.astype(jnp.int32), wa, wb, src)


def rows_fit(density, measured):
    rows = density.shape[0]
    groups = lax.axis_size("views")
    depth = lax.axis_size("depth")
    tile_width = density.shape[3]
    return (
        rows % groups == 0
        and (rows // groups) % depth == 0
        and tile_width % LANES == 0
        and 2 * HALO == LANES
        and density.shape[1] == 2
        and measured.shape[0] * groups % 2 == 0
        and tile_width >= 3 * measured.shape[0] * density.shape[2] * groups
    )


def per_device_rows(density, measured, shear_shift, shear_frac, spectrum, attenuation):
    row_total, materials, depth_here, tile_width = density.shape
    groups = lax.axis_size("views")
    depth_count = lax.axis_size("depth")
    views_here = measured.shape[0]
    views_all = views_here * groups
    depth_all = depth_here * depth_count
    rows_group = row_total // groups
    rows_here = rows_group // depth_count
    group = lax.axis_index("views")
    slab = lax.axis_index("depth")

    lower_weight = (1.0 - shear_frac).astype(jnp.bfloat16).astype(jnp.float32)
    upper_weight = shear_frac.astype(jnp.bfloat16).astype(jnp.float32)
    table = jnp.stack([shear_shift.astype(jnp.float32), lower_weight, upper_weight])
    entries = table.size
    observed = measured.reshape(views_here, groups, rows_group, tile_width)
    observed = lax.dynamic_slice_in_dim(observed, slab * rows_here, rows_here, 2)
    observed = jnp.transpose(observed, (1, 0, 2, 3)).reshape(groups, views_here * rows_here, tile_width)
    extra = jnp.pad(table.reshape(1, entries), ((0, 0), (0, tile_width - entries)))
    extra = jnp.broadcast_to(extra[None], (groups, 1, tile_width))
    observed = jnp.concatenate([observed, extra], axis=1)
    observed = lax.all_to_all(observed, "views", 0, 0, tiled=True)
    table = observed[:, views_here * rows_here, :entries].reshape(groups, 3, views_here, depth_here)
    table = jnp.transpose(table, (1, 0, 2, 3)).reshape(3, views_all, depth_here)
    observed = observed[:, : views_here * rows_here].reshape(views_all, rows_here, tile_width)

    channels = rows_here * materials
    mine = lax.dynamic_slice_in_dim(density, group * rows_group, rows_group, 0)
    mine = mine.reshape(depth_count, rows_here, materials, depth_here, tile_width)
    mine = jnp.transpose(mine, (0, 3, 1, 2, 4)).reshape(depth_count, depth_here * channels, tile_width)
    wide = table.size
    extra = jnp.pad(table.reshape(1, wide), ((0, 0), (0, tile_width - wide))).astype(jnp.bfloat16)
    extra = jnp.broadcast_to(extra[None], (depth_count, 1, tile_width))
    mine = jnp.concatenate([mine, extra], axis=1)
    mine = lax.all_to_all(mine, "depth", 0, 0, tiled=True)
    table = mine[:, depth_here * channels, :wide].astype(jnp.float32)
    table = table.reshape(depth_count, 3, views_all, depth_here)
    table = jnp.transpose(table, (1, 2, 0, 3)).reshape(3, views_all, depth_all)
    shift_all = table[0].astype(jnp.int32)
    lower_all = table[1]
    upper_all = table[2]
    mine = mine[:, : depth_here * channels].reshape(depth_all, channels, tile_width)
    padded = with_halo(mine, (("lat", 2),), HALO).astype(jnp.float32)

    sums = shear_apply(
        (shift_all + HALO).T, lower_all.T, upper_all.T, padded, tile_width
    )
    sums = (sums / depth_all).reshape(views_all, rows_here, materials, tile_width)
    grads = spectral(sums, observed, spectrum, attenuation, views_all)
    grads = grads.reshape(views_all, rows_here * materials, tile_width)
    padded_grads = with_halo(grads, (("lat", 2),), HALO).astype(jnp.float32)
    layers = shear_apply(
        HALO - 1 - shift_all, upper_all, lower_all, padded_grads, tile_width
    )
    layers = layers.reshape(depth_count, depth_here, rows_here, materials, tile_width)
    layers = exchange(layers, "depth")
    return jnp.transpose(layers, (0, 2, 3, 1, 4)).reshape(rows_group, materials, depth_here, tile_width)


def rows_fit_wide(density, measured):
    rows = density.shape[0]
    groups = lax.axis_size("views")
    parts = lax.axis_size("depth") * lax.axis_size("lat")
    tile_width = density.shape[3]
    return (
        rows % groups == 0
        and (rows // groups) % parts == 0
        and tile_width % LANES == 0
        and 2 * HALO == LANES
        and density.shape[1] == 2
        and measured.shape[0] * groups % 2 == 0
        and tile_width >= 3 * measured.shape[0] * density.shape[2]
        and ((rows // groups // parts) * density.shape[1] * density.shape[2]) % groups == 0
    )


def stack_halves(values, halves, tile_width):
    count, rows, materials, _ = values.shape
    padded = jnp.pad(values, ((0, 0), (0, 0), (0, 0), (HALO, HALO)))
    parts = [
        padded[..., h * tile_width : h * tile_width + tile_width + 2 * HALO] for h in range(halves)
    ]
    return jnp.stack(parts, axis=1).reshape(count, halves * rows * materials, tile_width + 2 * HALO)


def join_halves(values, halves, rows, materials):
    count, _, tile_width = values.shape
    values = values.reshape(count, halves, rows, materials, tile_width)
    return jnp.transpose(values, (0, 2, 3, 1, 4)).reshape(count, rows, materials, halves * tile_width)


def per_device_wide(density, measured, shear_shift, shear_frac, spectrum, attenuation):
    row_total, materials, depth_here, tile_width = density.shape
    groups = lax.axis_size("views")
    depth_count = lax.axis_size("depth")
    halves = lax.axis_size("lat")
    parts = depth_count * halves
    views_here = measured.shape[0]
    views_all = views_here * groups
    depth_all = depth_here * depth_count
    rows_group = row_total // groups
    rows_here = rows_group // parts
    group = lax.axis_index("views")
    slab = lax.axis_index("depth")
    half = lax.axis_index("lat")

    lower_weight = (1.0 - shear_frac).astype(jnp.bfloat16).astype(jnp.float32)
    upper_weight = shear_frac.astype(jnp.bfloat16).astype(jnp.float32)
    block = jnp.stack([shear_shift.astype(jnp.float32), lower_weight, upper_weight])
    entries = block.size
    observed = measured.reshape(views_here, groups, depth_count, halves, rows_here, tile_width)
    observed = lax.dynamic_index_in_dim(observed, slab, 2, keepdims=False)
    observed = jnp.transpose(observed, (1, 2, 0, 3, 4)).reshape(
        groups * halves, views_here * rows_here, tile_width
    )
    observed = lax.all_to_all(observed, ("views", "lat"), 0, 0, tiled=True)
    observed = observed.reshape(groups, halves, views_here, rows_here, tile_width)
    observed = jnp.transpose(observed, (0, 2, 3, 1, 4)).reshape(views_all, rows_here, halves * tile_width)

    chunk = rows_here * materials * depth_here * tile_width
    piece = chunk // groups
    mine = density.reshape(groups * parts, groups, piece)
    mine = lax.dynamic_index_in_dim(mine, group, 1, keepdims=False)
    mine = mine.reshape(groups * parts, piece // tile_width, tile_width)
    extra = jnp.pad(block.reshape(1, entries), ((0, 0), (0, tile_width - entries))).astype(jnp.bfloat16)
    extra = jnp.broadcast_to(extra[None], (groups * parts, 1, tile_width))
    mine = jnp.concatenate([mine, extra], axis=1)
    mine = lax.all_to_all(mine, ("views", "depth", "lat"), 0, 0, tiled=True)
    mine = mine.reshape(groups, depth_count, halves, piece // tile_width + 1, tile_width)
    table = mine[:, :, 0, piece // tile_width, :entries].astype(jnp.float32)
    table = table.reshape(groups, depth_count, 3, views_here, depth_here)
    table = jnp.transpose(table, (2, 0, 3, 1, 4)).reshape(3, views_all, depth_all)
    mine = mine[:, :, :, : piece // tile_width].reshape(groups, depth_count, halves, piece)
    mine = jnp.transpose(mine, (1, 2, 0, 3)).reshape(
        depth_count, halves, rows_here, materials, depth_here, tile_width
    )
    channels = materials * halves * rows_here
    mine = jnp.transpose(mine, (0, 4, 3, 1, 2, 5)).reshape(depth_all, channels, tile_width)
    mine = mine.astype(jnp.float32)
    target = observed.reshape(views_all // 2, 2, rows_here, halves, tile_width)
    target = jnp.transpose(target, (0, 1, 3, 2, 4)).reshape(views_all // 2, 2 * halves * rows_here, tile_width)
    emitted = jnp.log(jnp.sum(spectrum)).reshape(1)
    smem = pl.BlockSpec(memory_space=pltpu.SMEM)
    vmem = pl.BlockSpec(memory_space=pltpu.VMEM)
    grads = pl.pallas_call(
        functools.partial(forward_kernel, rows_here, halves, depth_all, views_all),
        out_shape=jax.ShapeDtypeStruct((views_all, channels, tile_width), jnp.float32),
        in_specs=[smem, smem, smem, smem, vmem, vmem],
        out_specs=vmem,
        scratch_shapes=[
            pltpu.VMEM((views_all, channels, tile_width), jnp.float32),
            pltpu.VMEM((depth_all, channels, tile_width + LANES), jnp.float32),
            pltpu.VMEM((depth_all, channels, tile_width + LANES), jnp.float32),
        ],
        interpret=INTERPRET,
    )(table, emitted, spectrum, attenuation, mine, target)
    layers = pl.pallas_call(
        functools.partial(backward_kernel, rows_here, halves),
        out_shape=jax.ShapeDtypeStruct((parts * rows_here * materials, depth_here, tile_width), jnp.float32),
        in_specs=[smem, vmem],
        out_specs=vmem,
        scratch_shapes=[
            pltpu.VMEM((views_all, channels, tile_width + LANES), jnp.float32),
            pltpu.VMEM((views_all, channels, tile_width + LANES), jnp.float32),
        ],
        interpret=INTERPRET,
    )(table, grads)
    layers = layers.reshape(parts, rows_here, materials, depth_here, tile_width)
    layers = lax.all_to_all(layers, ("depth", "lat"), 0, 0, tiled=True)
    return layers.reshape(rows_group, materials, depth_here, tile_width)


def per_device_any(density, measured, shear_shift, shear_frac, spectrum, attenuation):
    if rows_fit_wide(density, measured):
        return per_device_wide(density, measured, shear_shift, shear_frac, spectrum, attenuation)
    if rows_fit(density, measured):
        return per_device_rows(density, measured, shear_shift, shear_frac, spectrum, attenuation)
    return per_device(density, measured, shear_shift, shear_frac, spectrum, attenuation)


def solution(mesh):
    in_specs = (
        P(None, None, "depth", "lat"),
        P("views", None, "lat"),
        P("views", "depth"),
        P("views", "depth"),
        P(),
        P(),
    )
    out_specs = P("views", None, "depth", "lat")
    return jax.shard_map(
        per_device_any, mesh=mesh, in_specs=in_specs, out_specs=out_specs, check_vma=False
    )
```

```python
import functools
import jax
import jax.numpy as jnp
from jax import lax
from jax.sharding import PartitionSpec as P
from jax.experimental import pallas as pl
from jax.experimental.pallas import tpu as pltpu

HALO = 64


def with_halo(x, sides, width):
    for axis, dim in sides:
        size, length = (lax.axis_size(axis), x.shape[dim])
        up = [(i, (i + 1) % size) for i in range(size - 1)]
        down = [(j, i) for i, j in up]
        last = lax.slice_in_dim(x, length - width, length, axis=dim)
        first = lax.slice_in_dim(x, 0, width, axis=dim)
        before = lax.ppermute(last, axis, up)
        after = lax.ppermute(first, axis, down)
        x = jnp.concatenate([before, x, after], axis=dim)
    return x


def exchange(x, axis):
    count = lax.axis_size(axis)
    me = lax.axis_index(axis)
    result = x
    for step in range(1, count):
        pairs = [(i, (i + step) % count) for i in range(count)]
        part = lax.dynamic_index_in_dim(x, (me + step) % count, 0, keepdims=True)
        part = lax.ppermute(part, axis, pairs)
        result = lax.dynamic_update_index_in_dim(result, part, (me - step) % count, 0)
    return result


def band_forward(shear_shift, lower_weight, upper_weight, window, block_width):
    band_shape = (shear_shift.shape[1], window, shear_shift.shape[0], block_width)
    tap_index = lax.broadcasted_iota(jnp.int32, band_shape, 1)
    column = lax.broadcasted_iota(jnp.int32, band_shape, 3)
    anchor = (shear_shift.T + HALO)[:, None, :, None]
    nothing = jnp.zeros((), jnp.bfloat16)
    lower_part = jnp.where(tap_index == column + anchor, lower_weight.T[:, None, :, None], nothing)
    upper_part = jnp.where(
        tap_index == column + anchor + 1, upper_weight.T[:, None, :, None], nothing
    )
    return lower_part + upper_part


def band_backward(shear_shift, lower_weight, upper_weight, window, block_width):
    band_shape = (shear_shift.shape[0], window, shear_shift.shape[1], block_width)
    tap_index = lax.broadcasted_iota(jnp.int32, band_shape, 1)
    column = lax.broadcasted_iota(jnp.int32, band_shape, 3)
    anchor = (HALO - shear_shift)[:, None, :, None]
    nothing = jnp.zeros((), jnp.bfloat16)
    lower_part = jnp.where(tap_index == column + anchor, lower_weight[:, None, :, None], nothing)
    upper_part = jnp.where(
        tap_index == column + anchor - 1, upper_weight[:, None, :, None], nothing
    )
    return lower_part + upper_part


def spectral(path_sums, observed, spectrum, attenuation, views_all):
    view_count, row_count, materials, tile_width = path_sums.shape
    block_pixels = 4096
    path_water = path_sums[:, :, 0, :].reshape(-1, block_pixels)
    path_bone = path_sums[:, :, 1, :].reshape(-1, block_pixels)
    target_flat = observed.reshape(-1, block_pixels)
    coefficients = jnp.concatenate(
        [jnp.ones((1, spectrum.shape[0]), jnp.float32), attenuation], axis=0
    )
    emitted = jnp.log(jnp.sum(spectrum))

    def one_block(inputs):
        water_block, bone_block, target_block = inputs
        exponent = (
            attenuation[0][:, None] * water_block[None, :]
            + attenuation[1][:, None] * bone_block[None, :]
        )
        counts = spectrum[:, None] * jnp.exp(-exponent)
        moments = jnp.dot(coefficients, counts, precision=lax.Precision.HIGHEST)
        intensity = moments[0]
        residual = emitted - jnp.log(intensity) - target_block
        factor = residual / intensity / views_all
        return (moments[1:] * factor[None, :]).astype(jnp.bfloat16)

    stacked = lax.map(one_block, (path_water, path_bone, target_flat))
    gradients = jnp.swapaxes(stacked, 0, 1).reshape(materials, view_count, row_count, tile_width)
    return jnp.transpose(gradients, (1, 2, 0, 3))


def spectral_kernel(views_all, emitted_ref, spectrum_ref, attenuation_ref, water_ref, bone_ref, target_ref, out0_ref, out1_ref):
    rows, width = water_ref.shape
    energies = spectrum_ref.shape[0]
    block = 8

    def one_block(b, carry):
        lo = pl.multiple_of(b * block, block)
        water = water_ref[pl.ds(lo, block), :]
        bone = bone_ref[pl.ds(lo, block), :]

        def one_energy(e, sums):
            intensity, first, second = sums
            a0 = attenuation_ref[0, e]
            a1 = attenuation_ref[1, e]
            counts = spectrum_ref[e] * jnp.exp(-(a0 * water + a1 * bone))
            return (intensity + counts, first + a0 * counts, second + a1 * counts)

        zero = jnp.zeros((block, width), jnp.float32)
        intensity, first, second = lax.fori_loop(0, energies, one_energy, (zero, zero, zero), unroll=8)
        residual = emitted_ref[0] - jnp.log(intensity) - target_ref[pl.ds(lo, block), :]
        factor = residual / intensity / views_all
        out0_ref[pl.ds(lo, block), :] = (first * factor).astype(out0_ref.dtype)
        out1_ref[pl.ds(lo, block), :] = (second * factor).astype(out1_ref.dtype)
        return carry

    lax.fori_loop(0, rows // block, one_block, 0)


def spectral_pallas(path_sums, observed, spectrum, attenuation, views_all):
    view_count, row_count, materials, width_all = path_sums.shape
    pixels = view_count * row_count * width_all
    rows = pixels // LANES // 4
    water = path_sums[:, :, 0, :].reshape(rows, 4 * LANES)
    bone = path_sums[:, :, 1, :].reshape(rows, 4 * LANES)
    target = observed.reshape(rows, 4 * LANES)
    emitted = jnp.log(jnp.sum(spectrum)).reshape(1)
    smem = pl.BlockSpec(memory_space=pltpu.SMEM)
    vmem = pl.BlockSpec(memory_space=pltpu.VMEM)
    first, second = pl.pallas_call(
        functools.partial(spectral_kernel, views_all),
        out_shape=(
            jax.ShapeDtypeStruct((rows, 4 * LANES), jnp.bfloat16),
            jax.ShapeDtypeStruct((rows, 4 * LANES), jnp.bfloat16),
        ),
        in_specs=[smem, smem, smem, vmem, vmem, vmem],
        out_specs=(vmem, vmem),
        interpret=INTERPRET,
    )(emitted, spectrum, attenuation, water, bone, target)
    shape = (view_count, row_count, width_all)
    return jnp.stack([first.reshape(shape), second.reshape(shape)], axis=2)


def per_device(density, measured, shear_shift, shear_frac, spectrum, attenuation):
    row_total, materials, depth_here, tile_width = density.shape
    block_width = min(128, tile_width)
    block_count = tile_width // block_width
    window = block_width + 2 * HALO
    views_all = measured.shape[0] * lax.axis_size("views")
    depth_all = depth_here * lax.axis_size("depth")
    rows_out = row_total // lax.axis_size("views")
    lower_weight = (1.0 - shear_frac).astype(jnp.bfloat16)
    upper_weight = shear_frac.astype(jnp.bfloat16)
    rows_here = density.shape[0]
    padded = with_halo(density, (("lat", 3),), HALO)
    framed = jnp.stack(
        [
            padded[:, :, :, number * block_width : number * block_width + window]
            for number in range(block_count)
        ],
        axis=2,
    )
    forward_band = band_forward(shear_shift, lower_weight, upper_weight, window, block_width)
    partial_value = jnp.einsum(
        "ymnzi,zivc->vymnc", framed, forward_band, preferred_element_type=jnp.float32
    )
    partial_value = partial_value.reshape(shear_shift.shape[0], rows_here, materials, tile_width)
    shares = lax.psum_scatter(partial_value, "depth", scatter_dimension=3, tiled=True) / depth_all
    share_cols = shares.shape[3]
    observed = lax.dynamic_slice_in_dim(
        measured, lax.axis_index("depth") * share_cols, share_cols, 2
    )
    share_grads = spectral(shares, observed, spectrum, attenuation, views_all)
    path_grads = lax.all_gather(share_grads, "depth", axis=3, tiled=True)
    padded_grads = with_halo(path_grads, (("lat", 3),), HALO)
    framed_grads = jnp.stack(
        [
            padded_grads[:, :, :, number * block_width : number * block_width + window]
            for number in range(block_count)
        ],
        axis=3,
    )
    backward_band = band_backward(shear_shift, lower_weight, upper_weight, window, block_width)
    product = jnp.einsum(
        "vymni,vizc->ymznc", framed_grads, backward_band, preferred_element_type=jnp.float32
    )
    return lax.psum_scatter(
        product.reshape(rows_out * lax.axis_size("views"), materials, depth_here, tile_width),
        "views",
        scatter_dimension=0,
        tiled=True,
    )


LANES = 128
INTERPRET = False


def shear_kernel(rot_ref, thr_ref, wa_ref, wb_ref, src_ref, out_ref):
    outer_count, channels, width = src_ref.shape
    inner_count, _, out_width = out_ref.shape
    pieces = width // LANES
    out_pieces = out_width // LANES
    out_ref[...] = jnp.zeros(out_ref.shape, jnp.float32)
    lane = lax.broadcasted_iota(jnp.int32, (channels, LANES), 1)

    def outer(o, carry):
        cols = [src_ref[o, :, k * LANES : (k + 1) * LANES] for k in range(pieces)]
        turned = [pltpu.roll(c, LANES - 1, 1) for c in cols]
        nexts = [
            jnp.where(lane < LANES - 1, turned[k], turned[k + 1]) for k in range(pieces - 1)
        ] + [turned[pieces - 1]]
        for i in range(inner_count):
            wa = wa_ref[o, i]
            wb = wb_ref[o, i]
            mixed = [wa * cols[k] + wb * nexts[k] for k in range(pieces)]
            rolled = [pltpu.roll(m, rot_ref[o, i], 1) for m in mixed]
            keep = lane < thr_ref[o, i]
            for j in range(out_pieces):
                out_ref[i, :, j * LANES : (j + 1) * LANES] += jnp.where(
                    keep, rolled[j], rolled[j + 1]
                )
        return carry

    lax.fori_loop(0, outer_count, outer, 0)


def shear_table_kernel(forward, tab_ref, src_ref, out_ref):
    outer_count, channels, width = src_ref.shape
    inner_count, _, out_width = out_ref.shape
    pieces = width // LANES
    out_pieces = out_width // LANES
    out_ref[...] = jnp.zeros(out_ref.shape, jnp.float32)
    lane = lax.broadcasted_iota(jnp.int32, (channels, LANES), 1)

    def outer(o, carry):
        cols = [src_ref[o, :, k * LANES : (k + 1) * LANES] for k in range(pieces)]
        turned = [pltpu.roll(c, LANES - 1, 1) for c in cols]
        nexts = [
            jnp.where(lane < LANES - 1, turned[k], turned[k + 1]) for k in range(pieces - 1)
        ] + [turned[pieces - 1]]
        for i in range(inner_count):
            if forward:
                shift = tab_ref[0, i, o].astype(jnp.int32)
                wa = tab_ref[1, i, o]
                wb = tab_ref[2, i, o]
                offset = shift + HALO
            else:
                shift = tab_ref[0, o, i].astype(jnp.int32)
                wa = tab_ref[2, o, i]
                wb = tab_ref[1, o, i]
                offset = HALO - 1 - shift
            limit = LANES - offset
            amount = jnp.where(limit == LANES, 0, limit)
            mixed = [wa * cols[k] + wb * nexts[k] for k in range(pieces)]
            rolled = [pltpu.roll(m, amount, 1) for m in mixed]
            keep = lane < limit
            for j in range(out_pieces):
                out_ref[i, :, j * LANES : (j + 1) * LANES] += jnp.where(
                    keep, rolled[j], rolled[j + 1]
                )
        return carry

    lax.fori_loop(0, outer_count, outer, 0)


def shear_table(forward, table, src, inner_count, out_width):
    _, channels, _ = src.shape
    smem = pl.BlockSpec(memory_space=pltpu.SMEM)
    vmem = pl.BlockSpec(memory_space=pltpu.VMEM)
    return pl.pallas_call(
        functools.partial(shear_table_kernel, forward),
        out_shape=jax.ShapeDtypeStruct((inner_count, channels, out_width), jnp.float32),
        in_specs=[smem, vmem],
        out_specs=vmem,
        interpret=INTERPRET,
    )(table, src)


def halo_columns(ys, lane, half_of, rows_here, halves, channels):
    count = len(ys)
    turned = [pltpu.roll(y, HALO, 1) for y in ys]
    zero = jnp.zeros_like(ys[0])
    left = jnp.where(half_of >= 1, pltpu.roll(turned[count - 1], rows_here, 0), zero)
    right = jnp.where(half_of <= halves - 2, pltpu.roll(turned[0], channels - rows_here, 0), zero)
    edge = lane < HALO
    cols = [jnp.where(edge, left, turned[0])]
    cols += [jnp.where(edge, turned[k - 1], turned[k]) for k in range(1, count)]
    cols += [jnp.where(edge, turned[count - 1], right)]
    return cols


def shear_pass(forward, rows_here, halves, tab_ref, src_ref, acc_ref, cols_ref, nexts_ref):
    outer_count, channels, width = src_ref.shape
    inner_count = acc_ref.shape[0]
    pieces = width // LANES
    lane = lax.broadcasted_iota(jnp.int32, (channels, LANES), 1)
    half_of = (lax.broadcasted_iota(jnp.int32, (channels, LANES), 0) // rows_here) % halves

    def prepare(o, carry):
        ys = [src_ref[o, :, k * LANES : (k + 1) * LANES] for k in range(pieces)]
        cols = halo_columns(ys, lane, half_of, rows_here, halves, channels)
        turned = [pltpu.roll(c, LANES - 1, 1) for c in cols]
        nexts = [jnp.where(lane < LANES - 1, turned[k], turned[k + 1]) for k in range(pieces)]
        nexts.append(turned[pieces])
        for k in range(pieces + 1):
            cols_ref[o, :, k * LANES : (k + 1) * LANES] = cols[k]
            nexts_ref[o, :, k * LANES : (k + 1) * LANES] = nexts[k]
        return carry

    lax.fori_loop(0, outer_count, prepare, 0)

    for i in range(inner_count):

        def one_input(o, acc):
            if forward:
                shift = tab_ref[0, i, o].astype(jnp.int32)
                wa = tab_ref[1, i, o]
                wb = tab_ref[2, i, o]
                offset = shift + HALO
            else:
                shift = tab_ref[0, o, i].astype(jnp.int32)
                wa = tab_ref[2, o, i]
                wb = tab_ref[1, o, i]
                offset = HALO - 1 - shift
            limit = LANES - offset
            amount = jnp.where(limit == LANES, 0, limit)
            mixed = [
                wa * cols_ref[o, :, k * LANES : (k + 1) * LANES]
                + wb * nexts_ref[o, :, k * LANES : (k + 1) * LANES]
                for k in range(pieces + 1)
            ]
            rolled = [pltpu.roll(m, amount, 1) for m in mixed]
            keep = lane < limit
            return tuple(acc[j] + jnp.where(keep, rolled[j], rolled[j + 1]) for j in range(pieces))

        zero = jnp.zeros((channels, LANES), jnp.float32)
        acc = lax.fori_loop(0, outer_count, one_input, tuple(zero for _ in range(pieces)), unroll=True)
        for j in range(pieces):
            acc_ref[i, :, j * LANES : (j + 1) * LANES] = acc[j]


def scatter_pass(rows_here, halves, tab_ref, src_ref, out_ref, cols_ref, nexts_ref):
    outer_count, channels, width = src_ref.shape
    _, depth_here, _ = out_ref.shape
    materials = channels // (halves * rows_here)
    pieces = width // LANES
    lane = lax.broadcasted_iota(jnp.int32, (channels, LANES), 1)
    half_of = (lax.broadcasted_iota(jnp.int32, (channels, LANES), 0) // rows_here) % halves

    def prepare(o, carry):
        ys = [src_ref[o, :, k * LANES : (k + 1) * LANES] for k in range(pieces)]
        cols = halo_columns(ys, lane, half_of, rows_here, halves, channels)
        turned = [pltpu.roll(c, LANES - 1, 1) for c in cols]
        nexts = [jnp.where(lane < LANES - 1, turned[k], turned[k + 1]) for k in range(pieces)]
        nexts.append(turned[pieces])
        for k in range(pieces + 1):
            cols_ref[o, :, k * LANES : (k + 1) * LANES] = cols[k]
            nexts_ref[o, :, k * LANES : (k + 1) * LANES] = nexts[k]
        return carry

    lax.fori_loop(0, outer_count, prepare, 0)
    inner_count = tab_ref.shape[2]

    for i in range(inner_count):
        slab, level = divmod(i, depth_here)

        def one_view(o, acc):
            shift = tab_ref[0, o, i].astype(jnp.int32)
            wa = tab_ref[2, o, i]
            wb = tab_ref[1, o, i]
            offset = HALO - 1 - shift
            limit = LANES - offset
            amount = jnp.where(limit == LANES, 0, limit)
            mixed = [
                wa * cols_ref[o, :, k * LANES : (k + 1) * LANES]
                + wb * nexts_ref[o, :, k * LANES : (k + 1) * LANES]
                for k in range(pieces + 1)
            ]
            rolled = [pltpu.roll(m, amount, 1) for m in mixed]
            keep = lane < limit
            return tuple(acc[j] + jnp.where(keep, rolled[j], rolled[j + 1]) for j in range(pieces))

        zero = jnp.zeros((channels, LANES), jnp.float32)
        acc = lax.fori_loop(0, outer_count, one_view, tuple(zero for _ in range(pieces)), unroll=True)
        value = jnp.concatenate(acc, axis=1)
        for c in range(channels):
            material, rest = divmod(c, halves * rows_here)
            half, row = divmod(rest, rows_here)
            target = ((slab * halves + half) * rows_here + row) * materials + material
            out_ref[target, level : level + 1, :] = value[c : c + 1, :]


def forward_kernel(rows_here, halves, depth_all, views_all, tab_ref, emitted_ref, spectrum_ref,
                   attenuation_ref, src_ref, target_ref, out_ref, sums_ref, cols_ref, nexts_ref):
    shear_pass(True, rows_here, halves, tab_ref, src_ref, sums_ref, cols_ref, nexts_ref)
    _, channels, width = sums_ref.shape
    energies = spectrum_ref.shape[0]
    split = channels // 2
    low = lax.broadcasted_iota(jnp.int32, (channels, width), 0) < split

    def one_pair(p, carry):
        first_view = sums_ref[2 * p] / depth_all
        second_view = sums_ref[2 * p + 1] / depth_all
        water = jnp.where(low, first_view, pltpu.roll(second_view, split, 0))
        bone = jnp.where(low, pltpu.roll(first_view, split, 0), second_view)

        def one_energy(e, sums):
            intensity, first, second = sums
            a0 = attenuation_ref[0, e]
            a1 = attenuation_ref[1, e]
            counts = spectrum_ref[e] * jnp.exp((-a0) * water + (-a1) * bone)
            return (intensity + counts, first + a0 * counts, second + a1 * counts)

        zero = jnp.zeros((channels, width), jnp.float32)
        intensity, first, second = lax.fori_loop(0, energies, one_energy, (zero, zero, zero), unroll=True)
        residual = emitted_ref[0] - jnp.log(intensity) - target_ref[p]
        factor = residual / intensity / views_all
        first = (first * factor).astype(jnp.bfloat16).astype(jnp.float32)
        second = (second * factor).astype(jnp.bfloat16).astype(jnp.float32)
        out_ref[2 * p] = jnp.where(low, first, pltpu.roll(second, split, 0))
        out_ref[2 * p + 1] = jnp.where(low, pltpu.roll(first, split, 0), second)
        return carry

    lax.fori_loop(0, out_ref.shape[0] // 2, one_pair, 0)


def backward_kernel(rows_here, halves, tab_ref, src_ref, out_ref, cols_ref, nexts_ref):
    scatter_pass(rows_here, halves, tab_ref, src_ref, out_ref, cols_ref, nexts_ref)


def shear_apply(offset, wa, wb, src, out_width):
    outer_count, channels, width = src.shape
    inner_count = offset.shape[1]
    rot = (LANES - offset) % LANES
    thr = LANES - offset
    smem = pl.BlockSpec(memory_space=pltpu.SMEM)
    vmem = pl.BlockSpec(memory_space=pltpu.VMEM)
    return pl.pallas_call(
        shear_kernel,
        out_shape=jax.ShapeDtypeStruct((inner_count, channels, out_width), jnp.float32),
        in_specs=[smem, smem, smem, smem, vmem],
        out_specs=vmem,
        interpret=INTERPRET,
    )(rot.astype(jnp.int32), thr.astype(jnp.int32), wa, wb, src)


def rows_fit(density, measured):
    rows = density.shape[0]
    groups = lax.axis_size("views")
    depth = lax.axis_size("depth")
    tile_width = density.shape[3]
    return (
        rows % groups == 0
        and (rows // groups) % depth == 0
        and tile_width % LANES == 0
        and 2 * HALO == LANES
        and density.shape[1] == 2
        and measured.shape[0] * groups % 2 == 0
        and tile_width >= 3 * measured.shape[0] * density.shape[2] * groups
    )


def per_device_rows(density, measured, shear_shift, shear_frac, spectrum, attenuation):
    row_total, materials, depth_here, tile_width = density.shape
    groups = lax.axis_size("views")
    depth_count = lax.axis_size("depth")
    views_here = measured.shape[0]
    views_all = views_here * groups
    depth_all = depth_here * depth_count
    rows_group = row_total // groups
    rows_here = rows_group // depth_count
    group = lax.axis_index("views")
    slab = lax.axis_index("depth")

    lower_weight = (1.0 - shear_frac).astype(jnp.bfloat16).astype(jnp.float32)
    upper_weight = shear_frac.astype(jnp.bfloat16).astype(jnp.float32)
    table = jnp.stack([shear_shift.astype(jnp.float32), lower_weight, upper_weight])
    entries = table.size
    observed = measured.reshape(views_here, groups, rows_group, tile_width)
    observed = lax.dynamic_slice_in_dim(observed, slab * rows_here, rows_here, 2)
    observed = jnp.transpose(observed, (1, 0, 2, 3)).reshape(groups, views_here * rows_here, tile_width)
    extra = jnp.pad(table.reshape(1, entries), ((0, 0), (0, tile_width - entries)))
    extra = jnp.broadcast_to(extra[None], (groups, 1, tile_width))
    observed = jnp.concatenate([observed, extra], axis=1)
    observed = lax.all_to_all(observed, "views", 0, 0, tiled=True)
    table = observed[:, views_here * rows_here, :entries].reshape(groups, 3, views_here, depth_here)
    table = jnp.transpose(table, (1, 0, 2, 3)).reshape(3, views_all, depth_here)
    observed = observed[:, : views_here * rows_here].reshape(views_all, rows_here, tile_width)

    channels = rows_here * materials
    mine = lax.dynamic_slice_in_dim(density, group * rows_group, rows_group, 0)
    mine = mine.reshape(depth_count, rows_here, materials, depth_here, tile_width)
    mine = jnp.transpose(mine, (0, 3, 1, 2, 4)).reshape(depth_count, depth_here * channels, tile_width)
    wide = table.size
    extra = jnp.pad(table.reshape(1, wide), ((0, 0), (0, tile_width - wide))).astype(jnp.bfloat16)
    extra = jnp.broadcast_to(extra[None], (depth_count, 1, tile_width))
    mine = jnp.concatenate([mine, extra], axis=1)
    mine = lax.all_to_all(mine, "depth", 0, 0, tiled=True)
    table = mine[:, depth_here * channels, :wide].astype(jnp.float32)
    table = table.reshape(depth_count, 3, views_all, depth_here)
    table = jnp.transpose(table, (1, 2, 0, 3)).reshape(3, views_all, depth_all)
    shift_all = table[0].astype(jnp.int32)
    lower_all = table[1]
    upper_all = table[2]
    mine = mine[:, : depth_here * channels].reshape(depth_all, channels, tile_width)
    padded = with_halo(mine, (("lat", 2),), HALO).astype(jnp.float32)

    sums = shear_apply(
        (shift_all + HALO).T, lower_all.T, upper_all.T, padded, tile_width
    )
    sums = (sums / depth_all).reshape(views_all, rows_here, materials, tile_width)
    grads = spectral(sums, observed, spectrum, attenuation, views_all)
    grads = grads.reshape(views_all, rows_here * materials, tile_width)
    padded_grads = with_halo(grads, (("lat", 2),), HALO).astype(jnp.float32)
    layers = shear_apply(
        HALO - 1 - shift_all, upper_all, lower_all, padded_grads, tile_width
    )
    layers = layers.reshape(depth_count, depth_here, rows_here, materials, tile_width)
    layers = exchange(layers, "depth")
    return jnp.transpose(layers, (0, 2, 3, 1, 4)).reshape(rows_group, materials, depth_here, tile_width)


def rows_fit_wide(density, measured):
    rows = density.shape[0]
    groups = lax.axis_size("views")
    parts = lax.axis_size("depth") * lax.axis_size("lat")
    tile_width = density.shape[3]
    return (
        rows % groups == 0
        and (rows // groups) % parts == 0
        and tile_width % LANES == 0
        and 2 * HALO == LANES
        and density.shape[1] == 2
        and measured.shape[0] * groups % 2 == 0
        and tile_width >= 3 * measured.shape[0] * density.shape[2]
        and ((rows // groups // parts) * density.shape[1] * density.shape[2]) % groups == 0
    )


def stack_halves(values, halves, tile_width):
    count, rows, materials, _ = values.shape
    padded = jnp.pad(values, ((0, 0), (0, 0), (0, 0), (HALO, HALO)))
    parts = [
        padded[..., h * tile_width : h * tile_width + tile_width + 2 * HALO] for h in range(halves)
    ]
    return jnp.stack(parts, axis=1).reshape(count, halves * rows * materials, tile_width + 2 * HALO)


def join_halves(values, halves, rows, materials):
    count, _, tile_width = values.shape
    values = values.reshape(count, halves, rows, materials, tile_width)
    return jnp.transpose(values, (0, 2, 3, 1, 4)).reshape(count, rows, materials, halves * tile_width)


def per_device_wide(density, measured, shear_shift, shear_frac, spectrum, attenuation):
    row_total, materials, depth_here, tile_width = density.shape
    groups = lax.axis_size("views")
    depth_count = lax.axis_size("depth")
    halves = lax.axis_size("lat")
    parts = depth_count * halves
    views_here = measured.shape[0]
    views_all = views_here * groups
    depth_all = depth_here * depth_count
    rows_group = row_total // groups
    rows_here = rows_group // parts
    group = lax.axis_index("views")
    slab = lax.axis_index("depth")
    half = lax.axis_index("lat")

    lower_weight = (1.0 - shear_frac).astype(jnp.bfloat16).astype(jnp.float32)
    upper_weight = shear_frac.astype(jnp.bfloat16).astype(jnp.float32)
    block = jnp.stack([shear_shift.astype(jnp.float32), lower_weight, upper_weight])
    entries = block.size
    observed = measured.reshape(views_here, groups, depth_count, halves, rows_here, tile_width)
    observed = lax.dynamic_index_in_dim(observed, slab, 2, keepdims=False)
    observed = jnp.transpose(observed, (1, 2, 0, 3, 4)).reshape(
        groups * halves, views_here * rows_here, tile_width
    )
    observed = lax.all_to_all(observed, ("views", "lat"), 0, 0, tiled=True)
    observed = observed.reshape(groups, halves, views_here, rows_here, tile_width)
    observed = jnp.transpose(observed, (0, 2, 3, 1, 4)).reshape(views_all, rows_here, halves * tile_width)

    chunk = rows_here * materials * depth_here * tile_width
    piece = chunk // groups
    mine = density.reshape(groups * parts, groups, piece)
    mine = lax.dynamic_index_in_dim(mine, group, 1, keepdims=False)
    mine = mine.reshape(groups * parts, piece // tile_width, tile_width)
    extra = jnp.pad(block.reshape(1, entries), ((0, 0), (0, tile_width - entries))).astype(jnp.bfloat16)
    extra = jnp.broadcast_to(extra[None], (groups * parts, 1, tile_width))
    mine = jnp.concatenate([mine, extra], axis=1)
    mine = lax.all_to_all(mine, ("views", "depth", "lat"), 0, 0, tiled=True)
    mine = mine.reshape(groups, depth_count, halves, piece // tile_width + 1, tile_width)
    table = mine[:, :, 0, piece // tile_width, :entries].astype(jnp.float32)
    table = table.reshape(groups, depth_count, 3, views_here, depth_here)
    table = jnp.transpose(table, (2, 0, 3, 1, 4)).reshape(3, views_all, depth_all)
    mine = mine[:, :, :, : piece // tile_width].reshape(groups, depth_count, halves, piece)
    mine = jnp.transpose(mine, (1, 2, 0, 3)).reshape(
        depth_count, halves, rows_here, materials, depth_here, tile_width
    )
    channels = materials * halves * rows_here
    mine = jnp.transpose(mine, (0, 4, 3, 1, 2, 5)).reshape(depth_all, channels, tile_width)
    mine = mine.astype(jnp.float32)
    target = observed.reshape(views_all // 2, 2, rows_here, halves, tile_width)
    target = jnp.transpose(target, (0, 1, 3, 2, 4)).reshape(views_all // 2, 2 * halves * rows_here, tile_width)
    emitted = jnp.log(jnp.sum(spectrum)).reshape(1)
    smem = pl.BlockSpec(memory_space=pltpu.SMEM)
    vmem = pl.BlockSpec(memory_space=pltpu.VMEM)
    grads = pl.pallas_call(
        functools.partial(forward_kernel, rows_here, halves, depth_all, views_all),
        out_shape=jax.ShapeDtypeStruct((views_all, channels, tile_width), jnp.float32),
        in_specs=[smem, smem, smem, smem, vmem, vmem],
        out_specs=vmem,
        scratch_shapes=[
            pltpu.VMEM((views_all, channels, tile_width), jnp.float32),
            pltpu.VMEM((depth_all, channels, tile_width + LANES), jnp.float32),
            pltpu.VMEM((depth_all, channels, tile_width + LANES), jnp.float32),
        ],
        interpret=INTERPRET,
    )(table, emitted, spectrum, attenuation, mine, target)
    layers = pl.pallas_call(
        functools.partial(backward_kernel, rows_here, halves),
        out_shape=jax.ShapeDtypeStruct((parts * rows_here * materials, depth_here, tile_width), jnp.float32),
        in_specs=[smem, vmem],
        out_specs=vmem,
        scratch_shapes=[
            pltpu.VMEM((views_all, channels, tile_width + LANES), jnp.float32),
            pltpu.VMEM((views_all, channels, tile_width + LANES), jnp.float32),
        ],
        interpret=INTERPRET,
    )(table, grads)
    layers = layers.reshape(parts, rows_here, materials, depth_here, tile_width)
    layers = lax.all_to_all(layers, ("depth", "lat"), 0, 0, tiled=True)
    return layers.reshape(rows_group, materials, depth_here, tile_width)


def per_device_any(density, measured, shear_shift, shear_frac, spectrum, attenuation):
    if rows_fit_wide(density, measured):
        return per_device_wide(density, measured, shear_shift, shear_frac, spectrum, attenuation)
    if rows_fit(density, measured):
        return per_device_rows(density, measured, shear_shift, shear_frac, spectrum, attenuation)
    return per_device(density, measured, shear_shift, shear_frac, spectrum, attenuation)


def solution(mesh):
    in_specs = (
        P(None, None, "depth", "lat"),
        P("views", None, "lat"),
        P("views", "depth"),
        P("views", "depth"),
        P(),
        P(),
    )
    out_specs = P("views", None, "depth", "lat")
    return jax.shard_map(
        per_device_any, mesh=mesh, in_specs=in_specs, out_specs=out_specs, check_vma=False
    )
```

```python
import functools
import jax
import jax.numpy as jnp
from jax import lax
from jax.sharding import PartitionSpec as P
from jax.experimental import pallas as pl
from jax.experimental.pallas import tpu as pltpu

HALO = 64


def with_halo(x, sides, width):
    for axis, dim in sides:
        size, length = (lax.axis_size(axis), x.shape[dim])
        up = [(i, (i + 1) % size) for i in range(size - 1)]
        down = [(j, i) for i, j in up]
        last = lax.slice_in_dim(x, length - width, length, axis=dim)
        first = lax.slice_in_dim(x, 0, width, axis=dim)
        before = lax.ppermute(last, axis, up)
        after = lax.ppermute(first, axis, down)
        x = jnp.concatenate([before, x, after], axis=dim)
    return x


def exchange(x, axis):
    count = lax.axis_size(axis)
    me = lax.axis_index(axis)
    result = x
    for step in range(1, count):
        pairs = [(i, (i + step) % count) for i in range(count)]
        part = lax.dynamic_index_in_dim(x, (me + step) % count, 0, keepdims=True)
        part = lax.ppermute(part, axis, pairs)
        result = lax.dynamic_update_index_in_dim(result, part, (me - step) % count, 0)
    return result


def band_forward(shear_shift, lower_weight, upper_weight, window, block_width):
    band_shape = (shear_shift.shape[1], window, shear_shift.shape[0], block_width)
    tap_index = lax.broadcasted_iota(jnp.int32, band_shape, 1)
    column = lax.broadcasted_iota(jnp.int32, band_shape, 3)
    anchor = (shear_shift.T + HALO)[:, None, :, None]
    nothing = jnp.zeros((), jnp.bfloat16)
    lower_part = jnp.where(tap_index == column + anchor, lower_weight.T[:, None, :, None], nothing)
    upper_part = jnp.where(
        tap_index == column + anchor + 1, upper_weight.T[:, None, :, None], nothing
    )
    return lower_part + upper_part


def band_backward(shear_shift, lower_weight, upper_weight, window, block_width):
    band_shape = (shear_shift.shape[0], window, shear_shift.shape[1], block_width)
    tap_index = lax.broadcasted_iota(jnp.int32, band_shape, 1)
    column = lax.broadcasted_iota(jnp.int32, band_shape, 3)
    anchor = (HALO - shear_shift)[:, None, :, None]
    nothing = jnp.zeros((), jnp.bfloat16)
    lower_part = jnp.where(tap_index == column + anchor, lower_weight[:, None, :, None], nothing)
    upper_part = jnp.where(
        tap_index == column + anchor - 1, upper_weight[:, None, :, None], nothing
    )
    return lower_part + upper_part


def spectral(path_sums, observed, spectrum, attenuation, views_all):
    view_count, row_count, materials, tile_width = path_sums.shape
    block_pixels = 4096
    path_water = path_sums[:, :, 0, :].reshape(-1, block_pixels)
    path_bone = path_sums[:, :, 1, :].reshape(-1, block_pixels)
    target_flat = observed.reshape(-1, block_pixels)
    coefficients = jnp.concatenate(
        [jnp.ones((1, spectrum.shape[0]), jnp.float32), attenuation], axis=0
    )
    emitted = jnp.log(jnp.sum(spectrum))

    def one_block(inputs):
        water_block, bone_block, target_block = inputs
        exponent = (
            attenuation[0][:, None] * water_block[None, :]
            + attenuation[1][:, None] * bone_block[None, :]
        )
        counts = spectrum[:, None] * jnp.exp(-exponent)
        moments = jnp.dot(coefficients, counts, precision=lax.Precision.HIGHEST)
        intensity = moments[0]
        residual = emitted - jnp.log(intensity) - target_block
        factor = residual / intensity / views_all
        return (moments[1:] * factor[None, :]).astype(jnp.bfloat16)

    stacked = lax.map(one_block, (path_water, path_bone, target_flat))
    gradients = jnp.swapaxes(stacked, 0, 1).reshape(materials, view_count, row_count, tile_width)
    return jnp.transpose(gradients, (1, 2, 0, 3))


def spectral_kernel(views_all, emitted_ref, spectrum_ref, attenuation_ref, water_ref, bone_ref, target_ref, out0_ref, out1_ref):
    rows, width = water_ref.shape
    energies = spectrum_ref.shape[0]
    block = 8

    def one_block(b, carry):
        lo = pl.multiple_of(b * block, block)
        water = water_ref[pl.ds(lo, block), :]
        bone = bone_ref[pl.ds(lo, block), :]

        def one_energy(e, sums):
            intensity, first, second = sums
            a0 = attenuation_ref[0, e]
            a1 = attenuation_ref[1, e]
            counts = spectrum_ref[e] * jnp.exp(-(a0 * water + a1 * bone))
            return (intensity + counts, first + a0 * counts, second + a1 * counts)

        zero = jnp.zeros((block, width), jnp.float32)
        intensity, first, second = lax.fori_loop(0, energies, one_energy, (zero, zero, zero), unroll=8)
        residual = emitted_ref[0] - jnp.log(intensity) - target_ref[pl.ds(lo, block), :]
        factor = residual / intensity / views_all
        out0_ref[pl.ds(lo, block), :] = (first * factor).astype(out0_ref.dtype)
        out1_ref[pl.ds(lo, block), :] = (second * factor).astype(out1_ref.dtype)
        return carry

    lax.fori_loop(0, rows // block, one_block, 0)


def spectral_pallas(path_sums, observed, spectrum, attenuation, views_all):
    view_count, row_count, materials, width_all = path_sums.shape
    pixels = view_count * row_count * width_all
    rows = pixels // LANES // 4
    water = path_sums[:, :, 0, :].reshape(rows, 4 * LANES)
    bone = path_sums[:, :, 1, :].reshape(rows, 4 * LANES)
    target = observed.reshape(rows, 4 * LANES)
    emitted = jnp.log(jnp.sum(spectrum)).reshape(1)
    smem = pl.BlockSpec(memory_space=pltpu.SMEM)
    vmem = pl.BlockSpec(memory_space=pltpu.VMEM)
    first, second = pl.pallas_call(
        functools.partial(spectral_kernel, views_all),
        out_shape=(
            jax.ShapeDtypeStruct((rows, 4 * LANES), jnp.bfloat16),
            jax.ShapeDtypeStruct((rows, 4 * LANES), jnp.bfloat16),
        ),
        in_specs=[smem, smem, smem, vmem, vmem, vmem],
        out_specs=(vmem, vmem),
        interpret=INTERPRET,
    )(emitted, spectrum, attenuation, water, bone, target)
    shape = (view_count, row_count, width_all)
    return jnp.stack([first.reshape(shape), second.reshape(shape)], axis=2)


def per_device(density, measured, shear_shift, shear_frac, spectrum, attenuation):
    row_total, materials, depth_here, tile_width = density.shape
    block_width = min(128, tile_width)
    block_count = tile_width // block_width
    window = block_width + 2 * HALO
    views_all = measured.shape[0] * lax.axis_size("views")
    depth_all = depth_here * lax.axis_size("depth")
    rows_out = row_total // lax.axis_size("views")
    lower_weight = (1.0 - shear_frac).astype(jnp.bfloat16)
    upper_weight = shear_frac.astype(jnp.bfloat16)
    rows_here = density.shape[0]
    padded = with_halo(density, (("lat", 3),), HALO)
    framed = jnp.stack(
        [
            padded[:, :, :, number * block_width : number * block_width + window]
            for number in range(block_count)
        ],
        axis=2,
    )
    forward_band = band_forward(shear_shift, lower_weight, upper_weight, window, block_width)
    partial_value = jnp.einsum(
        "ymnzi,zivc->vymnc", framed, forward_band, preferred_element_type=jnp.float32
    )
    partial_value = partial_value.reshape(shear_shift.shape[0], rows_here, materials, tile_width)
    shares = lax.psum_scatter(partial_value, "depth", scatter_dimension=3, tiled=True) / depth_all
    share_cols = shares.shape[3]
    observed = lax.dynamic_slice_in_dim(
        measured, lax.axis_index("depth") * share_cols, share_cols, 2
    )
    share_grads = spectral(shares, observed, spectrum, attenuation, views_all)
    path_grads = lax.all_gather(share_grads, "depth", axis=3, tiled=True)
    padded_grads = with_halo(path_grads, (("lat", 3),), HALO)
    framed_grads = jnp.stack(
        [
            padded_grads[:, :, :, number * block_width : number * block_width + window]
            for number in range(block_count)
        ],
        axis=3,
    )
    backward_band = band_backward(shear_shift, lower_weight, upper_weight, window, block_width)
    product = jnp.einsum(
        "vymni,vizc->ymznc", framed_grads, backward_band, preferred_element_type=jnp.float32
    )
    return lax.psum_scatter(
        product.reshape(rows_out * lax.axis_size("views"), materials, depth_here, tile_width),
        "views",
        scatter_dimension=0,
        tiled=True,
    )


LANES = 128
INTERPRET = False


def shear_kernel(rot_ref, thr_ref, wa_ref, wb_ref, src_ref, out_ref):
    outer_count, channels, width = src_ref.shape
    inner_count, _, out_width = out_ref.shape
    pieces = width // LANES
    out_pieces = out_width // LANES
    out_ref[...] = jnp.zeros(out_ref.shape, jnp.float32)
    lane = lax.broadcasted_iota(jnp.int32, (channels, LANES), 1)

    def outer(o, carry):
        cols = [src_ref[o, :, k * LANES : (k + 1) * LANES] for k in range(pieces)]
        turned = [pltpu.roll(c, LANES - 1, 1) for c in cols]
        nexts = [
            jnp.where(lane < LANES - 1, turned[k], turned[k + 1]) for k in range(pieces - 1)
        ] + [turned[pieces - 1]]
        for i in range(inner_count):
            wa = wa_ref[o, i]
            wb = wb_ref[o, i]
            mixed = [wa * cols[k] + wb * nexts[k] for k in range(pieces)]
            rolled = [pltpu.roll(m, rot_ref[o, i], 1) for m in mixed]
            keep = lane < thr_ref[o, i]
            for j in range(out_pieces):
                out_ref[i, :, j * LANES : (j + 1) * LANES] += jnp.where(
                    keep, rolled[j], rolled[j + 1]
                )
        return carry

    lax.fori_loop(0, outer_count, outer, 0)


def shear_table_kernel(forward, tab_ref, src_ref, out_ref):
    outer_count, channels, width = src_ref.shape
    inner_count, _, out_width = out_ref.shape
    pieces = width // LANES
    out_pieces = out_width // LANES
    out_ref[...] = jnp.zeros(out_ref.shape, jnp.float32)
    lane = lax.broadcasted_iota(jnp.int32, (channels, LANES), 1)

    def outer(o, carry):
        cols = [src_ref[o, :, k * LANES : (k + 1) * LANES] for k in range(pieces)]
        turned = [pltpu.roll(c, LANES - 1, 1) for c in cols]
        nexts = [
            jnp.where(lane < LANES - 1, turned[k], turned[k + 1]) for k in range(pieces - 1)
        ] + [turned[pieces - 1]]
        for i in range(inner_count):
            if forward:
                shift = tab_ref[0, i, o].astype(jnp.int32)
                wa = tab_ref[1, i, o]
                wb = tab_ref[2, i, o]
                offset = shift + HALO
            else:
                shift = tab_ref[0, o, i].astype(jnp.int32)
                wa = tab_ref[2, o, i]
                wb = tab_ref[1, o, i]
                offset = HALO - 1 - shift
            limit = LANES - offset
            amount = jnp.where(limit == LANES, 0, limit)
            mixed = [wa * cols[k] + wb * nexts[k] for k in range(pieces)]
            rolled = [pltpu.roll(m, amount, 1) for m in mixed]
            keep = lane < limit
            for j in range(out_pieces):
                out_ref[i, :, j * LANES : (j + 1) * LANES] += jnp.where(
                    keep, rolled[j], rolled[j + 1]
                )
        return carry

    lax.fori_loop(0, outer_count, outer, 0)


def shear_table(forward, table, src, inner_count, out_width):
    _, channels, _ = src.shape
    smem = pl.BlockSpec(memory_space=pltpu.SMEM)
    vmem = pl.BlockSpec(memory_space=pltpu.VMEM)
    return pl.pallas_call(
        functools.partial(shear_table_kernel, forward),
        out_shape=jax.ShapeDtypeStruct((inner_count, channels, out_width), jnp.float32),
        in_specs=[smem, vmem],
        out_specs=vmem,
        interpret=INTERPRET,
    )(table, src)


def halo_columns(ys, lane, half_of, rows_here, halves, channels):
    count = len(ys)
    turned = [pltpu.roll(y, HALO, 1) for y in ys]
    zero = jnp.zeros_like(ys[0])
    left = jnp.where(half_of >= 1, pltpu.roll(turned[count - 1], rows_here, 0), zero)
    right = jnp.where(half_of <= halves - 2, pltpu.roll(turned[0], channels - rows_here, 0), zero)
    edge = lane < HALO
    cols = [jnp.where(edge, left, turned[0])]
    cols += [jnp.where(edge, turned[k - 1], turned[k]) for k in range(1, count)]
    cols += [jnp.where(edge, turned[count - 1], right)]
    return cols


def shear_pass(forward, rows_here, halves, tab_ref, src_ref, acc_ref, cols_ref, nexts_ref):
    outer_count, channels, width = src_ref.shape
    inner_count = acc_ref.shape[0]
    pieces = width // LANES
    lane = lax.broadcasted_iota(jnp.int32, (channels, LANES), 1)
    half_of = (lax.broadcasted_iota(jnp.int32, (channels, LANES), 0) // rows_here) % halves

    def prepare(o, carry):
        ys = [src_ref[o, :, k * LANES : (k + 1) * LANES] for k in range(pieces)]
        cols = halo_columns(ys, lane, half_of, rows_here, halves, channels)
        turned = [pltpu.roll(c, LANES - 1, 1) for c in cols]
        nexts = [jnp.where(lane < LANES - 1, turned[k], turned[k + 1]) for k in range(pieces)]
        nexts.append(turned[pieces])
        for k in range(pieces + 1):
            cols_ref[o, :, k * LANES : (k + 1) * LANES] = cols[k]
            nexts_ref[o, :, k * LANES : (k + 1) * LANES] = nexts[k]
        return carry

    lax.fori_loop(0, outer_count, prepare, 0)

    for i in range(inner_count):

        def one_input(o, acc):
            if forward:
                shift = tab_ref[0, i, o].astype(jnp.int32)
                wa = tab_ref[1, i, o]
                wb = tab_ref[2, i, o]
                offset = shift + HALO
            else:
                shift = tab_ref[0, o, i].astype(jnp.int32)
                wa = tab_ref[2, o, i]
                wb = tab_ref[1, o, i]
                offset = HALO - 1 - shift
            limit = LANES - offset
            amount = jnp.where(limit == LANES, 0, limit)
            mixed = [
                wa * cols_ref[o, :, k * LANES : (k + 1) * LANES]
                + wb * nexts_ref[o, :, k * LANES : (k + 1) * LANES]
                for k in range(pieces + 1)
            ]
            rolled = [pltpu.roll(m, amount, 1) for m in mixed]
            keep = lane < limit
            return tuple(acc[j] + jnp.where(keep, rolled[j], rolled[j + 1]) for j in range(pieces))

        zero = jnp.zeros((channels, LANES), jnp.float32)
        acc = lax.fori_loop(0, outer_count, one_input, tuple(zero for _ in range(pieces)), unroll=True)
        for j in range(pieces):
            acc_ref[i, :, j * LANES : (j + 1) * LANES] = acc[j]


def scatter_pass(rows_here, halves, tab_ref, src_ref, out_ref, cols_ref, nexts_ref):
    outer_count, channels, width = src_ref.shape
    _, depth_here, _ = out_ref.shape
    materials = channels // (halves * rows_here)
    pieces = width // LANES
    lane = lax.broadcasted_iota(jnp.int32, (channels, LANES), 1)
    half_of = (lax.broadcasted_iota(jnp.int32, (channels, LANES), 0) // rows_here) % halves

    def prepare(o, carry):
        ys = [src_ref[o, :, k * LANES : (k + 1) * LANES] for k in range(pieces)]
        cols = halo_columns(ys, lane, half_of, rows_here, halves, channels)
        turned = [pltpu.roll(c, LANES - 1, 1) for c in cols]
        nexts = [jnp.where(lane < LANES - 1, turned[k], turned[k + 1]) for k in range(pieces)]
        nexts.append(turned[pieces])
        for k in range(pieces + 1):
            cols_ref[o, :, k * LANES : (k + 1) * LANES] = cols[k]
            nexts_ref[o, :, k * LANES : (k + 1) * LANES] = nexts[k]
        return carry

    lax.fori_loop(0, outer_count, prepare, 0)
    inner_count = tab_ref.shape[2]

    for i in range(inner_count):
        slab, level = divmod(i, depth_here)

        def one_view(o, acc):
            shift = tab_ref[0, o, i].astype(jnp.int32)
            wa = tab_ref[2, o, i]
            wb = tab_ref[1, o, i]
            offset = HALO - 1 - shift
            limit = LANES - offset
            amount = jnp.where(limit == LANES, 0, limit)
            mixed = [
                wa * cols_ref[o, :, k * LANES : (k + 1) * LANES]
                + wb * nexts_ref[o, :, k * LANES : (k + 1) * LANES]
                for k in range(pieces + 1)
            ]
            rolled = [pltpu.roll(m, amount, 1) for m in mixed]
            keep = lane < limit
            return tuple(acc[j] + jnp.where(keep, rolled[j], rolled[j + 1]) for j in range(pieces))

        zero = jnp.zeros((channels, LANES), jnp.float32)
        acc = lax.fori_loop(0, outer_count, one_view, tuple(zero for _ in range(pieces)), unroll=True)
        value = jnp.concatenate(acc, axis=1)
        for c in range(channels):
            material, rest = divmod(c, halves * rows_here)
            half, row = divmod(rest, rows_here)
            target = ((slab * halves + half) * rows_here + row) * materials + material
            out_ref[target, level : level + 1, :] = value[c : c + 1, :]


def forward_kernel(rows_here, halves, depth_all, views_all, tab_ref, emitted_ref, spectrum_ref,
                   attenuation_ref, src_ref, target_ref, out_ref, sums_ref, cols_ref, nexts_ref):
    shear_pass(True, rows_here, halves, tab_ref, src_ref, sums_ref, cols_ref, nexts_ref)
    _, channels, width = sums_ref.shape
    energies = spectrum_ref.shape[0]
    split = channels // 2
    low = lax.broadcasted_iota(jnp.int32, (channels, width), 0) < split

    def one_pair(p, carry):
        first_view = sums_ref[2 * p] / depth_all
        second_view = sums_ref[2 * p + 1] / depth_all
        water = jnp.where(low, first_view, pltpu.roll(second_view, split, 0))
        bone = jnp.where(low, pltpu.roll(first_view, split, 0), second_view)

        def one_energy(e, sums):
            intensity, first, second = sums
            a0 = attenuation_ref[0, e]
            a1 = attenuation_ref[1, e]
            counts = spectrum_ref[e] * jnp.exp((-a0) * water + (-a1) * bone)
            return (intensity + counts, first + a0 * counts, second + a1 * counts)

        zero = jnp.zeros((channels, width), jnp.float32)
        intensity, first, second = lax.fori_loop(0, energies, one_energy, (zero, zero, zero), unroll=True)
        residual = emitted_ref[0] - jnp.log(intensity) - target_ref[p]
        factor = residual / intensity / views_all
        first = (first * factor).astype(jnp.bfloat16).astype(jnp.float32)
        second = (second * factor).astype(jnp.bfloat16).astype(jnp.float32)
        out_ref[2 * p] = jnp.where(low, first, pltpu.roll(second, split, 0))
        out_ref[2 * p + 1] = jnp.where(low, pltpu.roll(first, split, 0), second)
        return carry

    lax.fori_loop(0, out_ref.shape[0] // 2, one_pair, 0)


def backward_kernel(rows_here, halves, tab_ref, src_ref, out_ref, cols_ref, nexts_ref):
    scatter_pass(rows_here, halves, tab_ref, src_ref, out_ref, cols_ref, nexts_ref)


def shear_apply(offset, wa, wb, src, out_width):
    outer_count, channels, width = src.shape
    inner_count = offset.shape[1]
    rot = (LANES - offset) % LANES
    thr = LANES - offset
    smem = pl.BlockSpec(memory_space=pltpu.SMEM)
    vmem = pl.BlockSpec(memory_space=pltpu.VMEM)
    return pl.pallas_call(
        shear_kernel,
        out_shape=jax.ShapeDtypeStruct((inner_count, channels, out_width), jnp.float32),
        in_specs=[smem, smem, smem, smem, vmem],
        out_specs=vmem,
        interpret=INTERPRET,
    )(rot.astype(jnp.int32), thr.astype(jnp.int32), wa, wb, src)


def rows_fit(density, measured):
    rows = density.shape[0]
    groups = lax.axis_size("views")
    depth = lax.axis_size("depth")
    tile_width = density.shape[3]
    return (
        rows % groups == 0
        and (rows // groups) % depth == 0
        and tile_width % LANES == 0
        and 2 * HALO == LANES
        and density.shape[1] == 2
        and measured.shape[0] * groups % 2 == 0
        and tile_width >= 3 * measured.shape[0] * density.shape[2] * groups
    )


def per_device_rows(density, measured, shear_shift, shear_frac, spectrum, attenuation):
    row_total, materials, depth_here, tile_width = density.shape
    groups = lax.axis_size("views")
    depth_count = lax.axis_size("depth")
    views_here = measured.shape[0]
    views_all = views_here * groups
    depth_all = depth_here * depth_count
    rows_group = row_total // groups
    rows_here = rows_group // depth_count
    group = lax.axis_index("views")
    slab = lax.axis_index("depth")

    lower_weight = (1.0 - shear_frac).astype(jnp.bfloat16).astype(jnp.float32)
    upper_weight = shear_frac.astype(jnp.bfloat16).astype(jnp.float32)
    table = jnp.stack([shear_shift.astype(jnp.float32), lower_weight, upper_weight])
    entries = table.size
    observed = measured.reshape(views_here, groups, rows_group, tile_width)
    observed = lax.dynamic_slice_in_dim(observed, slab * rows_here, rows_here, 2)
    observed = jnp.transpose(observed, (1, 0, 2, 3)).reshape(groups, views_here * rows_here, tile_width)
    extra = jnp.pad(table.reshape(1, entries), ((0, 0), (0, tile_width - entries)))
    extra = jnp.broadcast_to(extra[None], (groups, 1, tile_width))
    observed = jnp.concatenate([observed, extra], axis=1)
    observed = lax.all_to_all(observed, "views", 0, 0, tiled=True)
    table = observed[:, views_here * rows_here, :entries].reshape(groups, 3, views_here, depth_here)
    table = jnp.transpose(table, (1, 0, 2, 3)).reshape(3, views_all, depth_here)
    observed = observed[:, : views_here * rows_here].reshape(views_all, rows_here, tile_width)

    channels = rows_here * materials
    mine = lax.dynamic_slice_in_dim(density, group * rows_group, rows_group, 0)
    mine = mine.reshape(depth_count, rows_here, materials, depth_here, tile_width)
    mine = jnp.transpose(mine, (0, 3, 1, 2, 4)).reshape(depth_count, depth_here * channels, tile_width)
    wide = table.size
    extra = jnp.pad(table.reshape(1, wide), ((0, 0), (0, tile_width - wide))).astype(jnp.bfloat16)
    extra = jnp.broadcast_to(extra[None], (depth_count, 1, tile_width))
    mine = jnp.concatenate([mine, extra], axis=1)
    mine = lax.all_to_all(mine, "depth", 0, 0, tiled=True)
    table = mine[:, depth_here * channels, :wide].astype(jnp.float32)
    table = table.reshape(depth_count, 3, views_all, depth_here)
    table = jnp.transpose(table, (1, 2, 0, 3)).reshape(3, views_all, depth_all)
    shift_all = table[0].astype(jnp.int32)
    lower_all = table[1]
    upper_all = table[2]
    mine = mine[:, : depth_here * channels].reshape(depth_all, channels, tile_width)
    padded = with_halo(mine, (("lat", 2),), HALO).astype(jnp.float32)

    sums = shear_apply(
        (shift_all + HALO).T, lower_all.T, upper_all.T, padded, tile_width
    )
    sums = (sums / depth_all).reshape(views_all, rows_here, materials, tile_width)
    grads = spectral(sums, observed, spectrum, attenuation, views_all)
    grads = grads.reshape(views_all, rows_here * materials, tile_width)
    padded_grads = with_halo(grads, (("lat", 2),), HALO).astype(jnp.float32)
    layers = shear_apply(
        HALO - 1 - shift_all, upper_all, lower_all, padded_grads, tile_width
    )
    layers = layers.reshape(depth_count, depth_here, rows_here, materials, tile_width)
    layers = exchange(layers, "depth")
    return jnp.transpose(layers, (0, 2, 3, 1, 4)).reshape(rows_group, materials, depth_here, tile_width)


def rows_fit_wide(density, measured):
    rows = density.shape[0]
    groups = lax.axis_size("views")
    parts = lax.axis_size("depth") * lax.axis_size("lat")
    tile_width = density.shape[3]
    return (
        rows % groups == 0
        and (rows // groups) % parts == 0
        and tile_width % LANES == 0
        and 2 * HALO == LANES
        and density.shape[1] == 2
        and measured.shape[0] * groups % 2 == 0
        and tile_width >= 3 * measured.shape[0] * density.shape[2]
        and ((rows // groups // parts) * density.shape[1] * density.shape[2]) % groups == 0
    )


def stack_halves(values, halves, tile_width):
    count, rows, materials, _ = values.shape
    padded = jnp.pad(values, ((0, 0), (0, 0), (0, 0), (HALO, HALO)))
    parts = [
        padded[..., h * tile_width : h * tile_width + tile_width + 2 * HALO] for h in range(halves)
    ]
    return jnp.stack(parts, axis=1).reshape(count, halves * rows * materials, tile_width + 2 * HALO)


def join_halves(values, halves, rows, materials):
    count, _, tile_width = values.shape
    values = values.reshape(count, halves, rows, materials, tile_width)
    return jnp.transpose(values, (0, 2, 3, 1, 4)).reshape(count, rows, materials, halves * tile_width)


def per_device_wide(density, measured, shear_shift, shear_frac, spectrum, attenuation):
    row_total, materials, depth_here, tile_width = density.shape
    groups = lax.axis_size("views")
    depth_count = lax.axis_size("depth")
    halves = lax.axis_size("lat")
    parts = depth_count * halves
    views_here = measured.shape[0]
    views_all = views_here * groups
    depth_all = depth_here * depth_count
    rows_group = row_total // groups
    rows_here = rows_group // parts
    group = lax.axis_index("views")
    slab = lax.axis_index("depth")
    half = lax.axis_index("lat")

    lower_weight = (1.0 - shear_frac).astype(jnp.bfloat16).astype(jnp.float32)
    upper_weight = shear_frac.astype(jnp.bfloat16).astype(jnp.float32)
    block = jnp.stack([shear_shift.astype(jnp.float32), lower_weight, upper_weight])
    entries = block.size
    span = halves * rows_here
    observed = jnp.stack(
        [
            lax.dynamic_slice_in_dim(measured, (g * depth_count + slab) * span, span, 1)
            for g in range(groups)
        ]
    )
    observed = observed.reshape(groups, views_here, halves, rows_here, tile_width)
    observed = jnp.transpose(observed, (0, 2, 1, 3, 4)).reshape(
        groups * halves, views_here * rows_here, tile_width
    )
    observed = lax.all_to_all(observed, ("views", "lat"), 0, 0, tiled=True)
    observed = observed.reshape(groups, halves, views_here, rows_here, tile_width)
    observed = jnp.transpose(observed, (0, 2, 3, 1, 4)).reshape(views_all, rows_here, halves * tile_width)

    chunk = rows_here * materials * depth_here * tile_width
    piece = chunk // groups
    mine = density.reshape(groups * parts, groups, piece)
    mine = lax.dynamic_index_in_dim(mine, group, 1, keepdims=False)
    mine = mine.reshape(groups * parts, piece // tile_width, tile_width)
    extra = jnp.pad(block.reshape(1, entries), ((0, 0), (0, tile_width - entries))).astype(jnp.bfloat16)
    extra = jnp.broadcast_to(extra[None], (groups * parts, 1, tile_width))
    mine = jnp.concatenate([mine, extra], axis=1)
    mine = lax.all_to_all(mine, ("views", "depth", "lat"), 0, 0, tiled=True)
    mine = mine.reshape(groups, depth_count, halves, piece // tile_width + 1, tile_width)
    table = mine[:, :, 0, piece // tile_width, :entries].astype(jnp.float32)
    table = table.reshape(groups, depth_count, 3, views_here, depth_here)
    table = jnp.transpose(table, (2, 0, 3, 1, 4)).reshape(3, views_all, depth_all)
    mine = mine[:, :, :, : piece // tile_width].reshape(groups, depth_count, halves, piece)
    mine = jnp.transpose(mine, (1, 2, 0, 3)).reshape(
        depth_count, halves, rows_here, materials, depth_here, tile_width
    )
    channels = materials * halves * rows_here
    mine = jnp.transpose(mine, (0, 4, 3, 1, 2, 5)).reshape(depth_all, channels, tile_width)
    mine = mine.astype(jnp.float32)
    target = observed.reshape(views_all // 2, 2, rows_here, halves, tile_width)
    target = jnp.transpose(target, (0, 1, 3, 2, 4)).reshape(views_all // 2, 2 * halves * rows_here, tile_width)
    emitted = jnp.log(jnp.sum(spectrum)).reshape(1)
    smem = pl.BlockSpec(memory_space=pltpu.SMEM)
    vmem = pl.BlockSpec(memory_space=pltpu.VMEM)
    grads = pl.pallas_call(
        functools.partial(forward_kernel, rows_here, halves, depth_all, views_all),
        out_shape=jax.ShapeDtypeStruct((views_all, channels, tile_width), jnp.float32),
        in_specs=[smem, smem, smem, smem, vmem, vmem],
        out_specs=vmem,
        scratch_shapes=[
            pltpu.VMEM((views_all, channels, tile_width), jnp.float32),
            pltpu.VMEM((depth_all, channels, tile_width + LANES), jnp.float32),
            pltpu.VMEM((depth_all, channels, tile_width + LANES), jnp.float32),
        ],
        interpret=INTERPRET,
    )(table, emitted, spectrum, attenuation, mine, target)
    layers = pl.pallas_call(
        functools.partial(backward_kernel, rows_here, halves),
        out_shape=jax.ShapeDtypeStruct((parts * rows_here * materials, depth_here, tile_width), jnp.float32),
        in_specs=[smem, vmem],
        out_specs=vmem,
        scratch_shapes=[
            pltpu.VMEM((views_all, channels, tile_width + LANES), jnp.float32),
            pltpu.VMEM((views_all, channels, tile_width + LANES), jnp.float32),
        ],
        interpret=INTERPRET,
    )(table, grads)
    layers = layers.reshape(parts, rows_here, materials, depth_here, tile_width)
    layers = lax.all_to_all(layers, ("depth", "lat"), 0, 0, tiled=True)
    return layers.reshape(rows_group, materials, depth_here, tile_width)


def per_device_any(density, measured, shear_shift, shear_frac, spectrum, attenuation):
    if rows_fit_wide(density, measured):
        return per_device_wide(density, measured, shear_shift, shear_frac, spectrum, attenuation)
    if rows_fit(density, measured):
        return per_device_rows(density, measured, shear_shift, shear_frac, spectrum, attenuation)
    return per_device(density, measured, shear_shift, shear_frac, spectrum, attenuation)


def solution(mesh):
    in_specs = (
        P(None, None, "depth", "lat"),
        P("views", None, "lat"),
        P("views", "depth"),
        P("views", "depth"),
        P(),
        P(),
    )
    out_specs = P("views", None, "depth", "lat")
    return jax.shard_map(
        per_device_any, mesh=mesh, in_specs=in_specs, out_specs=out_specs, check_vma=False
    )
```

```python
import functools
import jax
import jax.numpy as jnp
from jax import lax
from jax.sharding import PartitionSpec as P
from jax.experimental import pallas as pl
from jax.experimental.pallas import tpu as pltpu

HALO = 64


def with_halo(x, sides, width):
    for axis, dim in sides:
        size, length = (lax.axis_size(axis), x.shape[dim])
        up = [(i, (i + 1) % size) for i in range(size - 1)]
        down = [(j, i) for i, j in up]
        last = lax.slice_in_dim(x, length - width, length, axis=dim)
        first = lax.slice_in_dim(x, 0, width, axis=dim)
        before = lax.ppermute(last, axis, up)
        after = lax.ppermute(first, axis, down)
        x = jnp.concatenate([before, x, after], axis=dim)
    return x


def exchange(x, axis):
    count = lax.axis_size(axis)
    me = lax.axis_index(axis)
    result = x
    for step in range(1, count):
        pairs = [(i, (i + step) % count) for i in range(count)]
        part = lax.dynamic_index_in_dim(x, (me + step) % count, 0, keepdims=True)
        part = lax.ppermute(part, axis, pairs)
        result = lax.dynamic_update_index_in_dim(result, part, (me - step) % count, 0)
    return result


def band_forward(shear_shift, lower_weight, upper_weight, window, block_width):
    band_shape = (shear_shift.shape[1], window, shear_shift.shape[0], block_width)
    tap_index = lax.broadcasted_iota(jnp.int32, band_shape, 1)
    column = lax.broadcasted_iota(jnp.int32, band_shape, 3)
    anchor = (shear_shift.T + HALO)[:, None, :, None]
    nothing = jnp.zeros((), jnp.bfloat16)
    lower_part = jnp.where(tap_index == column + anchor, lower_weight.T[:, None, :, None], nothing)
    upper_part = jnp.where(
        tap_index == column + anchor + 1, upper_weight.T[:, None, :, None], nothing
    )
    return lower_part + upper_part


def band_backward(shear_shift, lower_weight, upper_weight, window, block_width):
    band_shape = (shear_shift.shape[0], window, shear_shift.shape[1], block_width)
    tap_index = lax.broadcasted_iota(jnp.int32, band_shape, 1)
    column = lax.broadcasted_iota(jnp.int32, band_shape, 3)
    anchor = (HALO - shear_shift)[:, None, :, None]
    nothing = jnp.zeros((), jnp.bfloat16)
    lower_part = jnp.where(tap_index == column + anchor, lower_weight[:, None, :, None], nothing)
    upper_part = jnp.where(
        tap_index == column + anchor - 1, upper_weight[:, None, :, None], nothing
    )
    return lower_part + upper_part


def spectral(path_sums, observed, spectrum, attenuation, views_all):
    view_count, row_count, materials, tile_width = path_sums.shape
    block_pixels = 4096
    path_water = path_sums[:, :, 0, :].reshape(-1, block_pixels)
    path_bone = path_sums[:, :, 1, :].reshape(-1, block_pixels)
    target_flat = observed.reshape(-1, block_pixels)
    coefficients = jnp.concatenate(
        [jnp.ones((1, spectrum.shape[0]), jnp.float32), attenuation], axis=0
    )
    emitted = jnp.log(jnp.sum(spectrum))

    def one_block(inputs):
        water_block, bone_block, target_block = inputs
        exponent = (
            attenuation[0][:, None] * water_block[None, :]
            + attenuation[1][:, None] * bone_block[None, :]
        )
        counts = spectrum[:, None] * jnp.exp(-exponent)
        moments = jnp.dot(coefficients, counts, precision=lax.Precision.HIGHEST)
        intensity = moments[0]
        residual = emitted - jnp.log(intensity) - target_block
        factor = residual / intensity / views_all
        return (moments[1:] * factor[None, :]).astype(jnp.bfloat16)

    stacked = lax.map(one_block, (path_water, path_bone, target_flat))
    gradients = jnp.swapaxes(stacked, 0, 1).reshape(materials, view_count, row_count, tile_width)
    return jnp.transpose(gradients, (1, 2, 0, 3))


def spectral_kernel(views_all, emitted_ref, spectrum_ref, attenuation_ref, water_ref, bone_ref, target_ref, out0_ref, out1_ref):
    rows, width = water_ref.shape
    energies = spectrum_ref.shape[0]
    block = 8

    def one_block(b, carry):
        lo = pl.multiple_of(b * block, block)
        water = water_ref[pl.ds(lo, block), :]
        bone = bone_ref[pl.ds(lo, block), :]

        def one_energy(e, sums):
            intensity, first, second = sums
            a0 = attenuation_ref[0, e]
            a1 = attenuation_ref[1, e]
            counts = spectrum_ref[e] * jnp.exp(-(a0 * water + a1 * bone))
            return (intensity + counts, first + a0 * counts, second + a1 * counts)

        zero = jnp.zeros((block, width), jnp.float32)
        intensity, first, second = lax.fori_loop(0, energies, one_energy, (zero, zero, zero), unroll=8)
        residual = emitted_ref[0] - jnp.log(intensity) - target_ref[pl.ds(lo, block), :]
        factor = residual / intensity / views_all
        out0_ref[pl.ds(lo, block), :] = (first * factor).astype(out0_ref.dtype)
        out1_ref[pl.ds(lo, block), :] = (second * factor).astype(out1_ref.dtype)
        return carry

    lax.fori_loop(0, rows // block, one_block, 0)


def spectral_pallas(path_sums, observed, spectrum, attenuation, views_all):
    view_count, row_count, materials, width_all = path_sums.shape
    pixels = view_count * row_count * width_all
    rows = pixels // LANES // 4
    water = path_sums[:, :, 0, :].reshape(rows, 4 * LANES)
    bone = path_sums[:, :, 1, :].reshape(rows, 4 * LANES)
    target = observed.reshape(rows, 4 * LANES)
    emitted = jnp.log(jnp.sum(spectrum)).reshape(1)
    smem = pl.BlockSpec(memory_space=pltpu.SMEM)
    vmem = pl.BlockSpec(memory_space=pltpu.VMEM)
    first, second = pl.pallas_call(
        functools.partial(spectral_kernel, views_all),
        out_shape=(
            jax.ShapeDtypeStruct((rows, 4 * LANES), jnp.bfloat16),
            jax.ShapeDtypeStruct((rows, 4 * LANES), jnp.bfloat16),
        ),
        in_specs=[smem, smem, smem, vmem, vmem, vmem],
        out_specs=(vmem, vmem),
        interpret=INTERPRET,
    )(emitted, spectrum, attenuation, water, bone, target)
    shape = (view_count, row_count, width_all)
    return jnp.stack([first.reshape(shape), second.reshape(shape)], axis=2)


def per_device(density, measured, shear_shift, shear_frac, spectrum, attenuation):
    row_total, materials, depth_here, tile_width = density.shape
    block_width = min(128, tile_width)
    block_count = tile_width // block_width
    window = block_width + 2 * HALO
    views_all = measured.shape[0] * lax.axis_size("views")
    depth_all = depth_here * lax.axis_size("depth")
    rows_out = row_total // lax.axis_size("views")
    lower_weight = (1.0 - shear_frac).astype(jnp.bfloat16)
    upper_weight = shear_frac.astype(jnp.bfloat16)
    rows_here = density.shape[0]
    padded = with_halo(density, (("lat", 3),), HALO)
    framed = jnp.stack(
        [
            padded[:, :, :, number * block_width : number * block_width + window]
            for number in range(block_count)
        ],
        axis=2,
    )
    forward_band = band_forward(shear_shift, lower_weight, upper_weight, window, block_width)
    partial_value = jnp.einsum(
        "ymnzi,zivc->vymnc", framed, forward_band, preferred_element_type=jnp.float32
    )
    partial_value = partial_value.reshape(shear_shift.shape[0], rows_here, materials, tile_width)
    shares = lax.psum_scatter(partial_value, "depth", scatter_dimension=3, tiled=True) / depth_all
    share_cols = shares.shape[3]
    observed = lax.dynamic_slice_in_dim(
        measured, lax.axis_index("depth") * share_cols, share_cols, 2
    )
    share_grads = spectral(shares, observed, spectrum, attenuation, views_all)
    path_grads = lax.all_gather(share_grads, "depth", axis=3, tiled=True)
    padded_grads = with_halo(path_grads, (("lat", 3),), HALO)
    framed_grads = jnp.stack(
        [
            padded_grads[:, :, :, number * block_width : number * block_width + window]
            for number in range(block_count)
        ],
        axis=3,
    )
    backward_band = band_backward(shear_shift, lower_weight, upper_weight, window, block_width)
    product = jnp.einsum(
        "vymni,vizc->ymznc", framed_grads, backward_band, preferred_element_type=jnp.float32
    )
    return lax.psum_scatter(
        product.reshape(rows_out * lax.axis_size("views"), materials, depth_here, tile_width),
        "views",
        scatter_dimension=0,
        tiled=True,
    )


LANES = 128
INTERPRET = False


def shear_kernel(rot_ref, thr_ref, wa_ref, wb_ref, src_ref, out_ref):
    outer_count, channels, width = src_ref.shape
    inner_count, _, out_width = out_ref.shape
    pieces = width // LANES
    out_pieces = out_width // LANES
    out_ref[...] = jnp.zeros(out_ref.shape, jnp.float32)
    lane = lax.broadcasted_iota(jnp.int32, (channels, LANES), 1)

    def outer(o, carry):
        cols = [src_ref[o, :, k * LANES : (k + 1) * LANES] for k in range(pieces)]
        turned = [pltpu.roll(c, LANES - 1, 1) for c in cols]
        nexts = [
            jnp.where(lane < LANES - 1, turned[k], turned[k + 1]) for k in range(pieces - 1)
        ] + [turned[pieces - 1]]
        for i in range(inner_count):
            wa = wa_ref[o, i]
            wb = wb_ref[o, i]
            mixed = [wa * cols[k] + wb * nexts[k] for k in range(pieces)]
            rolled = [pltpu.roll(m, rot_ref[o, i], 1) for m in mixed]
            keep = lane < thr_ref[o, i]
            for j in range(out_pieces):
                out_ref[i, :, j * LANES : (j + 1) * LANES] += jnp.where(
                    keep, rolled[j], rolled[j + 1]
                )
        return carry

    lax.fori_loop(0, outer_count, outer, 0)


def shear_table_kernel(forward, tab_ref, src_ref, out_ref):
    outer_count, channels, width = src_ref.shape
    inner_count, _, out_width = out_ref.shape
    pieces = width // LANES
    out_pieces = out_width // LANES
    out_ref[...] = jnp.zeros(out_ref.shape, jnp.float32)
    lane = lax.broadcasted_iota(jnp.int32, (channels, LANES), 1)

    def outer(o, carry):
        cols = [src_ref[o, :, k * LANES : (k + 1) * LANES] for k in range(pieces)]
        turned = [pltpu.roll(c, LANES - 1, 1) for c in cols]
        nexts = [
            jnp.where(lane < LANES - 1, turned[k], turned[k + 1]) for k in range(pieces - 1)
        ] + [turned[pieces - 1]]
        for i in range(inner_count):
            if forward:
                shift = tab_ref[0, i, o].astype(jnp.int32)
                wa = tab_ref[1, i, o]
                wb = tab_ref[2, i, o]
                offset = shift + HALO
            else:
                shift = tab_ref[0, o, i].astype(jnp.int32)
                wa = tab_ref[2, o, i]
                wb = tab_ref[1, o, i]
                offset = HALO - 1 - shift
            limit = LANES - offset
            amount = jnp.where(limit == LANES, 0, limit)
            mixed = [wa * cols[k] + wb * nexts[k] for k in range(pieces)]
            rolled = [pltpu.roll(m, amount, 1) for m in mixed]
            keep = lane < limit
            for j in range(out_pieces):
                out_ref[i, :, j * LANES : (j + 1) * LANES] += jnp.where(
                    keep, rolled[j], rolled[j + 1]
                )
        return carry

    lax.fori_loop(0, outer_count, outer, 0)


def shear_table(forward, table, src, inner_count, out_width):
    _, channels, _ = src.shape
    smem = pl.BlockSpec(memory_space=pltpu.SMEM)
    vmem = pl.BlockSpec(memory_space=pltpu.VMEM)
    return pl.pallas_call(
        functools.partial(shear_table_kernel, forward),
        out_shape=jax.ShapeDtypeStruct((inner_count, channels, out_width), jnp.float32),
        in_specs=[smem, vmem],
        out_specs=vmem,
        interpret=INTERPRET,
    )(table, src)


def halo_columns(ys, lane, half_of, rows_here, halves, channels):
    count = len(ys)
    turned = [pltpu.roll(y, HALO, 1) for y in ys]
    zero = jnp.zeros_like(ys[0])
    left = jnp.where(half_of >= 1, pltpu.roll(turned[count - 1], rows_here, 0), zero)
    right = jnp.where(half_of <= halves - 2, pltpu.roll(turned[0], channels - rows_here, 0), zero)
    edge = lane < HALO
    cols = [jnp.where(edge, left, turned[0])]
    cols += [jnp.where(edge, turned[k - 1], turned[k]) for k in range(1, count)]
    cols += [jnp.where(edge, turned[count - 1], right)]
    return cols


def shear_pass(forward, rows_here, halves, tab_ref, src_ref, acc_ref, cols_ref, nexts_ref):
    outer_count, channels, width = src_ref.shape
    inner_count = acc_ref.shape[0]
    pieces = width // LANES
    lane = lax.broadcasted_iota(jnp.int32, (channels, LANES), 1)
    half_of = (lax.broadcasted_iota(jnp.int32, (channels, LANES), 0) // rows_here) % halves

    def prepare(o, carry):
        ys = [src_ref[o, :, k * LANES : (k + 1) * LANES] for k in range(pieces)]
        cols = halo_columns(ys, lane, half_of, rows_here, halves, channels)
        turned = [pltpu.roll(c, LANES - 1, 1) for c in cols]
        nexts = [jnp.where(lane < LANES - 1, turned[k], turned[k + 1]) for k in range(pieces)]
        nexts.append(turned[pieces])
        for k in range(pieces + 1):
            cols_ref[o, :, k * LANES : (k + 1) * LANES] = cols[k]
            nexts_ref[o, :, k * LANES : (k + 1) * LANES] = nexts[k]
        return carry

    lax.fori_loop(0, outer_count, prepare, 0)

    for i in range(inner_count):

        def one_input(o, acc):
            if forward:
                shift = tab_ref[0, i, o].astype(jnp.int32)
                wa = tab_ref[1, i, o]
                wb = tab_ref[2, i, o]
                offset = shift + HALO
            else:
                shift = tab_ref[0, o, i].astype(jnp.int32)
                wa = tab_ref[2, o, i]
                wb = tab_ref[1, o, i]
                offset = HALO - 1 - shift
            limit = LANES - offset
            amount = jnp.where(limit == LANES, 0, limit)
            mixed = [
                wa * cols_ref[o, :, k * LANES : (k + 1) * LANES]
                + wb * nexts_ref[o, :, k * LANES : (k + 1) * LANES]
                for k in range(pieces + 1)
            ]
            rolled = [pltpu.roll(m, amount, 1) for m in mixed]
            keep = lane < limit
            return tuple(acc[j] + jnp.where(keep, rolled[j], rolled[j + 1]) for j in range(pieces))

        zero = jnp.zeros((channels, LANES), jnp.float32)
        acc = lax.fori_loop(0, outer_count, one_input, tuple(zero for _ in range(pieces)), unroll=True)
        for j in range(pieces):
            acc_ref[i, :, j * LANES : (j + 1) * LANES] = acc[j]


def scatter_pass(rows_here, halves, tab_ref, src_ref, out_ref, cols_ref, nexts_ref):
    outer_count, channels, width = src_ref.shape
    _, depth_here, _ = out_ref.shape
    materials = channels // (halves * rows_here)
    pieces = width // LANES
    lane = lax.broadcasted_iota(jnp.int32, (channels, LANES), 1)
    half_of = (lax.broadcasted_iota(jnp.int32, (channels, LANES), 0) // rows_here) % halves

    def prepare(o, carry):
        ys = [src_ref[o, :, k * LANES : (k + 1) * LANES] for k in range(pieces)]
        cols = halo_columns(ys, lane, half_of, rows_here, halves, channels)
        turned = [pltpu.roll(c, LANES - 1, 1) for c in cols]
        nexts = [jnp.where(lane < LANES - 1, turned[k], turned[k + 1]) for k in range(pieces)]
        nexts.append(turned[pieces])
        for k in range(pieces + 1):
            cols_ref[o, :, k * LANES : (k + 1) * LANES] = cols[k]
            nexts_ref[o, :, k * LANES : (k + 1) * LANES] = nexts[k]
        return carry

    lax.fori_loop(0, outer_count, prepare, 0)
    inner_count = tab_ref.shape[2]

    for i in range(inner_count):
        slab, level = divmod(i, depth_here)

        def one_view(o, acc):
            shift = tab_ref[0, o, i].astype(jnp.int32)
            wa = tab_ref[2, o, i]
            wb = tab_ref[1, o, i]
            offset = HALO - 1 - shift
            limit = LANES - offset
            amount = jnp.where(limit == LANES, 0, limit)
            mixed = [
                wa * cols_ref[o, :, k * LANES : (k + 1) * LANES]
                + wb * nexts_ref[o, :, k * LANES : (k + 1) * LANES]
                for k in range(pieces + 1)
            ]
            rolled = [pltpu.roll(m, amount, 1) for m in mixed]
            keep = lane < limit
            return tuple(acc[j] + jnp.where(keep, rolled[j], rolled[j + 1]) for j in range(pieces))

        zero = jnp.zeros((channels, LANES), jnp.float32)
        acc = lax.fori_loop(0, outer_count, one_view, tuple(zero for _ in range(pieces)), unroll=True)
        value = jnp.concatenate(acc, axis=1)
        for c in range(channels):
            material, rest = divmod(c, halves * rows_here)
            half, row = divmod(rest, rows_here)
            target = ((slab * halves + half) * rows_here + row) * materials + material
            out_ref[target, level : level + 1, :] = value[c : c + 1, :]


def forward_kernel(rows_here, halves, depth_all, views_all, tab_ref, emitted_ref, spectrum_ref,
                   attenuation_ref, src_ref, target_ref, out_ref, sums_ref, cols_ref, nexts_ref):
    shear_pass(True, rows_here, halves, tab_ref, src_ref, sums_ref, cols_ref, nexts_ref)
    _, channels, width = sums_ref.shape
    energies = spectrum_ref.shape[0]
    split = channels // 2
    low = lax.broadcasted_iota(jnp.int32, (channels, width), 0) < split

    def one_pair(p, carry):
        first_view = sums_ref[2 * p] / depth_all
        second_view = sums_ref[2 * p + 1] / depth_all
        water = jnp.where(low, first_view, pltpu.roll(second_view, split, 0))
        bone = jnp.where(low, pltpu.roll(first_view, split, 0), second_view)

        def one_energy(e, sums):
            intensity, first, second = sums
            a0 = attenuation_ref[0, e]
            a1 = attenuation_ref[1, e]
            counts = spectrum_ref[e] * jnp.exp((-a0) * water + (-a1) * bone)
            return (intensity + counts, first + a0 * counts, second + a1 * counts)

        zero = jnp.zeros((channels, width), jnp.float32)
        intensity, first, second = lax.fori_loop(0, energies, one_energy, (zero, zero, zero), unroll=True)
        residual = emitted_ref[0] - jnp.log(intensity) - target_ref[p]
        factor = residual / intensity / views_all
        first = (first * factor).astype(jnp.bfloat16).astype(jnp.float32)
        second = (second * factor).astype(jnp.bfloat16).astype(jnp.float32)
        out_ref[2 * p] = jnp.where(low, first, pltpu.roll(second, split, 0))
        out_ref[2 * p + 1] = jnp.where(low, pltpu.roll(first, split, 0), second)
        return carry

    lax.fori_loop(0, out_ref.shape[0] // 2, one_pair, 0)


def backward_kernel(rows_here, halves, tab_ref, src_ref, out_ref, cols_ref, nexts_ref):
    scatter_pass(rows_here, halves, tab_ref, src_ref, out_ref, cols_ref, nexts_ref)


def shear_apply(offset, wa, wb, src, out_width):
    outer_count, channels, width = src.shape
    inner_count = offset.shape[1]
    rot = (LANES - offset) % LANES
    thr = LANES - offset
    smem = pl.BlockSpec(memory_space=pltpu.SMEM)
    vmem = pl.BlockSpec(memory_space=pltpu.VMEM)
    return pl.pallas_call(
        shear_kernel,
        out_shape=jax.ShapeDtypeStruct((inner_count, channels, out_width), jnp.float32),
        in_specs=[smem, smem, smem, smem, vmem],
        out_specs=vmem,
        interpret=INTERPRET,
    )(rot.astype(jnp.int32), thr.astype(jnp.int32), wa, wb, src)


def rows_fit(density, measured):
    rows = density.shape[0]
    groups = lax.axis_size("views")
    depth = lax.axis_size("depth")
    tile_width = density.shape[3]
    return (
        rows % groups == 0
        and (rows // groups) % depth == 0
        and tile_width % LANES == 0
        and 2 * HALO == LANES
        and density.shape[1] == 2
        and measured.shape[0] * groups % 2 == 0
        and tile_width >= 3 * measured.shape[0] * density.shape[2] * groups
    )


def per_device_rows(density, measured, shear_shift, shear_frac, spectrum, attenuation):
    row_total, materials, depth_here, tile_width = density.shape
    groups = lax.axis_size("views")
    depth_count = lax.axis_size("depth")
    views_here = measured.shape[0]
    views_all = views_here * groups
    depth_all = depth_here * depth_count
    rows_group = row_total // groups
    rows_here = rows_group // depth_count
    group = lax.axis_index("views")
    slab = lax.axis_index("depth")

    lower_weight = (1.0 - shear_frac).astype(jnp.bfloat16).astype(jnp.float32)
    upper_weight = shear_frac.astype(jnp.bfloat16).astype(jnp.float32)
    table = jnp.stack([shear_shift.astype(jnp.float32), lower_weight, upper_weight])
    entries = table.size
    observed = measured.reshape(views_here, groups, rows_group, tile_width)
    observed = lax.dynamic_slice_in_dim(observed, slab * rows_here, rows_here, 2)
    observed = jnp.transpose(observed, (1, 0, 2, 3)).reshape(groups, views_here * rows_here, tile_width)
    extra = jnp.pad(table.reshape(1, entries), ((0, 0), (0, tile_width - entries)))
    extra = jnp.broadcast_to(extra[None], (groups, 1, tile_width))
    observed = jnp.concatenate([observed, extra], axis=1)
    observed = lax.all_to_all(observed, "views", 0, 0, tiled=True)
    table = observed[:, views_here * rows_here, :entries].reshape(groups, 3, views_here, depth_here)
    table = jnp.transpose(table, (1, 0, 2, 3)).reshape(3, views_all, depth_here)
    observed = observed[:, : views_here * rows_here].reshape(views_all, rows_here, tile_width)

    channels = rows_here * materials
    mine = lax.dynamic_slice_in_dim(density, group * rows_group, rows_group, 0)
    mine = mine.reshape(depth_count, rows_here, materials, depth_here, tile_width)
    mine = jnp.transpose(mine, (0, 3, 1, 2, 4)).reshape(depth_count, depth_here * channels, tile_width)
    wide = table.size
    extra = jnp.pad(table.reshape(1, wide), ((0, 0), (0, tile_width - wide))).astype(jnp.bfloat16)
    extra = jnp.broadcast_to(extra[None], (depth_count, 1, tile_width))
    mine = jnp.concatenate([mine, extra], axis=1)
    mine = lax.all_to_all(mine, "depth", 0, 0, tiled=True)
    table = mine[:, depth_here * channels, :wide].astype(jnp.float32)
    table = table.reshape(depth_count, 3, views_all, depth_here)
    table = jnp.transpose(table, (1, 2, 0, 3)).reshape(3, views_all, depth_all)
    shift_all = table[0].astype(jnp.int32)
    lower_all = table[1]
    upper_all = table[2]
    mine = mine[:, : depth_here * channels].reshape(depth_all, channels, tile_width)
    padded = with_halo(mine, (("lat", 2),), HALO).astype(jnp.float32)

    sums = shear_apply(
        (shift_all + HALO).T, lower_all.T, upper_all.T, padded, tile_width
    )
    sums = (sums / depth_all).reshape(views_all, rows_here, materials, tile_width)
    grads = spectral(sums, observed, spectrum, attenuation, views_all)
    grads = grads.reshape(views_all, rows_here * materials, tile_width)
    padded_grads = with_halo(grads, (("lat", 2),), HALO).astype(jnp.float32)
    layers = shear_apply(
        HALO - 1 - shift_all, upper_all, lower_all, padded_grads, tile_width
    )
    layers = layers.reshape(depth_count, depth_here, rows_here, materials, tile_width)
    layers = exchange(layers, "depth")
    return jnp.transpose(layers, (0, 2, 3, 1, 4)).reshape(rows_group, materials, depth_here, tile_width)


def rows_fit_wide(density, measured):
    rows = density.shape[0]
    groups = lax.axis_size("views")
    parts = lax.axis_size("depth") * lax.axis_size("lat")
    tile_width = density.shape[3]
    return (
        rows % groups == 0
        and (rows // groups) % parts == 0
        and tile_width % LANES == 0
        and 2 * HALO == LANES
        and density.shape[1] == 2
        and measured.shape[0] * groups % 2 == 0
        and tile_width >= 3 * measured.shape[0] * density.shape[2]
        and ((rows // groups // parts) * density.shape[1] * density.shape[2]) % groups == 0
    )


def stack_halves(values, halves, tile_width):
    count, rows, materials, _ = values.shape
    padded = jnp.pad(values, ((0, 0), (0, 0), (0, 0), (HALO, HALO)))
    parts = [
        padded[..., h * tile_width : h * tile_width + tile_width + 2 * HALO] for h in range(halves)
    ]
    return jnp.stack(parts, axis=1).reshape(count, halves * rows * materials, tile_width + 2 * HALO)


def join_halves(values, halves, rows, materials):
    count, _, tile_width = values.shape
    values = values.reshape(count, halves, rows, materials, tile_width)
    return jnp.transpose(values, (0, 2, 3, 1, 4)).reshape(count, rows, materials, halves * tile_width)


def per_device_wide(density, measured, shear_shift, shear_frac, spectrum, attenuation):
    row_total, materials, depth_here, tile_width = density.shape
    groups = lax.axis_size("views")
    depth_count = lax.axis_size("depth")
    halves = lax.axis_size("lat")
    parts = depth_count * halves
    views_here = measured.shape[0]
    views_all = views_here * groups
    depth_all = depth_here * depth_count
    rows_group = row_total // groups
    rows_here = rows_group // parts
    group = lax.axis_index("views")
    slab = lax.axis_index("depth")
    half = lax.axis_index("lat")

    lower_weight = (1.0 - shear_frac).astype(jnp.bfloat16).astype(jnp.float32)
    upper_weight = shear_frac.astype(jnp.bfloat16).astype(jnp.float32)
    block = jnp.stack([shear_shift.astype(jnp.float32), lower_weight, upper_weight])
    entries = block.size
    span = halves * rows_here
    observed = jnp.stack(
        [
            lax.dynamic_slice_in_dim(
                measured, (g * depth_count + slab) * span + h * rows_here, rows_here, 1
            ).reshape(views_here * rows_here, tile_width)
            for g in range(groups)
            for h in range(halves)
        ]
    )
    observed = lax.all_to_all(observed, ("views", "lat"), 0, 0, tiled=True)
    observed = observed.reshape(groups, halves, views_here, rows_here, tile_width)
    observed = jnp.transpose(observed, (0, 2, 3, 1, 4)).reshape(views_all, rows_here, halves * tile_width)

    chunk = rows_here * materials * depth_here * tile_width
    piece = chunk // groups
    mine = density.reshape(groups * parts, groups, piece)
    mine = lax.dynamic_index_in_dim(mine, group, 1, keepdims=False)
    mine = mine.reshape(groups * parts, piece // tile_width, tile_width)
    extra = jnp.pad(block.reshape(1, entries), ((0, 0), (0, tile_width - entries))).astype(jnp.bfloat16)
    extra = jnp.broadcast_to(extra[None], (groups * parts, 1, tile_width))
    mine = jnp.concatenate([mine, extra], axis=1)
    mine = lax.all_to_all(mine, ("views", "depth", "lat"), 0, 0, tiled=True)
    mine = mine.reshape(groups, depth_count, halves, piece // tile_width + 1, tile_width)
    table = mine[:, :, 0, piece // tile_width, :entries].astype(jnp.float32)
    table = table.reshape(groups, depth_count, 3, views_here, depth_here)
    table = jnp.transpose(table, (2, 0, 3, 1, 4)).reshape(3, views_all, depth_all)
    mine = mine[:, :, :, : piece // tile_width].reshape(groups, depth_count, halves, piece)
    mine = jnp.transpose(mine, (1, 2, 0, 3)).reshape(
        depth_count, halves, rows_here, materials, depth_here, tile_width
    )
    channels = materials * halves * rows_here
    mine = jnp.transpose(mine, (0, 4, 3, 1, 2, 5)).reshape(depth_all, channels, tile_width)
    mine = mine.astype(jnp.float32)
    target = observed.reshape(views_all // 2, 2, rows_here, halves, tile_width)
    target = jnp.transpose(target, (0, 1, 3, 2, 4)).reshape(views_all // 2, 2 * halves * rows_here, tile_width)
    emitted = jnp.log(jnp.sum(spectrum)).reshape(1)
    smem = pl.BlockSpec(memory_space=pltpu.SMEM)
    vmem = pl.BlockSpec(memory_space=pltpu.VMEM)
    grads = pl.pallas_call(
        functools.partial(forward_kernel, rows_here, halves, depth_all, views_all),
        out_shape=jax.ShapeDtypeStruct((views_all, channels, tile_width), jnp.float32),
        in_specs=[smem, smem, smem, smem, vmem, vmem],
        out_specs=vmem,
        scratch_shapes=[
            pltpu.VMEM((views_all, channels, tile_width), jnp.float32),
            pltpu.VMEM((depth_all, channels, tile_width + LANES), jnp.float32),
            pltpu.VMEM((depth_all, channels, tile_width + LANES), jnp.float32),
        ],
        interpret=INTERPRET,
    )(table, emitted, spectrum, attenuation, mine, target)
    layers = pl.pallas_call(
        functools.partial(backward_kernel, rows_here, halves),
        out_shape=jax.ShapeDtypeStruct((parts * rows_here * materials, depth_here, tile_width), jnp.float32),
        in_specs=[smem, vmem],
        out_specs=vmem,
        scratch_shapes=[
            pltpu.VMEM((views_all, channels, tile_width + LANES), jnp.float32),
            pltpu.VMEM((views_all, channels, tile_width + LANES), jnp.float32),
        ],
        interpret=INTERPRET,
    )(table, grads)
    layers = layers.reshape(parts, rows_here, materials, depth_here, tile_width)
    layers = lax.all_to_all(layers, ("depth", "lat"), 0, 0, tiled=True)
    return layers.reshape(rows_group, materials, depth_here, tile_width)


def per_device_any(density, measured, shear_shift, shear_frac, spectrum, attenuation):
    if rows_fit_wide(density, measured):
        return per_device_wide(density, measured, shear_shift, shear_frac, spectrum, attenuation)
    if rows_fit(density, measured):
        return per_device_rows(density, measured, shear_shift, shear_frac, spectrum, attenuation)
    return per_device(density, measured, shear_shift, shear_frac, spectrum, attenuation)


def solution(mesh):
    in_specs = (
        P(None, None, "depth", "lat"),
        P("views", None, "lat"),
        P("views", "depth"),
        P("views", "depth"),
        P(),
        P(),
    )
    out_specs = P("views", None, "depth", "lat")
    return jax.shard_map(
        per_device_any, mesh=mesh, in_specs=in_specs, out_specs=out_specs, check_vma=False
    )
```

```python
import functools
import jax
import jax.numpy as jnp
from jax import lax
from jax.sharding import PartitionSpec as P
from jax.experimental import pallas as pl
from jax.experimental.pallas import tpu as pltpu

HALO = 64


def with_halo(x, sides, width):
    for axis, dim in sides:
        size, length = (lax.axis_size(axis), x.shape[dim])
        up = [(i, (i + 1) % size) for i in range(size - 1)]
        down = [(j, i) for i, j in up]
        last = lax.slice_in_dim(x, length - width, length, axis=dim)
        first = lax.slice_in_dim(x, 0, width, axis=dim)
        before = lax.ppermute(last, axis, up)
        after = lax.ppermute(first, axis, down)
        x = jnp.concatenate([before, x, after], axis=dim)
    return x


def exchange(x, axis):
    count = lax.axis_size(axis)
    me = lax.axis_index(axis)
    result = x
    for step in range(1, count):
        pairs = [(i, (i + step) % count) for i in range(count)]
        part = lax.dynamic_index_in_dim(x, (me + step) % count, 0, keepdims=True)
        part = lax.ppermute(part, axis, pairs)
        result = lax.dynamic_update_index_in_dim(result, part, (me - step) % count, 0)
    return result


def band_forward(shear_shift, lower_weight, upper_weight, window, block_width):
    band_shape = (shear_shift.shape[1], window, shear_shift.shape[0], block_width)
    tap_index = lax.broadcasted_iota(jnp.int32, band_shape, 1)
    column = lax.broadcasted_iota(jnp.int32, band_shape, 3)
    anchor = (shear_shift.T + HALO)[:, None, :, None]
    nothing = jnp.zeros((), jnp.bfloat16)
    lower_part = jnp.where(tap_index == column + anchor, lower_weight.T[:, None, :, None], nothing)
    upper_part = jnp.where(
        tap_index == column + anchor + 1, upper_weight.T[:, None, :, None], nothing
    )
    return lower_part + upper_part


def band_backward(shear_shift, lower_weight, upper_weight, window, block_width):
    band_shape = (shear_shift.shape[0], window, shear_shift.shape[1], block_width)
    tap_index = lax.broadcasted_iota(jnp.int32, band_shape, 1)
    column = lax.broadcasted_iota(jnp.int32, band_shape, 3)
    anchor = (HALO - shear_shift)[:, None, :, None]
    nothing = jnp.zeros((), jnp.bfloat16)
    lower_part = jnp.where(tap_index == column + anchor, lower_weight[:, None, :, None], nothing)
    upper_part = jnp.where(
        tap_index == column + anchor - 1, upper_weight[:, None, :, None], nothing
    )
    return lower_part + upper_part


def spectral(path_sums, observed, spectrum, attenuation, views_all):
    view_count, row_count, materials, tile_width = path_sums.shape
    block_pixels = 4096
    path_water = path_sums[:, :, 0, :].reshape(-1, block_pixels)
    path_bone = path_sums[:, :, 1, :].reshape(-1, block_pixels)
    target_flat = observed.reshape(-1, block_pixels)
    coefficients = jnp.concatenate(
        [jnp.ones((1, spectrum.shape[0]), jnp.float32), attenuation], axis=0
    )
    emitted = jnp.log(jnp.sum(spectrum))

    def one_block(inputs):
        water_block, bone_block, target_block = inputs
        exponent = (
            attenuation[0][:, None] * water_block[None, :]
            + attenuation[1][:, None] * bone_block[None, :]
        )
        counts = spectrum[:, None] * jnp.exp(-exponent)
        moments = jnp.dot(coefficients, counts, precision=lax.Precision.HIGHEST)
        intensity = moments[0]
        residual = emitted - jnp.log(intensity) - target_block
        factor = residual / intensity / views_all
        return (moments[1:] * factor[None, :]).astype(jnp.bfloat16)

    stacked = lax.map(one_block, (path_water, path_bone, target_flat))
    gradients = jnp.swapaxes(stacked, 0, 1).reshape(materials, view_count, row_count, tile_width)
    return jnp.transpose(gradients, (1, 2, 0, 3))


def spectral_kernel(views_all, emitted_ref, spectrum_ref, attenuation_ref, water_ref, bone_ref, target_ref, out0_ref, out1_ref):
    rows, width = water_ref.shape
    energies = spectrum_ref.shape[0]
    block = 8

    def one_block(b, carry):
        lo = pl.multiple_of(b * block, block)
        water = water_ref[pl.ds(lo, block), :]
        bone = bone_ref[pl.ds(lo, block), :]

        def one_energy(e, sums):
            intensity, first, second = sums
            a0 = attenuation_ref[0, e]
            a1 = attenuation_ref[1, e]
            counts = spectrum_ref[e] * jnp.exp(-(a0 * water + a1 * bone))
            return (intensity + counts, first + a0 * counts, second + a1 * counts)

        zero = jnp.zeros((block, width), jnp.float32)
        intensity, first, second = lax.fori_loop(0, energies, one_energy, (zero, zero, zero), unroll=8)
        residual = emitted_ref[0] - jnp.log(intensity) - target_ref[pl.ds(lo, block), :]
        factor = residual / intensity / views_all
        out0_ref[pl.ds(lo, block), :] = (first * factor).astype(out0_ref.dtype)
        out1_ref[pl.ds(lo, block), :] = (second * factor).astype(out1_ref.dtype)
        return carry

    lax.fori_loop(0, rows // block, one_block, 0)


def spectral_pallas(path_sums, observed, spectrum, attenuation, views_all):
    view_count, row_count, materials, width_all = path_sums.shape
    pixels = view_count * row_count * width_all
    rows = pixels // LANES // 4
    water = path_sums[:, :, 0, :].reshape(rows, 4 * LANES)
    bone = path_sums[:, :, 1, :].reshape(rows, 4 * LANES)
    target = observed.reshape(rows, 4 * LANES)
    emitted = jnp.log(jnp.sum(spectrum)).reshape(1)
    smem = pl.BlockSpec(memory_space=pltpu.SMEM)
    vmem = pl.BlockSpec(memory_space=pltpu.VMEM)
    first, second = pl.pallas_call(
        functools.partial(spectral_kernel, views_all),
        out_shape=(
            jax.ShapeDtypeStruct((rows, 4 * LANES), jnp.bfloat16),
            jax.ShapeDtypeStruct((rows, 4 * LANES), jnp.bfloat16),
        ),
        in_specs=[smem, smem, smem, vmem, vmem, vmem],
        out_specs=(vmem, vmem),
        interpret=INTERPRET,
    )(emitted, spectrum, attenuation, water, bone, target)
    shape = (view_count, row_count, width_all)
    return jnp.stack([first.reshape(shape), second.reshape(shape)], axis=2)


def per_device(density, measured, shear_shift, shear_frac, spectrum, attenuation):
    row_total, materials, depth_here, tile_width = density.shape
    block_width = min(128, tile_width)
    block_count = tile_width // block_width
    window = block_width + 2 * HALO
    views_all = measured.shape[0] * lax.axis_size("views")
    depth_all = depth_here * lax.axis_size("depth")
    rows_out = row_total // lax.axis_size("views")
    lower_weight = (1.0 - shear_frac).astype(jnp.bfloat16)
    upper_weight = shear_frac.astype(jnp.bfloat16)
    rows_here = density.shape[0]
    padded = with_halo(density, (("lat", 3),), HALO)
    framed = jnp.stack(
        [
            padded[:, :, :, number * block_width : number * block_width + window]
            for number in range(block_count)
        ],
        axis=2,
    )
    forward_band = band_forward(shear_shift, lower_weight, upper_weight, window, block_width)
    partial_value = jnp.einsum(
        "ymnzi,zivc->vymnc", framed, forward_band, preferred_element_type=jnp.float32
    )
    partial_value = partial_value.reshape(shear_shift.shape[0], rows_here, materials, tile_width)
    shares = lax.psum_scatter(partial_value, "depth", scatter_dimension=3, tiled=True) / depth_all
    share_cols = shares.shape[3]
    observed = lax.dynamic_slice_in_dim(
        measured, lax.axis_index("depth") * share_cols, share_cols, 2
    )
    share_grads = spectral(shares, observed, spectrum, attenuation, views_all)
    path_grads = lax.all_gather(share_grads, "depth", axis=3, tiled=True)
    padded_grads = with_halo(path_grads, (("lat", 3),), HALO)
    framed_grads = jnp.stack(
        [
            padded_grads[:, :, :, number * block_width : number * block_width + window]
            for number in range(block_count)
        ],
        axis=3,
    )
    backward_band = band_backward(shear_shift, lower_weight, upper_weight, window, block_width)
    product = jnp.einsum(
        "vymni,vizc->ymznc", framed_grads, backward_band, preferred_element_type=jnp.float32
    )
    return lax.psum_scatter(
        product.reshape(rows_out * lax.axis_size("views"), materials, depth_here, tile_width),
        "views",
        scatter_dimension=0,
        tiled=True,
    )


LANES = 128
INTERPRET = False


def shear_kernel(rot_ref, thr_ref, wa_ref, wb_ref, src_ref, out_ref):
    outer_count, channels, width = src_ref.shape
    inner_count, _, out_width = out_ref.shape
    pieces = width // LANES
    out_pieces = out_width // LANES
    out_ref[...] = jnp.zeros(out_ref.shape, jnp.float32)
    lane = lax.broadcasted_iota(jnp.int32, (channels, LANES), 1)

    def outer(o, carry):
        cols = [src_ref[o, :, k * LANES : (k + 1) * LANES] for k in range(pieces)]
        turned = [pltpu.roll(c, LANES - 1, 1) for c in cols]
        nexts = [
            jnp.where(lane < LANES - 1, turned[k], turned[k + 1]) for k in range(pieces - 1)
        ] + [turned[pieces - 1]]
        for i in range(inner_count):
            wa = wa_ref[o, i]
            wb = wb_ref[o, i]
            mixed = [wa * cols[k] + wb * nexts[k] for k in range(pieces)]
            rolled = [pltpu.roll(m, rot_ref[o, i], 1) for m in mixed]
            keep = lane < thr_ref[o, i]
            for j in range(out_pieces):
                out_ref[i, :, j * LANES : (j + 1) * LANES] += jnp.where(
                    keep, rolled[j], rolled[j + 1]
                )
        return carry

    lax.fori_loop(0, outer_count, outer, 0)


def shear_table_kernel(forward, tab_ref, src_ref, out_ref):
    outer_count, channels, width = src_ref.shape
    inner_count, _, out_width = out_ref.shape
    pieces = width // LANES
    out_pieces = out_width // LANES
    out_ref[...] = jnp.zeros(out_ref.shape, jnp.float32)
    lane = lax.broadcasted_iota(jnp.int32, (channels, LANES), 1)

    def outer(o, carry):
        cols = [src_ref[o, :, k * LANES : (k + 1) * LANES] for k in range(pieces)]
        turned = [pltpu.roll(c, LANES - 1, 1) for c in cols]
        nexts = [
            jnp.where(lane < LANES - 1, turned[k], turned[k + 1]) for k in range(pieces - 1)
        ] + [turned[pieces - 1]]
        for i in range(inner_count):
            if forward:
                shift = tab_ref[0, i, o].astype(jnp.int32)
                wa = tab_ref[1, i, o]
                wb = tab_ref[2, i, o]
                offset = shift + HALO
            else:
                shift = tab_ref[0, o, i].astype(jnp.int32)
                wa = tab_ref[2, o, i]
                wb = tab_ref[1, o, i]
                offset = HALO - 1 - shift
            limit = LANES - offset
            amount = jnp.where(limit == LANES, 0, limit)
            mixed = [wa * cols[k] + wb * nexts[k] for k in range(pieces)]
            rolled = [pltpu.roll(m, amount, 1) for m in mixed]
            keep = lane < limit
            for j in range(out_pieces):
                out_ref[i, :, j * LANES : (j + 1) * LANES] += jnp.where(
                    keep, rolled[j], rolled[j + 1]
                )
        return carry

    lax.fori_loop(0, outer_count, outer, 0)


def shear_table(forward, table, src, inner_count, out_width):
    _, channels, _ = src.shape
    smem = pl.BlockSpec(memory_space=pltpu.SMEM)
    vmem = pl.BlockSpec(memory_space=pltpu.VMEM)
    return pl.pallas_call(
        functools.partial(shear_table_kernel, forward),
        out_shape=jax.ShapeDtypeStruct((inner_count, channels, out_width), jnp.float32),
        in_specs=[smem, vmem],
        out_specs=vmem,
        interpret=INTERPRET,
    )(table, src)


def halo_columns(ys, lane, half_of, rows_here, halves, channels):
    count = len(ys)
    turned = [pltpu.roll(y, HALO, 1) for y in ys]
    zero = jnp.zeros_like(ys[0])
    left = jnp.where(half_of >= 1, pltpu.roll(turned[count - 1], rows_here, 0), zero)
    right = jnp.where(half_of <= halves - 2, pltpu.roll(turned[0], channels - rows_here, 0), zero)
    edge = lane < HALO
    cols = [jnp.where(edge, left, turned[0])]
    cols += [jnp.where(edge, turned[k - 1], turned[k]) for k in range(1, count)]
    cols += [jnp.where(edge, turned[count - 1], right)]
    return cols


def shear_pass(forward, rows_here, halves, tab_ref, src_ref, acc_ref, cols_ref, nexts_ref):
    outer_count, channels, width = src_ref.shape
    inner_count = acc_ref.shape[0]
    pieces = width // LANES
    lane = lax.broadcasted_iota(jnp.int32, (channels, LANES), 1)
    half_of = (lax.broadcasted_iota(jnp.int32, (channels, LANES), 0) // rows_here) % halves

    def prepare(o, carry):
        ys = [src_ref[o, :, k * LANES : (k + 1) * LANES] for k in range(pieces)]
        cols = halo_columns(ys, lane, half_of, rows_here, halves, channels)
        turned = [pltpu.roll(c, LANES - 1, 1) for c in cols]
        nexts = [jnp.where(lane < LANES - 1, turned[k], turned[k + 1]) for k in range(pieces)]
        nexts.append(turned[pieces])
        for k in range(pieces + 1):
            cols_ref[o, :, k * LANES : (k + 1) * LANES] = cols[k]
            nexts_ref[o, :, k * LANES : (k + 1) * LANES] = nexts[k]
        return carry

    lax.fori_loop(0, outer_count, prepare, 0)

    for i in range(inner_count):

        def one_input(o, acc):
            if forward:
                shift = tab_ref[0, i, o].astype(jnp.int32)
                wa = tab_ref[1, i, o]
                wb = tab_ref[2, i, o]
                offset = shift + HALO
            else:
                shift = tab_ref[0, o, i].astype(jnp.int32)
                wa = tab_ref[2, o, i]
                wb = tab_ref[1, o, i]
                offset = HALO - 1 - shift
            limit = LANES - offset
            amount = jnp.where(limit == LANES, 0, limit)
            mixed = [
                wa * cols_ref[o, :, k * LANES : (k + 1) * LANES]
                + wb * nexts_ref[o, :, k * LANES : (k + 1) * LANES]
                for k in range(pieces + 1)
            ]
            rolled = [pltpu.roll(m, amount, 1) for m in mixed]
            keep = lane < limit
            return tuple(acc[j] + jnp.where(keep, rolled[j], rolled[j + 1]) for j in range(pieces))

        zero = jnp.zeros((channels, LANES), jnp.float32)
        acc = lax.fori_loop(0, outer_count, one_input, tuple(zero for _ in range(pieces)), unroll=True)
        for j in range(pieces):
            acc_ref[i, :, j * LANES : (j + 1) * LANES] = acc[j]


def scatter_pass(rows_here, halves, tab_ref, src_ref, out_ref, cols_ref, nexts_ref):
    outer_count, channels, width = src_ref.shape
    _, depth_here, _ = out_ref.shape
    materials = channels // (halves * rows_here)
    pieces = width // LANES
    lane = lax.broadcasted_iota(jnp.int32, (channels, LANES), 1)
    half_of = (lax.broadcasted_iota(jnp.int32, (channels, LANES), 0) // rows_here) % halves

    def prepare(o, carry):
        ys = [src_ref[o, :, k * LANES : (k + 1) * LANES] for k in range(pieces)]
        cols = halo_columns(ys, lane, half_of, rows_here, halves, channels)
        turned = [pltpu.roll(c, LANES - 1, 1) for c in cols]
        nexts = [jnp.where(lane < LANES - 1, turned[k], turned[k + 1]) for k in range(pieces)]
        nexts.append(turned[pieces])
        for k in range(pieces + 1):
            cols_ref[o, :, k * LANES : (k + 1) * LANES] = cols[k]
            nexts_ref[o, :, k * LANES : (k + 1) * LANES] = nexts[k]
        return carry

    lax.fori_loop(0, outer_count, prepare, 0)
    inner_count = tab_ref.shape[2]

    for i in range(inner_count):
        slab, level = divmod(i, depth_here)

        def one_view(o, acc):
            shift = tab_ref[0, o, i].astype(jnp.int32)
            wa = tab_ref[2, o, i]
            wb = tab_ref[1, o, i]
            offset = HALO - 1 - shift
            limit = LANES - offset
            amount = jnp.where(limit == LANES, 0, limit)
            mixed = [
                wa * cols_ref[o, :, k * LANES : (k + 1) * LANES]
                + wb * nexts_ref[o, :, k * LANES : (k + 1) * LANES]
                for k in range(pieces + 1)
            ]
            rolled = [pltpu.roll(m, amount, 1) for m in mixed]
            keep = lane < limit
            return tuple(acc[j] + jnp.where(keep, rolled[j], rolled[j + 1]) for j in range(pieces))

        zero = jnp.zeros((channels, LANES), jnp.float32)
        acc = lax.fori_loop(0, outer_count, one_view, tuple(zero for _ in range(pieces)), unroll=True)
        value = jnp.concatenate(acc, axis=1)
        for c in range(channels):
            material, rest = divmod(c, halves * rows_here)
            half, row = divmod(rest, rows_here)
            target = ((slab * halves + half) * rows_here + row) * materials + material
            out_ref[target, level : level + 1, :] = value[c : c + 1, :]


def forward_kernel(rows_here, halves, depth_all, views_all, tab_ref, emitted_ref, spectrum_ref,
                   attenuation_ref, src_ref, target_ref, out_ref, sums_ref, cols_ref, nexts_ref):
    shear_pass(True, rows_here, halves, tab_ref, src_ref, sums_ref, cols_ref, nexts_ref)
    _, channels, width = sums_ref.shape
    energies = spectrum_ref.shape[0]
    split = channels // 2
    low = lax.broadcasted_iota(jnp.int32, (channels, width), 0) < split

    def one_pair(p, carry):
        first_view = sums_ref[2 * p] / depth_all
        second_view = sums_ref[2 * p + 1] / depth_all
        water = jnp.where(low, first_view, pltpu.roll(second_view, split, 0))
        bone = jnp.where(low, pltpu.roll(first_view, split, 0), second_view)

        def one_energy(e, sums):
            intensity, first, second = sums
            a0 = attenuation_ref[0, e]
            a1 = attenuation_ref[1, e]
            counts = spectrum_ref[e] * jnp.exp((-a0) * water + (-a1) * bone)
            return (intensity + counts, first + a0 * counts, second + a1 * counts)

        zero = jnp.zeros((channels, width), jnp.float32)
        intensity, first, second = lax.fori_loop(0, energies, one_energy, (zero, zero, zero), unroll=True)
        residual = emitted_ref[0] - jnp.log(intensity) - target_ref[p]
        factor = residual / intensity / views_all
        first = (first * factor).astype(jnp.bfloat16).astype(jnp.float32)
        second = (second * factor).astype(jnp.bfloat16).astype(jnp.float32)
        out_ref[2 * p] = jnp.where(low, first, pltpu.roll(second, split, 0))
        out_ref[2 * p + 1] = jnp.where(low, pltpu.roll(first, split, 0), second)
        return carry

    lax.fori_loop(0, out_ref.shape[0] // 2, one_pair, 0, unroll=True)


def backward_kernel(rows_here, halves, tab_ref, src_ref, out_ref, cols_ref, nexts_ref):
    scatter_pass(rows_here, halves, tab_ref, src_ref, out_ref, cols_ref, nexts_ref)


def shear_apply(offset, wa, wb, src, out_width):
    outer_count, channels, width = src.shape
    inner_count = offset.shape[1]
    rot = (LANES - offset) % LANES
    thr = LANES - offset
    smem = pl.BlockSpec(memory_space=pltpu.SMEM)
    vmem = pl.BlockSpec(memory_space=pltpu.VMEM)
    return pl.pallas_call(
        shear_kernel,
        out_shape=jax.ShapeDtypeStruct((inner_count, channels, out_width), jnp.float32),
        in_specs=[smem, smem, smem, smem, vmem],
        out_specs=vmem,
        interpret=INTERPRET,
    )(rot.astype(jnp.int32), thr.astype(jnp.int32), wa, wb, src)


def rows_fit(density, measured):
    rows = density.shape[0]
    groups = lax.axis_size("views")
    depth = lax.axis_size("depth")
    tile_width = density.shape[3]
    return (
        rows % groups == 0
        and (rows // groups) % depth == 0
        and tile_width % LANES == 0
        and 2 * HALO == LANES
        and density.shape[1] == 2
        and measured.shape[0] * groups % 2 == 0
        and tile_width >= 3 * measured.shape[0] * density.shape[2] * groups
    )


def per_device_rows(density, measured, shear_shift, shear_frac, spectrum, attenuation):
    row_total, materials, depth_here, tile_width = density.shape
    groups = lax.axis_size("views")
    depth_count = lax.axis_size("depth")
    views_here = measured.shape[0]
    views_all = views_here * groups
    depth_all = depth_here * depth_count
    rows_group = row_total // groups
    rows_here = rows_group // depth_count
    group = lax.axis_index("views")
    slab = lax.axis_index("depth")

    lower_weight = (1.0 - shear_frac).astype(jnp.bfloat16).astype(jnp.float32)
    upper_weight = shear_frac.astype(jnp.bfloat16).astype(jnp.float32)
    table = jnp.stack([shear_shift.astype(jnp.float32), lower_weight, upper_weight])
    entries = table.size
    observed = measured.reshape(views_here, groups, rows_group, tile_width)
    observed = lax.dynamic_slice_in_dim(observed, slab * rows_here, rows_here, 2)
    observed = jnp.transpose(observed, (1, 0, 2, 3)).reshape(groups, views_here * rows_here, tile_width)
    extra = jnp.pad(table.reshape(1, entries), ((0, 0), (0, tile_width - entries)))
    extra = jnp.broadcast_to(extra[None], (groups, 1, tile_width))
    observed = jnp.concatenate([observed, extra], axis=1)
    observed = lax.all_to_all(observed, "views", 0, 0, tiled=True)
    table = observed[:, views_here * rows_here, :entries].reshape(groups, 3, views_here, depth_here)
    table = jnp.transpose(table, (1, 0, 2, 3)).reshape(3, views_all, depth_here)
    observed = observed[:, : views_here * rows_here].reshape(views_all, rows_here, tile_width)

    channels = rows_here * materials
    mine = lax.dynamic_slice_in_dim(density, group * rows_group, rows_group, 0)
    mine = mine.reshape(depth_count, rows_here, materials, depth_here, tile_width)
    mine = jnp.transpose(mine, (0, 3, 1, 2, 4)).reshape(depth_count, depth_here * channels, tile_width)
    wide = table.size
    extra = jnp.pad(table.reshape(1, wide), ((0, 0), (0, tile_width - wide))).astype(jnp.bfloat16)
    extra = jnp.broadcast_to(extra[None], (depth_count, 1, tile_width))
    mine = jnp.concatenate([mine, extra], axis=1)
    mine = lax.all_to_all(mine, "depth", 0, 0, tiled=True)
    table = mine[:, depth_here * channels, :wide].astype(jnp.float32)
    table = table.reshape(depth_count, 3, views_all, depth_here)
    table = jnp.transpose(table, (1, 2, 0, 3)).reshape(3, views_all, depth_all)
    shift_all = table[0].astype(jnp.int32)
    lower_all = table[1]
    upper_all = table[2]
    mine = mine[:, : depth_here * channels].reshape(depth_all, channels, tile_width)
    padded = with_halo(mine, (("lat", 2),), HALO).astype(jnp.float32)

    sums = shear_apply(
        (shift_all + HALO).T, lower_all.T, upper_all.T, padded, tile_width
    )
    sums = (sums / depth_all).reshape(views_all, rows_here, materials, tile_width)
    grads = spectral(sums, observed, spectrum, attenuation, views_all)
    grads = grads.reshape(views_all, rows_here * materials, tile_width)
    padded_grads = with_halo(grads, (("lat", 2),), HALO).astype(jnp.float32)
    layers = shear_apply(
        HALO - 1 - shift_all, upper_all, lower_all, padded_grads, tile_width
    )
    layers = layers.reshape(depth_count, depth_here, rows_here, materials, tile_width)
    layers = exchange(layers, "depth")
    return jnp.transpose(layers, (0, 2, 3, 1, 4)).reshape(rows_group, materials, depth_here, tile_width)


def rows_fit_wide(density, measured):
    rows = density.shape[0]
    groups = lax.axis_size("views")
    parts = lax.axis_size("depth") * lax.axis_size("lat")
    tile_width = density.shape[3]
    return (
        rows % groups == 0
        and (rows // groups) % parts == 0
        and tile_width % LANES == 0
        and 2 * HALO == LANES
        and density.shape[1] == 2
        and measured.shape[0] * groups % 2 == 0
        and tile_width >= 3 * measured.shape[0] * density.shape[2]
        and ((rows // groups // parts) * density.shape[1] * density.shape[2]) % groups == 0
    )


def stack_halves(values, halves, tile_width):
    count, rows, materials, _ = values.shape
    padded = jnp.pad(values, ((0, 0), (0, 0), (0, 0), (HALO, HALO)))
    parts = [
        padded[..., h * tile_width : h * tile_width + tile_width + 2 * HALO] for h in range(halves)
    ]
    return jnp.stack(parts, axis=1).reshape(count, halves * rows * materials, tile_width + 2 * HALO)


def join_halves(values, halves, rows, materials):
    count, _, tile_width = values.shape
    values = values.reshape(count, halves, rows, materials, tile_width)
    return jnp.transpose(values, (0, 2, 3, 1, 4)).reshape(count, rows, materials, halves * tile_width)


def per_device_wide(density, measured, shear_shift, shear_frac, spectrum, attenuation):
    row_total, materials, depth_here, tile_width = density.shape
    groups = lax.axis_size("views")
    depth_count = lax.axis_size("depth")
    halves = lax.axis_size("lat")
    parts = depth_count * halves
    views_here = measured.shape[0]
    views_all = views_here * groups
    depth_all = depth_here * depth_count
    rows_group = row_total // groups
    rows_here = rows_group // parts
    group = lax.axis_index("views")
    slab = lax.axis_index("depth")
    half = lax.axis_index("lat")

    lower_weight = (1.0 - shear_frac).astype(jnp.bfloat16).astype(jnp.float32)
    upper_weight = shear_frac.astype(jnp.bfloat16).astype(jnp.float32)
    block = jnp.stack([shear_shift.astype(jnp.float32), lower_weight, upper_weight])
    entries = block.size
    span = halves * rows_here
    observed = jnp.stack(
        [
            lax.dynamic_slice_in_dim(measured, (g * depth_count + slab) * span, span, 1)
            for g in range(groups)
        ]
    )
    observed = observed.reshape(groups, views_here, halves, rows_here, tile_width)
    observed = jnp.transpose(observed, (0, 2, 1, 3, 4)).reshape(
        groups * halves, views_here * rows_here, tile_width
    )
    observed = lax.all_to_all(observed, ("views", "lat"), 0, 0, tiled=True)
    observed = observed.reshape(groups, halves, views_here, rows_here, tile_width)
    observed = jnp.transpose(observed, (0, 2, 3, 1, 4)).reshape(views_all, rows_here, halves * tile_width)

    chunk = rows_here * materials * depth_here * tile_width
    piece = chunk // groups
    mine = density.reshape(groups * parts, groups, piece)
    mine = lax.dynamic_index_in_dim(mine, group, 1, keepdims=False)
    mine = mine.reshape(groups * parts, piece // tile_width, tile_width)
    extra = jnp.pad(block.reshape(1, entries), ((0, 0), (0, tile_width - entries))).astype(jnp.bfloat16)
    extra = jnp.broadcast_to(extra[None], (groups * parts, 1, tile_width))
    mine = jnp.concatenate([mine, extra], axis=1)
    mine = lax.all_to_all(mine, ("views", "depth", "lat"), 0, 0, tiled=True)
    mine = mine.reshape(groups, depth_count, halves, piece // tile_width + 1, tile_width)
    table = mine[:, :, 0, piece // tile_width, :entries].astype(jnp.float32)
    table = table.reshape(groups, depth_count, 3, views_here, depth_here)
    table = jnp.transpose(table, (2, 0, 3, 1, 4)).reshape(3, views_all, depth_all)
    mine = mine[:, :, :, : piece // tile_width].reshape(groups, depth_count, halves, piece)
    mine = jnp.transpose(mine, (1, 2, 0, 3)).reshape(
        depth_count, halves, rows_here, materials, depth_here, tile_width
    )
    channels = materials * halves * rows_here
    mine = jnp.transpose(mine, (0, 4, 3, 1, 2, 5)).reshape(depth_all, channels, tile_width)
    mine = mine.astype(jnp.float32)
    target = observed.reshape(views_all // 2, 2, rows_here, halves, tile_width)
    target = jnp.transpose(target, (0, 1, 3, 2, 4)).reshape(views_all // 2, 2 * halves * rows_here, tile_width)
    emitted = jnp.log(jnp.sum(spectrum)).reshape(1)
    smem = pl.BlockSpec(memory_space=pltpu.SMEM)
    vmem = pl.BlockSpec(memory_space=pltpu.VMEM)
    grads = pl.pallas_call(
        functools.partial(forward_kernel, rows_here, halves, depth_all, views_all),
        out_shape=jax.ShapeDtypeStruct((views_all, channels, tile_width), jnp.float32),
        in_specs=[smem, smem, smem, smem, vmem, vmem],
        out_specs=vmem,
        scratch_shapes=[
            pltpu.VMEM((views_all, channels, tile_width), jnp.float32),
            pltpu.VMEM((depth_all, channels, tile_width + LANES), jnp.float32),
            pltpu.VMEM((depth_all, channels, tile_width + LANES), jnp.float32),
        ],
        interpret=INTERPRET,
    )(table, emitted, spectrum, attenuation, mine, target)
    layers = pl.pallas_call(
        functools.partial(backward_kernel, rows_here, halves),
        out_shape=jax.ShapeDtypeStruct((parts * rows_here * materials, depth_here, tile_width), jnp.float32),
        in_specs=[smem, vmem],
        out_specs=vmem,
        scratch_shapes=[
            pltpu.VMEM((views_all, channels, tile_width + LANES), jnp.float32),
            pltpu.VMEM((views_all, channels, tile_width + LANES), jnp.float32),
        ],
        interpret=INTERPRET,
    )(table, grads)
    layers = layers.reshape(parts, rows_here, materials, depth_here, tile_width)
    layers = lax.all_to_all(layers, ("depth", "lat"), 0, 0, tiled=True)
    return layers.reshape(rows_group, materials, depth_here, tile_width)


def per_device_any(density, measured, shear_shift, shear_frac, spectrum, attenuation):
    if rows_fit_wide(density, measured):
        return per_device_wide(density, measured, shear_shift, shear_frac, spectrum, attenuation)
    if rows_fit(density, measured):
        return per_device_rows(density, measured, shear_shift, shear_frac, spectrum, attenuation)
    return per_device(density, measured, shear_shift, shear_frac, spectrum, attenuation)


def solution(mesh):
    in_specs = (
        P(None, None, "depth", "lat"),
        P("views", None, "lat"),
        P("views", "depth"),
        P("views", "depth"),
        P(),
        P(),
    )
    out_specs = P("views", None, "depth", "lat")
    return jax.shard_map(
        per_device_any, mesh=mesh, in_specs=in_specs, out_specs=out_specs, check_vma=False
    )
```

```python
import functools
import jax
import jax.numpy as jnp
from jax import lax
from jax.sharding import PartitionSpec as P
from jax.experimental import pallas as pl
from jax.experimental.pallas import tpu as pltpu

HALO = 64


def with_halo(x, sides, width):
    for axis, dim in sides:
        size, length = (lax.axis_size(axis), x.shape[dim])
        up = [(i, (i + 1) % size) for i in range(size - 1)]
        down = [(j, i) for i, j in up]
        last = lax.slice_in_dim(x, length - width, length, axis=dim)
        first = lax.slice_in_dim(x, 0, width, axis=dim)
        before = lax.ppermute(last, axis, up)
        after = lax.ppermute(first, axis, down)
        x = jnp.concatenate([before, x, after], axis=dim)
    return x


def exchange(x, axis):
    count = lax.axis_size(axis)
    me = lax.axis_index(axis)
    result = x
    for step in range(1, count):
        pairs = [(i, (i + step) % count) for i in range(count)]
        part = lax.dynamic_index_in_dim(x, (me + step) % count, 0, keepdims=True)
        part = lax.ppermute(part, axis, pairs)
        result = lax.dynamic_update_index_in_dim(result, part, (me - step) % count, 0)
    return result


def band_forward(shear_shift, lower_weight, upper_weight, window, block_width):
    band_shape = (shear_shift.shape[1], window, shear_shift.shape[0], block_width)
    tap_index = lax.broadcasted_iota(jnp.int32, band_shape, 1)
    column = lax.broadcasted_iota(jnp.int32, band_shape, 3)
    anchor = (shear_shift.T + HALO)[:, None, :, None]
    nothing = jnp.zeros((), jnp.bfloat16)
    lower_part = jnp.where(tap_index == column + anchor, lower_weight.T[:, None, :, None], nothing)
    upper_part = jnp.where(
        tap_index == column + anchor + 1, upper_weight.T[:, None, :, None], nothing
    )
    return lower_part + upper_part


def band_backward(shear_shift, lower_weight, upper_weight, window, block_width):
    band_shape = (shear_shift.shape[0], window, shear_shift.shape[1], block_width)
    tap_index = lax.broadcasted_iota(jnp.int32, band_shape, 1)
    column = lax.broadcasted_iota(jnp.int32, band_shape, 3)
    anchor = (HALO - shear_shift)[:, None, :, None]
    nothing = jnp.zeros((), jnp.bfloat16)
    lower_part = jnp.where(tap_index == column + anchor, lower_weight[:, None, :, None], nothing)
    upper_part = jnp.where(
        tap_index == column + anchor - 1, upper_weight[:, None, :, None], nothing
    )
    return lower_part + upper_part


def spectral(path_sums, observed, spectrum, attenuation, views_all):
    view_count, row_count, materials, tile_width = path_sums.shape
    block_pixels = 4096
    path_water = path_sums[:, :, 0, :].reshape(-1, block_pixels)
    path_bone = path_sums[:, :, 1, :].reshape(-1, block_pixels)
    target_flat = observed.reshape(-1, block_pixels)
    coefficients = jnp.concatenate(
        [jnp.ones((1, spectrum.shape[0]), jnp.float32), attenuation], axis=0
    )
    emitted = jnp.log(jnp.sum(spectrum))

    def one_block(inputs):
        water_block, bone_block, target_block = inputs
        exponent = (
            attenuation[0][:, None] * water_block[None, :]
            + attenuation[1][:, None] * bone_block[None, :]
        )
        counts = spectrum[:, None] * jnp.exp(-exponent)
        moments = jnp.dot(coefficients, counts, precision=lax.Precision.HIGHEST)
        intensity = moments[0]
        residual = emitted - jnp.log(intensity) - target_block
        factor = residual / intensity / views_all
        return (moments[1:] * factor[None, :]).astype(jnp.bfloat16)

    stacked = lax.map(one_block, (path_water, path_bone, target_flat))
    gradients = jnp.swapaxes(stacked, 0, 1).reshape(materials, view_count, row_count, tile_width)
    return jnp.transpose(gradients, (1, 2, 0, 3))


def spectral_kernel(views_all, emitted_ref, spectrum_ref, attenuation_ref, water_ref, bone_ref, target_ref, out0_ref, out1_ref):
    rows, width = water_ref.shape
    energies = spectrum_ref.shape[0]
    block = 8

    def one_block(b, carry):
        lo = pl.multiple_of(b * block, block)
        water = water_ref[pl.ds(lo, block), :]
        bone = bone_ref[pl.ds(lo, block), :]

        def one_energy(e, sums):
            intensity, first, second = sums
            a0 = attenuation_ref[0, e]
            a1 = attenuation_ref[1, e]
            counts = spectrum_ref[e] * jnp.exp(-(a0 * water + a1 * bone))
            return (intensity + counts, first + a0 * counts, second + a1 * counts)

        zero = jnp.zeros((block, width), jnp.float32)
        intensity, first, second = lax.fori_loop(0, energies, one_energy, (zero, zero, zero), unroll=8)
        residual = emitted_ref[0] - jnp.log(intensity) - target_ref[pl.ds(lo, block), :]
        factor = residual / intensity / views_all
        out0_ref[pl.ds(lo, block), :] = (first * factor).astype(out0_ref.dtype)
        out1_ref[pl.ds(lo, block), :] = (second * factor).astype(out1_ref.dtype)
        return carry

    lax.fori_loop(0, rows // block, one_block, 0)


def spectral_pallas(path_sums, observed, spectrum, attenuation, views_all):
    view_count, row_count, materials, width_all = path_sums.shape
    pixels = view_count * row_count * width_all
    rows = pixels // LANES // 4
    water = path_sums[:, :, 0, :].reshape(rows, 4 * LANES)
    bone = path_sums[:, :, 1, :].reshape(rows, 4 * LANES)
    target = observed.reshape(rows, 4 * LANES)
    emitted = jnp.log(jnp.sum(spectrum)).reshape(1)
    smem = pl.BlockSpec(memory_space=pltpu.SMEM)
    vmem = pl.BlockSpec(memory_space=pltpu.VMEM)
    first, second = pl.pallas_call(
        functools.partial(spectral_kernel, views_all),
        out_shape=(
            jax.ShapeDtypeStruct((rows, 4 * LANES), jnp.bfloat16),
            jax.ShapeDtypeStruct((rows, 4 * LANES), jnp.bfloat16),
        ),
        in_specs=[smem, smem, smem, vmem, vmem, vmem],
        out_specs=(vmem, vmem),
        interpret=INTERPRET,
    )(emitted, spectrum, attenuation, water, bone, target)
    shape = (view_count, row_count, width_all)
    return jnp.stack([first.reshape(shape), second.reshape(shape)], axis=2)


def per_device(density, measured, shear_shift, shear_frac, spectrum, attenuation):
    row_total, materials, depth_here, tile_width = density.shape
    block_width = min(128, tile_width)
    block_count = tile_width // block_width
    window = block_width + 2 * HALO
    views_all = measured.shape[0] * lax.axis_size("views")
    depth_all = depth_here * lax.axis_size("depth")
    rows_out = row_total // lax.axis_size("views")
    lower_weight = (1.0 - shear_frac).astype(jnp.bfloat16)
    upper_weight = shear_frac.astype(jnp.bfloat16)
    rows_here = density.shape[0]
    padded = with_halo(density, (("lat", 3),), HALO)
    framed = jnp.stack(
        [
            padded[:, :, :, number * block_width : number * block_width + window]
            for number in range(block_count)
        ],
        axis=2,
    )
    forward_band = band_forward(shear_shift, lower_weight, upper_weight, window, block_width)
    partial_value = jnp.einsum(
        "ymnzi,zivc->vymnc", framed, forward_band, preferred_element_type=jnp.float32
    )
    partial_value = partial_value.reshape(shear_shift.shape[0], rows_here, materials, tile_width)
    shares = lax.psum_scatter(partial_value, "depth", scatter_dimension=3, tiled=True) / depth_all
    share_cols = shares.shape[3]
    observed = lax.dynamic_slice_in_dim(
        measured, lax.axis_index("depth") * share_cols, share_cols, 2
    )
    share_grads = spectral(shares, observed, spectrum, attenuation, views_all)
    path_grads = lax.all_gather(share_grads, "depth", axis=3, tiled=True)
    padded_grads = with_halo(path_grads, (("lat", 3),), HALO)
    framed_grads = jnp.stack(
        [
            padded_grads[:, :, :, number * block_width : number * block_width + window]
            for number in range(block_count)
        ],
        axis=3,
    )
    backward_band = band_backward(shear_shift, lower_weight, upper_weight, window, block_width)
    product = jnp.einsum(
        "vymni,vizc->ymznc", framed_grads, backward_band, preferred_element_type=jnp.float32
    )
    return lax.psum_scatter(
        product.reshape(rows_out * lax.axis_size("views"), materials, depth_here, tile_width),
        "views",
        scatter_dimension=0,
        tiled=True,
    )


LANES = 128
INTERPRET = False


def shear_kernel(rot_ref, thr_ref, wa_ref, wb_ref, src_ref, out_ref):
    outer_count, channels, width = src_ref.shape
    inner_count, _, out_width = out_ref.shape
    pieces = width // LANES
    out_pieces = out_width // LANES
    out_ref[...] = jnp.zeros(out_ref.shape, jnp.float32)
    lane = lax.broadcasted_iota(jnp.int32, (channels, LANES), 1)

    def outer(o, carry):
        cols = [src_ref[o, :, k * LANES : (k + 1) * LANES] for k in range(pieces)]
        turned = [pltpu.roll(c, LANES - 1, 1) for c in cols]
        nexts = [
            jnp.where(lane < LANES - 1, turned[k], turned[k + 1]) for k in range(pieces - 1)
        ] + [turned[pieces - 1]]
        for i in range(inner_count):
            wa = wa_ref[o, i]
            wb = wb_ref[o, i]
            mixed = [wa * cols[k] + wb * nexts[k] for k in range(pieces)]
            rolled = [pltpu.roll(m, rot_ref[o, i], 1) for m in mixed]
            keep = lane < thr_ref[o, i]
            for j in range(out_pieces):
                out_ref[i, :, j * LANES : (j + 1) * LANES] += jnp.where(
                    keep, rolled[j], rolled[j + 1]
                )
        return carry

    lax.fori_loop(0, outer_count, outer, 0)


def shear_table_kernel(forward, tab_ref, src_ref, out_ref):
    outer_count, channels, width = src_ref.shape
    inner_count, _, out_width = out_ref.shape
    pieces = width // LANES
    out_pieces = out_width // LANES
    out_ref[...] = jnp.zeros(out_ref.shape, jnp.float32)
    lane = lax.broadcasted_iota(jnp.int32, (channels, LANES), 1)

    def outer(o, carry):
        cols = [src_ref[o, :, k * LANES : (k + 1) * LANES] for k in range(pieces)]
        turned = [pltpu.roll(c, LANES - 1, 1) for c in cols]
        nexts = [
            jnp.where(lane < LANES - 1, turned[k], turned[k + 1]) for k in range(pieces - 1)
        ] + [turned[pieces - 1]]
        for i in range(inner_count):
            if forward:
                shift = tab_ref[0, i, o].astype(jnp.int32)
                wa = tab_ref[1, i, o]
                wb = tab_ref[2, i, o]
                offset = shift + HALO
            else:
                shift = tab_ref[0, o, i].astype(jnp.int32)
                wa = tab_ref[2, o, i]
                wb = tab_ref[1, o, i]
                offset = HALO - 1 - shift
            limit = LANES - offset
            amount = jnp.where(limit == LANES, 0, limit)
            mixed = [wa * cols[k] + wb * nexts[k] for k in range(pieces)]
            rolled = [pltpu.roll(m, amount, 1) for m in mixed]
            keep = lane < limit
            for j in range(out_pieces):
                out_ref[i, :, j * LANES : (j + 1) * LANES] += jnp.where(
                    keep, rolled[j], rolled[j + 1]
                )
        return carry

    lax.fori_loop(0, outer_count, outer, 0)


def shear_table(forward, table, src, inner_count, out_width):
    _, channels, _ = src.shape
    smem = pl.BlockSpec(memory_space=pltpu.SMEM)
    vmem = pl.BlockSpec(memory_space=pltpu.VMEM)
    return pl.pallas_call(
        functools.partial(shear_table_kernel, forward),
        out_shape=jax.ShapeDtypeStruct((inner_count, channels, out_width), jnp.float32),
        in_specs=[smem, vmem],
        out_specs=vmem,
        interpret=INTERPRET,
    )(table, src)


def halo_columns(ys, lane, half_of, rows_here, halves, channels):
    count = len(ys)
    turned = [pltpu.roll(y, HALO, 1) for y in ys]
    zero = jnp.zeros_like(ys[0])
    left = jnp.where(half_of >= 1, pltpu.roll(turned[count - 1], rows_here, 0), zero)
    right = jnp.where(half_of <= halves - 2, pltpu.roll(turned[0], channels - rows_here, 0), zero)
    edge = lane < HALO
    cols = [jnp.where(edge, left, turned[0])]
    cols += [jnp.where(edge, turned[k - 1], turned[k]) for k in range(1, count)]
    cols += [jnp.where(edge, turned[count - 1], right)]
    return cols


def shear_pass(forward, rows_here, halves, tab_ref, src_ref, acc_ref, cols_ref, nexts_ref):
    outer_count, channels, width = src_ref.shape
    inner_count = acc_ref.shape[0]
    pieces = width // LANES
    lane = lax.broadcasted_iota(jnp.int32, (channels, LANES), 1)
    half_of = (lax.broadcasted_iota(jnp.int32, (channels, LANES), 0) // rows_here) % halves

    def prepare(o, carry):
        ys = [src_ref[o, :, k * LANES : (k + 1) * LANES] for k in range(pieces)]
        cols = halo_columns(ys, lane, half_of, rows_here, halves, channels)
        turned = [pltpu.roll(c, LANES - 1, 1) for c in cols]
        nexts = [jnp.where(lane < LANES - 1, turned[k], turned[k + 1]) for k in range(pieces)]
        nexts.append(turned[pieces])
        for k in range(pieces + 1):
            cols_ref[o, :, k * LANES : (k + 1) * LANES] = cols[k]
            nexts_ref[o, :, k * LANES : (k + 1) * LANES] = nexts[k]
        return carry

    lax.fori_loop(0, outer_count, prepare, 0, unroll=True)

    for i in range(inner_count):

        def one_input(o, acc):
            if forward:
                shift = tab_ref[0, i, o].astype(jnp.int32)
                wa = tab_ref[1, i, o]
                wb = tab_ref[2, i, o]
                offset = shift + HALO
            else:
                shift = tab_ref[0, o, i].astype(jnp.int32)
                wa = tab_ref[2, o, i]
                wb = tab_ref[1, o, i]
                offset = HALO - 1 - shift
            limit = LANES - offset
            amount = jnp.where(limit == LANES, 0, limit)
            mixed = [
                wa * cols_ref[o, :, k * LANES : (k + 1) * LANES]
                + wb * nexts_ref[o, :, k * LANES : (k + 1) * LANES]
                for k in range(pieces + 1)
            ]
            rolled = [pltpu.roll(m, amount, 1) for m in mixed]
            keep = lane < limit
            return tuple(acc[j] + jnp.where(keep, rolled[j], rolled[j + 1]) for j in range(pieces))

        zero = jnp.zeros((channels, LANES), jnp.float32)
        acc = lax.fori_loop(0, outer_count, one_input, tuple(zero for _ in range(pieces)), unroll=True)
        for j in range(pieces):
            acc_ref[i, :, j * LANES : (j + 1) * LANES] = acc[j]


def scatter_pass(rows_here, halves, tab_ref, src_ref, out_ref, cols_ref, nexts_ref):
    outer_count, channels, width = src_ref.shape
    _, depth_here, _ = out_ref.shape
    materials = channels // (halves * rows_here)
    pieces = width // LANES
    lane = lax.broadcasted_iota(jnp.int32, (channels, LANES), 1)
    half_of = (lax.broadcasted_iota(jnp.int32, (channels, LANES), 0) // rows_here) % halves

    def prepare(o, carry):
        ys = [src_ref[o, :, k * LANES : (k + 1) * LANES] for k in range(pieces)]
        cols = halo_columns(ys, lane, half_of, rows_here, halves, channels)
        turned = [pltpu.roll(c, LANES - 1, 1) for c in cols]
        nexts = [jnp.where(lane < LANES - 1, turned[k], turned[k + 1]) for k in range(pieces)]
        nexts.append(turned[pieces])
        for k in range(pieces + 1):
            cols_ref[o, :, k * LANES : (k + 1) * LANES] = cols[k]
            nexts_ref[o, :, k * LANES : (k + 1) * LANES] = nexts[k]
        return carry

    lax.fori_loop(0, outer_count, prepare, 0, unroll=True)
    inner_count = tab_ref.shape[2]

    for i in range(inner_count):
        slab, level = divmod(i, depth_here)

        def one_view(o, acc):
            shift = tab_ref[0, o, i].astype(jnp.int32)
            wa = tab_ref[2, o, i]
            wb = tab_ref[1, o, i]
            offset = HALO - 1 - shift
            limit = LANES - offset
            amount = jnp.where(limit == LANES, 0, limit)
            mixed = [
                wa * cols_ref[o, :, k * LANES : (k + 1) * LANES]
                + wb * nexts_ref[o, :, k * LANES : (k + 1) * LANES]
                for k in range(pieces + 1)
            ]
            rolled = [pltpu.roll(m, amount, 1) for m in mixed]
            keep = lane < limit
            return tuple(acc[j] + jnp.where(keep, rolled[j], rolled[j + 1]) for j in range(pieces))

        zero = jnp.zeros((channels, LANES), jnp.float32)
        acc = lax.fori_loop(0, outer_count, one_view, tuple(zero for _ in range(pieces)), unroll=True)
        value = jnp.concatenate(acc, axis=1)
        for c in range(channels):
            material, rest = divmod(c, halves * rows_here)
            half, row = divmod(rest, rows_here)
            target = ((slab * halves + half) * rows_here + row) * materials + material
            out_ref[target, level : level + 1, :] = value[c : c + 1, :]


def scaled(value, count):
    if count & (count - 1) == 0:
        return value * (1.0 / count)
    return value / count


def forward_kernel(rows_here, halves, depth_all, views_all, tab_ref, emitted_ref, spectrum_ref,
                   attenuation_ref, src_ref, target_ref, out_ref, sums_ref, cols_ref, nexts_ref):
    shear_pass(True, rows_here, halves, tab_ref, src_ref, sums_ref, cols_ref, nexts_ref)
    _, channels, width = sums_ref.shape
    energies = spectrum_ref.shape[0]
    split = channels // 2
    low = lax.broadcasted_iota(jnp.int32, (channels, width), 0) < split

    def one_pair(p, carry):
        first_view = scaled(sums_ref[2 * p], depth_all)
        second_view = scaled(sums_ref[2 * p + 1], depth_all)
        water = jnp.where(low, first_view, pltpu.roll(second_view, split, 0))
        bone = jnp.where(low, pltpu.roll(first_view, split, 0), second_view)

        def one_energy(e, sums):
            intensity, first, second = sums
            a0 = attenuation_ref[0, e]
            a1 = attenuation_ref[1, e]
            counts = spectrum_ref[e] * jnp.exp((-a0) * water + (-a1) * bone)
            return (intensity + counts, first + a0 * counts, second + a1 * counts)

        zero = jnp.zeros((channels, width), jnp.float32)
        intensity, first, second = lax.fori_loop(0, energies, one_energy, (zero, zero, zero), unroll=True)
        residual = emitted_ref[0] - jnp.log(intensity) - target_ref[p]
        factor = scaled(residual / intensity, views_all)
        first = (first * factor).astype(jnp.bfloat16).astype(jnp.float32)
        second = (second * factor).astype(jnp.bfloat16).astype(jnp.float32)
        out_ref[2 * p] = jnp.where(low, first, pltpu.roll(second, split, 0))
        out_ref[2 * p + 1] = jnp.where(low, pltpu.roll(first, split, 0), second)
        return carry

    lax.fori_loop(0, out_ref.shape[0] // 2, one_pair, 0, unroll=True)


def backward_kernel(rows_here, halves, tab_ref, src_ref, out_ref, cols_ref, nexts_ref):
    scatter_pass(rows_here, halves, tab_ref, src_ref, out_ref, cols_ref, nexts_ref)


def shear_apply(offset, wa, wb, src, out_width):
    outer_count, channels, width = src.shape
    inner_count = offset.shape[1]
    rot = (LANES - offset) % LANES
    thr = LANES - offset
    smem = pl.BlockSpec(memory_space=pltpu.SMEM)
    vmem = pl.BlockSpec(memory_space=pltpu.VMEM)
    return pl.pallas_call(
        shear_kernel,
        out_shape=jax.ShapeDtypeStruct((inner_count, channels, out_width), jnp.float32),
        in_specs=[smem, smem, smem, smem, vmem],
        out_specs=vmem,
        interpret=INTERPRET,
    )(rot.astype(jnp.int32), thr.astype(jnp.int32), wa, wb, src)


def rows_fit(density, measured):
    rows = density.shape[0]
    groups = lax.axis_size("views")
    depth = lax.axis_size("depth")
    tile_width = density.shape[3]
    return (
        rows % groups == 0
        and (rows // groups) % depth == 0
        and tile_width % LANES == 0
        and 2 * HALO == LANES
        and density.shape[1] == 2
        and measured.shape[0] * groups % 2 == 0
        and tile_width >= 3 * measured.shape[0] * density.shape[2] * groups
    )


def per_device_rows(density, measured, shear_shift, shear_frac, spectrum, attenuation):
    row_total, materials, depth_here, tile_width = density.shape
    groups = lax.axis_size("views")
    depth_count = lax.axis_size("depth")
    views_here = measured.shape[0]
    views_all = views_here * groups
    depth_all = depth_here * depth_count
    rows_group = row_total // groups
    rows_here = rows_group // depth_count
    group = lax.axis_index("views")
    slab = lax.axis_index("depth")

    lower_weight = (1.0 - shear_frac).astype(jnp.bfloat16).astype(jnp.float32)
    upper_weight = shear_frac.astype(jnp.bfloat16).astype(jnp.float32)
    table = jnp.stack([shear_shift.astype(jnp.float32), lower_weight, upper_weight])
    entries = table.size
    observed = measured.reshape(views_here, groups, rows_group, tile_width)
    observed = lax.dynamic_slice_in_dim(observed, slab * rows_here, rows_here, 2)
    observed = jnp.transpose(observed, (1, 0, 2, 3)).reshape(groups, views_here * rows_here, tile_width)
    extra = jnp.pad(table.reshape(1, entries), ((0, 0), (0, tile_width - entries)))
    extra = jnp.broadcast_to(extra[None], (groups, 1, tile_width))
    observed = jnp.concatenate([observed, extra], axis=1)
    observed = lax.all_to_all(observed, "views", 0, 0, tiled=True)
    table = observed[:, views_here * rows_here, :entries].reshape(groups, 3, views_here, depth_here)
    table = jnp.transpose(table, (1, 0, 2, 3)).reshape(3, views_all, depth_here)
    observed = observed[:, : views_here * rows_here].reshape(views_all, rows_here, tile_width)

    channels = rows_here * materials
    mine = lax.dynamic_slice_in_dim(density, group * rows_group, rows_group, 0)
    mine = mine.reshape(depth_count, rows_here, materials, depth_here, tile_width)
    mine = jnp.transpose(mine, (0, 3, 1, 2, 4)).reshape(depth_count, depth_here * channels, tile_width)
    wide = table.size
    extra = jnp.pad(table.reshape(1, wide), ((0, 0), (0, tile_width - wide))).astype(jnp.bfloat16)
    extra = jnp.broadcast_to(extra[None], (depth_count, 1, tile_width))
    mine = jnp.concatenate([mine, extra], axis=1)
    mine = lax.all_to_all(mine, "depth", 0, 0, tiled=True)
    table = mine[:, depth_here * channels, :wide].astype(jnp.float32)
    table = table.reshape(depth_count, 3, views_all, depth_here)
    table = jnp.transpose(table, (1, 2, 0, 3)).reshape(3, views_all, depth_all)
    shift_all = table[0].astype(jnp.int32)
    lower_all = table[1]
    upper_all = table[2]
    mine = mine[:, : depth_here * channels].reshape(depth_all, channels, tile_width)
    padded = with_halo(mine, (("lat", 2),), HALO).astype(jnp.float32)

    sums = shear_apply(
        (shift_all + HALO).T, lower_all.T, upper_all.T, padded, tile_width
    )
    sums = (sums / depth_all).reshape(views_all, rows_here, materials, tile_width)
    grads = spectral(sums, observed, spectrum, attenuation, views_all)
    grads = grads.reshape(views_all, rows_here * materials, tile_width)
    padded_grads = with_halo(grads, (("lat", 2),), HALO).astype(jnp.float32)
    layers = shear_apply(
        HALO - 1 - shift_all, upper_all, lower_all, padded_grads, tile_width
    )
    layers = layers.reshape(depth_count, depth_here, rows_here, materials, tile_width)
    layers = exchange(layers, "depth")
    return jnp.transpose(layers, (0, 2, 3, 1, 4)).reshape(rows_group, materials, depth_here, tile_width)


def rows_fit_wide(density, measured):
    rows = density.shape[0]
    groups = lax.axis_size("views")
    parts = lax.axis_size("depth") * lax.axis_size("lat")
    tile_width = density.shape[3]
    return (
        rows % groups == 0
        and (rows // groups) % parts == 0
        and tile_width % LANES == 0
        and 2 * HALO == LANES
        and density.shape[1] == 2
        and measured.shape[0] * groups % 2 == 0
        and tile_width >= 3 * measured.shape[0] * density.shape[2]
        and ((rows // groups // parts) * density.shape[1] * density.shape[2]) % groups == 0
    )


def stack_halves(values, halves, tile_width):
    count, rows, materials, _ = values.shape
    padded = jnp.pad(values, ((0, 0), (0, 0), (0, 0), (HALO, HALO)))
    parts = [
        padded[..., h * tile_width : h * tile_width + tile_width + 2 * HALO] for h in range(halves)
    ]
    return jnp.stack(parts, axis=1).reshape(count, halves * rows * materials, tile_width + 2 * HALO)


def join_halves(values, halves, rows, materials):
    count, _, tile_width = values.shape
    values = values.reshape(count, halves, rows, materials, tile_width)
    return jnp.transpose(values, (0, 2, 3, 1, 4)).reshape(count, rows, materials, halves * tile_width)


def per_device_wide(density, measured, shear_shift, shear_frac, spectrum, attenuation):
    row_total, materials, depth_here, tile_width = density.shape
    groups = lax.axis_size("views")
    depth_count = lax.axis_size("depth")
    halves = lax.axis_size("lat")
    parts = depth_count * halves
    views_here = measured.shape[0]
    views_all = views_here * groups
    depth_all = depth_here * depth_count
    rows_group = row_total // groups
    rows_here = rows_group // parts
    group = lax.axis_index("views")
    slab = lax.axis_index("depth")
    half = lax.axis_index("lat")

    lower_weight = (1.0 - shear_frac).astype(jnp.bfloat16).astype(jnp.float32)
    upper_weight = shear_frac.astype(jnp.bfloat16).astype(jnp.float32)
    block = jnp.stack([shear_shift.astype(jnp.float32), lower_weight, upper_weight])
    entries = block.size
    span = halves * rows_here
    observed = jnp.stack(
        [
            lax.dynamic_slice_in_dim(measured, (g * depth_count + slab) * span, span, 1)
            for g in range(groups)
        ]
    )
    observed = observed.reshape(groups, views_here, halves, rows_here, tile_width)
    observed = jnp.transpose(observed, (0, 2, 1, 3, 4)).reshape(
        groups * halves, views_here * rows_here, tile_width
    )
    observed = lax.all_to_all(observed, ("views", "lat"), 0, 0, tiled=True)
    observed = observed.reshape(groups, halves, views_here, rows_here, tile_width)
    observed = jnp.transpose(observed, (0, 2, 3, 1, 4)).reshape(views_all, rows_here, halves * tile_width)

    chunk = rows_here * materials * depth_here * tile_width
    piece = chunk // groups
    mine = density.reshape(groups * parts, groups, piece)
    mine = lax.dynamic_index_in_dim(mine, group, 1, keepdims=False)
    mine = mine.reshape(groups * parts, piece // tile_width, tile_width)
    extra = jnp.pad(block.reshape(1, entries), ((0, 0), (0, tile_width - entries))).astype(jnp.bfloat16)
    extra = jnp.broadcast_to(extra[None], (groups * parts, 1, tile_width))
    mine = jnp.concatenate([mine, extra], axis=1)
    mine = lax.all_to_all(mine, ("views", "depth", "lat"), 0, 0, tiled=True)
    mine = mine.reshape(groups, depth_count, halves, piece // tile_width + 1, tile_width)
    table = mine[:, :, 0, piece // tile_width, :entries].astype(jnp.float32)
    table = table.reshape(groups, depth_count, 3, views_here, depth_here)
    table = jnp.transpose(table, (2, 0, 3, 1, 4)).reshape(3, views_all, depth_all)
    mine = mine[:, :, :, : piece // tile_width].reshape(groups, depth_count, halves, piece)
    mine = jnp.transpose(mine, (1, 2, 0, 3)).reshape(
        depth_count, halves, rows_here, materials, depth_here, tile_width
    )
    channels = materials * halves * rows_here
    mine = jnp.transpose(mine, (0, 4, 3, 1, 2, 5)).reshape(depth_all, channels, tile_width)
    mine = mine.astype(jnp.float32)
    target = observed.reshape(views_all // 2, 2, rows_here, halves, tile_width)
    target = jnp.transpose(target, (0, 1, 3, 2, 4)).reshape(views_all // 2, 2 * halves * rows_here, tile_width)
    emitted = jnp.log(jnp.sum(spectrum)).reshape(1)
    smem = pl.BlockSpec(memory_space=pltpu.SMEM)
    vmem = pl.BlockSpec(memory_space=pltpu.VMEM)
    grads = pl.pallas_call(
        functools.partial(forward_kernel, rows_here, halves, depth_all, views_all),
        out_shape=jax.ShapeDtypeStruct((views_all, channels, tile_width), jnp.float32),
        in_specs=[smem, smem, smem, smem, vmem, vmem],
        out_specs=vmem,
        scratch_shapes=[
            pltpu.VMEM((views_all, channels, tile_width), jnp.float32),
            pltpu.VMEM((depth_all, channels, tile_width + LANES), jnp.float32),
            pltpu.VMEM((depth_all, channels, tile_width + LANES), jnp.float32),
        ],
        interpret=INTERPRET,
    )(table, emitted, spectrum, attenuation, mine, target)
    layers = pl.pallas_call(
        functools.partial(backward_kernel, rows_here, halves),
        out_shape=jax.ShapeDtypeStruct((parts * rows_here * materials, depth_here, tile_width), jnp.float32),
        in_specs=[smem, vmem],
        out_specs=vmem,
        scratch_shapes=[
            pltpu.VMEM((views_all, channels, tile_width + LANES), jnp.float32),
            pltpu.VMEM((views_all, channels, tile_width + LANES), jnp.float32),
        ],
        interpret=INTERPRET,
    )(table, grads)
    layers = layers.reshape(parts, rows_here, materials, depth_here, tile_width)
    layers = lax.all_to_all(layers, ("depth", "lat"), 0, 0, tiled=True)
    return layers.reshape(rows_group, materials, depth_here, tile_width)


def per_device_any(density, measured, shear_shift, shear_frac, spectrum, attenuation):
    if rows_fit_wide(density, measured):
        return per_device_wide(density, measured, shear_shift, shear_frac, spectrum, attenuation)
    if rows_fit(density, measured):
        return per_device_rows(density, measured, shear_shift, shear_frac, spectrum, attenuation)
    return per_device(density, measured, shear_shift, shear_frac, spectrum, attenuation)


def solution(mesh):
    in_specs = (
        P(None, None, "depth", "lat"),
        P("views", None, "lat"),
        P("views", "depth"),
        P("views", "depth"),
        P(),
        P(),
    )
    out_specs = P("views", None, "depth", "lat")
    return jax.shard_map(
        per_device_any, mesh=mesh, in_specs=in_specs, out_specs=out_specs, check_vma=False
    )
```

```python
import functools
import jax
import jax.numpy as jnp
from jax import lax
from jax.sharding import PartitionSpec as P
from jax.experimental import pallas as pl
from jax.experimental.pallas import tpu as pltpu

HALO = 64


def with_halo(x, sides, width):
    for axis, dim in sides:
        size, length = (lax.axis_size(axis), x.shape[dim])
        up = [(i, (i + 1) % size) for i in range(size - 1)]
        down = [(j, i) for i, j in up]
        last = lax.slice_in_dim(x, length - width, length, axis=dim)
        first = lax.slice_in_dim(x, 0, width, axis=dim)
        before = lax.ppermute(last, axis, up)
        after = lax.ppermute(first, axis, down)
        x = jnp.concatenate([before, x, after], axis=dim)
    return x


def exchange(x, axis):
    count = lax.axis_size(axis)
    me = lax.axis_index(axis)
    result = x
    for step in range(1, count):
        pairs = [(i, (i + step) % count) for i in range(count)]
        part = lax.dynamic_index_in_dim(x, (me + step) % count, 0, keepdims=True)
        part = lax.ppermute(part, axis, pairs)
        result = lax.dynamic_update_index_in_dim(result, part, (me - step) % count, 0)
    return result


def band_forward(shear_shift, lower_weight, upper_weight, window, block_width):
    band_shape = (shear_shift.shape[1], window, shear_shift.shape[0], block_width)
    tap_index = lax.broadcasted_iota(jnp.int32, band_shape, 1)
    column = lax.broadcasted_iota(jnp.int32, band_shape, 3)
    anchor = (shear_shift.T + HALO)[:, None, :, None]
    nothing = jnp.zeros((), jnp.bfloat16)
    lower_part = jnp.where(tap_index == column + anchor, lower_weight.T[:, None, :, None], nothing)
    upper_part = jnp.where(
        tap_index == column + anchor + 1, upper_weight.T[:, None, :, None], nothing
    )
    return lower_part + upper_part


def band_backward(shear_shift, lower_weight, upper_weight, window, block_width):
    band_shape = (shear_shift.shape[0], window, shear_shift.shape[1], block_width)
    tap_index = lax.broadcasted_iota(jnp.int32, band_shape, 1)
    column = lax.broadcasted_iota(jnp.int32, band_shape, 3)
    anchor = (HALO - shear_shift)[:, None, :, None]
    nothing = jnp.zeros((), jnp.bfloat16)
    lower_part = jnp.where(tap_index == column + anchor, lower_weight[:, None, :, None], nothing)
    upper_part = jnp.where(
        tap_index == column + anchor - 1, upper_weight[:, None, :, None], nothing
    )
    return lower_part + upper_part


def spectral(path_sums, observed, spectrum, attenuation, views_all):
    view_count, row_count, materials, tile_width = path_sums.shape
    block_pixels = 4096
    path_water = path_sums[:, :, 0, :].reshape(-1, block_pixels)
    path_bone = path_sums[:, :, 1, :].reshape(-1, block_pixels)
    target_flat = observed.reshape(-1, block_pixels)
    coefficients = jnp.concatenate(
        [jnp.ones((1, spectrum.shape[0]), jnp.float32), attenuation], axis=0
    )
    emitted = jnp.log(jnp.sum(spectrum))

    def one_block(inputs):
        water_block, bone_block, target_block = inputs
        exponent = (
            attenuation[0][:, None] * water_block[None, :]
            + attenuation[1][:, None] * bone_block[None, :]
        )
        counts = spectrum[:, None] * jnp.exp(-exponent)
        moments = jnp.dot(coefficients, counts, precision=lax.Precision.HIGHEST)
        intensity = moments[0]
        residual = emitted - jnp.log(intensity) - target_block
        factor = residual / intensity / views_all
        return (moments[1:] * factor[None, :]).astype(jnp.bfloat16)

    stacked = lax.map(one_block, (path_water, path_bone, target_flat))
    gradients = jnp.swapaxes(stacked, 0, 1).reshape(materials, view_count, row_count, tile_width)
    return jnp.transpose(gradients, (1, 2, 0, 3))


def spectral_kernel(views_all, emitted_ref, spectrum_ref, attenuation_ref, water_ref, bone_ref, target_ref, out0_ref, out1_ref):
    rows, width = water_ref.shape
    energies = spectrum_ref.shape[0]
    block = 8

    def one_block(b, carry):
        lo = pl.multiple_of(b * block, block)
        water = water_ref[pl.ds(lo, block), :]
        bone = bone_ref[pl.ds(lo, block), :]

        def one_energy(e, sums):
            intensity, first, second = sums
            a0 = attenuation_ref[0, e]
            a1 = attenuation_ref[1, e]
            counts = spectrum_ref[e] * jnp.exp(-(a0 * water + a1 * bone))
            return (intensity + counts, first + a0 * counts, second + a1 * counts)

        zero = jnp.zeros((block, width), jnp.float32)
        intensity, first, second = lax.fori_loop(0, energies, one_energy, (zero, zero, zero), unroll=8)
        residual = emitted_ref[0] - jnp.log(intensity) - target_ref[pl.ds(lo, block), :]
        factor = residual / intensity / views_all
        out0_ref[pl.ds(lo, block), :] = (first * factor).astype(out0_ref.dtype)
        out1_ref[pl.ds(lo, block), :] = (second * factor).astype(out1_ref.dtype)
        return carry

    lax.fori_loop(0, rows // block, one_block, 0)


def spectral_pallas(path_sums, observed, spectrum, attenuation, views_all):
    view_count, row_count, materials, width_all = path_sums.shape
    pixels = view_count * row_count * width_all
    rows = pixels // LANES // 4
    water = path_sums[:, :, 0, :].reshape(rows, 4 * LANES)
    bone = path_sums[:, :, 1, :].reshape(rows, 4 * LANES)
    target = observed.reshape(rows, 4 * LANES)
    emitted = jnp.log(jnp.sum(spectrum)).reshape(1)
    smem = pl.BlockSpec(memory_space=pltpu.SMEM)
    vmem = pl.BlockSpec(memory_space=pltpu.VMEM)
    first, second = pl.pallas_call(
        functools.partial(spectral_kernel, views_all),
        out_shape=(
            jax.ShapeDtypeStruct((rows, 4 * LANES), jnp.bfloat16),
            jax.ShapeDtypeStruct((rows, 4 * LANES), jnp.bfloat16),
        ),
        in_specs=[smem, smem, smem, vmem, vmem, vmem],
        out_specs=(vmem, vmem),
        interpret=INTERPRET,
    )(emitted, spectrum, attenuation, water, bone, target)
    shape = (view_count, row_count, width_all)
    return jnp.stack([first.reshape(shape), second.reshape(shape)], axis=2)


def per_device(density, measured, shear_shift, shear_frac, spectrum, attenuation):
    row_total, materials, depth_here, tile_width = density.shape
    block_width = min(128, tile_width)
    block_count = tile_width // block_width
    window = block_width + 2 * HALO
    views_all = measured.shape[0] * lax.axis_size("views")
    depth_all = depth_here * lax.axis_size("depth")
    rows_out = row_total // lax.axis_size("views")
    lower_weight = (1.0 - shear_frac).astype(jnp.bfloat16)
    upper_weight = shear_frac.astype(jnp.bfloat16)
    rows_here = density.shape[0]
    padded = with_halo(density, (("lat", 3),), HALO)
    framed = jnp.stack(
        [
            padded[:, :, :, number * block_width : number * block_width + window]
            for number in range(block_count)
        ],
        axis=2,
    )
    forward_band = band_forward(shear_shift, lower_weight, upper_weight, window, block_width)
    partial_value = jnp.einsum(
        "ymnzi,zivc->vymnc", framed, forward_band, preferred_element_type=jnp.float32
    )
    partial_value = partial_value.reshape(shear_shift.shape[0], rows_here, materials, tile_width)
    shares = lax.psum_scatter(partial_value, "depth", scatter_dimension=3, tiled=True) / depth_all
    share_cols = shares.shape[3]
    observed = lax.dynamic_slice_in_dim(
        measured, lax.axis_index("depth") * share_cols, share_cols, 2
    )
    share_grads = spectral(shares, observed, spectrum, attenuation, views_all)
    path_grads = lax.all_gather(share_grads, "depth", axis=3, tiled=True)
    padded_grads = with_halo(path_grads, (("lat", 3),), HALO)
    framed_grads = jnp.stack(
        [
            padded_grads[:, :, :, number * block_width : number * block_width + window]
            for number in range(block_count)
        ],
        axis=3,
    )
    backward_band = band_backward(shear_shift, lower_weight, upper_weight, window, block_width)
    product = jnp.einsum(
        "vymni,vizc->ymznc", framed_grads, backward_band, preferred_element_type=jnp.float32
    )
    return lax.psum_scatter(
        product.reshape(rows_out * lax.axis_size("views"), materials, depth_here, tile_width),
        "views",
        scatter_dimension=0,
        tiled=True,
    )


LANES = 128
INTERPRET = False


def shear_kernel(rot_ref, thr_ref, wa_ref, wb_ref, src_ref, out_ref):
    outer_count, channels, width = src_ref.shape
    inner_count, _, out_width = out_ref.shape
    pieces = width // LANES
    out_pieces = out_width // LANES
    out_ref[...] = jnp.zeros(out_ref.shape, jnp.float32)
    lane = lax.broadcasted_iota(jnp.int32, (channels, LANES), 1)

    def outer(o, carry):
        cols = [src_ref[o, :, k * LANES : (k + 1) * LANES] for k in range(pieces)]
        turned = [pltpu.roll(c, LANES - 1, 1) for c in cols]
        nexts = [
            jnp.where(lane < LANES - 1, turned[k], turned[k + 1]) for k in range(pieces - 1)
        ] + [turned[pieces - 1]]
        for i in range(inner_count):
            wa = wa_ref[o, i]
            wb = wb_ref[o, i]
            mixed = [wa * cols[k] + wb * nexts[k] for k in range(pieces)]
            rolled = [pltpu.roll(m, rot_ref[o, i], 1) for m in mixed]
            keep = lane < thr_ref[o, i]
            for j in range(out_pieces):
                out_ref[i, :, j * LANES : (j + 1) * LANES] += jnp.where(
                    keep, rolled[j], rolled[j + 1]
                )
        return carry

    lax.fori_loop(0, outer_count, outer, 0)


def shear_table_kernel(forward, tab_ref, src_ref, out_ref):
    outer_count, channels, width = src_ref.shape
    inner_count, _, out_width = out_ref.shape
    pieces = width // LANES
    out_pieces = out_width // LANES
    out_ref[...] = jnp.zeros(out_ref.shape, jnp.float32)
    lane = lax.broadcasted_iota(jnp.int32, (channels, LANES), 1)

    def outer(o, carry):
        cols = [src_ref[o, :, k * LANES : (k + 1) * LANES] for k in range(pieces)]
        turned = [pltpu.roll(c, LANES - 1, 1) for c in cols]
        nexts = [
            jnp.where(lane < LANES - 1, turned[k], turned[k + 1]) for k in range(pieces - 1)
        ] + [turned[pieces - 1]]
        for i in range(inner_count):
            if forward:
                shift = tab_ref[0, i, o].astype(jnp.int32)
                wa = tab_ref[1, i, o]
                wb = tab_ref[2, i, o]
                offset = shift + HALO
            else:
                shift = tab_ref[0, o, i].astype(jnp.int32)
                wa = tab_ref[2, o, i]
                wb = tab_ref[1, o, i]
                offset = HALO - 1 - shift
            limit = LANES - offset
            amount = jnp.where(limit == LANES, 0, limit)
            mixed = [wa * cols[k] + wb * nexts[k] for k in range(pieces)]
            rolled = [pltpu.roll(m, amount, 1) for m in mixed]
            keep = lane < limit
            for j in range(out_pieces):
                out_ref[i, :, j * LANES : (j + 1) * LANES] += jnp.where(
                    keep, rolled[j], rolled[j + 1]
                )
        return carry

    lax.fori_loop(0, outer_count, outer, 0)


def shear_table(forward, table, src, inner_count, out_width):
    _, channels, _ = src.shape
    smem = pl.BlockSpec(memory_space=pltpu.SMEM)
    vmem = pl.BlockSpec(memory_space=pltpu.VMEM)
    return pl.pallas_call(
        functools.partial(shear_table_kernel, forward),
        out_shape=jax.ShapeDtypeStruct((inner_count, channels, out_width), jnp.float32),
        in_specs=[smem, vmem],
        out_specs=vmem,
        interpret=INTERPRET,
    )(table, src)


def halo_columns(ys, lane, half_of, rows_here, halves, channels):
    count = len(ys)
    turned = [pltpu.roll(y, HALO, 1) for y in ys]
    zero = jnp.zeros_like(ys[0])
    left = jnp.where(half_of >= 1, pltpu.roll(turned[count - 1], rows_here, 0), zero)
    right = jnp.where(half_of <= halves - 2, pltpu.roll(turned[0], channels - rows_here, 0), zero)
    edge = lane < HALO
    cols = [jnp.where(edge, left, turned[0])]
    cols += [jnp.where(edge, turned[k - 1], turned[k]) for k in range(1, count)]
    cols += [jnp.where(edge, turned[count - 1], right)]
    return cols


def table_entry(tab_ref, kind, view, level, views_here, depth_here):
    block = views_here * depth_here
    return tab_ref[
        view // views_here,
        level // depth_here,
        kind * block + (view % views_here) * depth_here + level % depth_here,
    ]


def shear_pass(forward, rows_here, halves, tab_ref, src_ref, acc_ref, cols_ref, nexts_ref):
    outer_count, channels, width = src_ref.shape
    inner_count = acc_ref.shape[0]
    pieces = width // LANES
    lane = lax.broadcasted_iota(jnp.int32, (channels, LANES), 1)
    half_of = (lax.broadcasted_iota(jnp.int32, (channels, LANES), 0) // rows_here) % halves

    def prepare(o, carry):
        ys = [src_ref[o, :, k * LANES : (k + 1) * LANES] for k in range(pieces)]
        cols = halo_columns(ys, lane, half_of, rows_here, halves, channels)
        turned = [pltpu.roll(c, LANES - 1, 1) for c in cols]
        nexts = [jnp.where(lane < LANES - 1, turned[k], turned[k + 1]) for k in range(pieces)]
        nexts.append(turned[pieces])
        for k in range(pieces + 1):
            cols_ref[o, :, k * LANES : (k + 1) * LANES] = cols[k]
            nexts_ref[o, :, k * LANES : (k + 1) * LANES] = nexts[k]
        return carry

    lax.fori_loop(0, outer_count, prepare, 0, unroll=True)

    views_here = tab_ref.shape[2] // 3 // (outer_count // tab_ref.shape[1] if forward else inner_count // tab_ref.shape[1])
    depth_here = (outer_count if forward else inner_count) // tab_ref.shape[1]

    def tab(kind, view, level):
        return table_entry(tab_ref, kind, view, level, views_here, depth_here)

    for i in range(inner_count):

        def one_input(o, acc):
            if forward:
                shift = tab(0, i, o).astype(jnp.int32)
                wa = tab(1, i, o)
                wb = tab(2, i, o)
                offset = shift + HALO
            else:
                shift = tab(0, o, i).astype(jnp.int32)
                wa = tab(2, o, i)
                wb = tab(1, o, i)
                offset = HALO - 1 - shift
            limit = LANES - offset
            amount = jnp.where(limit == LANES, 0, limit)
            mixed = [
                wa * cols_ref[o, :, k * LANES : (k + 1) * LANES]
                + wb * nexts_ref[o, :, k * LANES : (k + 1) * LANES]
                for k in range(pieces + 1)
            ]
            rolled = [pltpu.roll(m, amount, 1) for m in mixed]
            keep = lane < limit
            return tuple(acc[j] + jnp.where(keep, rolled[j], rolled[j + 1]) for j in range(pieces))

        zero = jnp.zeros((channels, LANES), jnp.float32)
        acc = lax.fori_loop(0, outer_count, one_input, tuple(zero for _ in range(pieces)), unroll=True)
        for j in range(pieces):
            acc_ref[i, :, j * LANES : (j + 1) * LANES] = acc[j]


def scatter_pass(rows_here, halves, tab_ref, src_ref, out_ref, cols_ref, nexts_ref):
    outer_count, channels, width = src_ref.shape
    _, depth_here, _ = out_ref.shape
    materials = channels // (halves * rows_here)
    pieces = width // LANES
    lane = lax.broadcasted_iota(jnp.int32, (channels, LANES), 1)
    half_of = (lax.broadcasted_iota(jnp.int32, (channels, LANES), 0) // rows_here) % halves

    def prepare(o, carry):
        ys = [src_ref[o, :, k * LANES : (k + 1) * LANES] for k in range(pieces)]
        cols = halo_columns(ys, lane, half_of, rows_here, halves, channels)
        turned = [pltpu.roll(c, LANES - 1, 1) for c in cols]
        nexts = [jnp.where(lane < LANES - 1, turned[k], turned[k + 1]) for k in range(pieces)]
        nexts.append(turned[pieces])
        for k in range(pieces + 1):
            cols_ref[o, :, k * LANES : (k + 1) * LANES] = cols[k]
            nexts_ref[o, :, k * LANES : (k + 1) * LANES] = nexts[k]
        return carry

    lax.fori_loop(0, outer_count, prepare, 0, unroll=True)
    inner_count = tab_ref.shape[1] * depth_here
    views_here = tab_ref.shape[2] // 3 // depth_here

    def tab(kind, view, z):
        return table_entry(tab_ref, kind, view, z, views_here, depth_here)

    for i in range(inner_count):
        slab, level = divmod(i, depth_here)

        def one_view(o, acc):
            shift = tab(0, o, i).astype(jnp.int32)
            wa = tab(2, o, i)
            wb = tab(1, o, i)
            offset = HALO - 1 - shift
            limit = LANES - offset
            amount = jnp.where(limit == LANES, 0, limit)
            mixed = [
                wa * cols_ref[o, :, k * LANES : (k + 1) * LANES]
                + wb * nexts_ref[o, :, k * LANES : (k + 1) * LANES]
                for k in range(pieces + 1)
            ]
            rolled = [pltpu.roll(m, amount, 1) for m in mixed]
            keep = lane < limit
            return tuple(acc[j] + jnp.where(keep, rolled[j], rolled[j + 1]) for j in range(pieces))

        zero = jnp.zeros((channels, LANES), jnp.float32)
        acc = lax.fori_loop(0, outer_count, one_view, tuple(zero for _ in range(pieces)), unroll=True)
        value = jnp.concatenate(acc, axis=1)
        for c in range(channels):
            material, rest = divmod(c, halves * rows_here)
            half, row = divmod(rest, rows_here)
            target = ((slab * halves + half) * rows_here + row) * materials + material
            out_ref[target, level : level + 1, :] = value[c : c + 1, :]


def scaled(value, count):
    if count & (count - 1) == 0:
        return value * (1.0 / count)
    return value / count


def forward_kernel(rows_here, halves, depth_all, views_all, tab_ref, emitted_ref, spectrum_ref,
                   attenuation_ref, src_ref, target_ref, out_ref, sums_ref, cols_ref, nexts_ref):
    shear_pass(True, rows_here, halves, tab_ref, src_ref, sums_ref, cols_ref, nexts_ref)
    _, channels, width = sums_ref.shape
    energies = spectrum_ref.shape[0]
    split = channels // 2
    low = lax.broadcasted_iota(jnp.int32, (channels, width), 0) < split

    def one_pair(p, carry):
        first_view = scaled(sums_ref[2 * p], depth_all)
        second_view = scaled(sums_ref[2 * p + 1], depth_all)
        water = jnp.where(low, first_view, pltpu.roll(second_view, split, 0))
        bone = jnp.where(low, pltpu.roll(first_view, split, 0), second_view)

        def one_energy(e, sums):
            intensity, first, second = sums
            a0 = attenuation_ref[0, e]
            a1 = attenuation_ref[1, e]
            counts = spectrum_ref[e] * jnp.exp((-a0) * water + (-a1) * bone)
            return (intensity + counts, first + a0 * counts, second + a1 * counts)

        zero = jnp.zeros((channels, width), jnp.float32)
        intensity, first, second = lax.fori_loop(0, energies, one_energy, (zero, zero, zero), unroll=True)
        residual = emitted_ref[0] - jnp.log(intensity) - target_ref[p]
        factor = scaled(residual / intensity, views_all)
        first = (first * factor).astype(jnp.bfloat16).astype(jnp.float32)
        second = (second * factor).astype(jnp.bfloat16).astype(jnp.float32)
        out_ref[2 * p] = jnp.where(low, first, pltpu.roll(second, split, 0))
        out_ref[2 * p + 1] = jnp.where(low, pltpu.roll(first, split, 0), second)
        return carry

    lax.fori_loop(0, out_ref.shape[0] // 2, one_pair, 0, unroll=True)


def backward_kernel(rows_here, halves, tab_ref, src_ref, out_ref, cols_ref, nexts_ref):
    scatter_pass(rows_here, halves, tab_ref, src_ref, out_ref, cols_ref, nexts_ref)


def shear_apply(offset, wa, wb, src, out_width):
    outer_count, channels, width = src.shape
    inner_count = offset.shape[1]
    rot = (LANES - offset) % LANES
    thr = LANES - offset
    smem = pl.BlockSpec(memory_space=pltpu.SMEM)
    vmem = pl.BlockSpec(memory_space=pltpu.VMEM)
    return pl.pallas_call(
        shear_kernel,
        out_shape=jax.ShapeDtypeStruct((inner_count, channels, out_width), jnp.float32),
        in_specs=[smem, smem, smem, smem, vmem],
        out_specs=vmem,
        interpret=INTERPRET,
    )(rot.astype(jnp.int32), thr.astype(jnp.int32), wa, wb, src)


def rows_fit(density, measured):
    rows = density.shape[0]
    groups = lax.axis_size("views")
    depth = lax.axis_size("depth")
    tile_width = density.shape[3]
    return (
        rows % groups == 0
        and (rows // groups) % depth == 0
        and tile_width % LANES == 0
        and 2 * HALO == LANES
        and density.shape[1] == 2
        and measured.shape[0] * groups % 2 == 0
        and tile_width >= 3 * measured.shape[0] * density.shape[2] * groups
    )


def per_device_rows(density, measured, shear_shift, shear_frac, spectrum, attenuation):
    row_total, materials, depth_here, tile_width = density.shape
    groups = lax.axis_size("views")
    depth_count = lax.axis_size("depth")
    views_here = measured.shape[0]
    views_all = views_here * groups
    depth_all = depth_here * depth_count
    rows_group = row_total // groups
    rows_here = rows_group // depth_count
    group = lax.axis_index("views")
    slab = lax.axis_index("depth")

    lower_weight = (1.0 - shear_frac).astype(jnp.bfloat16).astype(jnp.float32)
    upper_weight = shear_frac.astype(jnp.bfloat16).astype(jnp.float32)
    table = jnp.stack([shear_shift.astype(jnp.float32), lower_weight, upper_weight])
    entries = table.size
    observed = measured.reshape(views_here, groups, rows_group, tile_width)
    observed = lax.dynamic_slice_in_dim(observed, slab * rows_here, rows_here, 2)
    observed = jnp.transpose(observed, (1, 0, 2, 3)).reshape(groups, views_here * rows_here, tile_width)
    extra = jnp.pad(table.reshape(1, entries), ((0, 0), (0, tile_width - entries)))
    extra = jnp.broadcast_to(extra[None], (groups, 1, tile_width))
    observed = jnp.concatenate([observed, extra], axis=1)
    observed = lax.all_to_all(observed, "views", 0, 0, tiled=True)
    table = observed[:, views_here * rows_here, :entries].reshape(groups, 3, views_here, depth_here)
    table = jnp.transpose(table, (1, 0, 2, 3)).reshape(3, views_all, depth_here)
    observed = observed[:, : views_here * rows_here].reshape(views_all, rows_here, tile_width)

    channels = rows_here * materials
    mine = lax.dynamic_slice_in_dim(density, group * rows_group, rows_group, 0)
    mine = mine.reshape(depth_count, rows_here, materials, depth_here, tile_width)
    mine = jnp.transpose(mine, (0, 3, 1, 2, 4)).reshape(depth_count, depth_here * channels, tile_width)
    wide = table.size
    extra = jnp.pad(table.reshape(1, wide), ((0, 0), (0, tile_width - wide))).astype(jnp.bfloat16)
    extra = jnp.broadcast_to(extra[None], (depth_count, 1, tile_width))
    mine = jnp.concatenate([mine, extra], axis=1)
    mine = lax.all_to_all(mine, "depth", 0, 0, tiled=True)
    table = mine[:, depth_here * channels, :wide].astype(jnp.float32)
    table = table.reshape(depth_count, 3, views_all, depth_here)
    table = jnp.transpose(table, (1, 2, 0, 3)).reshape(3, views_all, depth_all)
    shift_all = table[0].astype(jnp.int32)
    lower_all = table[1]
    upper_all = table[2]
    mine = mine[:, : depth_here * channels].reshape(depth_all, channels, tile_width)
    padded = with_halo(mine, (("lat", 2),), HALO).astype(jnp.float32)

    sums = shear_apply(
        (shift_all + HALO).T, lower_all.T, upper_all.T, padded, tile_width
    )
    sums = (sums / depth_all).reshape(views_all, rows_here, materials, tile_width)
    grads = spectral(sums, observed, spectrum, attenuation, views_all)
    grads = grads.reshape(views_all, rows_here * materials, tile_width)
    padded_grads = with_halo(grads, (("lat", 2),), HALO).astype(jnp.float32)
    layers = shear_apply(
        HALO - 1 - shift_all, upper_all, lower_all, padded_grads, tile_width
    )
    layers = layers.reshape(depth_count, depth_here, rows_here, materials, tile_width)
    layers = exchange(layers, "depth")
    return jnp.transpose(layers, (0, 2, 3, 1, 4)).reshape(rows_group, materials, depth_here, tile_width)


def rows_fit_wide(density, measured):
    rows = density.shape[0]
    groups = lax.axis_size("views")
    parts = lax.axis_size("depth") * lax.axis_size("lat")
    tile_width = density.shape[3]
    return (
        rows % groups == 0
        and (rows // groups) % parts == 0
        and tile_width % LANES == 0
        and 2 * HALO == LANES
        and density.shape[1] == 2
        and measured.shape[0] * groups % 2 == 0
        and tile_width >= 3 * measured.shape[0] * density.shape[2]
        and ((rows // groups // parts) * density.shape[1] * density.shape[2]) % groups == 0
    )


def stack_halves(values, halves, tile_width):
    count, rows, materials, _ = values.shape
    padded = jnp.pad(values, ((0, 0), (0, 0), (0, 0), (HALO, HALO)))
    parts = [
        padded[..., h * tile_width : h * tile_width + tile_width + 2 * HALO] for h in range(halves)
    ]
    return jnp.stack(parts, axis=1).reshape(count, halves * rows * materials, tile_width + 2 * HALO)


def join_halves(values, halves, rows, materials):
    count, _, tile_width = values.shape
    values = values.reshape(count, halves, rows, materials, tile_width)
    return jnp.transpose(values, (0, 2, 3, 1, 4)).reshape(count, rows, materials, halves * tile_width)


def per_device_wide(density, measured, shear_shift, shear_frac, spectrum, attenuation):
    row_total, materials, depth_here, tile_width = density.shape
    groups = lax.axis_size("views")
    depth_count = lax.axis_size("depth")
    halves = lax.axis_size("lat")
    parts = depth_count * halves
    views_here = measured.shape[0]
    views_all = views_here * groups
    depth_all = depth_here * depth_count
    rows_group = row_total // groups
    rows_here = rows_group // parts
    group = lax.axis_index("views")
    slab = lax.axis_index("depth")
    half = lax.axis_index("lat")

    lower_weight = (1.0 - shear_frac).astype(jnp.bfloat16).astype(jnp.float32)
    upper_weight = shear_frac.astype(jnp.bfloat16).astype(jnp.float32)
    block = jnp.stack([shear_shift.astype(jnp.float32), lower_weight, upper_weight])
    entries = block.size
    span = halves * rows_here
    observed = jnp.stack(
        [
            lax.dynamic_slice_in_dim(measured, (g * depth_count + slab) * span, span, 1)
            for g in range(groups)
        ]
    )
    observed = observed.reshape(groups, views_here, halves, rows_here, tile_width)
    observed = jnp.transpose(observed, (0, 2, 1, 3, 4)).reshape(
        groups * halves, views_here * rows_here, tile_width
    )
    observed = lax.all_to_all(observed, ("views", "lat"), 0, 0, tiled=True)
    observed = observed.reshape(groups, halves, views_here, rows_here, tile_width)
    observed = jnp.transpose(observed, (0, 2, 3, 1, 4)).reshape(views_all, rows_here, halves * tile_width)

    chunk = rows_here * materials * depth_here * tile_width
    piece = chunk // groups
    mine = density.reshape(groups * parts, groups, piece)
    mine = lax.dynamic_index_in_dim(mine, group, 1, keepdims=False)
    mine = mine.reshape(groups * parts, piece // tile_width, tile_width)
    extra = jnp.pad(block.reshape(1, entries), ((0, 0), (0, tile_width - entries))).astype(jnp.bfloat16)
    extra = jnp.broadcast_to(extra[None], (groups * parts, 1, tile_width))
    mine = jnp.concatenate([mine, extra], axis=1)
    mine = lax.all_to_all(mine, ("views", "depth", "lat"), 0, 0, tiled=True)
    mine = mine.reshape(groups, depth_count, halves, piece // tile_width + 1, tile_width)
    table = mine[:, :, 0, piece // tile_width, :entries].astype(jnp.float32)
    mine = mine[:, :, :, : piece // tile_width].reshape(groups, depth_count, halves, piece)
    mine = jnp.transpose(mine, (1, 2, 0, 3)).reshape(
        depth_count, halves, rows_here, materials, depth_here, tile_width
    )
    channels = materials * halves * rows_here
    mine = jnp.transpose(mine, (0, 4, 3, 1, 2, 5)).reshape(depth_all, channels, tile_width)
    mine = mine.astype(jnp.float32)
    target = observed.reshape(views_all // 2, 2, rows_here, halves, tile_width)
    target = jnp.transpose(target, (0, 1, 3, 2, 4)).reshape(views_all // 2, 2 * halves * rows_here, tile_width)
    emitted = jnp.log(jnp.sum(spectrum)).reshape(1)
    smem = pl.BlockSpec(memory_space=pltpu.SMEM)
    vmem = pl.BlockSpec(memory_space=pltpu.VMEM)
    grads = pl.pallas_call(
        functools.partial(forward_kernel, rows_here, halves, depth_all, views_all),
        out_shape=jax.ShapeDtypeStruct((views_all, channels, tile_width), jnp.float32),
        in_specs=[smem, smem, smem, smem, vmem, vmem],
        out_specs=vmem,
        scratch_shapes=[
            pltpu.VMEM((views_all, channels, tile_width), jnp.float32),
            pltpu.VMEM((depth_all, channels, tile_width + LANES), jnp.float32),
            pltpu.VMEM((depth_all, channels, tile_width + LANES), jnp.float32),
        ],
        interpret=INTERPRET,
    )(table, emitted, spectrum, attenuation, mine, target)
    layers = pl.pallas_call(
        functools.partial(backward_kernel, rows_here, halves),
        out_shape=jax.ShapeDtypeStruct((parts * rows_here * materials, depth_here, tile_width), jnp.float32),
        in_specs=[smem, vmem],
        out_specs=vmem,
        scratch_shapes=[
            pltpu.VMEM((views_all, channels, tile_width + LANES), jnp.float32),
            pltpu.VMEM((views_all, channels, tile_width + LANES), jnp.float32),
        ],
        interpret=INTERPRET,
    )(table, grads)
    layers = layers.reshape(parts, rows_here, materials, depth_here, tile_width)
    layers = lax.all_to_all(layers, ("depth", "lat"), 0, 0, tiled=True)
    return layers.reshape(rows_group, materials, depth_here, tile_width)


def per_device_any(density, measured, shear_shift, shear_frac, spectrum, attenuation):
    if rows_fit_wide(density, measured):
        return per_device_wide(density, measured, shear_shift, shear_frac, spectrum, attenuation)
    if rows_fit(density, measured):
        return per_device_rows(density, measured, shear_shift, shear_frac, spectrum, attenuation)
    return per_device(density, measured, shear_shift, shear_frac, spectrum, attenuation)


def solution(mesh):
    in_specs = (
        P(None, None, "depth", "lat"),
        P("views", None, "lat"),
        P("views", "depth"),
        P("views", "depth"),
        P(),
        P(),
    )
    out_specs = P("views", None, "depth", "lat")
    return jax.shard_map(
        per_device_any, mesh=mesh, in_specs=in_specs, out_specs=out_specs, check_vma=False
    )
```
